32 devices in a mesh: dp: 8 (over z, x), qy: 2 (over y), qx: 2 (over core).
Axes of the slice: x: 2, y: 2, z: 4, core: 2. Of those that a mesh axis runs over, the one named last changes fastest.
Arguments:
- tokens: bfloat16 [8, 56, 56, 384], P('dp', 'qy', 'qx'), may hold values from -6 to 6
- crop_ids: int32 [8, 56, 56], P('dp'), may hold values from -1 to 3, as said below
- merge_order: int32 [4], replicated, may hold values from 0 to 3, each once
- owner_list: int32 [192], replicated, may hold values from 0 to 191, each once
- w_qkv: bfloat16 [384, 1152], replicated, may hold values from -0.3125 to 0.3125
- w_proj: bfloat16 [384, 384], replicated, may hold values from -1.25 to 1.25
- w_fc1: bfloat16 [384, 1536], replicated, may hold values from -0.3125 to 0.3125
- w_fc2: bfloat16 [1536, 384], replicated, may hold values from -0.15625 to 0.15625
- small_params: float32 [3564], replicated
- small_first: float32 [3564], replicated, may hold values from -384 to 384
- small_second: float32 [3564], replicated, may hold values from 2007.04 to 16056.32
- master_blocks: float32 [192, 96, 96], P('dp'), may hold values from -0.625 to 0.625
- first_moment: float32 [192, 96, 96], P('dp'), may hold values from -384 to 384
- second_moment: float32 [192, 96, 96], P('dp'), may hold values from 2007.04 to 16056.32
- basis_left: float32 [192, 96, 96], P('dp'), as said below
- basis_right: float32 [192, 96, 96], P('dp'), as said below
- merged_grad: bfloat16 [8, 784, 1536], P('dp', ('qy', 'qx')), may hold values from -6 to 6
Outputs:
- merged: bfloat16 [8, 784, 1536], P('dp', ('qy', 'qx'))
- grad_tokens: bfloat16 [8, 56, 56, 384], P('dp', 'qy', 'qx')
- weight_grads: float32 [192, 96, 96], P('dp')
- new_master: float32 [192, 96, 96], P('dp')
- new_first: float32 [192, 96, 96], P('dp')
- new_second: float32 [192, 96, 96], P('dp')
- master_low: bfloat16 [192, 96, 96], P('dp')
- small_grad: float32 [3564], replicated
- small_first_new: float32 [3564], replicated
- small_second_new: float32 [3564], replicated
- small_new: float32 [3564], replicated
- layer_stats: float32 [2], replicated
The draws below stay inside these ranges and needn't reach their ends.
Inputs may be any that keep to these rules, and one draw needn't show every extreme that they name: `crop_ids`: each canvas holds tokens of several crops; -1 marks padding tokens, present on every canvas. `basis_left`: each block is orthogonal. `basis_right`: each block is orthogonal.
All inputs are finite; a program needn't handle non-finite values.
Results may differ from the reference program's by a relative error of at most 0.014.
Values may be sent and summed in bfloat16 or wider, within the bound.
No kernel may reach another device: no remote copies, remote signals or barrier semaphores. Data moves between devices by JAX's collectives and lax.ppermute only.
A program may use at most 128 MiB of HBM per device.

```python
import math
from functools import partial
import jax
import jax.numpy as jnp
from jax import lax

C = 384
HEADS = 12
HEAD_DIM = 32
FF = 1536
WIN = 7
SHIFT = 3
BLK = 96
QH = 28
BATCH = 8
ROWS = 56
COLS = 56
TOKENS = 25088
RELS = 169
SMALLN = 3564
NBLK = 192
N_QY = 2
N_QX = 2


def draw_crop_ids(key, part):
    subkeys = jax.random.split(key, 4)
    cut_row = jax.random.randint(subkeys[0], (BATCH, 1, 1), WIN, ROWS - WIN)
    cut_col = jax.random.randint(subkeys[1], (BATCH, 1, 1), WIN, COLS - WIN)
    pad_row = jax.random.randint(subkeys[2], (BATCH, 1, 1), 1, 5)
    pad_col = jax.random.randint(subkeys[3], (BATCH, 1, 1), 1, 5)
    row_place = jnp.arange(ROWS, dtype=jnp.int32)[None, :, None]
    col_place = jnp.arange(COLS, dtype=jnp.int32)[None, None, :]
    crop_number = 2 * (row_place >= cut_row).astype(jnp.int32) + (col_place >= cut_col).astype(jnp.int32)
    padded = (row_place >= ROWS - pad_row) | (col_place >= COLS - pad_col)
    return jnp.where(padded, -1, crop_number).astype(jnp.int32)


def draw_small_params(key, part):
    subkeys = jax.random.split(key, 3)
    gains = 1.0 + 0.1 * jax.random.normal(subkeys[0], (2, C), jnp.float32)
    offsets = 0.3 * jax.random.normal(subkeys[1], (2, C), jnp.float32)
    table = jax.random.normal(subkeys[2], (HEADS * RELS,), jnp.float32)
    return jnp.concatenate([gains[0], offsets[0], gains[1], offsets[1], table])


def orthogonal_blocks(key):
    result = jnp.broadcast_to(jnp.eye(BLK, dtype=jnp.float32), (NBLK, BLK, BLK))
    for house_turn in range(4):
        vector = jax.random.normal(jax.random.fold_in(key, house_turn), (NBLK, BLK), jnp.float32)
        norm_sq = jnp.sum(vector * vector, -1, keepdims=True)
        product = jnp.einsum('sij,sj->si', result, vector)
        result = result - 2.0 * product[:, :, None] * vector[:, None, :] / norm_sq[:, :, None]
    return result


def draw_basis_left(key, part):
    return orthogonal_blocks(jax.random.fold_in(key, 11))


def draw_basis_right(key, part):
    return orthogonal_blocks(jax.random.fold_in(key, 23))


def block_scale(rng, extent, cuts, low, largest):
    def one(dim, shards_of):
        heights = jax.random.uniform(jax.random.fold_in(jax.random.fold_in(rng, 6), dim), (shards_of,), jnp.float32, low / len(cuts), largest / len(cuts))
        return jnp.repeat(jnp.exp(heights), extent[dim] // shards_of).reshape((-1,) + (1,) * (len(extent) - dim - 1))

    factor_of = one(*cuts[0])
    for cut in cuts[1:]:
        factor_of = factor_of * one(*cut)
    return factor_of


def gaussian(key, shape, deviation, most, cuts=(), kind=jnp.bfloat16):
    level = block_scale(key, shape, cuts, -0.22, 0.18) if cuts else 1.0
    array = jax.random.normal(key, shape, jnp.float32) * deviation * level
    return jnp.minimum(jnp.maximum(array, -most), most).astype(kind)


def setup_inputs(seed: int = 0) -> dict:
    key_list = jax.random.split(jax.random.key(seed), 18)
    return {
        "tokens": gaussian(key_list[0], (BATCH, ROWS, COLS, C), 1.0, 6.0, ((0, 8), (1, 2), (2, 2))),
        "crop_ids": draw_crop_ids(jax.random.fold_in(key_list[17], 71), 0),
        "merge_order": jax.random.permutation(key_list[2], N_QY * N_QX).astype(jnp.int32),
        "owner_list": jax.random.permutation(key_list[3], NBLK).astype(jnp.int32),
        "w_qkv": gaussian(key_list[4], (C, 3 * C), C ** -0.5, 0.3125),
        "w_proj": gaussian(key_list[5], (C, C), (C // 16) ** -0.5, 1.25),
        "w_fc1": gaussian(key_list[6], (C, FF), C ** -0.5, 0.3125),
        "w_fc2": gaussian(key_list[7], (FF, C), FF ** -0.5, 0.15625),
        "small_params": draw_small_params(jax.random.fold_in(key_list[17], 71), 0),
        "small_first": gaussian(key_list[9], (SMALLN,), (0.4 * TOKENS ** 0.5), 384.0, (), jnp.float32),
        "small_second": jnp.clip(jnp.exp(jax.random.uniform(key_list[10], (SMALLN,), jnp.float32, math.log(2007.04), math.log(16056.32))), 2007.04, 16056.32),
        "master_blocks": gaussian(key_list[11], (NBLK, BLK, BLK), 0.04, 0.625, ((0, 8),), jnp.float32),
        "first_moment": gaussian(key_list[12], (NBLK, BLK, BLK), (0.4 * TOKENS ** 0.5), 384.0, ((0, 8),), jnp.float32),
        "second_moment": jnp.clip(jnp.exp(math.log(16056.32) - 2.0794415 * jax.random.uniform(key_list[13], (NBLK, BLK, BLK), jnp.float32) ** block_scale(key_list[13], (NBLK, BLK, BLK), ((0, 8),), -0.2, 0.2)), 2007.04, 16056.32),
        "basis_left": draw_basis_left(jax.random.fold_in(key_list[17], 71), 0),
        "basis_right": draw_basis_right(jax.random.fold_in(key_list[17], 71), 0),
        "merged_grad": gaussian(key_list[16], (BATCH, QH * QH, N_QY * N_QX * C), 1.0, 6.0, ((0, 8), (1, 4))),
    }


BETA_ONE = 0.5
BETA_TWO = 0.6
ADAM_EPSILON = 1e-08
RATE_BLOCKS = 0.04
RATE_SMALL = 0.2
MASK_FILL = -1e+30
NORM_EPSILON = 1e-05
PRECISE = lax.Precision.HIGHEST

@jax.custom_vjp
def low(v):
    return lax.optimization_barrier(v.astype(jnp.bfloat16)).astype(jnp.float32)

@jax.custom_vjp
def low_back(v):
    return v

def low_keep(v):
    return (low(v), None)

def low_pass(kept, grad):
    return (grad,)

def back_keep(v):
    return (v, None)

def back_low(kept, grad):
    return (low(grad),)
low.defvjp(low_keep, low_pass)
low_back.defvjp(back_keep, back_low)

def layer_norm(tensor, gain, offset):
    center = tensor - lax.optimization_barrier(jnp.mean(tensor, -1, keepdims=True))
    spread = lax.optimization_barrier(jnp.mean(center * center, -1, keepdims=True))
    return center * lax.rsqrt(spread + NORM_EPSILON) * gain + offset

def windows_of(tensor):
    batch, rows_all, cols_all, channels = tensor.shape
    shaped = tensor.reshape(batch, rows_all // WIN, WIN, cols_all // WIN, WIN, channels)
    return shaped.transpose(0, 1, 3, 2, 4, 5).reshape(batch, rows_all // WIN * (cols_all // WIN), WIN * WIN, channels)

def windows_back(tensor, rows_all, cols_all):
    batch = tensor.shape[0]
    channels = tensor.shape[-1]
    shaped = tensor.reshape(batch, rows_all // WIN, cols_all // WIN, WIN, WIN, channels)
    return shaped.transpose(0, 1, 3, 2, 4, 5).reshape(batch, rows_all, cols_all, channels)

def relative_index():
    places = jnp.arange(WIN * WIN, dtype=jnp.int32)
    row_of = places // WIN
    col_of = places % WIN
    return (row_of[:, None] - row_of[None, :] + WIN - 1) * (2 * WIN - 1) + (col_of[:, None] - col_of[None, :] + WIN - 1)

def region_of(places, full):
    return jnp.where(places < full - WIN, 0, jnp.where(places < full - SHIFT, 1, 2)).astype(jnp.int32)

def attend(pair, rel_bias):
    mixed, labels = pair
    windows = mixed.shape[0]
    grouped = mixed.reshape(windows, WIN * WIN, 3, HEADS, HEAD_DIM)
    queries = grouped[:, :, 0]
    key_vecs = grouped[:, :, 1]
    values = grouped[:, :, 2]
    scores = jnp.einsum('wqhd,wkhd->whqk', queries, key_vecs, precision=PRECISE) * HEAD_DIM ** (-0.5) + rel_bias[None]
    scores = low_back(scores)
    allowed = labels[:, None, :, None] == labels[:, None, None, :]
    scores = jnp.where(allowed, scores, MASK_FILL)
    row_max = lax.optimization_barrier(jnp.max(scores, -1, keepdims=True))
    exp_scores = jnp.exp(scores - row_max)
    soft_weights = exp_scores / lax.optimization_barrier(jnp.sum(exp_scores, -1, keepdims=True))
    attended = jnp.einsum('whqk,wkhd->wqhd', low(soft_weights), values, precision=PRECISE)
    return attended.reshape(windows, WIN * WIN, HEADS * HEAD_DIM)

def blocks_of(matrix):
    row_blocks = matrix.shape[0] // BLK
    col_blocks = matrix.shape[1] // BLK
    return matrix.reshape(row_blocks, BLK, col_blocks, BLK).transpose(0, 2, 1, 3).reshape(row_blocks * col_blocks, BLK, BLK)

def rotate_update(grads, master, first, second, left, right):
    turned = jnp.einsum('sji,sjk->sik', left, grads, precision=PRECISE)
    turned = jnp.einsum('sik,skl->sil', turned, right, precision=PRECISE)
    new_first = BETA_ONE * first + (1.0 - BETA_ONE) * turned
    new_second = BETA_TWO * second + (1.0 - BETA_TWO) * turned * turned
    direction = new_first / (jnp.sqrt(new_second) + ADAM_EPSILON)
    back = jnp.einsum('sij,sjk->sik', left, direction, precision=PRECISE)
    back = jnp.einsum('sik,slk->sil', back, right, precision=PRECISE)
    return (new_first, new_second, master - RATE_BLOCKS * back)

def small_update(grads, params, first, second):
    new_first = BETA_ONE * first + (1.0 - BETA_ONE) * grads
    new_second = BETA_TWO * second + (1.0 - BETA_TWO) * grads * grads
    direction = new_first / (jnp.sqrt(new_second) + ADAM_EPSILON)
    return (new_first, new_second, params - RATE_SMALL * direction)

def reference(tokens, crop_ids, merge_order, owner_list, w_qkv, w_proj, w_fc1, w_fc2, small_params, small_first, small_second, master_blocks, first_moment, second_moment, basis_left, basis_right, merged_grad):
    quarters = N_QY * N_QX
    rolled = jnp.roll(crop_ids, (-SHIFT, -SHIFT), (1, 2))
    region_row = region_of(jnp.arange(ROWS, dtype=jnp.int32), ROWS)
    region_col = region_of(jnp.arange(COLS, dtype=jnp.int32), COLS)
    labels = (rolled + 1) * 9 + region_row[None, :, None] * 3 + region_col[None, None, :]
    win_labels = windows_of(labels[..., None])[..., 0]
    index_table = relative_index()

    def forward(inputs, weight_qkv, weight_proj, weight_one, weight_two, small):
        gain_one = small[0:C]
        offset_one = small[C:2 * C]
        gain_two = small[2 * C:3 * C]
        offset_two = small[3 * C:4 * C]
        table = small[4 * C:].reshape(HEADS, RELS)
        rel_bias = table[:, index_table]
        shifted = jnp.roll(inputs, (-SHIFT, -SHIFT), (1, 2))
        residual = windows_of(shifted)
        act_one = low(layer_norm(residual, gain_one, offset_one))
        mixed = low(low_back(jnp.einsum('bwtc,cf->bwtf', act_one, weight_qkv, precision=PRECISE)))
        attended = lax.map(jax.checkpoint(partial(attend, rel_bias=rel_bias)), (mixed, win_labels))
        attended = low(low_back(attended))
        branch_one = low_back(jnp.einsum('bwtc,cf->bwtf', attended, weight_proj, precision=PRECISE))
        hidden = residual + branch_one
        act_two = low(layer_norm(hidden, gain_two, offset_two))
        pre_gelu = low_back(jnp.einsum('bwtc,cf->bwtf', act_two, weight_one, precision=PRECISE))
        gelu_low = low(jax.nn.gelu(pre_gelu, approximate=False))
        branch_two = low_back(jnp.einsum('bwtf,fc->bwtc', gelu_low, weight_two, precision=PRECISE))
        output = hidden + branch_two
        valid = (win_labels >= 9).astype(jnp.float32)[..., None]
        sums = (jnp.sum(valid * output * output), jnp.sum(valid * (branch_one * branch_one + branch_two * branch_two)), jnp.sum(valid) * C)
        restored = jnp.roll(windows_back(output, ROWS, COLS), (SHIFT, SHIFT), (1, 2))
        return (restored, sums)
    output, pull, sums = jax.vjp(forward, tokens.astype(jnp.float32), w_qkv.astype(jnp.float32), w_proj.astype(jnp.float32), w_fc1.astype(jnp.float32), w_fc2.astype(jnp.float32), small_params, has_aux=True)
    output_low = output.astype(jnp.bfloat16)
    quads = [output_low[:, row_group * QH:(row_group + 1) * QH, col_group * QH:(col_group + 1) * QH].reshape(BATCH, QH * QH, C) for row_group in range(N_QY) for col_group in range(N_QX)]
    stacked = jnp.stack(quads, 2)
    merged = jnp.take(stacked, merge_order, axis=2).reshape(BATCH, QH * QH, quarters * C)
    quarter_ids = jnp.arange(quarters, dtype=jnp.int32)
    source_pick = lax.optimization_barrier(jnp.sum(quarter_ids[:, None] * (merge_order[:, None] == quarter_ids[None, :]).astype(jnp.int32), 0))
    incoming = merged_grad.reshape(BATCH, QH * QH, quarters, C)
    unordered = jnp.take(incoming, source_pick, axis=2)
    pieces = [jnp.concatenate([unordered[:, :, row_group * N_QX + col_group].reshape(BATCH, QH, QH, C) for col_group in range(N_QX)], 2) for row_group in range(N_QY)]
    cotangent = jnp.concatenate(pieces, 1).astype(jnp.float32)
    grads = pull(cotangent)
    grad_tokens = grads[0].astype(jnp.bfloat16)
    every_block = jnp.concatenate([blocks_of(grads[1]), blocks_of(grads[2]), blocks_of(grads[3]), blocks_of(grads[4])], 0)
    slot_grads = jnp.take(every_block, owner_list, axis=0)
    new_first, new_second, new_master = rotate_update(slot_grads, master_blocks, first_moment, second_moment, basis_left, basis_right)
    small_first_new, small_second_new, small_new = small_update(grads[5], small_params, small_first, small_second)
    stats = jnp.stack([jnp.sqrt(sums[0] / sums[2]), jnp.sqrt(sums[1] / (2.0 * sums[2]))])
    return (merged, grad_tokens, slot_grads, new_master, new_first, new_second, new_master.astype(jnp.bfloat16), grads[5], small_first_new, small_second_new, small_new, stats)
```

```python
from functools import partial

import jax
import jax.numpy as jnp
from jax import lax
from jax.sharding import PartitionSpec as P

HEADS = 12
WIN = 7
SHIFT = 3
BLK = 96


BETA_ONE = 0.5
BETA_TWO = 0.6
ADAM_EPSILON = 1e-08
RATE_BLOCKS = 0.04
RATE_SMALL = 0.2
MASK_FILL = -1e30
NORM_EPSILON = 1e-05
PRECISE = lax.Precision.HIGHEST


def passed_along(value, axis, steps):
    count = lax.axis_size(axis)
    pairs = [(source, (source + steps) % count) for source in range(count)]
    return lax.ppermute(value, axis, pairs)


def partner_of(value, axis, mask):
    count = lax.axis_size(axis)
    pairs = [(source, source ^ mask) for source in range(count)]
    return lax.ppermute(value, axis, pairs)


def device_bits():
    bits = [("qx", 1), ("qy", 1)]
    for power in range(lax.axis_size("dp").bit_length() - 1):
        bits.append(("dp", 1 << power))
    return bits


def bit_of(axis, mask):
    return (lax.axis_index(axis) & mask) != 0


def halve(part, names, bit, extra=None):
    place = names.index(bit)
    mine = bit_of(*bit).astype(jnp.int32)
    keep = jnp.take(part, mine, axis=place)
    send = jnp.take(part, 1 - mine, axis=place)
    if extra is None:
        arrived = partner_of(send.astype(jnp.bfloat16), *bit)
        return keep + arrived.astype(jnp.float32), None
    arrived, extra_in = partner_of((send.astype(jnp.bfloat16), extra), *bit)
    return keep + arrived.astype(jnp.float32), extra + extra_in


def reduce_to_owners(slots, small):
    groups = lax.axis_size("dp")
    dp_bits = groups.bit_length() - 1
    n_qy, n_qx = lax.axis_size("qy"), lax.axis_size("qx")
    per_group = slots.size // groups
    per_device = per_group // (n_qy * n_qx)
    cross = [("qy", 1)] + [("dp", 1 << power) for power in range(dp_bits)]
    parts = min(4, len(cross))
    names = [("dp", 1 << power) for power in reversed(range(dp_bits))] + [("qy", 1), ("qx", 1)]
    shaped = slots.reshape([2] * dp_bits + [n_qy, n_qx, parts, per_device // parts])
    shaped = jnp.moveaxis(shaped, dp_bits + 2, 0)
    pieces = [shaped[index] for index in range(parts)]
    piece_names = [list(names) for _ in range(parts)]
    orders = [[("qx", 1)] + cross[index:] + cross[:index] for index in range(parts)]
    for stage in range(len(names)):
        for index in range(parts):
            bit = orders[index][stage]
            carry = small if index == 0 else None
            pieces[index], carried = halve(pieces[index], piece_names[index], bit, carry)
            piece_names[index].remove(bit)
            if index == 0:
                small = carried
    chunk = jnp.concatenate([piece.reshape(-1) for piece in pieces])
    other = partner_of(chunk, "qy", 1)
    pair = jnp.where(bit_of("qy", 1), jnp.stack([other, chunk]), jnp.stack([chunk, other]))
    other = partner_of(pair, "qx", 1)
    quad = jnp.where(bit_of("qx", 1), jnp.stack([other, pair], 1), jnp.stack([pair, other], 1))
    return quad.reshape(-1, BLK, BLK), small


def cut_along(value, dim, devices):
    before, after = (value.shape[:dim], value.shape[dim + 1 :])
    return jnp.moveaxis(value.reshape(*before, devices, -1, *after), dim, 0)


def sent_and_summed(value, axis, dim):
    pieces = cut_along(value, dim, lax.axis_size(axis))
    arrived = lax.all_to_all(pieces, axis, split_axis=0, concat_axis=0, tiled=True)
    return arrived.astype(jnp.float32).sum(axis=0)


def norm_stats(tensor):
    center = tensor - jnp.mean(tensor, -1, keepdims=True)
    inverse = lax.rsqrt(jnp.mean(center * center, -1, keepdims=True) + NORM_EPSILON)
    return (center * inverse, inverse)


def norm_back(grad_act, normed, inverse, gain):
    scaled = grad_act * gain
    mean_one = jnp.mean(scaled, -1, keepdims=True)
    mean_two = jnp.mean(scaled * normed, -1, keepdims=True)
    return inverse * (scaled - mean_one - normed * mean_two)


def to_windows(tensor):
    canvases, rows_side, cols_side, channels = tensor.shape
    shaped = tensor.reshape(canvases, rows_side // WIN, WIN, cols_side // WIN, WIN, channels)
    return shaped.transpose(0, 1, 3, 2, 4, 5).reshape(
        canvases * (rows_side // WIN) * (cols_side // WIN), WIN * WIN, channels
    )


def from_windows(tensor, canvases, rows_side, cols_side):
    channels = tensor.shape[-1]
    shaped = tensor.reshape(canvases, rows_side // WIN, cols_side // WIN, WIN, WIN, channels)
    return shaped.transpose(0, 1, 3, 2, 4, 5).reshape(canvases, rows_side, cols_side, channels)


def relative_index():
    places = jnp.arange(WIN * WIN, dtype=jnp.int32)
    row_of = places // WIN
    col_of = places % WIN
    return (row_of[:, None] - row_of[None, :] + WIN - 1) * (2 * WIN - 1) + (
        col_of[:, None] - col_of[None, :] + WIN - 1
    )


def region_of(places, full):
    return jnp.where(places < full - WIN, 0, jnp.where(places < full - SHIFT, 1, 2)).astype(
        jnp.int32
    )


def advance(tensor):
    upper = passed_along(tensor[:, :SHIFT], "qy", -1)
    tensor = jnp.concatenate([tensor[:, SHIFT:], upper], 1)
    leftmost = passed_along(tensor[:, :, :SHIFT], "qx", -1)
    return jnp.concatenate([tensor[:, :, SHIFT:], leftmost], 2)


def retreat(tensor):
    lowest = passed_along(tensor[:, -SHIFT:], "qy", 1)
    tensor = jnp.concatenate([lowest, tensor[:, :-SHIFT]], 1)
    rightmost = passed_along(tensor[:, :, -SHIFT:], "qx", 1)
    return jnp.concatenate([rightmost, tensor[:, :, :-SHIFT]], 2)


def blocks_of(matrix):
    row_blocks = matrix.shape[0] // BLK
    col_blocks = matrix.shape[1] // BLK
    return (
        matrix.reshape(row_blocks, BLK, col_blocks, BLK)
        .transpose(0, 2, 1, 3)
        .reshape(row_blocks * col_blocks, BLK, BLK)
    )


def rotate_update(grads, master, first, second, left, right):
    turned = jnp.einsum("sji,sjk->sik", left, grads, precision=PRECISE)
    turned = jnp.einsum("sik,skl->sil", turned, right, precision=PRECISE)
    new_first = BETA_ONE * first + (1.0 - BETA_ONE) * turned
    new_second = BETA_TWO * second + (1.0 - BETA_TWO) * turned * turned
    direction = new_first / (jnp.sqrt(new_second) + ADAM_EPSILON)
    back = jnp.einsum("sij,sjk->sik", left, direction, precision=PRECISE)
    back = jnp.einsum("sik,slk->sil", back, right, precision=PRECISE)
    return (new_first, new_second, master - RATE_BLOCKS * back)


def small_update(grads, params, first, second):
    new_first = BETA_ONE * first + (1.0 - BETA_ONE) * grads
    new_second = BETA_TWO * second + (1.0 - BETA_TWO) * grads * grads
    direction = new_first / (jnp.sqrt(new_second) + ADAM_EPSILON)
    return (new_first, new_second, params - RATE_SMALL * direction)


def local(
    tokens,
    crop_ids,
    merge_order,
    owner_list,
    w_qkv,
    w_proj,
    w_fc1,
    w_fc2,
    small_params,
    small_first,
    small_second,
    master_blocks,
    first_moment,
    second_moment,
    basis_left,
    basis_right,
    merged_grad,
):
    canvases, quad_side, quad_cols, features = tokens.shape
    head_dim = features // HEADS
    score_scale = head_dim ** (-0.5)
    window_area = WIN * WIN
    quarters = lax.axis_size(("qy", "qx"))
    share_rows = quad_side * quad_cols // quarters
    row_base = lax.axis_index("qy") * quad_side
    col_base = lax.axis_index("qx") * quad_cols
    rolled = jnp.roll(crop_ids, (-SHIFT, -SHIFT), (1, 2))
    local_ids = lax.dynamic_slice(
        rolled, (jnp.int32(0), row_base, col_base), (canvases, quad_side, quad_cols)
    )
    region_row = region_of(
        row_base + jnp.arange(quad_side, dtype=jnp.int32), quad_side * lax.axis_size("qy")
    )
    region_col = region_of(
        col_base + jnp.arange(quad_cols, dtype=jnp.int32), quad_cols * lax.axis_size("qx")
    )
    labels = (local_ids + 1) * 9 + region_row[None, :, None] * 3 + region_col[None, None, :]
    win_labels = to_windows(labels[..., None])[..., 0]
    window_count = win_labels.shape[0]
    allowed = win_labels[:, None, :, None] == win_labels[:, None, None, :]
    valid = (win_labels >= 9).reshape(-1).astype(jnp.float32)[:, None]
    gain_one = small_params[0:features]
    offset_one = small_params[features : 2 * features]
    gain_two = small_params[2 * features : 3 * features]
    offset_two = small_params[3 * features : 4 * features]
    table = small_params[4 * features :].reshape(HEADS, -1)
    onehot = (
        relative_index().reshape(-1)[:, None]
        == jnp.arange(table.shape[1], dtype=jnp.int32)[None, :]
    ).astype(jnp.float32)
    rel_bias = jnp.einsum("hr,pr->hp", table, onehot, precision=PRECISE).reshape(
        HEADS, window_area, window_area
    )

    def score_of(queries, key_vecs):
        raw = (
            jnp.einsum("wqhd,wkhd->whqk", queries, key_vecs, preferred_element_type=jnp.float32)
            * score_scale
            + rel_bias[None]
        )
        return jnp.where(allowed, raw, MASK_FILL)

    residual = to_windows(advance(tokens)).reshape(-1, features).astype(jnp.float32)
    normed_one, inverse_one = norm_stats(residual)
    act_one = (normed_one * gain_one + offset_one).astype(jnp.bfloat16)
    mixed = jnp.dot(act_one, w_qkv, preferred_element_type=jnp.float32).astype(jnp.bfloat16)
    grouped = mixed.reshape(window_count, window_area, 3, HEADS, head_dim)
    queries = grouped[:, :, 0]
    key_vecs = grouped[:, :, 1]
    values = grouped[:, :, 2]
    scores = score_of(queries, key_vecs)
    row_max = jnp.max(scores, -1, keepdims=True)
    exp_scores = jnp.exp(scores - row_max)
    exp_total = jnp.sum(exp_scores, -1, keepdims=True)
    log_total = row_max + jnp.log(exp_total)
    probs_low = (exp_scores / exp_total).astype(jnp.bfloat16)
    attended = jnp.einsum("whqk,wkhd->wqhd", probs_low, values, preferred_element_type=jnp.float32)
    attended = attended.reshape(-1, features).astype(jnp.bfloat16)
    branch_one = jnp.dot(attended, w_proj, preferred_element_type=jnp.float32)
    hidden = residual + branch_one
    normed_two, inverse_two = norm_stats(hidden)
    act_two = (normed_two * gain_two + offset_two).astype(jnp.bfloat16)
    pre_gelu = jnp.dot(act_two, w_fc1, preferred_element_type=jnp.float32)
    gelu_low = jax.nn.gelu(pre_gelu, approximate=False).astype(jnp.bfloat16)
    branch_two = jnp.dot(gelu_low, w_fc2, preferred_element_type=jnp.float32)
    output = hidden + branch_two
    stat_terms = jnp.stack(
        [
            jnp.sum(valid * output * output),
            jnp.sum(valid * (branch_one * branch_one + branch_two * branch_two)),
            jnp.sum(valid) * features,
        ]
    )
    output_low = output.astype(jnp.bfloat16).reshape(window_count, window_area, features)
    restored = retreat(from_windows(output_low, canvases, quad_side, quad_cols))
    flat_out = restored.reshape(canvases, quarters, share_rows, features)
    arrived = lax.all_to_all(flat_out, ("qy", "qx"), 1, 1, tiled=True)
    merged = jnp.take(arrived, merge_order, axis=1).transpose(0, 2, 1, 3).reshape(
        canvases, share_rows, quarters * features
    )
    quarter_ids = jnp.arange(quarters, dtype=jnp.int32)
    source_pick = jnp.sum(
        quarter_ids[:, None] * (merge_order[:, None] == quarter_ids[None, :]).astype(jnp.int32), 0
    )
    incoming = merged_grad.reshape(canvases, share_rows, quarters, features)
    unordered = jnp.take(incoming, source_pick, axis=2).transpose(0, 2, 1, 3)
    returned = lax.all_to_all(unordered, ("qy", "qx"), 1, 1, tiled=True)
    grad_orig = returned.reshape(canvases, quad_side, quad_cols, features)
    grad_out = to_windows(advance(grad_orig)).reshape(-1, features)
    grad_fc2 = jnp.einsum("rf,rc->fc", gelu_low, grad_out, preferred_element_type=jnp.float32)
    grad_gelu = jnp.einsum("rc,fc->rf", grad_out, w_fc2, preferred_element_type=jnp.float32)
    gelu_pull = jax.vjp(partial(jax.nn.gelu, approximate=False), pre_gelu)[1]
    grad_pre = gelu_pull(grad_gelu)[0].astype(jnp.bfloat16)
    grad_fc1 = jnp.einsum("rc,rf->cf", act_two, grad_pre, preferred_element_type=jnp.float32)
    grad_act_two = jnp.einsum("rf,cf->rc", grad_pre, w_fc1, preferred_element_type=jnp.float32)
    grad_hidden = grad_out.astype(jnp.float32) + norm_back(
        grad_act_two, normed_two, inverse_two, gain_two
    )
    grad_branch = grad_hidden.astype(jnp.bfloat16)
    grad_proj = jnp.einsum("rc,rd->cd", attended, grad_branch, preferred_element_type=jnp.float32)
    grad_attended = jnp.einsum(
        "rd,cd->rc", grad_branch, w_proj, preferred_element_type=jnp.float32
    ).astype(jnp.bfloat16)
    grad_attended = grad_attended.reshape(window_count, window_area, HEADS, head_dim)
    probs = jnp.exp(score_of(queries, key_vecs) - log_total)
    grad_probs = jnp.einsum(
        "wqhd,wkhd->whqk", grad_attended, values, preferred_element_type=jnp.float32
    )
    grad_values = jnp.einsum(
        "whqk,wqhd->wkhd", probs_low, grad_attended, preferred_element_type=jnp.float32
    )
    grad_scores = (probs * (grad_probs - jnp.sum(probs * grad_probs, -1, keepdims=True))).astype(
        jnp.bfloat16
    )
    grad_bias = jnp.sum(grad_scores.astype(jnp.float32), 0).reshape(HEADS, -1)
    grad_table = jnp.dot(grad_bias, onehot, precision=PRECISE)
    grad_queries = (
        jnp.einsum("whqk,wkhd->wqhd", grad_scores, key_vecs, preferred_element_type=jnp.float32)
        * score_scale
    )
    grad_keys = (
        jnp.einsum("whqk,wqhd->wkhd", grad_scores, queries, preferred_element_type=jnp.float32)
        * score_scale
    )
    grad_mixed = (
        jnp.stack([grad_queries, grad_keys, grad_values], 2)
        .astype(jnp.bfloat16)
        .reshape(-1, 3 * features)
    )
    grad_qkv = jnp.einsum("rc,rf->cf", act_one, grad_mixed, preferred_element_type=jnp.float32)
    grad_act_one = jnp.einsum("rf,cf->rc", grad_mixed, w_qkv, preferred_element_type=jnp.float32)
    grad_input = grad_hidden + norm_back(grad_act_one, normed_one, inverse_one, gain_one)
    grad_low = grad_input.astype(jnp.bfloat16).reshape(window_count, window_area, features)
    grad_tokens = retreat(from_windows(grad_low, canvases, quad_side, quad_cols))
    small_local = jnp.concatenate(
        [
            jnp.sum(grad_act_one * normed_one, 0),
            jnp.sum(grad_act_one, 0),
            jnp.sum(grad_act_two * normed_two, 0),
            jnp.sum(grad_act_two, 0),
            grad_table.reshape(-1),
        ]
    )
    every_block = jnp.concatenate(
        [blocks_of(grad_qkv), blocks_of(grad_proj), blocks_of(grad_fc1), blocks_of(grad_fc2)], 0
    )
    slot_blocks = jnp.take(every_block, owner_list, axis=0)
    owned_grads, small_all = reduce_to_owners(
        slot_blocks, jnp.concatenate([small_local, stat_terms])
    )
    small_total = small_all[: small_local.shape[0]]
    stat_total = small_all[small_local.shape[0] :]
    new_first, new_second, new_master = rotate_update(
        owned_grads, master_blocks, first_moment, second_moment, basis_left, basis_right
    )
    small_first_new, small_second_new, small_new = small_update(
        small_total, small_params, small_first, small_second
    )
    stats = jnp.stack(
        [jnp.sqrt(stat_total[0] / stat_total[2]), jnp.sqrt(stat_total[1] / (2.0 * stat_total[2]))]
    )
    return (
        merged,
        grad_tokens,
        owned_grads,
        new_master,
        new_first,
        new_second,
        new_master.astype(jnp.bfloat16),
        small_total,
        small_first_new,
        small_second_new,
        small_new,
        stats,
    )


def solution(mesh):
    placed = (
        P("dp", "qy", "qx", None),
        P("dp", None, None),
        P(),
        P(),
        P(),
        P(),
        P(),
        P(),
        P(),
        P(),
        P(),
        P("dp", None, None),
        P("dp", None, None),
        P("dp", None, None),
        P("dp", None, None),
        P("dp", None, None),
        P("dp", ("qy", "qx"), None),
    )
    return jax.shard_map(
        local,
        mesh=mesh,
        in_specs=placed,
        out_specs=(
            P("dp", ("qy", "qx"), None),
            P("dp", "qy", "qx", None),
            P("dp", None, None),
            P("dp", None, None),
            P("dp", None, None),
            P("dp", None, None),
            P("dp", None, None),
            P(),
            P(),
            P(),
            P(),
            P(),
        ),
        check_vma=False,
    )
```

```python
from functools import partial

import jax
import jax.numpy as jnp
from jax import lax
from jax.sharding import PartitionSpec as P

HEADS = 12
WIN = 7
SHIFT = 3
BLK = 96


BETA_ONE = 0.5
BETA_TWO = 0.6
ADAM_EPSILON = 1e-08
RATE_BLOCKS = 0.04
RATE_SMALL = 0.2
MASK_FILL = -1e30
NORM_EPSILON = 1e-05
PRECISE = lax.Precision.HIGHEST


def passed_along(value, axis, steps):
    count = lax.axis_size(axis)
    pairs = [(source, (source + steps) % count) for source in range(count)]
    return lax.ppermute(value, axis, pairs)


def partner_of(value, axis, mask):
    count = lax.axis_size(axis)
    pairs = [(source, source ^ mask) for source in range(count)]
    return lax.ppermute(value, axis, pairs)


def bit_of(axis, mask):
    return ((lax.axis_index(axis) & mask) != 0).astype(jnp.int32)


LANES = 128
PARTS = 3


def lane_blocks(matrix):
    row_blocks, col_blocks = matrix.shape[0] // BLK, matrix.shape[1] // BLK
    shaped = matrix.reshape(row_blocks, BLK, col_blocks, BLK).transpose(0, 2, 1, 3)
    return shaped.reshape(row_blocks * col_blocks, BLK * BLK // LANES, LANES)


def reduce_to_owners(parted, small):
    groups = lax.axis_size("dp")
    dp_bits = groups.bit_length() - 1
    n_qy, n_qx = lax.axis_size("qy"), lax.axis_size("qx")
    count, depth = parted[0].shape[0], parted[0].shape[1]
    per_group = count // groups
    names = [("dp", 1 << power) for power in reversed(range(dp_bits))] + [("qy", 1), ("qx", 1)]
    cross = [("qy", 1)] + [("dp", 1 << power) for power in range(dp_bits)]
    pieces, piece_names, orders = [], [], []
    for index, part in enumerate(parted):
        pieces.append(
            part.reshape([2] * dp_bits + [n_qy, n_qx, per_group * depth // (n_qy * n_qx), LANES])
        )
        piece_names.append(list(names))
        turn = index % len(cross)
        orders.append([("qx", 1)] + cross[turn:] + cross[:turn])
    for stage in range(len(names)):
        for index in range(len(pieces)):
            bit = orders[index][stage]
            place = piece_names[index].index(bit)
            mine = bit_of(*bit)
            keep = lax.dynamic_index_in_dim(pieces[index], mine, place, keepdims=False)
            send = lax.dynamic_index_in_dim(pieces[index], 1 - mine, place, keepdims=False)
            piece_names[index].remove(bit)
            arrived = partner_of(send.astype(jnp.bfloat16), *bit)
            pieces[index] = keep + arrived.astype(jnp.float32)
            if index == 0:
                small = small + partner_of(small, *bit)
                pieces[0], small = lax.optimization_barrier((pieces[0], small))
    chunk = jnp.stack(pieces)
    other = partner_of(chunk, "qy", 1)
    pair = jnp.where(bit_of("qy", 1) == 1, jnp.stack([other, chunk], 1), jnp.stack([chunk, other], 1))
    other = partner_of(pair, "qx", 1)
    quad = jnp.where(bit_of("qx", 1) == 1, jnp.stack([other, pair], 2), jnp.stack([pair, other], 2))
    quad = quad.reshape(len(pieces), per_group, depth, LANES).transpose(1, 0, 2, 3)
    return quad.reshape(per_group, BLK, BLK), small


def cut_along(value, dim, devices):
    before, after = (value.shape[:dim], value.shape[dim + 1 :])
    return jnp.moveaxis(value.reshape(*before, devices, -1, *after), dim, 0)


def sent_and_summed(value, axis, dim):
    pieces = cut_along(value, dim, lax.axis_size(axis))
    arrived = lax.all_to_all(pieces, axis, split_axis=0, concat_axis=0, tiled=True)
    return arrived.astype(jnp.float32).sum(axis=0)


def norm_stats(tensor):
    center = tensor - jnp.mean(tensor, -1, keepdims=True)
    inverse = lax.rsqrt(jnp.mean(center * center, -1, keepdims=True) + NORM_EPSILON)
    return (center * inverse, inverse)


def norm_back(grad_act, normed, inverse, gain):
    scaled = grad_act * gain
    mean_one = jnp.mean(scaled, -1, keepdims=True)
    mean_two = jnp.mean(scaled * normed, -1, keepdims=True)
    return inverse * (scaled - mean_one - normed * mean_two)


def to_windows(tensor):
    canvases, rows_side, cols_side, channels = tensor.shape
    shaped = tensor.reshape(canvases, rows_side // WIN, WIN, cols_side // WIN, WIN, channels)
    return shaped.transpose(0, 1, 3, 2, 4, 5).reshape(
        canvases * (rows_side // WIN) * (cols_side // WIN), WIN * WIN, channels
    )


def from_windows(tensor, canvases, rows_side, cols_side):
    channels = tensor.shape[-1]
    shaped = tensor.reshape(canvases, rows_side // WIN, cols_side // WIN, WIN, WIN, channels)
    return shaped.transpose(0, 1, 3, 2, 4, 5).reshape(canvases, rows_side, cols_side, channels)


def relative_index():
    places = jnp.arange(WIN * WIN, dtype=jnp.int32)
    row_of = places // WIN
    col_of = places % WIN
    return (row_of[:, None] - row_of[None, :] + WIN - 1) * (2 * WIN - 1) + (
        col_of[:, None] - col_of[None, :] + WIN - 1
    )


def region_of(places, full):
    return jnp.where(places < full - WIN, 0, jnp.where(places < full - SHIFT, 1, 2)).astype(
        jnp.int32
    )


def advance(tensor):
    upper = passed_along(tensor[:, :SHIFT], "qy", -1)
    tensor = jnp.concatenate([tensor[:, SHIFT:], upper], 1)
    leftmost = passed_along(tensor[:, :, :SHIFT], "qx", -1)
    return jnp.concatenate([tensor[:, :, SHIFT:], leftmost], 2)


def retreat(tensor):
    lowest = passed_along(tensor[:, -SHIFT:], "qy", 1)
    tensor = jnp.concatenate([lowest, tensor[:, :-SHIFT]], 1)
    rightmost = passed_along(tensor[:, :, -SHIFT:], "qx", 1)
    return jnp.concatenate([rightmost, tensor[:, :, :-SHIFT]], 2)


def blocks_of(matrix):
    row_blocks = matrix.shape[0] // BLK
    col_blocks = matrix.shape[1] // BLK
    return (
        matrix.reshape(row_blocks, BLK, col_blocks, BLK)
        .transpose(0, 2, 1, 3)
        .reshape(row_blocks * col_blocks, BLK, BLK)
    )


def rotate_update(grads, master, first, second, left, right):
    turned = jnp.einsum("sji,sjk->sik", left, grads, precision=PRECISE)
    turned = jnp.einsum("sik,skl->sil", turned, right, precision=PRECISE)
    new_first = BETA_ONE * first + (1.0 - BETA_ONE) * turned
    new_second = BETA_TWO * second + (1.0 - BETA_TWO) * turned * turned
    direction = new_first / (jnp.sqrt(new_second) + ADAM_EPSILON)
    back = jnp.einsum("sij,sjk->sik", left, direction, precision=PRECISE)
    back = jnp.einsum("sik,slk->sil", back, right, precision=PRECISE)
    return (new_first, new_second, master - RATE_BLOCKS * back)


def small_update(grads, params, first, second):
    new_first = BETA_ONE * first + (1.0 - BETA_ONE) * grads
    new_second = BETA_TWO * second + (1.0 - BETA_TWO) * grads * grads
    direction = new_first / (jnp.sqrt(new_second) + ADAM_EPSILON)
    return (new_first, new_second, params - RATE_SMALL * direction)


def local(
    tokens,
    crop_ids,
    merge_order,
    owner_list,
    w_qkv,
    w_proj,
    w_fc1,
    w_fc2,
    small_params,
    small_first,
    small_second,
    master_blocks,
    first_moment,
    second_moment,
    basis_left,
    basis_right,
    merged_grad,
):
    canvases, quad_side, quad_cols, features = tokens.shape
    head_dim = features // HEADS
    score_scale = head_dim ** (-0.5)
    window_area = WIN * WIN
    quarters = lax.axis_size(("qy", "qx"))
    share_rows = quad_side * quad_cols // quarters
    row_base = lax.axis_index("qy") * quad_side
    col_base = lax.axis_index("qx") * quad_cols
    rolled = jnp.roll(crop_ids, (-SHIFT, -SHIFT), (1, 2))
    local_ids = lax.dynamic_slice(
        rolled, (jnp.int32(0), row_base, col_base), (canvases, quad_side, quad_cols)
    )
    region_row = region_of(
        row_base + jnp.arange(quad_side, dtype=jnp.int32), quad_side * lax.axis_size("qy")
    )
    region_col = region_of(
        col_base + jnp.arange(quad_cols, dtype=jnp.int32), quad_cols * lax.axis_size("qx")
    )
    labels = (local_ids + 1) * 9 + region_row[None, :, None] * 3 + region_col[None, None, :]
    win_labels = to_windows(labels[..., None])[..., 0]
    window_count = win_labels.shape[0]
    allowed = win_labels[:, None, :, None] == win_labels[:, None, None, :]
    valid = (win_labels >= 9).reshape(-1).astype(jnp.float32)[:, None]
    gain_one = small_params[0:features]
    offset_one = small_params[features : 2 * features]
    gain_two = small_params[2 * features : 3 * features]
    offset_two = small_params[3 * features : 4 * features]
    table = small_params[4 * features :].reshape(HEADS, -1)
    onehot = (
        relative_index().reshape(-1)[:, None]
        == jnp.arange(table.shape[1], dtype=jnp.int32)[None, :]
    ).astype(jnp.float32)
    rel_bias = jnp.einsum("hr,pr->hp", table, onehot, precision=PRECISE).reshape(
        HEADS, window_area, window_area
    )

    def score_of(queries, key_vecs):
        raw = (
            jnp.einsum("wqhd,wkhd->whqk", queries, key_vecs, preferred_element_type=jnp.float32)
            * score_scale
            + rel_bias[None]
        )
        return jnp.where(allowed, raw, MASK_FILL)

    residual = to_windows(advance(tokens)).reshape(-1, features).astype(jnp.float32)
    normed_one, inverse_one = norm_stats(residual)
    act_one = (normed_one * gain_one + offset_one).astype(jnp.bfloat16)
    mixed = jnp.dot(act_one, w_qkv, preferred_element_type=jnp.float32).astype(jnp.bfloat16)
    grouped = mixed.reshape(window_count, window_area, 3, HEADS, head_dim)
    queries = grouped[:, :, 0]
    key_vecs = grouped[:, :, 1]
    values = grouped[:, :, 2]
    scores = score_of(queries, key_vecs)
    row_max = jnp.max(scores, -1, keepdims=True)
    exp_scores = jnp.exp(scores - row_max)
    exp_total = jnp.sum(exp_scores, -1, keepdims=True)
    log_total = row_max + jnp.log(exp_total)
    probs_low = (exp_scores / exp_total).astype(jnp.bfloat16)
    attended = jnp.einsum("whqk,wkhd->wqhd", probs_low, values, preferred_element_type=jnp.float32)
    attended = attended.reshape(-1, features).astype(jnp.bfloat16)
    branch_one = jnp.dot(attended, w_proj, preferred_element_type=jnp.float32)
    hidden = residual + branch_one
    normed_two, inverse_two = norm_stats(hidden)
    act_two = (normed_two * gain_two + offset_two).astype(jnp.bfloat16)
    pre_gelu = jnp.dot(act_two, w_fc1, preferred_element_type=jnp.float32)
    gelu_low = jax.nn.gelu(pre_gelu, approximate=False).astype(jnp.bfloat16)
    branch_two = jnp.dot(gelu_low, w_fc2, preferred_element_type=jnp.float32)
    output = hidden + branch_two
    stat_terms = jnp.stack(
        [
            jnp.sum(valid * output * output),
            jnp.sum(valid * (branch_one * branch_one + branch_two * branch_two)),
            jnp.sum(valid) * features,
        ]
    )
    output_low = output.astype(jnp.bfloat16).reshape(window_count, window_area, features)
    restored = retreat(from_windows(output_low, canvases, quad_side, quad_cols))
    flat_out = restored.reshape(canvases, quarters, share_rows, features)
    arrived = lax.all_to_all(flat_out, ("qy", "qx"), 1, 1, tiled=True)
    merged = jnp.take(arrived, merge_order, axis=1, mode="clip").transpose(0, 2, 1, 3).reshape(
        canvases, share_rows, quarters * features
    )
    quarter_ids = jnp.arange(quarters, dtype=jnp.int32)
    source_pick = jnp.sum(
        quarter_ids[:, None] * (merge_order[:, None] == quarter_ids[None, :]).astype(jnp.int32), 0
    )
    incoming = merged_grad.reshape(canvases, share_rows, quarters, features)
    unordered = jnp.take(incoming, source_pick, axis=2, mode="clip").transpose(0, 2, 1, 3)
    returned = lax.all_to_all(unordered, ("qy", "qx"), 1, 1, tiled=True)
    grad_orig = returned.reshape(canvases, quad_side, quad_cols, features)
    grad_out = to_windows(advance(grad_orig)).reshape(-1, features)
    grad_fc2 = jnp.einsum("rf,rc->fc", gelu_low, grad_out, preferred_element_type=jnp.float32)
    grad_gelu = jnp.einsum("rc,fc->rf", grad_out, w_fc2, preferred_element_type=jnp.float32)
    gelu_pull = jax.vjp(partial(jax.nn.gelu, approximate=False), pre_gelu)[1]
    grad_pre = gelu_pull(grad_gelu)[0].astype(jnp.bfloat16)
    grad_fc1 = jnp.einsum("rc,rf->cf", act_two, grad_pre, preferred_element_type=jnp.float32)
    grad_act_two = jnp.einsum("rf,cf->rc", grad_pre, w_fc1, preferred_element_type=jnp.float32)
    grad_hidden = grad_out.astype(jnp.float32) + norm_back(
        grad_act_two, normed_two, inverse_two, gain_two
    )
    grad_branch = grad_hidden.astype(jnp.bfloat16)
    grad_proj = jnp.einsum("rc,rd->cd", attended, grad_branch, preferred_element_type=jnp.float32)
    grad_attended = jnp.einsum(
        "rd,cd->rc", grad_branch, w_proj, preferred_element_type=jnp.float32
    ).astype(jnp.bfloat16)
    grad_attended = grad_attended.reshape(window_count, window_area, HEADS, head_dim)
    probs = jnp.exp(score_of(queries, key_vecs) - log_total)
    grad_probs = jnp.einsum(
        "wqhd,wkhd->whqk", grad_attended, values, preferred_element_type=jnp.float32
    )
    grad_values = jnp.einsum(
        "whqk,wqhd->wkhd", probs_low, grad_attended, preferred_element_type=jnp.float32
    )
    grad_scores = (probs * (grad_probs - jnp.sum(probs * grad_probs, -1, keepdims=True))).astype(
        jnp.bfloat16
    )
    grad_bias = jnp.sum(grad_scores.astype(jnp.float32), 0).reshape(HEADS, -1)
    grad_table = jnp.dot(grad_bias, onehot, precision=PRECISE)
    grad_queries = (
        jnp.einsum("whqk,wkhd->wqhd", grad_scores, key_vecs, preferred_element_type=jnp.float32)
        * score_scale
    )
    grad_keys = (
        jnp.einsum("whqk,wqhd->wkhd", grad_scores, queries, preferred_element_type=jnp.float32)
        * score_scale
    )
    grad_mixed = (
        jnp.stack([grad_queries, grad_keys, grad_values], 2)
        .astype(jnp.bfloat16)
        .reshape(-1, 3 * features)
    )
    grad_qkv = jnp.einsum("rc,rf->cf", act_one, grad_mixed, preferred_element_type=jnp.float32)
    grad_act_one = jnp.einsum("rf,cf->rc", grad_mixed, w_qkv, preferred_element_type=jnp.float32)
    grad_input = grad_hidden + norm_back(grad_act_one, normed_one, inverse_one, gain_one)
    grad_low = grad_input.astype(jnp.bfloat16).reshape(window_count, window_area, features)
    grad_tokens = retreat(from_windows(grad_low, canvases, quad_side, quad_cols))
    small_local = jnp.concatenate(
        [
            jnp.sum(grad_act_one * normed_one, 0),
            jnp.sum(grad_act_one, 0),
            jnp.sum(grad_act_two * normed_two, 0),
            jnp.sum(grad_act_two, 0),
            grad_table.reshape(-1),
        ]
    )
    every_block = jnp.concatenate(
        [lane_blocks(grad_qkv), lane_blocks(grad_proj), lane_blocks(grad_fc1), lane_blocks(grad_fc2)],
        0,
    )
    depth = every_block.shape[1] // PARTS
    parted = [
        jnp.take(every_block[:, index * depth : (index + 1) * depth], owner_list, axis=0, mode="clip")
        for index in range(PARTS)
    ]
    owned_grads, small_all = reduce_to_owners(parted, jnp.concatenate([small_local, stat_terms]))
    small_total = small_all[: small_local.shape[0]]
    stat_total = small_all[small_local.shape[0] :]
    new_first, new_second, new_master = rotate_update(
        owned_grads, master_blocks, first_moment, second_moment, basis_left, basis_right
    )
    small_first_new, small_second_new, small_new = small_update(
        small_total, small_params, small_first, small_second
    )
    stats = jnp.stack(
        [jnp.sqrt(stat_total[0] / stat_total[2]), jnp.sqrt(stat_total[1] / (2.0 * stat_total[2]))]
    )
    return (
        merged,
        grad_tokens,
        owned_grads,
        new_master,
        new_first,
        new_second,
        new_master.astype(jnp.bfloat16),
        small_total,
        small_first_new,
        small_second_new,
        small_new,
        stats,
    )


def solution(mesh):
    placed = (
        P("dp", "qy", "qx", None),
        P("dp", None, None),
        P(),
        P(),
        P(),
        P(),
        P(),
        P(),
        P(),
        P(),
        P(),
        P("dp", None, None),
        P("dp", None, None),
        P("dp", None, None),
        P("dp", None, None),
        P("dp", None, None),
        P("dp", ("qy", "qx"), None),
    )
    return jax.shard_map(
        local,
        mesh=mesh,
        in_specs=placed,
        out_specs=(
            P("dp", ("qy", "qx"), None),
            P("dp", "qy", "qx", None),
            P("dp", None, None),
            P("dp", None, None),
            P("dp", None, None),
            P("dp", None, None),
            P("dp", None, None),
            P(),
            P(),
            P(),
            P(),
            P(),
        ),
        check_vma=False,
    )
```

```python
import functools
from functools import partial

import jax
import jax.numpy as jnp
from jax import lax
from jax.experimental import pallas as pl
from jax.experimental.pallas import tpu as pltpu
from jax.sharding import PartitionSpec as P

HEADS = 12
WIN = 7
SHIFT = 3
BLK = 96


BETA_ONE = 0.5
BETA_TWO = 0.6
ADAM_EPSILON = 1e-08
RATE_BLOCKS = 0.04
RATE_SMALL = 0.2
MASK_FILL = -1e30
NORM_EPSILON = 1e-05
PRECISE = lax.Precision.HIGHEST


def passed_along(value, axis, steps):
    count = lax.axis_size(axis)
    pairs = [(source, (source + steps) % count) for source in range(count)]
    return lax.ppermute(value, axis, pairs)


def partner_of(value, axis, mask):
    count = lax.axis_size(axis)
    pairs = [(source, source ^ mask) for source in range(count)]
    return lax.ppermute(value, axis, pairs)


def bit_of(axis, mask):
    return ((lax.axis_index(axis) & mask) != 0).astype(jnp.int32)


LANES = 128
PARTS = 3
GROUP = 4
SPAN = 392


def _masked_scores(q4, k4, lane, j, bias, allowed, scale):
    qj = jnp.where(lane == j, q4, jnp.zeros_like(q4))
    raw = lax.dot_general(qj, k4, (((1,), (1,)), ((), ())), preferred_element_type=jnp.float32)
    return jnp.where(allowed, raw * scale + bias, MASK_FILL)


def _fwd_kernel(mix_ref, bias_ref, kc_ref, kr_ref, out_ref, lse_ref, *, scale, blocks):
    width = HEADS * 32
    lane = lax.broadcasted_iota(jnp.int32, (1, LANES), 1) // 32
    head_lane = lax.broadcasted_iota(jnp.int32, (1, LANES), 1)
    for b in range(blocks):
        rows = pl.ds(b * SPAN, SPAN)
        allowed = kc_ref[b] == kr_ref[b]
        lse_all = jnp.zeros((SPAN, LANES), jnp.float32)
        for g in range(HEADS // GROUP):
            q4 = mix_ref[rows, pl.ds(g * LANES, LANES)]
            k4 = mix_ref[rows, pl.ds(width + g * LANES, LANES)]
            v4 = mix_ref[rows, pl.ds(2 * width + g * LANES, LANES)]
            acc = jnp.zeros((SPAN, LANES), jnp.float32)
            for j in range(GROUP):
                h = g * GROUP + j
                s = _masked_scores(q4, k4, lane, j, bias_ref[h], allowed, scale)
                top = jnp.max(s, -1, keepdims=True)
                e = jnp.exp(s - top)
                total = jnp.sum(e, -1, keepdims=True)
                probs = (e / total).astype(jnp.bfloat16)
                vj = jnp.where(lane == j, v4, jnp.zeros_like(v4))
                acc = acc + jnp.dot(probs, vj, preferred_element_type=jnp.float32)
                lse_all = jnp.where(head_lane == h, top + jnp.log(total), lse_all)
            out_ref[rows, pl.ds(g * LANES, LANES)] = acc.astype(out_ref.dtype)
        lse_ref[b] = lse_all


def _bwd_kernel(mix_ref, grad_ref, lse_ref, bias_ref, kc_ref, kr_ref, gmix_ref, dbias_ref, *, scale, blocks):
    width = HEADS * 32
    lane = lax.broadcasted_iota(jnp.int32, (1, LANES), 1) // 32
    head_lane = lax.broadcasted_iota(jnp.int32, (1, LANES), 1)
    for b in range(blocks):
        rows = pl.ds(b * SPAN, SPAN)
        allowed = kc_ref[b] == kr_ref[b]
        lse_all = lse_ref[b]
        for g in range(HEADS // GROUP):
            q4 = mix_ref[rows, pl.ds(g * LANES, LANES)]
            k4 = mix_ref[rows, pl.ds(width + g * LANES, LANES)]
            v4 = mix_ref[rows, pl.ds(2 * width + g * LANES, LANES)]
            d4 = grad_ref[rows, pl.ds(g * LANES, LANES)]
            gq = jnp.zeros((SPAN, LANES), jnp.float32)
            gk = jnp.zeros((SPAN, LANES), jnp.float32)
            gv = jnp.zeros((SPAN, LANES), jnp.float32)
            for j in range(GROUP):
                h = g * GROUP + j
                s = _masked_scores(q4, k4, lane, j, bias_ref[h], allowed, scale)
                lse = jnp.sum(jnp.where(head_lane == h, lse_all, 0.0), -1, keepdims=True)
                probs = jnp.exp(s - lse)
                dj = jnp.where(lane == j, d4, jnp.zeros_like(d4))
                dprobs = lax.dot_general(dj, v4, (((1,), (1,)), ((), ())), preferred_element_type=jnp.float32)
                inner = jnp.sum(probs * dprobs, -1, keepdims=True)
                dscores = (probs * (dprobs - inner)).astype(jnp.bfloat16)
                if b == 0:
                    dbias_ref[h] = dscores.astype(jnp.float32)
                else:
                    dbias_ref[h] = dbias_ref[h] + dscores.astype(jnp.float32)
                kj = jnp.where(lane == j, k4, jnp.zeros_like(k4))
                qj = jnp.where(lane == j, q4, jnp.zeros_like(q4))
                gq = gq + jnp.dot(dscores, kj, preferred_element_type=jnp.float32)
                gk = gk + lax.dot_general(dscores, qj, (((0,), (0,)), ((), ())), preferred_element_type=jnp.float32)
                gv = gv + lax.dot_general(probs.astype(jnp.bfloat16), dj, (((0,), (0,)), ((), ())), preferred_element_type=jnp.float32)
            gmix_ref[rows, pl.ds(g * LANES, LANES)] = (gq * scale).astype(gmix_ref.dtype)
            gmix_ref[rows, pl.ds(width + g * LANES, LANES)] = (gk * scale).astype(gmix_ref.dtype)
            gmix_ref[rows, pl.ds(2 * width + g * LANES, LANES)] = gv.astype(gmix_ref.dtype)


def _vmem():
    return pl.BlockSpec(memory_space=pltpu.VMEM)


def attention_fwd(mixed, bias, key_col, key_row, scale):
    tokens = mixed.shape[0]
    blocks = tokens // SPAN
    kernel = functools.partial(_fwd_kernel, scale=scale, blocks=blocks)
    return pl.pallas_call(
        kernel,
        out_shape=(
            jax.ShapeDtypeStruct((tokens, HEADS * 32), jnp.bfloat16),
            jax.ShapeDtypeStruct((blocks, SPAN, LANES), jnp.float32),
        ),
        in_specs=[_vmem()] * 4,
        out_specs=(_vmem(), _vmem()),
        compiler_params=pltpu.CompilerParams(vmem_limit_bytes=48 * 1024 * 1024),
    )(mixed, bias, key_col, key_row)


def attention_bwd(mixed, grad_att, lse, bias, key_col, key_row, scale):
    tokens = mixed.shape[0]
    blocks = tokens // SPAN
    kernel = functools.partial(_bwd_kernel, scale=scale, blocks=blocks)
    return pl.pallas_call(
        kernel,
        out_shape=(
            jax.ShapeDtypeStruct(mixed.shape, jnp.bfloat16),
            jax.ShapeDtypeStruct(bias.shape, jnp.float32),
        ),
        in_specs=[_vmem()] * 6,
        out_specs=(_vmem(), _vmem()),
        compiler_params=pltpu.CompilerParams(vmem_limit_bytes=56 * 1024 * 1024),
    )(mixed, grad_att, lse, bias, key_col, key_row)


def lane_blocks(matrix):
    row_blocks, col_blocks = matrix.shape[0] // BLK, matrix.shape[1] // BLK
    shaped = matrix.reshape(row_blocks, BLK, col_blocks, BLK).transpose(0, 2, 1, 3)
    return shaped.reshape(row_blocks * col_blocks, BLK * BLK // LANES, LANES)


def reduce_to_owners(parted, small):
    groups = lax.axis_size("dp")
    dp_bits = groups.bit_length() - 1
    n_qy, n_qx = lax.axis_size("qy"), lax.axis_size("qx")
    count, depth = parted[0].shape[0], parted[0].shape[1]
    per_group = count // groups
    names = [("dp", 1 << power) for power in reversed(range(dp_bits))] + [("qy", 1), ("qx", 1)]
    cross = [("qy", 1)] + [("dp", 1 << power) for power in range(dp_bits)]
    pieces, piece_names, orders = [], [], []
    for index, part in enumerate(parted):
        pieces.append(
            part.reshape([2] * dp_bits + [n_qy, n_qx, per_group * depth // (n_qy * n_qx), LANES])
        )
        piece_names.append(list(names))
        turn = index % len(cross)
        orders.append([("qx", 1)] + cross[turn:] + cross[:turn])
    for stage in range(len(names)):
        for index in range(len(pieces)):
            bit = orders[index][stage]
            place = piece_names[index].index(bit)
            mine = bit_of(*bit)
            keep = lax.dynamic_index_in_dim(pieces[index], mine, place, keepdims=False)
            send = lax.dynamic_index_in_dim(pieces[index], 1 - mine, place, keepdims=False)
            piece_names[index].remove(bit)
            arrived = partner_of(send.astype(jnp.bfloat16), *bit)
            pieces[index] = keep + arrived.astype(jnp.float32)
            if index == 0:
                small = small + partner_of(small, *bit)
                pieces[0], small = lax.optimization_barrier((pieces[0], small))
    chunk = jnp.stack(pieces)
    other = partner_of(chunk, "qy", 1)
    pair = jnp.where(bit_of("qy", 1) == 1, jnp.stack([other, chunk], 1), jnp.stack([chunk, other], 1))
    other = partner_of(pair, "qx", 1)
    quad = jnp.where(bit_of("qx", 1) == 1, jnp.stack([other, pair], 2), jnp.stack([pair, other], 2))
    quad = quad.reshape(len(pieces), per_group, depth, LANES).transpose(1, 0, 2, 3)
    return quad.reshape(per_group, BLK, BLK), small


def cut_along(value, dim, devices):
    before, after = (value.shape[:dim], value.shape[dim + 1 :])
    return jnp.moveaxis(value.reshape(*before, devices, -1, *after), dim, 0)


def sent_and_summed(value, axis, dim):
    pieces = cut_along(value, dim, lax.axis_size(axis))
    arrived = lax.all_to_all(pieces, axis, split_axis=0, concat_axis=0, tiled=True)
    return arrived.astype(jnp.float32).sum(axis=0)


def norm_stats(tensor):
    center = tensor - jnp.mean(tensor, -1, keepdims=True)
    inverse = lax.rsqrt(jnp.mean(center * center, -1, keepdims=True) + NORM_EPSILON)
    return (center * inverse, inverse)


def norm_back(grad_act, normed, inverse, gain):
    scaled = grad_act * gain
    mean_one = jnp.mean(scaled, -1, keepdims=True)
    mean_two = jnp.mean(scaled * normed, -1, keepdims=True)
    return inverse * (scaled - mean_one - normed * mean_two)


def to_windows(tensor):
    canvases, rows_side, cols_side, channels = tensor.shape
    shaped = tensor.reshape(canvases, rows_side // WIN, WIN, cols_side // WIN, WIN, channels)
    return shaped.transpose(0, 1, 3, 2, 4, 5).reshape(
        canvases * (rows_side // WIN) * (cols_side // WIN), WIN * WIN, channels
    )


def from_windows(tensor, canvases, rows_side, cols_side):
    channels = tensor.shape[-1]
    shaped = tensor.reshape(canvases, rows_side // WIN, cols_side // WIN, WIN, WIN, channels)
    return shaped.transpose(0, 1, 3, 2, 4, 5).reshape(canvases, rows_side, cols_side, channels)


def relative_index():
    places = jnp.arange(WIN * WIN, dtype=jnp.int32)
    row_of = places // WIN
    col_of = places % WIN
    return (row_of[:, None] - row_of[None, :] + WIN - 1) * (2 * WIN - 1) + (
        col_of[:, None] - col_of[None, :] + WIN - 1
    )


def region_of(places, full):
    return jnp.where(places < full - WIN, 0, jnp.where(places < full - SHIFT, 1, 2)).astype(
        jnp.int32
    )


def advance(tensor):
    upper = passed_along(tensor[:, :SHIFT], "qy", -1)
    tensor = jnp.concatenate([tensor[:, SHIFT:], upper], 1)
    leftmost = passed_along(tensor[:, :, :SHIFT], "qx", -1)
    return jnp.concatenate([tensor[:, :, SHIFT:], leftmost], 2)


def retreat(tensor):
    lowest = passed_along(tensor[:, -SHIFT:], "qy", 1)
    tensor = jnp.concatenate([lowest, tensor[:, :-SHIFT]], 1)
    rightmost = passed_along(tensor[:, :, -SHIFT:], "qx", 1)
    return jnp.concatenate([rightmost, tensor[:, :, :-SHIFT]], 2)


def blocks_of(matrix):
    row_blocks = matrix.shape[0] // BLK
    col_blocks = matrix.shape[1] // BLK
    return (
        matrix.reshape(row_blocks, BLK, col_blocks, BLK)
        .transpose(0, 2, 1, 3)
        .reshape(row_blocks * col_blocks, BLK, BLK)
    )


def rotate_update(grads, master, first, second, left, right):
    turned = jnp.einsum("sji,sjk->sik", left, grads, precision=PRECISE)
    turned = jnp.einsum("sik,skl->sil", turned, right, precision=PRECISE)
    new_first = BETA_ONE * first + (1.0 - BETA_ONE) * turned
    new_second = BETA_TWO * second + (1.0 - BETA_TWO) * turned * turned
    direction = new_first / (jnp.sqrt(new_second) + ADAM_EPSILON)
    back = jnp.einsum("sij,sjk->sik", left, direction, precision=PRECISE)
    back = jnp.einsum("sik,slk->sil", back, right, precision=PRECISE)
    return (new_first, new_second, master - RATE_BLOCKS * back)


def small_update(grads, params, first, second):
    new_first = BETA_ONE * first + (1.0 - BETA_ONE) * grads
    new_second = BETA_TWO * second + (1.0 - BETA_TWO) * grads * grads
    direction = new_first / (jnp.sqrt(new_second) + ADAM_EPSILON)
    return (new_first, new_second, params - RATE_SMALL * direction)


def local(
    tokens,
    crop_ids,
    merge_order,
    owner_list,
    w_qkv,
    w_proj,
    w_fc1,
    w_fc2,
    small_params,
    small_first,
    small_second,
    master_blocks,
    first_moment,
    second_moment,
    basis_left,
    basis_right,
    merged_grad,
):
    canvases, quad_side, quad_cols, features = tokens.shape
    head_dim = features // HEADS
    score_scale = head_dim ** (-0.5)
    window_area = WIN * WIN
    quarters = lax.axis_size(("qy", "qx"))
    share_rows = quad_side * quad_cols // quarters
    row_base = lax.axis_index("qy") * quad_side
    col_base = lax.axis_index("qx") * quad_cols
    rolled = jnp.roll(crop_ids, (-SHIFT, -SHIFT), (1, 2))
    local_ids = lax.dynamic_slice(
        rolled, (jnp.int32(0), row_base, col_base), (canvases, quad_side, quad_cols)
    )
    region_row = region_of(
        row_base + jnp.arange(quad_side, dtype=jnp.int32), quad_side * lax.axis_size("qy")
    )
    region_col = region_of(
        col_base + jnp.arange(quad_cols, dtype=jnp.int32), quad_cols * lax.axis_size("qx")
    )
    labels = (local_ids + 1) * 9 + region_row[None, :, None] * 3 + region_col[None, None, :]
    win_labels = to_windows(labels[..., None])[..., 0]
    window_count = win_labels.shape[0]
    valid = (win_labels >= 9).reshape(-1).astype(jnp.float32)[:, None]
    gain_one = small_params[0:features]
    offset_one = small_params[features : 2 * features]
    gain_two = small_params[2 * features : 3 * features]
    offset_two = small_params[3 * features : 4 * features]
    table = small_params[4 * features :].reshape(HEADS, -1)
    onehot = (
        relative_index().reshape(-1)[:, None]
        == jnp.arange(table.shape[1], dtype=jnp.int32)[None, :]
    ).astype(jnp.float32)
    rel_bias = jnp.einsum("hr,pr->hp", table, onehot, precision=PRECISE).reshape(
        HEADS, window_area, window_area
    )

    residual = to_windows(advance(tokens)).reshape(-1, features).astype(jnp.float32)
    normed_one, inverse_one = norm_stats(residual)
    act_one = (normed_one * gain_one + offset_one).astype(jnp.bfloat16)
    mixed = jnp.dot(act_one, w_qkv, preferred_element_type=jnp.float32).astype(jnp.bfloat16)
    per_span = SPAN // window_area
    window_slot = jnp.arange(window_count, dtype=jnp.int32) % per_span
    span_keys = (win_labels * per_span + window_slot[:, None]).reshape(-1, SPAN)
    key_col, key_row = span_keys[:, :, None], span_keys[:, None, :]
    dense_bias = jnp.tile(rel_bias, (1, per_span, per_span))
    attended, log_total = attention_fwd(mixed, dense_bias, key_col, key_row, score_scale)
    branch_one = jnp.dot(attended, w_proj, preferred_element_type=jnp.float32)
    hidden = residual + branch_one
    normed_two, inverse_two = norm_stats(hidden)
    act_two = (normed_two * gain_two + offset_two).astype(jnp.bfloat16)
    pre_gelu = jnp.dot(act_two, w_fc1, preferred_element_type=jnp.float32)
    gelu_low = jax.nn.gelu(pre_gelu, approximate=False).astype(jnp.bfloat16)
    branch_two = jnp.dot(gelu_low, w_fc2, preferred_element_type=jnp.float32)
    output = hidden + branch_two
    stat_terms = jnp.stack(
        [
            jnp.sum(valid * output * output),
            jnp.sum(valid * (branch_one * branch_one + branch_two * branch_two)),
            jnp.sum(valid) * features,
        ]
    )
    output_low = output.astype(jnp.bfloat16).reshape(window_count, window_area, features)
    restored = retreat(from_windows(output_low, canvases, quad_side, quad_cols))
    flat_out = restored.reshape(canvases, quarters, share_rows, features)
    arrived = lax.all_to_all(flat_out, ("qy", "qx"), 1, 1, tiled=True)
    merged = jnp.take(arrived, merge_order, axis=1, mode="clip").transpose(0, 2, 1, 3).reshape(
        canvases, share_rows, quarters * features
    )
    quarter_ids = jnp.arange(quarters, dtype=jnp.int32)
    source_pick = jnp.sum(
        quarter_ids[:, None] * (merge_order[:, None] == quarter_ids[None, :]).astype(jnp.int32), 0
    )
    incoming = merged_grad.reshape(canvases, share_rows, quarters, features)
    unordered = jnp.take(incoming, source_pick, axis=2, mode="clip").transpose(0, 2, 1, 3)
    returned = lax.all_to_all(unordered, ("qy", "qx"), 1, 1, tiled=True)
    grad_orig = returned.reshape(canvases, quad_side, quad_cols, features)
    grad_out = to_windows(advance(grad_orig)).reshape(-1, features)
    grad_fc2 = jnp.einsum("rf,rc->fc", gelu_low, grad_out, preferred_element_type=jnp.float32)
    grad_gelu = jnp.einsum("rc,fc->rf", grad_out, w_fc2, preferred_element_type=jnp.float32)
    gelu_pull = jax.vjp(partial(jax.nn.gelu, approximate=False), pre_gelu)[1]
    grad_pre = gelu_pull(grad_gelu)[0].astype(jnp.bfloat16)
    grad_fc1 = jnp.einsum("rc,rf->cf", act_two, grad_pre, preferred_element_type=jnp.float32)
    grad_act_two = jnp.einsum("rf,cf->rc", grad_pre, w_fc1, preferred_element_type=jnp.float32)
    grad_hidden = grad_out.astype(jnp.float32) + norm_back(
        grad_act_two, normed_two, inverse_two, gain_two
    )
    grad_branch = grad_hidden.astype(jnp.bfloat16)
    grad_proj = jnp.einsum("rc,rd->cd", attended, grad_branch, preferred_element_type=jnp.float32)
    grad_attended = jnp.einsum(
        "rd,cd->rc", grad_branch, w_proj, preferred_element_type=jnp.float32
    ).astype(jnp.bfloat16)
    grad_mixed, dense_grad_bias = attention_bwd(
        mixed, grad_attended, log_total, dense_bias, key_col, key_row, score_scale
    )
    dense_grad_bias = dense_grad_bias.reshape(HEADS, per_span, window_area, per_span, window_area)
    grad_bias = sum(dense_grad_bias[:, index, :, index, :] for index in range(per_span))
    grad_table = jnp.dot(grad_bias.reshape(HEADS, -1), onehot, precision=PRECISE)
    grad_qkv = jnp.einsum("rc,rf->cf", act_one, grad_mixed, preferred_element_type=jnp.float32)
    grad_act_one = jnp.einsum("rf,cf->rc", grad_mixed, w_qkv, preferred_element_type=jnp.float32)
    grad_input = grad_hidden + norm_back(grad_act_one, normed_one, inverse_one, gain_one)
    grad_low = grad_input.astype(jnp.bfloat16).reshape(window_count, window_area, features)
    grad_tokens = retreat(from_windows(grad_low, canvases, quad_side, quad_cols))
    small_local = jnp.concatenate(
        [
            jnp.sum(grad_act_one * normed_one, 0),
            jnp.sum(grad_act_one, 0),
            jnp.sum(grad_act_two * normed_two, 0),
            jnp.sum(grad_act_two, 0),
            grad_table.reshape(-1),
        ]
    )
    every_block = jnp.concatenate(
        [lane_blocks(grad_qkv), lane_blocks(grad_proj), lane_blocks(grad_fc1), lane_blocks(grad_fc2)],
        0,
    )
    depth = every_block.shape[1] // PARTS
    parted = [
        jnp.take(every_block[:, index * depth : (index + 1) * depth], owner_list, axis=0, mode="clip")
        for index in range(PARTS)
    ]
    owned_grads, small_all = reduce_to_owners(parted, jnp.concatenate([small_local, stat_terms]))
    small_total = small_all[: small_local.shape[0]]
    stat_total = small_all[small_local.shape[0] :]
    new_first, new_second, new_master = rotate_update(
        owned_grads, master_blocks, first_moment, second_moment, basis_left, basis_right
    )
    small_first_new, small_second_new, small_new = small_update(
        small_total, small_params, small_first, small_second
    )
    stats = jnp.stack(
        [jnp.sqrt(stat_total[0] / stat_total[2]), jnp.sqrt(stat_total[1] / (2.0 * stat_total[2]))]
    )
    return (
        merged,
        grad_tokens,
        owned_grads,
        new_master,
        new_first,
        new_second,
        new_master.astype(jnp.bfloat16),
        small_total,
        small_first_new,
        small_second_new,
        small_new,
        stats,
    )


def solution(mesh):
    placed = (
        P("dp", "qy", "qx", None),
        P("dp", None, None),
        P(),
        P(),
        P(),
        P(),
        P(),
        P(),
        P(),
        P(),
        P(),
        P("dp", None, None),
        P("dp", None, None),
        P("dp", None, None),
        P("dp", None, None),
        P("dp", None, None),
        P("dp", ("qy", "qx"), None),
    )
    return jax.shard_map(
        local,
        mesh=mesh,
        in_specs=placed,
        out_specs=(
            P("dp", ("qy", "qx"), None),
            P("dp", "qy", "qx", None),
            P("dp", None, None),
            P("dp", None, None),
            P("dp", None, None),
            P("dp", None, None),
            P("dp", None, None),
            P(),
            P(),
            P(),
            P(),
            P(),
        ),
        check_vma=False,
    )
```

```python
import functools
from functools import partial

import jax
import jax.numpy as jnp
from jax import lax
from jax.experimental import pallas as pl
from jax.experimental.pallas import tpu as pltpu
from jax.sharding import PartitionSpec as P

HEADS = 12
WIN = 7
SHIFT = 3
BLK = 96


BETA_ONE = 0.5
BETA_TWO = 0.6
ADAM_EPSILON = 1e-08
RATE_BLOCKS = 0.04
RATE_SMALL = 0.2
MASK_FILL = -1e30
NORM_EPSILON = 1e-05
PRECISE = lax.Precision.HIGHEST


def passed_along(value, axis, steps):
    count = lax.axis_size(axis)
    pairs = [(source, (source + steps) % count) for source in range(count)]
    return lax.ppermute(value, axis, pairs)


def partner_of(value, axis, mask):
    count = lax.axis_size(axis)
    pairs = [(source, source ^ mask) for source in range(count)]
    return lax.ppermute(value, axis, pairs)


def bit_of(axis, mask):
    return ((lax.axis_index(axis) & mask) != 0).astype(jnp.int32)


LANES = 128
PARTS = 3
GROUP = 4
SPAN = 392


def _masked_scores(q4, k4, lane, j, bias, allowed, scale):
    qj = jnp.where(lane == j, q4, jnp.zeros_like(q4))
    raw = lax.dot_general(qj, k4, (((1,), (1,)), ((), ())), preferred_element_type=jnp.float32)
    return jnp.where(allowed, raw * scale + bias, MASK_FILL)


def _fwd_kernel(mix_ref, bias_ref, kc_ref, kr_ref, out_ref, lse_ref, *, scale, blocks):
    width = HEADS * 32
    lane = lax.broadcasted_iota(jnp.int32, (1, LANES), 1) // 32
    head_lane = lax.broadcasted_iota(jnp.int32, (1, LANES), 1)
    for b in range(blocks):
        rows = pl.ds(b * SPAN, SPAN)
        allowed = kc_ref[b] == kr_ref[b]
        lse_all = jnp.zeros((SPAN, LANES), jnp.float32)
        for g in range(HEADS // GROUP):
            q4 = mix_ref[rows, pl.ds(g * LANES, LANES)]
            k4 = mix_ref[rows, pl.ds(width + g * LANES, LANES)]
            v4 = mix_ref[rows, pl.ds(2 * width + g * LANES, LANES)]
            acc = jnp.zeros((SPAN, LANES), jnp.float32)
            for j in range(GROUP):
                h = g * GROUP + j
                s = _masked_scores(q4, k4, lane, j, bias_ref[h], allowed, scale)
                top = jnp.max(s, -1, keepdims=True)
                e = jnp.exp(s - top)
                total = jnp.sum(e, -1, keepdims=True)
                probs = (e / total).astype(jnp.bfloat16)
                vj = jnp.where(lane == j, v4, jnp.zeros_like(v4))
                acc = acc + jnp.dot(probs, vj, preferred_element_type=jnp.float32)
                lse_all = jnp.where(head_lane == h, top + jnp.log(total), lse_all)
            out_ref[rows, pl.ds(g * LANES, LANES)] = acc.astype(out_ref.dtype)
        lse_ref[b] = lse_all


def _bwd_kernel(mix_ref, grad_ref, lse_ref, bias_ref, kc_ref, kr_ref, gmix_ref, dbias_ref, *, scale, blocks):
    width = HEADS * 32
    lane = lax.broadcasted_iota(jnp.int32, (1, LANES), 1) // 32
    head_lane = lax.broadcasted_iota(jnp.int32, (1, LANES), 1)
    for b in range(blocks):
        rows = pl.ds(b * SPAN, SPAN)
        allowed = kc_ref[b] == kr_ref[b]
        lse_all = lse_ref[b]
        for g in range(HEADS // GROUP):
            q4 = mix_ref[rows, pl.ds(g * LANES, LANES)]
            k4 = mix_ref[rows, pl.ds(width + g * LANES, LANES)]
            v4 = mix_ref[rows, pl.ds(2 * width + g * LANES, LANES)]
            d4 = grad_ref[rows, pl.ds(g * LANES, LANES)]
            gq = jnp.zeros((SPAN, LANES), jnp.float32)
            gk = jnp.zeros((SPAN, LANES), jnp.float32)
            gv = jnp.zeros((SPAN, LANES), jnp.float32)
            for j in range(GROUP):
                h = g * GROUP + j
                s = _masked_scores(q4, k4, lane, j, bias_ref[h], allowed, scale)
                lse = jnp.sum(jnp.where(head_lane == h, lse_all, 0.0), -1, keepdims=True)
                probs = jnp.exp(s - lse)
                dj = jnp.where(lane == j, d4, jnp.zeros_like(d4))
                dprobs = lax.dot_general(dj, v4, (((1,), (1,)), ((), ())), preferred_element_type=jnp.float32)
                inner = jnp.sum(probs * dprobs, -1, keepdims=True)
                dscores = (probs * (dprobs - inner)).astype(jnp.bfloat16)
                if b == 0:
                    dbias_ref[h] = dscores.astype(jnp.float32)
                else:
                    dbias_ref[h] = dbias_ref[h] + dscores.astype(jnp.float32)
                kj = jnp.where(lane == j, k4, jnp.zeros_like(k4))
                qj = jnp.where(lane == j, q4, jnp.zeros_like(q4))
                gq = gq + jnp.dot(dscores, kj, preferred_element_type=jnp.float32)
                gk = gk + lax.dot_general(dscores, qj, (((0,), (0,)), ((), ())), preferred_element_type=jnp.float32)
                gv = gv + lax.dot_general(probs.astype(jnp.bfloat16), dj, (((0,), (0,)), ((), ())), preferred_element_type=jnp.float32)
            gmix_ref[rows, pl.ds(g * LANES, LANES)] = (gq * scale).astype(gmix_ref.dtype)
            gmix_ref[rows, pl.ds(width + g * LANES, LANES)] = (gk * scale).astype(gmix_ref.dtype)
            gmix_ref[rows, pl.ds(2 * width + g * LANES, LANES)] = gv.astype(gmix_ref.dtype)


def _vmem():
    return pl.BlockSpec(memory_space=pltpu.VMEM)


def attention_fwd(mixed, bias, key_col, key_row, scale):
    tokens = mixed.shape[0]
    blocks = tokens // SPAN
    kernel = functools.partial(_fwd_kernel, scale=scale, blocks=blocks)
    return pl.pallas_call(
        kernel,
        out_shape=(
            jax.ShapeDtypeStruct((tokens, HEADS * 32), jnp.bfloat16),
            jax.ShapeDtypeStruct((blocks, SPAN, LANES), jnp.float32),
        ),
        in_specs=[_vmem()] * 4,
        out_specs=(_vmem(), _vmem()),
        compiler_params=pltpu.CompilerParams(vmem_limit_bytes=48 * 1024 * 1024),
    )(mixed, bias, key_col, key_row)


def attention_bwd(mixed, grad_att, lse, bias, key_col, key_row, scale):
    tokens = mixed.shape[0]
    blocks = tokens // SPAN
    kernel = functools.partial(_bwd_kernel, scale=scale, blocks=blocks)
    return pl.pallas_call(
        kernel,
        out_shape=(
            jax.ShapeDtypeStruct(mixed.shape, jnp.bfloat16),
            jax.ShapeDtypeStruct(bias.shape, jnp.float32),
        ),
        in_specs=[_vmem()] * 6,
        out_specs=(_vmem(), _vmem()),
        compiler_params=pltpu.CompilerParams(vmem_limit_bytes=56 * 1024 * 1024),
    )(mixed, grad_att, lse, bias, key_col, key_row)


def lane_blocks(matrix):
    row_blocks, col_blocks = matrix.shape[0] // BLK, matrix.shape[1] // BLK
    shaped = matrix.reshape(row_blocks, BLK, col_blocks, BLK).transpose(0, 2, 1, 3)
    return shaped.reshape(row_blocks * col_blocks, BLK * BLK // LANES, LANES)


def reduce_to_owners(parted, small):
    groups = lax.axis_size("dp")
    dp_bits = groups.bit_length() - 1
    n_qy, n_qx = lax.axis_size("qy"), lax.axis_size("qx")
    count, depth = parted[0].shape[0], parted[0].shape[1]
    per_group = count // groups
    names = [("dp", 1 << power) for power in reversed(range(dp_bits))] + [("qy", 1), ("qx", 1)]
    cross = [("qy", 1)] + [("dp", 1 << power) for power in range(dp_bits)]
    pieces, piece_names, orders = [], [], []
    for index, part in enumerate(parted):
        pieces.append(
            part.reshape([2] * dp_bits + [n_qy, n_qx, per_group * depth // (n_qy * n_qx), LANES])
        )
        piece_names.append(list(names))
        turn = index % len(cross)
        orders.append([("qx", 1)] + cross[turn:] + cross[:turn])
    for stage in range(len(names)):
        for index in range(len(pieces)):
            bit = orders[index][stage]
            place = piece_names[index].index(bit)
            mine = bit_of(*bit)
            keep = lax.dynamic_index_in_dim(pieces[index], mine, place, keepdims=False)
            send = lax.dynamic_index_in_dim(pieces[index], 1 - mine, place, keepdims=False)
            piece_names[index].remove(bit)
            arrived = partner_of(send.astype(jnp.bfloat16), *bit)
            pieces[index] = keep + arrived.astype(jnp.float32)
            if index == 0:
                small = small + partner_of(small, *bit)
                pieces[0], small = lax.optimization_barrier((pieces[0], small))
    chunk = jnp.stack(pieces)
    other = partner_of(chunk, "qy", 1)
    pair = jnp.where(bit_of("qy", 1) == 1, jnp.stack([other, chunk], 1), jnp.stack([chunk, other], 1))
    other = partner_of(pair, "qx", 1)
    quad = jnp.where(bit_of("qx", 1) == 1, jnp.stack([other, pair], 2), jnp.stack([pair, other], 2))
    quad = quad.reshape(len(pieces), per_group, depth, LANES).transpose(1, 0, 2, 3)
    return quad.reshape(per_group, BLK, BLK), small


def cut_along(value, dim, devices):
    before, after = (value.shape[:dim], value.shape[dim + 1 :])
    return jnp.moveaxis(value.reshape(*before, devices, -1, *after), dim, 0)


def sent_and_summed(value, axis, dim):
    pieces = cut_along(value, dim, lax.axis_size(axis))
    arrived = lax.all_to_all(pieces, axis, split_axis=0, concat_axis=0, tiled=True)
    return arrived.astype(jnp.float32).sum(axis=0)


def norm_stats(tensor):
    center = tensor - jnp.mean(tensor, -1, keepdims=True)
    inverse = lax.rsqrt(jnp.mean(center * center, -1, keepdims=True) + NORM_EPSILON)
    return (center * inverse, inverse)


def norm_back(grad_act, normed, inverse, gain):
    scaled = grad_act * gain
    mean_one = jnp.mean(scaled, -1, keepdims=True)
    mean_two = jnp.mean(scaled * normed, -1, keepdims=True)
    return inverse * (scaled - mean_one - normed * mean_two)


def to_windows(tensor):
    canvases, rows_side, cols_side, channels = tensor.shape
    shaped = tensor.reshape(canvases, rows_side // WIN, WIN, cols_side // WIN, WIN, channels)
    return shaped.transpose(0, 1, 3, 2, 4, 5).reshape(
        canvases * (rows_side // WIN) * (cols_side // WIN), WIN * WIN, channels
    )


def from_windows(tensor, canvases, rows_side, cols_side):
    channels = tensor.shape[-1]
    shaped = tensor.reshape(canvases, rows_side // WIN, cols_side // WIN, WIN, WIN, channels)
    return shaped.transpose(0, 1, 3, 2, 4, 5).reshape(canvases, rows_side, cols_side, channels)


def relative_index():
    places = jnp.arange(WIN * WIN, dtype=jnp.int32)
    row_of = places // WIN
    col_of = places % WIN
    return (row_of[:, None] - row_of[None, :] + WIN - 1) * (2 * WIN - 1) + (
        col_of[:, None] - col_of[None, :] + WIN - 1
    )


def region_of(places, full):
    return jnp.where(places < full - WIN, 0, jnp.where(places < full - SHIFT, 1, 2)).astype(
        jnp.int32
    )


def advance(tensor):
    upper = passed_along(tensor[:, :SHIFT], "qy", -1)
    tensor = jnp.concatenate([tensor[:, SHIFT:], upper], 1)
    leftmost = passed_along(tensor[:, :, :SHIFT], "qx", -1)
    return jnp.concatenate([tensor[:, :, SHIFT:], leftmost], 2)


def retreat(tensor):
    lowest = passed_along(tensor[:, -SHIFT:], "qy", 1)
    tensor = jnp.concatenate([lowest, tensor[:, :-SHIFT]], 1)
    rightmost = passed_along(tensor[:, :, -SHIFT:], "qx", 1)
    return jnp.concatenate([rightmost, tensor[:, :, :-SHIFT]], 2)


def blocks_of(matrix):
    row_blocks = matrix.shape[0] // BLK
    col_blocks = matrix.shape[1] // BLK
    return (
        matrix.reshape(row_blocks, BLK, col_blocks, BLK)
        .transpose(0, 2, 1, 3)
        .reshape(row_blocks * col_blocks, BLK, BLK)
    )


def rotate_update(grads, master, first, second, left, right):
    turned = jnp.einsum("sji,sjk->sik", left, grads, precision=PRECISE)
    turned = jnp.einsum("sik,skl->sil", turned, right, precision=PRECISE)
    new_first = BETA_ONE * first + (1.0 - BETA_ONE) * turned
    new_second = BETA_TWO * second + (1.0 - BETA_TWO) * turned * turned
    direction = new_first / (jnp.sqrt(new_second) + ADAM_EPSILON)
    back = jnp.einsum("sij,sjk->sik", left, direction, precision=PRECISE)
    back = jnp.einsum("sik,slk->sil", back, right, precision=PRECISE)
    return (new_first, new_second, master - RATE_BLOCKS * back)


def small_update(grads, params, first, second):
    new_first = BETA_ONE * first + (1.0 - BETA_ONE) * grads
    new_second = BETA_TWO * second + (1.0 - BETA_TWO) * grads * grads
    direction = new_first / (jnp.sqrt(new_second) + ADAM_EPSILON)
    return (new_first, new_second, params - RATE_SMALL * direction)


def local(
    tokens,
    crop_ids,
    merge_order,
    owner_list,
    w_qkv,
    w_proj,
    w_fc1,
    w_fc2,
    small_params,
    small_first,
    small_second,
    master_blocks,
    first_moment,
    second_moment,
    basis_left,
    basis_right,
    merged_grad,
):
    canvases, quad_side, quad_cols, features = tokens.shape
    head_dim = features // HEADS
    score_scale = head_dim ** (-0.5)
    window_area = WIN * WIN
    quarters = lax.axis_size(("qy", "qx"))
    share_rows = quad_side * quad_cols // quarters
    row_base = lax.axis_index("qy") * quad_side
    col_base = lax.axis_index("qx") * quad_cols
    rolled = jnp.roll(crop_ids, (-SHIFT, -SHIFT), (1, 2))
    local_ids = lax.dynamic_slice(
        rolled, (jnp.int32(0), row_base, col_base), (canvases, quad_side, quad_cols)
    )
    region_row = region_of(
        row_base + jnp.arange(quad_side, dtype=jnp.int32), quad_side * lax.axis_size("qy")
    )
    region_col = region_of(
        col_base + jnp.arange(quad_cols, dtype=jnp.int32), quad_cols * lax.axis_size("qx")
    )
    labels = (local_ids + 1) * 9 + region_row[None, :, None] * 3 + region_col[None, None, :]
    win_labels = to_windows(labels[..., None])[..., 0]
    window_count = win_labels.shape[0]
    valid = (win_labels >= 9).reshape(-1).astype(jnp.float32)[:, None]
    gain_one = small_params[0:features]
    offset_one = small_params[features : 2 * features]
    gain_two = small_params[2 * features : 3 * features]
    offset_two = small_params[3 * features : 4 * features]
    table = small_params[4 * features :].reshape(HEADS, -1)
    onehot = (
        relative_index().reshape(-1)[:, None]
        == jnp.arange(table.shape[1], dtype=jnp.int32)[None, :]
    ).astype(jnp.float32)
    rel_bias = jnp.einsum("hr,pr->hp", table, onehot, precision=PRECISE).reshape(
        HEADS, window_area, window_area
    )

    residual = to_windows(advance(tokens)).reshape(-1, features).astype(jnp.float32)
    normed_one, inverse_one = norm_stats(residual)
    act_one = (normed_one * gain_one + offset_one).astype(jnp.bfloat16)
    mixed = jnp.dot(act_one, w_qkv, preferred_element_type=jnp.float32).astype(jnp.bfloat16)
    per_span = SPAN // window_area
    window_slot = jnp.arange(window_count, dtype=jnp.int32) % per_span
    span_keys = (win_labels * per_span + window_slot[:, None]).reshape(-1, SPAN)
    key_col, key_row = span_keys[:, :, None], span_keys[:, None, :]
    spread = (
        jnp.arange(SPAN, dtype=jnp.int32)[:, None] % window_area
        == jnp.arange(window_area, dtype=jnp.int32)[None, :]
    ).astype(jnp.float32)
    dense_bias = jnp.einsum(
        "hti,ui->htu",
        jnp.einsum("ti,hij->htj", spread, rel_bias, precision=PRECISE),
        spread,
        precision=PRECISE,
    )
    attended, log_total = attention_fwd(mixed, dense_bias, key_col, key_row, score_scale)
    branch_one = jnp.dot(attended, w_proj, preferred_element_type=jnp.float32)
    hidden = residual + branch_one
    normed_two, inverse_two = norm_stats(hidden)
    act_two = (normed_two * gain_two + offset_two).astype(jnp.bfloat16)
    pre_gelu = jnp.dot(act_two, w_fc1, preferred_element_type=jnp.float32)
    gelu_low = jax.nn.gelu(pre_gelu, approximate=False).astype(jnp.bfloat16)
    branch_two = jnp.dot(gelu_low, w_fc2, preferred_element_type=jnp.float32)
    output = hidden + branch_two
    stat_terms = jnp.stack(
        [
            jnp.sum(valid * output * output),
            jnp.sum(valid * (branch_one * branch_one + branch_two * branch_two)),
            jnp.sum(valid) * features,
        ]
    )
    output_low = output.astype(jnp.bfloat16).reshape(window_count, window_area, features)
    restored = retreat(from_windows(output_low, canvases, quad_side, quad_cols))
    flat_out = restored.reshape(canvases, quarters, share_rows, features)
    arrived = lax.all_to_all(flat_out, ("qy", "qx"), 1, 1, tiled=True)
    merged = jnp.take(arrived, merge_order, axis=1, mode="clip").transpose(0, 2, 1, 3).reshape(
        canvases, share_rows, quarters * features
    )
    quarter_ids = jnp.arange(quarters, dtype=jnp.int32)
    source_pick = jnp.sum(
        quarter_ids[:, None] * (merge_order[:, None] == quarter_ids[None, :]).astype(jnp.int32), 0
    )
    incoming = merged_grad.reshape(canvases, share_rows, quarters, features)
    unordered = jnp.take(incoming, source_pick, axis=2, mode="clip").transpose(0, 2, 1, 3)
    returned = lax.all_to_all(unordered, ("qy", "qx"), 1, 1, tiled=True)
    grad_orig = returned.reshape(canvases, quad_side, quad_cols, features)
    grad_out = to_windows(advance(grad_orig)).reshape(-1, features)
    grad_fc2 = jnp.einsum("rf,rc->fc", gelu_low, grad_out, preferred_element_type=jnp.float32)
    grad_gelu = jnp.einsum("rc,fc->rf", grad_out, w_fc2, preferred_element_type=jnp.float32)
    gelu_pull = jax.vjp(partial(jax.nn.gelu, approximate=False), pre_gelu)[1]
    grad_pre = gelu_pull(grad_gelu)[0].astype(jnp.bfloat16)
    grad_fc1 = jnp.einsum("rc,rf->cf", act_two, grad_pre, preferred_element_type=jnp.float32)
    grad_act_two = jnp.einsum("rf,cf->rc", grad_pre, w_fc1, preferred_element_type=jnp.float32)
    grad_hidden = grad_out.astype(jnp.float32) + norm_back(
        grad_act_two, normed_two, inverse_two, gain_two
    )
    grad_branch = grad_hidden.astype(jnp.bfloat16)
    grad_proj = jnp.einsum("rc,rd->cd", attended, grad_branch, preferred_element_type=jnp.float32)
    grad_attended = jnp.einsum(
        "rd,cd->rc", grad_branch, w_proj, preferred_element_type=jnp.float32
    ).astype(jnp.bfloat16)
    grad_mixed, dense_grad_bias = attention_bwd(
        mixed, grad_attended, log_total, dense_bias, key_col, key_row, score_scale
    )
    grad_bias = jnp.einsum(
        "ti,htj->hij",
        spread,
        jnp.einsum("htu,uj->htj", dense_grad_bias, spread, precision=PRECISE),
        precision=PRECISE,
    )
    grad_table = jnp.dot(grad_bias.reshape(HEADS, -1), onehot, precision=PRECISE)
    grad_qkv = jnp.einsum("rc,rf->cf", act_one, grad_mixed, preferred_element_type=jnp.float32)
    grad_act_one = jnp.einsum("rf,cf->rc", grad_mixed, w_qkv, preferred_element_type=jnp.float32)
    grad_input = grad_hidden + norm_back(grad_act_one, normed_one, inverse_one, gain_one)
    grad_low = grad_input.astype(jnp.bfloat16).reshape(window_count, window_area, features)
    grad_tokens = retreat(from_windows(grad_low, canvases, quad_side, quad_cols))
    small_local = jnp.concatenate(
        [
            jnp.sum(grad_act_one * normed_one, 0),
            jnp.sum(grad_act_one, 0),
            jnp.sum(grad_act_two * normed_two, 0),
            jnp.sum(grad_act_two, 0),
            grad_table.reshape(-1),
        ]
    )
    every_block = jnp.concatenate(
        [lane_blocks(grad_qkv), lane_blocks(grad_proj), lane_blocks(grad_fc1), lane_blocks(grad_fc2)],
        0,
    )
    depth = every_block.shape[1] // PARTS
    parted = [
        jnp.take(every_block[:, index * depth : (index + 1) * depth], owner_list, axis=0, mode="clip")
        for index in range(PARTS)
    ]
    owned_grads, small_all = reduce_to_owners(parted, jnp.concatenate([small_local, stat_terms]))
    small_total = small_all[: small_local.shape[0]]
    stat_total = small_all[small_local.shape[0] :]
    new_first, new_second, new_master = rotate_update(
        owned_grads, master_blocks, first_moment, second_moment, basis_left, basis_right
    )
    small_first_new, small_second_new, small_new = small_update(
        small_total, small_params, small_first, small_second
    )
    stats = jnp.stack(
        [jnp.sqrt(stat_total[0] / stat_total[2]), jnp.sqrt(stat_total[1] / (2.0 * stat_total[2]))]
    )
    return (
        merged,
        grad_tokens,
        owned_grads,
        new_master,
        new_first,
        new_second,
        new_master.astype(jnp.bfloat16),
        small_total,
        small_first_new,
        small_second_new,
        small_new,
        stats,
    )


def solution(mesh):
    placed = (
        P("dp", "qy", "qx", None),
        P("dp", None, None),
        P(),
        P(),
        P(),
        P(),
        P(),
        P(),
        P(),
        P(),
        P(),
        P("dp", None, None),
        P("dp", None, None),
        P("dp", None, None),
        P("dp", None, None),
        P("dp", None, None),
        P("dp", ("qy", "qx"), None),
    )
    return jax.shard_map(
        local,
        mesh=mesh,
        in_specs=placed,
        out_specs=(
            P("dp", ("qy", "qx"), None),
            P("dp", "qy", "qx", None),
            P("dp", None, None),
            P("dp", None, None),
            P("dp", None, None),
            P("dp", None, None),
            P("dp", None, None),
            P(),
            P(),
            P(),
            P(),
            P(),
        ),
        check_vma=False,
    )
```

```python
import functools
from functools import partial

import jax
import jax.numpy as jnp
from jax import lax
from jax.experimental import pallas as pl
from jax.experimental.pallas import tpu as pltpu
from jax.sharding import PartitionSpec as P

HEADS = 12
WIN = 7
SHIFT = 3
BLK = 96


BETA_ONE = 0.5
BETA_TWO = 0.6
ADAM_EPSILON = 1e-08
RATE_BLOCKS = 0.04
RATE_SMALL = 0.2
MASK_FILL = -1e30
NORM_EPSILON = 1e-05
PRECISE = lax.Precision.HIGHEST


def passed_along(value, axis, steps):
    count = lax.axis_size(axis)
    pairs = [(source, (source + steps) % count) for source in range(count)]
    return lax.ppermute(value, axis, pairs)


def partner_of(value, axis, mask):
    count = lax.axis_size(axis)
    pairs = [(source, source ^ mask) for source in range(count)]
    return lax.ppermute(value, axis, pairs)


def bit_of(axis, mask):
    return ((lax.axis_index(axis) & mask) != 0).astype(jnp.int32)


LANES = 128
PARTS = 3
GROUP = 4
SPAN = 392
CHUNK = 56
AREA = 49


def _chunks():
    out = []
    for start in range(0, SPAN, CHUNK):
        first, last = start // AREA, (start + CHUNK - 1) // AREA
        low = (first * AREA) // LANES * LANES
        high = min(-(-((last + 1) * AREA) // LANES) * LANES, SPAN)
        out.append((start, low, high))
    return out


def _fwd_kernel(mix_ref, bias_ref, kc_ref, kr_ref, out_ref, lse_ref, *, scale, blocks):
    width = HEADS * 32
    lane = lax.broadcasted_iota(jnp.int32, (1, LANES), 1) // 32
    head_lane = lax.broadcasted_iota(jnp.int32, (1, LANES), 1)
    for b in range(blocks):
        base = b * SPAN
        for start, low, high in _chunks():
            rows = pl.ds(base + start, CHUNK)
            cols = pl.ds(base + low, high - low)
            allowed = kc_ref[b, pl.ds(start, CHUNK), :] == kr_ref[b, :, pl.ds(low, high - low)]
            lse_all = jnp.zeros((CHUNK, LANES), jnp.float32)
            for g in range(HEADS // GROUP):
                q4 = mix_ref[rows, pl.ds(g * LANES, LANES)]
                k4 = mix_ref[cols, pl.ds(width + g * LANES, LANES)].astype(jnp.bfloat16)
                v4 = mix_ref[cols, pl.ds(2 * width + g * LANES, LANES)]
                acc = jnp.zeros((CHUNK, LANES), jnp.float32)
                for j in range(GROUP):
                    h = g * GROUP + j
                    qj = jnp.where(lane == j, q4, 0.0).astype(jnp.bfloat16)
                    raw = lax.dot_general(qj, k4, (((1,), (1,)), ((), ())), preferred_element_type=jnp.float32)
                    bias = bias_ref[h, pl.ds(start, CHUNK), pl.ds(low, high - low)]
                    s = jnp.where(allowed, raw * scale + bias, MASK_FILL)
                    top = jnp.max(s, -1, keepdims=True)
                    e = jnp.exp(s - top)
                    total = jnp.sum(e, -1, keepdims=True)
                    probs = (e / total).astype(jnp.bfloat16)
                    vj = jnp.where(lane == j, v4, 0.0).astype(jnp.bfloat16)
                    acc = acc + jnp.dot(probs, vj, preferred_element_type=jnp.float32)
                    lse_all = jnp.where(head_lane == h, top + jnp.log(total), lse_all)
                out_ref[rows, pl.ds(g * LANES, LANES)] = acc.astype(out_ref.dtype)
            lse_ref[b, pl.ds(start, CHUNK), :] = lse_all


def _bwd_kernel(mix_ref, grad_ref, lse_ref, bias_ref, kc_ref, kr_ref, gmix_ref, dbias_ref, gk_acc, gv_acc, *, scale, blocks):
    width = HEADS * 32
    lane = lax.broadcasted_iota(jnp.int32, (1, LANES), 1) // 32
    head_lane = lax.broadcasted_iota(jnp.int32, (1, LANES), 1)
    dbias_ref[...] = jnp.zeros_like(dbias_ref)
    for b in range(blocks):
        base = b * SPAN
        gk_acc[...] = jnp.zeros_like(gk_acc)
        gv_acc[...] = jnp.zeros_like(gv_acc)
        for start, low, high in _chunks():
            rows = pl.ds(base + start, CHUNK)
            cols = pl.ds(base + low, high - low)
            allowed = kc_ref[b, pl.ds(start, CHUNK), :] == kr_ref[b, :, pl.ds(low, high - low)]
            lse_all = lse_ref[b, pl.ds(start, CHUNK), :]
            for g in range(HEADS // GROUP):
                q4 = mix_ref[rows, pl.ds(g * LANES, LANES)]
                k4 = mix_ref[cols, pl.ds(width + g * LANES, LANES)].astype(jnp.bfloat16)
                v4 = mix_ref[cols, pl.ds(2 * width + g * LANES, LANES)].astype(jnp.bfloat16)
                d4 = grad_ref[rows, pl.ds(g * LANES, LANES)]
                gq = jnp.zeros((CHUNK, LANES), jnp.float32)
                gk = jnp.zeros((high - low, LANES), jnp.float32)
                gv = jnp.zeros((high - low, LANES), jnp.float32)
                for j in range(GROUP):
                    h = g * GROUP + j
                    qj = jnp.where(lane == j, q4, 0.0).astype(jnp.bfloat16)
                    raw = lax.dot_general(qj, k4, (((1,), (1,)), ((), ())), preferred_element_type=jnp.float32)
                    bias = bias_ref[h, pl.ds(start, CHUNK), pl.ds(low, high - low)]
                    s = jnp.where(allowed, raw * scale + bias, MASK_FILL)
                    lse = jnp.sum(jnp.where(head_lane == h, lse_all, 0.0), -1, keepdims=True)
                    probs = jnp.exp(s - lse)
                    dj = jnp.where(lane == j, d4, 0.0).astype(jnp.bfloat16)
                    dprobs = lax.dot_general(dj, v4, (((1,), (1,)), ((), ())), preferred_element_type=jnp.float32)
                    inner = jnp.sum(probs * dprobs, -1, keepdims=True)
                    dscores = (probs * (dprobs - inner)).astype(jnp.bfloat16)
                    region = (h, pl.ds(start, CHUNK), pl.ds(low, high - low))
                    dbias_ref[region] = dbias_ref[region] + dscores.astype(jnp.float32)
                    kj = jnp.where(lane == j, k4, jnp.zeros_like(k4))
                    gq = gq + jnp.dot(dscores, kj, preferred_element_type=jnp.float32)
                    gk = gk + lax.dot_general(dscores, qj, (((0,), (0,)), ((), ())), preferred_element_type=jnp.float32)
                    gv = gv + lax.dot_general(probs.astype(jnp.bfloat16), dj, (((0,), (0,)), ((), ())), preferred_element_type=jnp.float32)
                gmix_ref[rows, pl.ds(g * LANES, LANES)] = (gq * scale).astype(gmix_ref.dtype)
                part = (pl.ds(low, high - low), pl.ds(g * LANES, LANES))
                gk_acc[part] = gk_acc[part] + gk
                gv_acc[part] = gv_acc[part] + gv
        for g in range(HEADS // GROUP):
            every = (pl.ds(base, SPAN), pl.ds(width + g * LANES, LANES))
            gmix_ref[every] = (gk_acc[:, pl.ds(g * LANES, LANES)] * scale).astype(gmix_ref.dtype)
            every = (pl.ds(base, SPAN), pl.ds(2 * width + g * LANES, LANES))
            gmix_ref[every] = gv_acc[:, pl.ds(g * LANES, LANES)].astype(gmix_ref.dtype)


def _vmem():
    return pl.BlockSpec(memory_space=pltpu.VMEM)


def attention_fwd(mixed, bias, key_col, key_row, scale):
    tokens = mixed.shape[0]
    blocks = tokens // SPAN
    kernel = functools.partial(_fwd_kernel, scale=scale, blocks=blocks)
    return pl.pallas_call(
        kernel,
        out_shape=(
            jax.ShapeDtypeStruct((tokens, HEADS * 32), jnp.bfloat16),
            jax.ShapeDtypeStruct((blocks, SPAN, LANES), jnp.float32),
        ),
        in_specs=[_vmem()] * 4,
        out_specs=(_vmem(), _vmem()),
        compiler_params=pltpu.CompilerParams(vmem_limit_bytes=48 * 1024 * 1024),
    )(mixed.astype(jnp.float32), bias, key_col, key_row)


def attention_bwd(mixed, grad_att, lse, bias, key_col, key_row, scale):
    tokens = mixed.shape[0]
    blocks = tokens // SPAN
    kernel = functools.partial(_bwd_kernel, scale=scale, blocks=blocks)
    return pl.pallas_call(
        kernel,
        out_shape=(
            jax.ShapeDtypeStruct(mixed.shape, jnp.bfloat16),
            jax.ShapeDtypeStruct(bias.shape, jnp.float32),
        ),
        in_specs=[_vmem()] * 6,
        out_specs=(_vmem(), _vmem()),
        scratch_shapes=[pltpu.VMEM((SPAN, HEADS * 32), jnp.float32)] * 2,
        compiler_params=pltpu.CompilerParams(vmem_limit_bytes=56 * 1024 * 1024),
    )(mixed.astype(jnp.float32), grad_att.astype(jnp.float32), lse, bias, key_col, key_row)


def lane_blocks(matrix):
    row_blocks, col_blocks = matrix.shape[0] // BLK, matrix.shape[1] // BLK
    shaped = matrix.reshape(row_blocks, BLK, col_blocks, BLK).transpose(0, 2, 1, 3)
    return shaped.reshape(row_blocks * col_blocks, BLK * BLK // LANES, LANES)


def reduce_to_owners(parted, small):
    groups = lax.axis_size("dp")
    dp_bits = groups.bit_length() - 1
    n_qy, n_qx = lax.axis_size("qy"), lax.axis_size("qx")
    count, depth = parted[0].shape[0], parted[0].shape[1]
    per_group = count // groups
    names = [("dp", 1 << power) for power in reversed(range(dp_bits))] + [("qy", 1), ("qx", 1)]
    cross = [("qy", 1)] + [("dp", 1 << power) for power in range(dp_bits)]
    pieces, piece_names, orders = [], [], []
    for index, part in enumerate(parted):
        pieces.append(
            part.reshape([2] * dp_bits + [n_qy, n_qx, per_group * depth // (n_qy * n_qx), LANES])
        )
        piece_names.append(list(names))
        turn = index % len(cross)
        orders.append([("qx", 1)] + cross[turn:] + cross[:turn])
    for stage in range(len(names)):
        for index in range(len(pieces)):
            bit = orders[index][stage]
            place = piece_names[index].index(bit)
            mine = bit_of(*bit)
            keep = lax.dynamic_index_in_dim(pieces[index], mine, place, keepdims=False)
            send = lax.dynamic_index_in_dim(pieces[index], 1 - mine, place, keepdims=False)
            piece_names[index].remove(bit)
            arrived = partner_of(send.astype(jnp.bfloat16), *bit)
            pieces[index] = keep + arrived.astype(jnp.float32)
            if index == 0:
                small = small + partner_of(small, *bit)
                pieces[0], small = lax.optimization_barrier((pieces[0], small))
    chunk = jnp.stack(pieces)
    other = partner_of(chunk, "qy", 1)
    pair = jnp.where(bit_of("qy", 1) == 1, jnp.stack([other, chunk], 1), jnp.stack([chunk, other], 1))
    other = partner_of(pair, "qx", 1)
    quad = jnp.where(bit_of("qx", 1) == 1, jnp.stack([other, pair], 2), jnp.stack([pair, other], 2))
    quad = quad.reshape(len(pieces), per_group, depth, LANES).transpose(1, 0, 2, 3)
    return quad.reshape(per_group, BLK, BLK), small


def cut_along(value, dim, devices):
    before, after = (value.shape[:dim], value.shape[dim + 1 :])
    return jnp.moveaxis(value.reshape(*before, devices, -1, *after), dim, 0)


def sent_and_summed(value, axis, dim):
    pieces = cut_along(value, dim, lax.axis_size(axis))
    arrived = lax.all_to_all(pieces, axis, split_axis=0, concat_axis=0, tiled=True)
    return arrived.astype(jnp.float32).sum(axis=0)


def norm_stats(tensor):
    center = tensor - jnp.mean(tensor, -1, keepdims=True)
    inverse = lax.rsqrt(jnp.mean(center * center, -1, keepdims=True) + NORM_EPSILON)
    return (center * inverse, inverse)


def norm_back(grad_act, normed, inverse, gain):
    scaled = grad_act * gain
    mean_one = jnp.mean(scaled, -1, keepdims=True)
    mean_two = jnp.mean(scaled * normed, -1, keepdims=True)
    return inverse * (scaled - mean_one - normed * mean_two)


def to_windows(tensor):
    canvases, rows_side, cols_side, channels = tensor.shape
    shaped = tensor.reshape(canvases, rows_side // WIN, WIN, cols_side // WIN, WIN, channels)
    return shaped.transpose(0, 1, 3, 2, 4, 5).reshape(
        canvases * (rows_side // WIN) * (cols_side // WIN), WIN * WIN, channels
    )


def from_windows(tensor, canvases, rows_side, cols_side):
    channels = tensor.shape[-1]
    shaped = tensor.reshape(canvases, rows_side // WIN, cols_side // WIN, WIN, WIN, channels)
    return shaped.transpose(0, 1, 3, 2, 4, 5).reshape(canvases, rows_side, cols_side, channels)


def relative_index():
    places = jnp.arange(WIN * WIN, dtype=jnp.int32)
    row_of = places // WIN
    col_of = places % WIN
    return (row_of[:, None] - row_of[None, :] + WIN - 1) * (2 * WIN - 1) + (
        col_of[:, None] - col_of[None, :] + WIN - 1
    )


def region_of(places, full):
    return jnp.where(places < full - WIN, 0, jnp.where(places < full - SHIFT, 1, 2)).astype(
        jnp.int32
    )


def advance(tensor):
    upper = passed_along(tensor[:, :SHIFT], "qy", -1)
    tensor = jnp.concatenate([tensor[:, SHIFT:], upper], 1)
    leftmost = passed_along(tensor[:, :, :SHIFT], "qx", -1)
    return jnp.concatenate([tensor[:, :, SHIFT:], leftmost], 2)


def retreat(tensor):
    lowest = passed_along(tensor[:, -SHIFT:], "qy", 1)
    tensor = jnp.concatenate([lowest, tensor[:, :-SHIFT]], 1)
    rightmost = passed_along(tensor[:, :, -SHIFT:], "qx", 1)
    return jnp.concatenate([rightmost, tensor[:, :, :-SHIFT]], 2)


def blocks_of(matrix):
    row_blocks = matrix.shape[0] // BLK
    col_blocks = matrix.shape[1] // BLK
    return (
        matrix.reshape(row_blocks, BLK, col_blocks, BLK)
        .transpose(0, 2, 1, 3)
        .reshape(row_blocks * col_blocks, BLK, BLK)
    )


def rotate_update(grads, master, first, second, left, right):
    turned = jnp.einsum("sji,sjk->sik", left, grads, precision=PRECISE)
    turned = jnp.einsum("sik,skl->sil", turned, right, precision=PRECISE)
    new_first = BETA_ONE * first + (1.0 - BETA_ONE) * turned
    new_second = BETA_TWO * second + (1.0 - BETA_TWO) * turned * turned
    direction = new_first / (jnp.sqrt(new_second) + ADAM_EPSILON)
    back = jnp.einsum("sij,sjk->sik", left, direction, precision=PRECISE)
    back = jnp.einsum("sik,slk->sil", back, right, precision=PRECISE)
    return (new_first, new_second, master - RATE_BLOCKS * back)


def small_update(grads, params, first, second):
    new_first = BETA_ONE * first + (1.0 - BETA_ONE) * grads
    new_second = BETA_TWO * second + (1.0 - BETA_TWO) * grads * grads
    direction = new_first / (jnp.sqrt(new_second) + ADAM_EPSILON)
    return (new_first, new_second, params - RATE_SMALL * direction)


def local(
    tokens,
    crop_ids,
    merge_order,
    owner_list,
    w_qkv,
    w_proj,
    w_fc1,
    w_fc2,
    small_params,
    small_first,
    small_second,
    master_blocks,
    first_moment,
    second_moment,
    basis_left,
    basis_right,
    merged_grad,
):
    canvases, quad_side, quad_cols, features = tokens.shape
    head_dim = features // HEADS
    score_scale = head_dim ** (-0.5)
    window_area = WIN * WIN
    quarters = lax.axis_size(("qy", "qx"))
    share_rows = quad_side * quad_cols // quarters
    row_base = lax.axis_index("qy") * quad_side
    col_base = lax.axis_index("qx") * quad_cols
    rolled = jnp.roll(crop_ids, (-SHIFT, -SHIFT), (1, 2))
    local_ids = lax.dynamic_slice(
        rolled, (jnp.int32(0), row_base, col_base), (canvases, quad_side, quad_cols)
    )
    region_row = region_of(
        row_base + jnp.arange(quad_side, dtype=jnp.int32), quad_side * lax.axis_size("qy")
    )
    region_col = region_of(
        col_base + jnp.arange(quad_cols, dtype=jnp.int32), quad_cols * lax.axis_size("qx")
    )
    labels = (local_ids + 1) * 9 + region_row[None, :, None] * 3 + region_col[None, None, :]
    win_labels = to_windows(labels[..., None])[..., 0]
    window_count = win_labels.shape[0]
    valid = (win_labels >= 9).reshape(-1).astype(jnp.float32)[:, None]
    gain_one = small_params[0:features]
    offset_one = small_params[features : 2 * features]
    gain_two = small_params[2 * features : 3 * features]
    offset_two = small_params[3 * features : 4 * features]
    table = small_params[4 * features :].reshape(HEADS, -1)
    onehot = (
        relative_index().reshape(-1)[:, None]
        == jnp.arange(table.shape[1], dtype=jnp.int32)[None, :]
    ).astype(jnp.float32)
    rel_bias = jnp.einsum("hr,pr->hp", table, onehot, precision=PRECISE).reshape(
        HEADS, window_area, window_area
    )

    residual = to_windows(advance(tokens)).reshape(-1, features).astype(jnp.float32)
    normed_one, inverse_one = norm_stats(residual)
    act_one = (normed_one * gain_one + offset_one).astype(jnp.bfloat16)
    mixed = jnp.dot(act_one, w_qkv, preferred_element_type=jnp.float32).astype(jnp.bfloat16)
    per_span = SPAN // window_area
    window_slot = jnp.arange(window_count, dtype=jnp.int32) % per_span
    span_keys = (win_labels * per_span + window_slot[:, None]).reshape(-1, SPAN)
    key_col, key_row = span_keys[:, :, None], span_keys[:, None, :]
    spread = (
        jnp.arange(SPAN, dtype=jnp.int32)[:, None] % window_area
        == jnp.arange(window_area, dtype=jnp.int32)[None, :]
    ).astype(jnp.float32)
    dense_bias = jnp.einsum(
        "hti,ui->htu",
        jnp.einsum("ti,hij->htj", spread, rel_bias, precision=PRECISE),
        spread,
        precision=PRECISE,
    )
    attended, log_total = attention_fwd(mixed, dense_bias, key_col, key_row, score_scale)
    branch_one = jnp.dot(attended, w_proj, preferred_element_type=jnp.float32)
    hidden = residual + branch_one
    normed_two, inverse_two = norm_stats(hidden)
    act_two = (normed_two * gain_two + offset_two).astype(jnp.bfloat16)
    pre_gelu = jnp.dot(act_two, w_fc1, preferred_element_type=jnp.float32)
    gelu_low = jax.nn.gelu(pre_gelu, approximate=False).astype(jnp.bfloat16)
    branch_two = jnp.dot(gelu_low, w_fc2, preferred_element_type=jnp.float32)
    output = hidden + branch_two
    stat_terms = jnp.stack(
        [
            jnp.sum(valid * output * output),
            jnp.sum(valid * (branch_one * branch_one + branch_two * branch_two)),
            jnp.sum(valid) * features,
        ]
    )
    output_low = output.astype(jnp.bfloat16).reshape(window_count, window_area, features)
    restored = retreat(from_windows(output_low, canvases, quad_side, quad_cols))
    flat_out = restored.reshape(canvases, quarters, share_rows, features)
    arrived = lax.all_to_all(flat_out, ("qy", "qx"), 1, 1, tiled=True)
    merged = jnp.take(arrived, merge_order, axis=1, mode="clip").transpose(0, 2, 1, 3).reshape(
        canvases, share_rows, quarters * features
    )
    quarter_ids = jnp.arange(quarters, dtype=jnp.int32)
    source_pick = jnp.sum(
        quarter_ids[:, None] * (merge_order[:, None] == quarter_ids[None, :]).astype(jnp.int32), 0
    )
    incoming = merged_grad.reshape(canvases, share_rows, quarters, features)
    unordered = jnp.take(incoming, source_pick, axis=2, mode="clip").transpose(0, 2, 1, 3)
    returned = lax.all_to_all(unordered, ("qy", "qx"), 1, 1, tiled=True)
    grad_orig = returned.reshape(canvases, quad_side, quad_cols, features)
    grad_out = to_windows(advance(grad_orig)).reshape(-1, features)
    grad_fc2 = jnp.einsum("rf,rc->fc", gelu_low, grad_out, preferred_element_type=jnp.float32)
    grad_gelu = jnp.einsum("rc,fc->rf", grad_out, w_fc2, preferred_element_type=jnp.float32)
    gelu_pull = jax.vjp(partial(jax.nn.gelu, approximate=False), pre_gelu)[1]
    grad_pre = gelu_pull(grad_gelu)[0].astype(jnp.bfloat16)
    grad_fc1 = jnp.einsum("rc,rf->cf", act_two, grad_pre, preferred_element_type=jnp.float32)
    grad_act_two = jnp.einsum("rf,cf->rc", grad_pre, w_fc1, preferred_element_type=jnp.float32)
    grad_hidden = grad_out.astype(jnp.float32) + norm_back(
        grad_act_two, normed_two, inverse_two, gain_two
    )
    grad_branch = grad_hidden.astype(jnp.bfloat16)
    grad_proj = jnp.einsum("rc,rd->cd", attended, grad_branch, preferred_element_type=jnp.float32)
    grad_attended = jnp.einsum(
        "rd,cd->rc", grad_branch, w_proj, preferred_element_type=jnp.float32
    ).astype(jnp.bfloat16)
    grad_mixed, dense_grad_bias = attention_bwd(
        mixed, grad_attended, log_total, dense_bias, key_col, key_row, score_scale
    )
    grad_bias = jnp.einsum(
        "ti,htj->hij",
        spread,
        jnp.einsum("htu,uj->htj", dense_grad_bias, spread, precision=PRECISE),
        precision=PRECISE,
    )
    grad_table = jnp.dot(grad_bias.reshape(HEADS, -1), onehot, precision=PRECISE)
    grad_qkv = jnp.einsum("rc,rf->cf", act_one, grad_mixed, preferred_element_type=jnp.float32)
    grad_act_one = jnp.einsum("rf,cf->rc", grad_mixed, w_qkv, preferred_element_type=jnp.float32)
    grad_input = grad_hidden + norm_back(grad_act_one, normed_one, inverse_one, gain_one)
    grad_low = grad_input.astype(jnp.bfloat16).reshape(window_count, window_area, features)
    grad_tokens = retreat(from_windows(grad_low, canvases, quad_side, quad_cols))
    small_local = jnp.concatenate(
        [
            jnp.sum(grad_act_one * normed_one, 0),
            jnp.sum(grad_act_one, 0),
            jnp.sum(grad_act_two * normed_two, 0),
            jnp.sum(grad_act_two, 0),
            grad_table.reshape(-1),
        ]
    )
    every_block = jnp.concatenate(
        [lane_blocks(grad_qkv), lane_blocks(grad_proj), lane_blocks(grad_fc1), lane_blocks(grad_fc2)],
        0,
    )
    depth = every_block.shape[1] // PARTS
    parted = [
        jnp.take(every_block[:, index * depth : (index + 1) * depth], owner_list, axis=0, mode="clip")
        for index in range(PARTS)
    ]
    owned_grads, small_all = reduce_to_owners(parted, jnp.concatenate([small_local, stat_terms]))
    small_total = small_all[: small_local.shape[0]]
    stat_total = small_all[small_local.shape[0] :]
    new_first, new_second, new_master = rotate_update(
        owned_grads, master_blocks, first_moment, second_moment, basis_left, basis_right
    )
    small_first_new, small_second_new, small_new = small_update(
        small_total, small_params, small_first, small_second
    )
    stats = jnp.stack(
        [jnp.sqrt(stat_total[0] / stat_total[2]), jnp.sqrt(stat_total[1] / (2.0 * stat_total[2]))]
    )
    return (
        merged,
        grad_tokens,
        owned_grads,
        new_master,
        new_first,
        new_second,
        new_master.astype(jnp.bfloat16),
        small_total,
        small_first_new,
        small_second_new,
        small_new,
        stats,
    )


def solution(mesh):
    placed = (
        P("dp", "qy", "qx", None),
        P("dp", None, None),
        P(),
        P(),
        P(),
        P(),
        P(),
        P(),
        P(),
        P(),
        P(),
        P("dp", None, None),
        P("dp", None, None),
        P("dp", None, None),
        P("dp", None, None),
        P("dp", None, None),
        P("dp", ("qy", "qx"), None),
    )
    return jax.shard_map(
        local,
        mesh=mesh,
        in_specs=placed,
        out_specs=(
            P("dp", ("qy", "qx"), None),
            P("dp", "qy", "qx", None),
            P("dp", None, None),
            P("dp", None, None),
            P("dp", None, None),
            P("dp", None, None),
            P("dp", None, None),
            P(),
            P(),
            P(),
            P(),
            P(),
        ),
        check_vma=False,
    )
```

```python
import functools
from functools import partial

import numpy as np

import jax
import jax.numpy as jnp
from jax import lax
from jax.experimental import pallas as pl
from jax.experimental.pallas import tpu as pltpu
from jax.sharding import PartitionSpec as P

HEADS = 12
WIN = 7
SHIFT = 3
BLK = 96


BETA_ONE = 0.5
BETA_TWO = 0.6
ADAM_EPSILON = 1e-08
RATE_BLOCKS = 0.04
RATE_SMALL = 0.2
MASK_FILL = -1e30
NORM_EPSILON = 1e-05
PRECISE = lax.Precision.HIGHEST


def passed_along(value, axis, steps):
    count = lax.axis_size(axis)
    pairs = [(source, (source + steps) % count) for source in range(count)]
    return lax.ppermute(value, axis, pairs)


def partner_of(value, axis, mask):
    count = lax.axis_size(axis)
    pairs = [(source, source ^ mask) for source in range(count)]
    return lax.ppermute(value, axis, pairs)


def bit_of(axis, mask):
    return ((lax.axis_index(axis) & mask) != 0).astype(jnp.int32)


LANES = 128
PARTS = 3
GROUP = 4
LANES = 128
MASK_FILL = -1e30
SPAN = 392


def _masked_scores(q4, k4, lane, j, bias, allowed, scale):
    qj = jnp.where(lane == j, q4, jnp.zeros_like(q4))
    raw = lax.dot_general(qj, k4, (((1,), (1,)), ((), ())), preferred_element_type=jnp.float32)
    return jnp.where(allowed, raw * scale + bias, MASK_FILL)


def _fwd_kernel(mix_ref, bias_ref, kc_ref, kr_ref, out_ref, lse_ref, *, scale, blocks):
    width = HEADS * 32
    lane = lax.broadcasted_iota(jnp.int32, (1, LANES), 1) // 32
    head_lane = lax.broadcasted_iota(jnp.int32, (1, LANES), 1)
    for b in range(blocks):
        rows = pl.ds(b * SPAN, SPAN)
        allowed = kc_ref[b] == kr_ref[b]
        lse_all = jnp.zeros((SPAN, LANES), jnp.float32)
        for g in range(HEADS // GROUP):
            q4 = mix_ref[rows, pl.ds(g * LANES, LANES)]
            k4 = mix_ref[rows, pl.ds(width + g * LANES, LANES)]
            v4 = mix_ref[rows, pl.ds(2 * width + g * LANES, LANES)]
            acc = jnp.zeros((SPAN, LANES), jnp.float32)
            for j in range(GROUP):
                h = g * GROUP + j
                s = _masked_scores(q4, k4, lane, j, bias_ref[h], allowed, scale)
                top = jnp.max(s, -1, keepdims=True)
                e = jnp.exp(s - top)
                total = jnp.sum(e, -1, keepdims=True)
                probs = (e / total).astype(jnp.bfloat16)
                vj = jnp.where(lane == j, v4, jnp.zeros_like(v4))
                acc = acc + jnp.dot(probs, vj, preferred_element_type=jnp.float32)
                lse_all = jnp.where(head_lane == h, top + jnp.log(total), lse_all)
            out_ref[rows, pl.ds(g * LANES, LANES)] = acc.astype(out_ref.dtype)
        lse_ref[b] = lse_all


def _bwd_kernel(mix_ref, grad_ref, lse_ref, bias_ref, kc_ref, kr_ref, gmix_ref, dbias_ref, *, scale, blocks):
    width = HEADS * 32
    lane = lax.broadcasted_iota(jnp.int32, (1, LANES), 1) // 32
    head_lane = lax.broadcasted_iota(jnp.int32, (1, LANES), 1)
    for b in range(blocks):
        rows = pl.ds(b * SPAN, SPAN)
        allowed = kc_ref[b] == kr_ref[b]
        lse_all = lse_ref[b]
        for g in range(HEADS // GROUP):
            q4 = mix_ref[rows, pl.ds(g * LANES, LANES)]
            k4 = mix_ref[rows, pl.ds(width + g * LANES, LANES)]
            v4 = mix_ref[rows, pl.ds(2 * width + g * LANES, LANES)]
            d4 = grad_ref[rows, pl.ds(g * LANES, LANES)]
            gq = jnp.zeros((SPAN, LANES), jnp.float32)
            gk = jnp.zeros((SPAN, LANES), jnp.float32)
            gv = jnp.zeros((SPAN, LANES), jnp.float32)
            for j in range(GROUP):
                h = g * GROUP + j
                s = _masked_scores(q4, k4, lane, j, bias_ref[h], allowed, scale)
                lse = jnp.sum(jnp.where(head_lane == h, lse_all, 0.0), -1, keepdims=True)
                probs = jnp.exp(s - lse)
                dj = jnp.where(lane == j, d4, jnp.zeros_like(d4))
                dprobs = lax.dot_general(dj, v4, (((1,), (1,)), ((), ())), preferred_element_type=jnp.float32)
                inner = jnp.sum(probs * dprobs, -1, keepdims=True)
                dscores = (probs * (dprobs - inner)).astype(jnp.bfloat16)
                if b == 0:
                    dbias_ref[h] = dscores.astype(jnp.float32)
                else:
                    dbias_ref[h] = dbias_ref[h] + dscores.astype(jnp.float32)
                kj = jnp.where(lane == j, k4, jnp.zeros_like(k4))
                qj = jnp.where(lane == j, q4, jnp.zeros_like(q4))
                gq = gq + jnp.dot(dscores, kj, preferred_element_type=jnp.float32)
                gk = gk + lax.dot_general(dscores, qj, (((0,), (0,)), ((), ())), preferred_element_type=jnp.float32)
                gv = gv + lax.dot_general(probs.astype(jnp.bfloat16), dj, (((0,), (0,)), ((), ())), preferred_element_type=jnp.float32)
            gmix_ref[rows, pl.ds(g * LANES, LANES)] = (gq * scale).astype(gmix_ref.dtype)
            gmix_ref[rows, pl.ds(width + g * LANES, LANES)] = (gk * scale).astype(gmix_ref.dtype)
            gmix_ref[rows, pl.ds(2 * width + g * LANES, LANES)] = gv.astype(gmix_ref.dtype)


def _vmem():
    return pl.BlockSpec(memory_space=pltpu.VMEM)


def attention_fwd(mixed, bias, key_col, key_row, scale):
    tokens = mixed.shape[0]
    blocks = tokens // SPAN
    kernel = functools.partial(_fwd_kernel, scale=scale, blocks=blocks)
    return pl.pallas_call(
        kernel,
        out_shape=(
            jax.ShapeDtypeStruct((tokens, HEADS * 32), jnp.bfloat16),
            jax.ShapeDtypeStruct((blocks, SPAN, LANES), jnp.float32),
        ),
        in_specs=[_vmem()] * 4,
        out_specs=(_vmem(), _vmem()),
        compiler_params=pltpu.CompilerParams(vmem_limit_bytes=48 * 1024 * 1024),
    )(mixed, bias, key_col, key_row)


def attention_bwd(mixed, grad_att, lse, bias, key_col, key_row, scale):
    tokens = mixed.shape[0]
    blocks = tokens // SPAN
    kernel = functools.partial(_bwd_kernel, scale=scale, blocks=blocks)
    return pl.pallas_call(
        kernel,
        out_shape=(
            jax.ShapeDtypeStruct(mixed.shape, jnp.bfloat16),
            jax.ShapeDtypeStruct(bias.shape, jnp.float32),
        ),
        in_specs=[_vmem()] * 6,
        out_specs=(_vmem(), _vmem()),
        compiler_params=pltpu.CompilerParams(vmem_limit_bytes=56 * 1024 * 1024),
    )(mixed, grad_att, lse, bias, key_col, key_row)


def lane_blocks(matrix):
    row_blocks, col_blocks = matrix.shape[0] // BLK, matrix.shape[1] // BLK
    shaped = matrix.reshape(row_blocks, BLK, col_blocks, BLK).transpose(0, 2, 1, 3)
    return shaped.reshape(row_blocks * col_blocks, BLK * BLK // LANES, LANES)


ROWS = 112
SQRT_HALF = float(np.sqrt(0.5))
INV_SQRT_TAU = float(1.0 / np.sqrt(2.0 * np.pi))


def _norm(tensor):
    center = tensor - jnp.mean(tensor, -1, keepdims=True)
    inverse = lax.rsqrt(jnp.mean(center * center, -1, keepdims=True) + NORM_EPSILON)
    return center * inverse, inverse


def _mlp_fwd_kernel(att_ref, res_ref, valid_ref, wp_ref, gain_ref, off_ref, w1_ref, w2_ref,
                    hid_ref, act_ref, gelu_ref, out_ref, stat_ref):
    step = pl.program_id(0)
    branch_one = jnp.dot(att_ref[...], wp_ref[...], preferred_element_type=jnp.float32)
    hidden = res_ref[...] + branch_one
    normed, _ = _norm(hidden)
    act = (normed * gain_ref[...] + off_ref[...]).astype(jnp.bfloat16)
    pre = jnp.dot(act, w1_ref[...], preferred_element_type=jnp.float32)
    gelu = ((0.5 * pre) * (1.0 + lax.erf(pre * SQRT_HALF))).astype(jnp.bfloat16)
    branch_two = jnp.dot(gelu, w2_ref[...], preferred_element_type=jnp.float32)
    output = hidden + branch_two
    valid = valid_ref[...]
    first = jnp.sum(valid * output * output)
    second = jnp.sum(valid * (branch_one * branch_one + branch_two * branch_two))
    lane = lax.broadcasted_iota(jnp.int32, (8, 128), 1)
    row = lax.broadcasted_iota(jnp.int32, (8, 128), 0)
    here = jnp.where((row == 0) & (lane == 0), first, 0.0) + jnp.where((row == 0) & (lane == 1), second, 0.0)

    @pl.when(step == 0)
    def _():
        stat_ref[...] = jnp.zeros_like(stat_ref)

    stat_ref[...] = stat_ref[...] + here
    hid_ref[...] = hidden
    act_ref[...] = act
    gelu_ref[...] = gelu
    out_ref[...] = output.astype(out_ref.dtype)


def _mlp_bwd_kernel(gout_ref, hid_ref, act_ref, gain_ref, w1_ref, w2_ref, wp_ref,
                    gpre_ref, ghid_ref, gbr_ref, gatt_ref, small_ref):
    step = pl.program_id(0)
    contract_last = (((1,), (1,)), ((), ()))
    pre = jnp.dot(act_ref[...], w1_ref[...], preferred_element_type=jnp.float32)
    grad_out = gout_ref[...]
    grad_gelu = lax.dot_general(grad_out, w2_ref[...], contract_last, preferred_element_type=jnp.float32)
    cdf = 0.5 * (1.0 + lax.erf(pre * SQRT_HALF))
    pdf = jnp.exp(-0.5 * pre * pre) * INV_SQRT_TAU
    grad_pre = (grad_gelu * (cdf + pre * pdf)).astype(jnp.bfloat16)
    grad_act = lax.dot_general(grad_pre, w1_ref[...], contract_last, preferred_element_type=jnp.float32)
    normed, inverse = _norm(hid_ref[...])
    scaled = grad_act * gain_ref[...]
    mean_one = jnp.mean(scaled, -1, keepdims=True)
    mean_two = jnp.mean(scaled * normed, -1, keepdims=True)
    grad_hidden = grad_out.astype(jnp.float32) + inverse * (scaled - mean_one - normed * mean_two)
    grad_branch = grad_hidden.astype(jnp.bfloat16)
    grad_att = lax.dot_general(grad_branch, wp_ref[...], contract_last, preferred_element_type=jnp.float32)
    sums = jnp.concatenate(
        [jnp.sum(grad_act * normed, 0, keepdims=True), jnp.sum(grad_act, 0, keepdims=True),
         jnp.zeros((6, grad_act.shape[1]), jnp.float32)], 0)

    @pl.when(step == 0)
    def _():
        small_ref[...] = jnp.zeros_like(small_ref)

    small_ref[...] = small_ref[...] + sums
    gpre_ref[...] = grad_pre
    ghid_ref[...] = grad_hidden
    gbr_ref[...] = grad_branch
    gatt_ref[...] = grad_att.astype(gatt_ref.dtype)


def _rows(width):
    return pl.BlockSpec((ROWS, width), lambda i: (i, 0))


def _whole(shape):
    return pl.BlockSpec(shape, lambda i: (0,) * len(shape))


def mlp_fwd(attended, residual, valid, w_proj, gain, offset, w_fc1, w_fc2):
    tokens, width = residual.shape
    hidden_width = w_fc1.shape[1]
    return pl.pallas_call(
        _mlp_fwd_kernel,
        grid=(tokens // ROWS,),
        out_shape=(
            jax.ShapeDtypeStruct((tokens, width), jnp.float32),
            jax.ShapeDtypeStruct((tokens, width), jnp.bfloat16),
            jax.ShapeDtypeStruct((tokens, hidden_width), jnp.bfloat16),
            jax.ShapeDtypeStruct((tokens, width), jnp.bfloat16),
            jax.ShapeDtypeStruct((8, 128), jnp.float32),
        ),
        in_specs=[_rows(width), _rows(width), _rows(1), _whole(w_proj.shape), _whole((1, width)),
                  _whole((1, width)), _whole(w_fc1.shape), _whole(w_fc2.shape)],
        out_specs=(_rows(width), _rows(width), _rows(hidden_width), _rows(width), _whole((8, 128))),
        compiler_params=pltpu.CompilerParams(dimension_semantics=("arbitrary",), vmem_limit_bytes=48 * 1024 * 1024),
    )(attended, residual, valid, w_proj, gain.reshape(1, -1), offset.reshape(1, -1), w_fc1, w_fc2)


def mlp_bwd(grad_out, hidden, act_two, gain, w_fc1, w_fc2, w_proj):
    tokens, width = hidden.shape
    hidden_width = w_fc1.shape[1]
    return pl.pallas_call(
        _mlp_bwd_kernel,
        grid=(tokens // ROWS,),
        out_shape=(
            jax.ShapeDtypeStruct((tokens, hidden_width), jnp.bfloat16),
            jax.ShapeDtypeStruct((tokens, width), jnp.float32),
            jax.ShapeDtypeStruct((tokens, width), jnp.bfloat16),
            jax.ShapeDtypeStruct((tokens, width), jnp.bfloat16),
            jax.ShapeDtypeStruct((8, width), jnp.float32),
        ),
        in_specs=[_rows(width), _rows(width), _rows(width), _whole((1, width)), _whole(w_fc1.shape),
                  _whole(w_fc2.shape), _whole(w_proj.shape)],
        out_specs=(_rows(hidden_width), _rows(width), _rows(width), _rows(width), _whole((8, width))),
        compiler_params=pltpu.CompilerParams(dimension_semantics=("arbitrary",), vmem_limit_bytes=48 * 1024 * 1024),
    )(grad_out, hidden, act_two, gain.reshape(1, -1), w_fc1, w_fc2, w_proj)


def reduce_to_owners(parted, small):
    groups = lax.axis_size("dp")
    dp_bits = groups.bit_length() - 1
    n_qy, n_qx = lax.axis_size("qy"), lax.axis_size("qx")
    count, depth = parted[0].shape[0], parted[0].shape[1]
    per_group = count // groups
    names = [("dp", 1 << power) for power in reversed(range(dp_bits))] + [("qy", 1), ("qx", 1)]
    cross = [("qy", 1)] + [("dp", 1 << power) for power in range(dp_bits)]
    pieces, piece_names, orders = [], [], []
    for index, part in enumerate(parted):
        pieces.append(
            part.reshape([2] * dp_bits + [n_qy, n_qx, per_group * depth // (n_qy * n_qx), LANES])
        )
        piece_names.append(list(names))
        turn = index % len(cross)
        orders.append([("qx", 1)] + cross[turn:] + cross[:turn])
    for stage in range(len(names)):
        for index in range(len(pieces)):
            bit = orders[index][stage]
            place = piece_names[index].index(bit)
            mine = bit_of(*bit)
            keep = lax.dynamic_index_in_dim(pieces[index], mine, place, keepdims=False)
            send = lax.dynamic_index_in_dim(pieces[index], 1 - mine, place, keepdims=False)
            piece_names[index].remove(bit)
            arrived = partner_of(send.astype(jnp.bfloat16), *bit)
            pieces[index] = keep + arrived.astype(jnp.float32)
            if index == 0:
                small = small + partner_of(small, *bit)
                pieces[0], small = lax.optimization_barrier((pieces[0], small))
    chunk = jnp.stack(pieces)
    other = partner_of(chunk, "qy", 1)
    pair = jnp.where(bit_of("qy", 1) == 1, jnp.stack([other, chunk], 1), jnp.stack([chunk, other], 1))
    other = partner_of(pair, "qx", 1)
    quad = jnp.where(bit_of("qx", 1) == 1, jnp.stack([other, pair], 2), jnp.stack([pair, other], 2))
    quad = quad.reshape(len(pieces), per_group, depth, LANES).transpose(1, 0, 2, 3)
    return quad.reshape(per_group, BLK, BLK), small


def cut_along(value, dim, devices):
    before, after = (value.shape[:dim], value.shape[dim + 1 :])
    return jnp.moveaxis(value.reshape(*before, devices, -1, *after), dim, 0)


def sent_and_summed(value, axis, dim):
    pieces = cut_along(value, dim, lax.axis_size(axis))
    arrived = lax.all_to_all(pieces, axis, split_axis=0, concat_axis=0, tiled=True)
    return arrived.astype(jnp.float32).sum(axis=0)


def norm_stats(tensor):
    center = tensor - jnp.mean(tensor, -1, keepdims=True)
    inverse = lax.rsqrt(jnp.mean(center * center, -1, keepdims=True) + NORM_EPSILON)
    return (center * inverse, inverse)


def norm_back(grad_act, normed, inverse, gain):
    scaled = grad_act * gain
    mean_one = jnp.mean(scaled, -1, keepdims=True)
    mean_two = jnp.mean(scaled * normed, -1, keepdims=True)
    return inverse * (scaled - mean_one - normed * mean_two)


def to_windows(tensor):
    canvases, rows_side, cols_side, channels = tensor.shape
    shaped = tensor.reshape(canvases, rows_side // WIN, WIN, cols_side // WIN, WIN, channels)
    return shaped.transpose(0, 1, 3, 2, 4, 5).reshape(
        canvases * (rows_side // WIN) * (cols_side // WIN), WIN * WIN, channels
    )


def from_windows(tensor, canvases, rows_side, cols_side):
    channels = tensor.shape[-1]
    shaped = tensor.reshape(canvases, rows_side // WIN, cols_side // WIN, WIN, WIN, channels)
    return shaped.transpose(0, 1, 3, 2, 4, 5).reshape(canvases, rows_side, cols_side, channels)


def relative_index():
    places = jnp.arange(WIN * WIN, dtype=jnp.int32)
    row_of = places // WIN
    col_of = places % WIN
    return (row_of[:, None] - row_of[None, :] + WIN - 1) * (2 * WIN - 1) + (
        col_of[:, None] - col_of[None, :] + WIN - 1
    )


def region_of(places, full):
    return jnp.where(places < full - WIN, 0, jnp.where(places < full - SHIFT, 1, 2)).astype(
        jnp.int32
    )


def advance(tensor):
    upper = passed_along(tensor[:, :SHIFT], "qy", -1)
    tensor = jnp.concatenate([tensor[:, SHIFT:], upper], 1)
    leftmost = passed_along(tensor[:, :, :SHIFT], "qx", -1)
    return jnp.concatenate([tensor[:, :, SHIFT:], leftmost], 2)


def retreat(tensor):
    lowest = passed_along(tensor[:, -SHIFT:], "qy", 1)
    tensor = jnp.concatenate([lowest, tensor[:, :-SHIFT]], 1)
    rightmost = passed_along(tensor[:, :, -SHIFT:], "qx", 1)
    return jnp.concatenate([rightmost, tensor[:, :, :-SHIFT]], 2)


def blocks_of(matrix):
    row_blocks = matrix.shape[0] // BLK
    col_blocks = matrix.shape[1] // BLK
    return (
        matrix.reshape(row_blocks, BLK, col_blocks, BLK)
        .transpose(0, 2, 1, 3)
        .reshape(row_blocks * col_blocks, BLK, BLK)
    )


def rotate_update(grads, master, first, second, left, right):
    turned = jnp.einsum("sji,sjk->sik", left, grads, precision=PRECISE)
    turned = jnp.einsum("sik,skl->sil", turned, right, precision=PRECISE)
    new_first = BETA_ONE * first + (1.0 - BETA_ONE) * turned
    new_second = BETA_TWO * second + (1.0 - BETA_TWO) * turned * turned
    direction = new_first / (jnp.sqrt(new_second) + ADAM_EPSILON)
    back = jnp.einsum("sij,sjk->sik", left, direction, precision=PRECISE)
    back = jnp.einsum("sik,slk->sil", back, right, precision=PRECISE)
    return (new_first, new_second, master - RATE_BLOCKS * back)


def small_update(grads, params, first, second):
    new_first = BETA_ONE * first + (1.0 - BETA_ONE) * grads
    new_second = BETA_TWO * second + (1.0 - BETA_TWO) * grads * grads
    direction = new_first / (jnp.sqrt(new_second) + ADAM_EPSILON)
    return (new_first, new_second, params - RATE_SMALL * direction)


def local(
    tokens,
    crop_ids,
    merge_order,
    owner_list,
    w_qkv,
    w_proj,
    w_fc1,
    w_fc2,
    small_params,
    small_first,
    small_second,
    master_blocks,
    first_moment,
    second_moment,
    basis_left,
    basis_right,
    merged_grad,
):
    canvases, quad_side, quad_cols, features = tokens.shape
    head_dim = features // HEADS
    score_scale = head_dim ** (-0.5)
    window_area = WIN * WIN
    quarters = lax.axis_size(("qy", "qx"))
    share_rows = quad_side * quad_cols // quarters
    row_base = lax.axis_index("qy") * quad_side
    col_base = lax.axis_index("qx") * quad_cols
    rolled = jnp.roll(crop_ids, (-SHIFT, -SHIFT), (1, 2))
    local_ids = lax.dynamic_slice(
        rolled, (jnp.int32(0), row_base, col_base), (canvases, quad_side, quad_cols)
    )
    region_row = region_of(
        row_base + jnp.arange(quad_side, dtype=jnp.int32), quad_side * lax.axis_size("qy")
    )
    region_col = region_of(
        col_base + jnp.arange(quad_cols, dtype=jnp.int32), quad_cols * lax.axis_size("qx")
    )
    labels = (local_ids + 1) * 9 + region_row[None, :, None] * 3 + region_col[None, None, :]
    win_labels = to_windows(labels[..., None])[..., 0]
    window_count = win_labels.shape[0]
    valid = (win_labels >= 9).reshape(-1).astype(jnp.float32)[:, None]
    gain_one = small_params[0:features]
    offset_one = small_params[features : 2 * features]
    gain_two = small_params[2 * features : 3 * features]
    offset_two = small_params[3 * features : 4 * features]
    table = small_params[4 * features :].reshape(HEADS, -1)
    onehot = (
        relative_index().reshape(-1)[:, None]
        == jnp.arange(table.shape[1], dtype=jnp.int32)[None, :]
    ).astype(jnp.float32)
    rel_bias = jnp.einsum("hr,pr->hp", table, onehot, precision=PRECISE).reshape(
        HEADS, window_area, window_area
    )

    residual = to_windows(advance(tokens)).reshape(-1, features).astype(jnp.float32)
    normed_one, inverse_one = norm_stats(residual)
    act_one = (normed_one * gain_one + offset_one).astype(jnp.bfloat16)
    mixed = jnp.dot(act_one, w_qkv, preferred_element_type=jnp.float32).astype(jnp.bfloat16)
    per_span = SPAN // window_area
    window_slot = jnp.arange(window_count, dtype=jnp.int32) % per_span
    span_keys = (win_labels * per_span + window_slot[:, None]).reshape(-1, SPAN)
    key_col, key_row = span_keys[:, :, None], span_keys[:, None, :]
    spread = (
        jnp.arange(SPAN, dtype=jnp.int32)[:, None] % window_area
        == jnp.arange(window_area, dtype=jnp.int32)[None, :]
    ).astype(jnp.float32)
    dense_bias = jnp.einsum(
        "hti,ui->htu",
        jnp.einsum("ti,hij->htj", spread, rel_bias, precision=PRECISE),
        spread,
        precision=PRECISE,
    )
    attended, log_total = attention_fwd(mixed, dense_bias, key_col, key_row, score_scale)
    hidden, act_two, gelu_low, output_flat, stat_block = mlp_fwd(
        attended, residual, valid, w_proj, gain_two, offset_two, w_fc1, w_fc2
    )
    stat_terms = jnp.stack([stat_block[0, 0], stat_block[0, 1], jnp.sum(valid) * features])
    output_low = output_flat.reshape(window_count, window_area, features)
    restored = retreat(from_windows(output_low, canvases, quad_side, quad_cols))
    flat_out = restored.reshape(canvases, quarters, share_rows, features)
    arrived = lax.all_to_all(flat_out, ("qy", "qx"), 1, 1, tiled=True)
    merged = jnp.take(arrived, merge_order, axis=1, mode="clip").transpose(0, 2, 1, 3).reshape(
        canvases, share_rows, quarters * features
    )
    quarter_ids = jnp.arange(quarters, dtype=jnp.int32)
    source_pick = jnp.sum(
        quarter_ids[:, None] * (merge_order[:, None] == quarter_ids[None, :]).astype(jnp.int32), 0
    )
    incoming = merged_grad.reshape(canvases, share_rows, quarters, features)
    unordered = jnp.take(incoming, source_pick, axis=2, mode="clip").transpose(0, 2, 1, 3)
    returned = lax.all_to_all(unordered, ("qy", "qx"), 1, 1, tiled=True)
    grad_orig = returned.reshape(canvases, quad_side, quad_cols, features)
    grad_out = to_windows(advance(grad_orig)).reshape(-1, features)
    grad_pre, grad_hidden, grad_branch, grad_attended, small_two = mlp_bwd(
        grad_out, hidden, act_two, gain_two, w_fc1, w_fc2, w_proj
    )
    grad_fc2 = jnp.einsum("rf,rc->fc", gelu_low, grad_out, preferred_element_type=jnp.float32)
    grad_fc1 = jnp.einsum("rc,rf->cf", act_two, grad_pre, preferred_element_type=jnp.float32)
    grad_proj = jnp.einsum("rc,rd->cd", attended, grad_branch, preferred_element_type=jnp.float32)
    grad_mixed, dense_grad_bias = attention_bwd(
        mixed, grad_attended, log_total, dense_bias, key_col, key_row, score_scale
    )
    grad_bias = jnp.einsum(
        "ti,htj->hij",
        spread,
        jnp.einsum("htu,uj->htj", dense_grad_bias, spread, precision=PRECISE),
        precision=PRECISE,
    )
    grad_table = jnp.dot(grad_bias.reshape(HEADS, -1), onehot, precision=PRECISE)
    grad_qkv = jnp.einsum("rc,rf->cf", act_one, grad_mixed, preferred_element_type=jnp.float32)
    grad_act_one = jnp.einsum("rf,cf->rc", grad_mixed, w_qkv, preferred_element_type=jnp.float32)
    grad_input = grad_hidden + norm_back(grad_act_one, normed_one, inverse_one, gain_one)
    grad_low = grad_input.astype(jnp.bfloat16).reshape(window_count, window_area, features)
    grad_tokens = retreat(from_windows(grad_low, canvases, quad_side, quad_cols))
    small_local = jnp.concatenate(
        [
            jnp.sum(grad_act_one * normed_one, 0),
            jnp.sum(grad_act_one, 0),
            small_two[0],
            small_two[1],
            grad_table.reshape(-1),
        ]
    )
    every_block = jnp.concatenate(
        [lane_blocks(grad_qkv), lane_blocks(grad_proj), lane_blocks(grad_fc1), lane_blocks(grad_fc2)],
        0,
    )
    depth = every_block.shape[1] // PARTS
    parted = [
        jnp.take(every_block[:, index * depth : (index + 1) * depth], owner_list, axis=0, mode="clip")
        for index in range(PARTS)
    ]
    owned_grads, small_all = reduce_to_owners(parted, jnp.concatenate([small_local, stat_terms]))
    small_total = small_all[: small_local.shape[0]]
    stat_total = small_all[small_local.shape[0] :]
    new_first, new_second, new_master = rotate_update(
        owned_grads, master_blocks, first_moment, second_moment, basis_left, basis_right
    )
    small_first_new, small_second_new, small_new = small_update(
        small_total, small_params, small_first, small_second
    )
    stats = jnp.stack(
        [jnp.sqrt(stat_total[0] / stat_total[2]), jnp.sqrt(stat_total[1] / (2.0 * stat_total[2]))]
    )
    return (
        merged,
        grad_tokens,
        owned_grads,
        new_master,
        new_first,
        new_second,
        new_master.astype(jnp.bfloat16),
        small_total,
        small_first_new,
        small_second_new,
        small_new,
        stats,
    )


def solution(mesh):
    placed = (
        P("dp", "qy", "qx", None),
        P("dp", None, None),
        P(),
        P(),
        P(),
        P(),
        P(),
        P(),
        P(),
        P(),
        P(),
        P("dp", None, None),
        P("dp", None, None),
        P("dp", None, None),
        P("dp", None, None),
        P("dp", None, None),
        P("dp", ("qy", "qx"), None),
    )
    return jax.shard_map(
        local,
        mesh=mesh,
        in_specs=placed,
        out_specs=(
            P("dp", ("qy", "qx"), None),
            P("dp", "qy", "qx", None),
            P("dp", None, None),
            P("dp", None, None),
            P("dp", None, None),
            P("dp", None, None),
            P("dp", None, None),
            P(),
            P(),
            P(),
            P(),
            P(),
        ),
        check_vma=False,
    )
```

```python
import functools
from functools import partial

import numpy as np

import jax
import jax.numpy as jnp
from jax import lax
from jax.experimental import pallas as pl
from jax.experimental.pallas import tpu as pltpu
from jax.sharding import PartitionSpec as P

HEADS = 12
WIN = 7
SHIFT = 3
BLK = 96


BETA_ONE = 0.5
BETA_TWO = 0.6
ADAM_EPSILON = 1e-08
RATE_BLOCKS = 0.04
RATE_SMALL = 0.2
MASK_FILL = -1e30
NORM_EPSILON = 1e-05
PRECISE = lax.Precision.HIGHEST


def passed_along(value, axis, steps):
    count = lax.axis_size(axis)
    pairs = [(source, (source + steps) % count) for source in range(count)]
    return lax.ppermute(value, axis, pairs)


def partner_of(value, axis, mask):
    count = lax.axis_size(axis)
    pairs = [(source, source ^ mask) for source in range(count)]
    return lax.ppermute(value, axis, pairs)


def bit_of(axis, mask):
    return ((lax.axis_index(axis) & mask) != 0).astype(jnp.int32)


LANES = 128
PARTS = 1
GROUP = 4
LANES = 128
MASK_FILL = -1e30
SPAN = 392


def _masked_scores(q4, k4, lane, j, bias, allowed, scale):
    qj = jnp.where(lane == j, q4, jnp.zeros_like(q4))
    raw = lax.dot_general(qj, k4, (((1,), (1,)), ((), ())), preferred_element_type=jnp.float32)
    return jnp.where(allowed, raw * scale + bias, MASK_FILL)


def _fwd_kernel(mix_ref, bias_ref, kc_ref, kr_ref, out_ref, lse_ref, *, scale, blocks):
    width = HEADS * 32
    lane = lax.broadcasted_iota(jnp.int32, (1, LANES), 1) // 32
    head_lane = lax.broadcasted_iota(jnp.int32, (1, LANES), 1)
    for b in range(blocks):
        rows = pl.ds(b * SPAN, SPAN)
        allowed = kc_ref[b] == kr_ref[b]
        lse_all = jnp.zeros((SPAN, LANES), jnp.float32)
        for g in range(HEADS // GROUP):
            q4 = mix_ref[rows, pl.ds(g * LANES, LANES)]
            k4 = mix_ref[rows, pl.ds(width + g * LANES, LANES)]
            v4 = mix_ref[rows, pl.ds(2 * width + g * LANES, LANES)]
            acc = jnp.zeros((SPAN, LANES), jnp.float32)
            for j in range(GROUP):
                h = g * GROUP + j
                s = _masked_scores(q4, k4, lane, j, bias_ref[h], allowed, scale)
                top = jnp.max(s, -1, keepdims=True)
                e = jnp.exp(s - top)
                total = jnp.sum(e, -1, keepdims=True)
                probs = (e / total).astype(jnp.bfloat16)
                vj = jnp.where(lane == j, v4, jnp.zeros_like(v4))
                acc = acc + jnp.dot(probs, vj, preferred_element_type=jnp.float32)
                lse_all = jnp.where(head_lane == h, top + jnp.log(total), lse_all)
            out_ref[rows, pl.ds(g * LANES, LANES)] = acc.astype(out_ref.dtype)
        lse_ref[b] = lse_all


def _bwd_kernel(mix_ref, grad_ref, lse_ref, bias_ref, kc_ref, kr_ref, gmix_ref, dbias_ref, *, scale, blocks):
    width = HEADS * 32
    lane = lax.broadcasted_iota(jnp.int32, (1, LANES), 1) // 32
    head_lane = lax.broadcasted_iota(jnp.int32, (1, LANES), 1)
    for b in range(blocks):
        rows = pl.ds(b * SPAN, SPAN)
        allowed = kc_ref[b] == kr_ref[b]
        lse_all = lse_ref[b]
        for g in range(HEADS // GROUP):
            q4 = mix_ref[rows, pl.ds(g * LANES, LANES)]
            k4 = mix_ref[rows, pl.ds(width + g * LANES, LANES)]
            v4 = mix_ref[rows, pl.ds(2 * width + g * LANES, LANES)]
            d4 = grad_ref[rows, pl.ds(g * LANES, LANES)]
            gq = jnp.zeros((SPAN, LANES), jnp.float32)
            gk = jnp.zeros((SPAN, LANES), jnp.float32)
            gv = jnp.zeros((SPAN, LANES), jnp.float32)
            for j in range(GROUP):
                h = g * GROUP + j
                s = _masked_scores(q4, k4, lane, j, bias_ref[h], allowed, scale)
                lse = jnp.sum(jnp.where(head_lane == h, lse_all, 0.0), -1, keepdims=True)
                probs = jnp.exp(s - lse)
                dj = jnp.where(lane == j, d4, jnp.zeros_like(d4))
                dprobs = lax.dot_general(dj, v4, (((1,), (1,)), ((), ())), preferred_element_type=jnp.float32)
                inner = jnp.sum(probs * dprobs, -1, keepdims=True)
                dscores = (probs * (dprobs - inner)).astype(jnp.bfloat16)
                if b == 0:
                    dbias_ref[h] = dscores.astype(jnp.float32)
                else:
                    dbias_ref[h] = dbias_ref[h] + dscores.astype(jnp.float32)
                kj = jnp.where(lane == j, k4, jnp.zeros_like(k4))
                qj = jnp.where(lane == j, q4, jnp.zeros_like(q4))
                gq = gq + jnp.dot(dscores, kj, preferred_element_type=jnp.float32)
                gk = gk + lax.dot_general(dscores, qj, (((0,), (0,)), ((), ())), preferred_element_type=jnp.float32)
                gv = gv + lax.dot_general(probs.astype(jnp.bfloat16), dj, (((0,), (0,)), ((), ())), preferred_element_type=jnp.float32)
            gmix_ref[rows, pl.ds(g * LANES, LANES)] = (gq * scale).astype(gmix_ref.dtype)
            gmix_ref[rows, pl.ds(width + g * LANES, LANES)] = (gk * scale).astype(gmix_ref.dtype)
            gmix_ref[rows, pl.ds(2 * width + g * LANES, LANES)] = gv.astype(gmix_ref.dtype)


def _vmem():
    return pl.BlockSpec(memory_space=pltpu.VMEM)


def attention_fwd(mixed, bias, key_col, key_row, scale):
    tokens = mixed.shape[0]
    blocks = tokens // SPAN
    kernel = functools.partial(_fwd_kernel, scale=scale, blocks=blocks)
    return pl.pallas_call(
        kernel,
        out_shape=(
            jax.ShapeDtypeStruct((tokens, HEADS * 32), jnp.bfloat16),
            jax.ShapeDtypeStruct((blocks, SPAN, LANES), jnp.float32),
        ),
        in_specs=[_vmem()] * 4,
        out_specs=(_vmem(), _vmem()),
        compiler_params=pltpu.CompilerParams(vmem_limit_bytes=48 * 1024 * 1024),
    )(mixed, bias, key_col, key_row)


def attention_bwd(mixed, grad_att, lse, bias, key_col, key_row, scale):
    tokens = mixed.shape[0]
    blocks = tokens // SPAN
    kernel = functools.partial(_bwd_kernel, scale=scale, blocks=blocks)
    return pl.pallas_call(
        kernel,
        out_shape=(
            jax.ShapeDtypeStruct(mixed.shape, jnp.bfloat16),
            jax.ShapeDtypeStruct(bias.shape, jnp.float32),
        ),
        in_specs=[_vmem()] * 6,
        out_specs=(_vmem(), _vmem()),
        compiler_params=pltpu.CompilerParams(vmem_limit_bytes=56 * 1024 * 1024),
    )(mixed, grad_att, lse, bias, key_col, key_row)


def lane_blocks(matrix):
    row_blocks, col_blocks = matrix.shape[0] // BLK, matrix.shape[1] // BLK
    shaped = matrix.reshape(row_blocks, BLK, col_blocks, BLK).transpose(0, 2, 1, 3)
    return shaped.reshape(row_blocks * col_blocks, BLK * BLK // LANES, LANES)


ROWS = 112
SQRT_HALF = float(np.sqrt(0.5))
INV_SQRT_TAU = float(1.0 / np.sqrt(2.0 * np.pi))


def _norm(tensor):
    center = tensor - jnp.mean(tensor, -1, keepdims=True)
    inverse = lax.rsqrt(jnp.mean(center * center, -1, keepdims=True) + NORM_EPSILON)
    return center * inverse, inverse


def _mlp_fwd_kernel(att_ref, res_ref, valid_ref, wp_ref, gain_ref, off_ref, w1_ref, w2_ref,
                    hid_ref, act_ref, gelu_ref, out_ref, stat_ref):
    step = pl.program_id(0)
    branch_one = jnp.dot(att_ref[...], wp_ref[...], preferred_element_type=jnp.float32)
    hidden = res_ref[...] + branch_one
    normed, _ = _norm(hidden)
    act = (normed * gain_ref[...] + off_ref[...]).astype(jnp.bfloat16)
    pre = jnp.dot(act, w1_ref[...], preferred_element_type=jnp.float32)
    gelu = ((0.5 * pre) * (1.0 + lax.erf(pre * SQRT_HALF))).astype(jnp.bfloat16)
    branch_two = jnp.dot(gelu, w2_ref[...], preferred_element_type=jnp.float32)
    output = hidden + branch_two
    valid = valid_ref[...]
    first = jnp.sum(valid * output * output)
    second = jnp.sum(valid * (branch_one * branch_one + branch_two * branch_two))
    lane = lax.broadcasted_iota(jnp.int32, (8, 128), 1)
    row = lax.broadcasted_iota(jnp.int32, (8, 128), 0)
    here = jnp.where((row == 0) & (lane == 0), first, 0.0) + jnp.where((row == 0) & (lane == 1), second, 0.0)

    @pl.when(step == 0)
    def _():
        stat_ref[...] = jnp.zeros_like(stat_ref)

    stat_ref[...] = stat_ref[...] + here
    hid_ref[...] = hidden
    act_ref[...] = act
    gelu_ref[...] = gelu
    out_ref[...] = output.astype(out_ref.dtype)


def _mlp_bwd_kernel(gout_ref, hid_ref, act_ref, gain_ref, w1_ref, w2_ref, wp_ref,
                    gpre_ref, ghid_ref, gbr_ref, gatt_ref, small_ref):
    step = pl.program_id(0)
    contract_last = (((1,), (1,)), ((), ()))
    pre = jnp.dot(act_ref[...], w1_ref[...], preferred_element_type=jnp.float32)
    grad_out = gout_ref[...]
    grad_gelu = lax.dot_general(grad_out, w2_ref[...], contract_last, preferred_element_type=jnp.float32)
    cdf = 0.5 * (1.0 + lax.erf(pre * SQRT_HALF))
    pdf = jnp.exp(-0.5 * pre * pre) * INV_SQRT_TAU
    grad_pre = (grad_gelu * (cdf + pre * pdf)).astype(jnp.bfloat16)
    grad_act = lax.dot_general(grad_pre, w1_ref[...], contract_last, preferred_element_type=jnp.float32)
    normed, inverse = _norm(hid_ref[...])
    scaled = grad_act * gain_ref[...]
    mean_one = jnp.mean(scaled, -1, keepdims=True)
    mean_two = jnp.mean(scaled * normed, -1, keepdims=True)
    grad_hidden = grad_out.astype(jnp.float32) + inverse * (scaled - mean_one - normed * mean_two)
    grad_branch = grad_hidden.astype(jnp.bfloat16)
    grad_att = lax.dot_general(grad_branch, wp_ref[...], contract_last, preferred_element_type=jnp.float32)
    sums = jnp.concatenate(
        [jnp.sum(grad_act * normed, 0, keepdims=True), jnp.sum(grad_act, 0, keepdims=True),
         jnp.zeros((6, grad_act.shape[1]), jnp.float32)], 0)

    @pl.when(step == 0)
    def _():
        small_ref[...] = jnp.zeros_like(small_ref)

    small_ref[...] = small_ref[...] + sums
    gpre_ref[...] = grad_pre
    ghid_ref[...] = grad_hidden
    gbr_ref[...] = grad_branch
    gatt_ref[...] = grad_att.astype(gatt_ref.dtype)


def _rows(width):
    return pl.BlockSpec((ROWS, width), lambda i: (i, 0))


def _whole(shape):
    return pl.BlockSpec(shape, lambda i: (0,) * len(shape))


def mlp_fwd(attended, residual, valid, w_proj, gain, offset, w_fc1, w_fc2):
    tokens, width = residual.shape
    hidden_width = w_fc1.shape[1]
    return pl.pallas_call(
        _mlp_fwd_kernel,
        grid=(tokens // ROWS,),
        out_shape=(
            jax.ShapeDtypeStruct((tokens, width), jnp.float32),
            jax.ShapeDtypeStruct((tokens, width), jnp.bfloat16),
            jax.ShapeDtypeStruct((tokens, hidden_width), jnp.bfloat16),
            jax.ShapeDtypeStruct((tokens, width), jnp.bfloat16),
            jax.ShapeDtypeStruct((8, 128), jnp.float32),
        ),
        in_specs=[_rows(width), _rows(width), _rows(1), _whole(w_proj.shape), _whole((1, width)),
                  _whole((1, width)), _whole(w_fc1.shape), _whole(w_fc2.shape)],
        out_specs=(_rows(width), _rows(width), _rows(hidden_width), _rows(width), _whole((8, 128))),
        compiler_params=pltpu.CompilerParams(dimension_semantics=("arbitrary",), vmem_limit_bytes=48 * 1024 * 1024),
    )(attended, residual, valid, w_proj, gain.reshape(1, -1), offset.reshape(1, -1), w_fc1, w_fc2)


def mlp_bwd(grad_out, hidden, act_two, gain, w_fc1, w_fc2, w_proj):
    tokens, width = hidden.shape
    hidden_width = w_fc1.shape[1]
    return pl.pallas_call(
        _mlp_bwd_kernel,
        grid=(tokens // ROWS,),
        out_shape=(
            jax.ShapeDtypeStruct((tokens, hidden_width), jnp.bfloat16),
            jax.ShapeDtypeStruct((tokens, width), jnp.float32),
            jax.ShapeDtypeStruct((tokens, width), jnp.bfloat16),
            jax.ShapeDtypeStruct((tokens, width), jnp.bfloat16),
            jax.ShapeDtypeStruct((8, width), jnp.float32),
        ),
        in_specs=[_rows(width), _rows(width), _rows(width), _whole((1, width)), _whole(w_fc1.shape),
                  _whole(w_fc2.shape), _whole(w_proj.shape)],
        out_specs=(_rows(hidden_width), _rows(width), _rows(width), _rows(width), _whole((8, width))),
        compiler_params=pltpu.CompilerParams(dimension_semantics=("arbitrary",), vmem_limit_bytes=48 * 1024 * 1024),
    )(grad_out, hidden, act_two, gain.reshape(1, -1), w_fc1, w_fc2, w_proj)


def reduce_to_owners(parted, small):
    groups = lax.axis_size("dp")
    dp_bits = groups.bit_length() - 1
    n_qy, n_qx = lax.axis_size("qy"), lax.axis_size("qx")
    count, depth = parted[0].shape[0], parted[0].shape[1]
    per_group = count // groups
    names = [("dp", 1 << power) for power in reversed(range(dp_bits))] + [("qy", 1), ("qx", 1)]
    cross = [("qy", 1)] + [("dp", 1 << power) for power in range(dp_bits)]
    pieces, piece_names, orders = [], [], []
    for index, part in enumerate(parted):
        pieces.append(
            part.reshape([2] * dp_bits + [n_qy, n_qx, per_group * depth // (n_qy * n_qx), LANES])
        )
        piece_names.append(list(names))
        turn = index % len(cross)
        orders.append([("qx", 1)] + cross[turn:] + cross[:turn])
    for stage in range(len(names)):
        for index in range(len(pieces)):
            bit = orders[index][stage]
            place = piece_names[index].index(bit)
            mine = bit_of(*bit)
            keep = lax.dynamic_index_in_dim(pieces[index], mine, place, keepdims=False)
            send = lax.dynamic_index_in_dim(pieces[index], 1 - mine, place, keepdims=False)
            piece_names[index].remove(bit)
            arrived = partner_of(send.astype(jnp.bfloat16), *bit)
            pieces[index] = keep + arrived.astype(jnp.float32)
            if index == 0:
                small = small + partner_of(small, *bit)
                pieces[0], small = lax.optimization_barrier((pieces[0], small))
    chunk = jnp.stack(pieces)
    other = partner_of(chunk, "qy", 1)
    pair = jnp.where(bit_of("qy", 1) == 1, jnp.stack([other, chunk], 1), jnp.stack([chunk, other], 1))
    other = partner_of(pair, "qx", 1)
    quad = jnp.where(bit_of("qx", 1) == 1, jnp.stack([other, pair], 2), jnp.stack([pair, other], 2))
    quad = quad.reshape(len(pieces), per_group, depth, LANES).transpose(1, 0, 2, 3)
    return quad.reshape(per_group, BLK, BLK), small


def cut_along(value, dim, devices):
    before, after = (value.shape[:dim], value.shape[dim + 1 :])
    return jnp.moveaxis(value.reshape(*before, devices, -1, *after), dim, 0)


def sent_and_summed(value, axis, dim):
    pieces = cut_along(value, dim, lax.axis_size(axis))
    arrived = lax.all_to_all(pieces, axis, split_axis=0, concat_axis=0, tiled=True)
    return arrived.astype(jnp.float32).sum(axis=0)


def norm_stats(tensor):
    center = tensor - jnp.mean(tensor, -1, keepdims=True)
    inverse = lax.rsqrt(jnp.mean(center * center, -1, keepdims=True) + NORM_EPSILON)
    return (center * inverse, inverse)


def norm_back(grad_act, normed, inverse, gain):
    scaled = grad_act * gain
    mean_one = jnp.mean(scaled, -1, keepdims=True)
    mean_two = jnp.mean(scaled * normed, -1, keepdims=True)
    return inverse * (scaled - mean_one - normed * mean_two)


def to_windows(tensor):
    canvases, rows_side, cols_side, channels = tensor.shape
    shaped = tensor.reshape(canvases, rows_side // WIN, WIN, cols_side // WIN, WIN, channels)
    return shaped.transpose(0, 1, 3, 2, 4, 5).reshape(
        canvases * (rows_side // WIN) * (cols_side // WIN), WIN * WIN, channels
    )


def from_windows(tensor, canvases, rows_side, cols_side):
    channels = tensor.shape[-1]
    shaped = tensor.reshape(canvases, rows_side // WIN, cols_side // WIN, WIN, WIN, channels)
    return shaped.transpose(0, 1, 3, 2, 4, 5).reshape(canvases, rows_side, cols_side, channels)


def relative_index():
    places = jnp.arange(WIN * WIN, dtype=jnp.int32)
    row_of = places // WIN
    col_of = places % WIN
    return (row_of[:, None] - row_of[None, :] + WIN - 1) * (2 * WIN - 1) + (
        col_of[:, None] - col_of[None, :] + WIN - 1
    )


def region_of(places, full):
    return jnp.where(places < full - WIN, 0, jnp.where(places < full - SHIFT, 1, 2)).astype(
        jnp.int32
    )


def advance(tensor):
    upper = passed_along(tensor[:, :SHIFT], "qy", -1)
    tensor = jnp.concatenate([tensor[:, SHIFT:], upper], 1)
    leftmost = passed_along(tensor[:, :, :SHIFT], "qx", -1)
    return jnp.concatenate([tensor[:, :, SHIFT:], leftmost], 2)


def retreat(tensor):
    lowest = passed_along(tensor[:, -SHIFT:], "qy", 1)
    tensor = jnp.concatenate([lowest, tensor[:, :-SHIFT]], 1)
    rightmost = passed_along(tensor[:, :, -SHIFT:], "qx", 1)
    return jnp.concatenate([rightmost, tensor[:, :, :-SHIFT]], 2)


def blocks_of(matrix):
    row_blocks = matrix.shape[0] // BLK
    col_blocks = matrix.shape[1] // BLK
    return (
        matrix.reshape(row_blocks, BLK, col_blocks, BLK)
        .transpose(0, 2, 1, 3)
        .reshape(row_blocks * col_blocks, BLK, BLK)
    )


def rotate_update(grads, master, first, second, left, right):
    turned = jnp.einsum("sji,sjk->sik", left, grads, precision=PRECISE)
    turned = jnp.einsum("sik,skl->sil", turned, right, precision=PRECISE)
    new_first = BETA_ONE * first + (1.0 - BETA_ONE) * turned
    new_second = BETA_TWO * second + (1.0 - BETA_TWO) * turned * turned
    direction = new_first / (jnp.sqrt(new_second) + ADAM_EPSILON)
    back = jnp.einsum("sij,sjk->sik", left, direction, precision=PRECISE)
    back = jnp.einsum("sik,slk->sil", back, right, precision=PRECISE)
    return (new_first, new_second, master - RATE_BLOCKS * back)


def small_update(grads, params, first, second):
    new_first = BETA_ONE * first + (1.0 - BETA_ONE) * grads
    new_second = BETA_TWO * second + (1.0 - BETA_TWO) * grads * grads
    direction = new_first / (jnp.sqrt(new_second) + ADAM_EPSILON)
    return (new_first, new_second, params - RATE_SMALL * direction)


def local(
    tokens,
    crop_ids,
    merge_order,
    owner_list,
    w_qkv,
    w_proj,
    w_fc1,
    w_fc2,
    small_params,
    small_first,
    small_second,
    master_blocks,
    first_moment,
    second_moment,
    basis_left,
    basis_right,
    merged_grad,
):
    canvases, quad_side, quad_cols, features = tokens.shape
    head_dim = features // HEADS
    score_scale = head_dim ** (-0.5)
    window_area = WIN * WIN
    quarters = lax.axis_size(("qy", "qx"))
    share_rows = quad_side * quad_cols // quarters
    row_base = lax.axis_index("qy") * quad_side
    col_base = lax.axis_index("qx") * quad_cols
    rolled = jnp.roll(crop_ids, (-SHIFT, -SHIFT), (1, 2))
    local_ids = lax.dynamic_slice(
        rolled, (jnp.int32(0), row_base, col_base), (canvases, quad_side, quad_cols)
    )
    region_row = region_of(
        row_base + jnp.arange(quad_side, dtype=jnp.int32), quad_side * lax.axis_size("qy")
    )
    region_col = region_of(
        col_base + jnp.arange(quad_cols, dtype=jnp.int32), quad_cols * lax.axis_size("qx")
    )
    labels = (local_ids + 1) * 9 + region_row[None, :, None] * 3 + region_col[None, None, :]
    win_labels = to_windows(labels[..., None])[..., 0]
    window_count = win_labels.shape[0]
    valid = (win_labels >= 9).reshape(-1).astype(jnp.float32)[:, None]
    gain_one = small_params[0:features]
    offset_one = small_params[features : 2 * features]
    gain_two = small_params[2 * features : 3 * features]
    offset_two = small_params[3 * features : 4 * features]
    table = small_params[4 * features :].reshape(HEADS, -1)
    onehot = (
        relative_index().reshape(-1)[:, None]
        == jnp.arange(table.shape[1], dtype=jnp.int32)[None, :]
    ).astype(jnp.float32)
    rel_bias = jnp.einsum("hr,pr->hp", table, onehot, precision=PRECISE).reshape(
        HEADS, window_area, window_area
    )

    residual = to_windows(advance(tokens)).reshape(-1, features).astype(jnp.float32)
    normed_one, inverse_one = norm_stats(residual)
    act_one = (normed_one * gain_one + offset_one).astype(jnp.bfloat16)
    mixed = jnp.dot(act_one, w_qkv, preferred_element_type=jnp.float32).astype(jnp.bfloat16)
    per_span = SPAN // window_area
    window_slot = jnp.arange(window_count, dtype=jnp.int32) % per_span
    span_keys = (win_labels * per_span + window_slot[:, None]).reshape(-1, SPAN)
    key_col, key_row = span_keys[:, :, None], span_keys[:, None, :]
    spread = (
        jnp.arange(SPAN, dtype=jnp.int32)[:, None] % window_area
        == jnp.arange(window_area, dtype=jnp.int32)[None, :]
    ).astype(jnp.float32)
    dense_bias = jnp.einsum(
        "hti,ui->htu",
        jnp.einsum("ti,hij->htj", spread, rel_bias, precision=PRECISE),
        spread,
        precision=PRECISE,
    )
    attended, log_total = attention_fwd(mixed, dense_bias, key_col, key_row, score_scale)
    hidden, act_two, gelu_low, output_flat, stat_block = mlp_fwd(
        attended, residual, valid, w_proj, gain_two, offset_two, w_fc1, w_fc2
    )
    stat_terms = jnp.stack([stat_block[0, 0], stat_block[0, 1], jnp.sum(valid) * features])
    output_low = output_flat.reshape(window_count, window_area, features)
    restored = retreat(from_windows(output_low, canvases, quad_side, quad_cols))
    flat_out = restored.reshape(canvases, quarters, share_rows, features)
    arrived = lax.all_to_all(flat_out, ("qy", "qx"), 1, 1, tiled=True)
    merged = jnp.take(arrived, merge_order, axis=1, mode="clip").transpose(0, 2, 1, 3).reshape(
        canvases, share_rows, quarters * features
    )
    quarter_ids = jnp.arange(quarters, dtype=jnp.int32)
    source_pick = jnp.sum(
        quarter_ids[:, None] * (merge_order[:, None] == quarter_ids[None, :]).astype(jnp.int32), 0
    )
    incoming = merged_grad.reshape(canvases, share_rows, quarters, features)
    unordered = jnp.take(incoming, source_pick, axis=2, mode="clip").transpose(0, 2, 1, 3)
    returned = lax.all_to_all(unordered, ("qy", "qx"), 1, 1, tiled=True)
    grad_orig = returned.reshape(canvases, quad_side, quad_cols, features)
    grad_out = to_windows(advance(grad_orig)).reshape(-1, features)
    grad_pre, grad_hidden, grad_branch, grad_attended, small_two = mlp_bwd(
        grad_out, hidden, act_two, gain_two, w_fc1, w_fc2, w_proj
    )
    grad_fc2 = jnp.einsum("rf,rc->fc", gelu_low, grad_out, preferred_element_type=jnp.float32)
    grad_fc1 = jnp.einsum("rc,rf->cf", act_two, grad_pre, preferred_element_type=jnp.float32)
    grad_proj = jnp.einsum("rc,rd->cd", attended, grad_branch, preferred_element_type=jnp.float32)
    grad_mixed, dense_grad_bias = attention_bwd(
        mixed, grad_attended, log_total, dense_bias, key_col, key_row, score_scale
    )
    grad_bias = jnp.einsum(
        "ti,htj->hij",
        spread,
        jnp.einsum("htu,uj->htj", dense_grad_bias, spread, precision=PRECISE),
        precision=PRECISE,
    )
    grad_table = jnp.dot(grad_bias.reshape(HEADS, -1), onehot, precision=PRECISE)
    grad_qkv = jnp.einsum("rc,rf->cf", act_one, grad_mixed, preferred_element_type=jnp.float32)
    grad_act_one = jnp.einsum("rf,cf->rc", grad_mixed, w_qkv, preferred_element_type=jnp.float32)
    grad_input = grad_hidden + norm_back(grad_act_one, normed_one, inverse_one, gain_one)
    grad_low = grad_input.astype(jnp.bfloat16).reshape(window_count, window_area, features)
    grad_tokens = retreat(from_windows(grad_low, canvases, quad_side, quad_cols))
    small_local = jnp.concatenate(
        [
            jnp.sum(grad_act_one * normed_one, 0),
            jnp.sum(grad_act_one, 0),
            small_two[0],
            small_two[1],
            grad_table.reshape(-1),
        ]
    )
    every_block = jnp.concatenate(
        [lane_blocks(grad_qkv), lane_blocks(grad_proj), lane_blocks(grad_fc1), lane_blocks(grad_fc2)],
        0,
    )
    depth = every_block.shape[1] // PARTS
    parted = [
        jnp.take(every_block[:, index * depth : (index + 1) * depth], owner_list, axis=0, mode="clip")
        for index in range(PARTS)
    ]
    owned_grads, small_all = reduce_to_owners(parted, jnp.concatenate([small_local, stat_terms]))
    small_total = small_all[: small_local.shape[0]]
    stat_total = small_all[small_local.shape[0] :]
    new_first, new_second, new_master = rotate_update(
        owned_grads, master_blocks, first_moment, second_moment, basis_left, basis_right
    )
    small_first_new, small_second_new, small_new = small_update(
        small_total, small_params, small_first, small_second
    )
    stats = jnp.stack(
        [jnp.sqrt(stat_total[0] / stat_total[2]), jnp.sqrt(stat_total[1] / (2.0 * stat_total[2]))]
    )
    return (
        merged,
        grad_tokens,
        owned_grads,
        new_master,
        new_first,
        new_second,
        new_master.astype(jnp.bfloat16),
        small_total,
        small_first_new,
        small_second_new,
        small_new,
        stats,
    )


def solution(mesh):
    placed = (
        P("dp", "qy", "qx", None),
        P("dp", None, None),
        P(),
        P(),
        P(),
        P(),
        P(),
        P(),
        P(),
        P(),
        P(),
        P("dp", None, None),
        P("dp", None, None),
        P("dp", None, None),
        P("dp", None, None),
        P("dp", None, None),
        P("dp", ("qy", "qx"), None),
    )
    return jax.shard_map(
        local,
        mesh=mesh,
        in_specs=placed,
        out_specs=(
            P("dp", ("qy", "qx"), None),
            P("dp", "qy", "qx", None),
            P("dp", None, None),
            P("dp", None, None),
            P("dp", None, None),
            P("dp", None, None),
            P("dp", None, None),
            P(),
            P(),
            P(),
            P(),
            P(),
        ),
        check_vma=False,
    )
```

```python
import functools
from functools import partial

import numpy as np

import jax
import jax.numpy as jnp
from jax import lax
from jax.experimental import pallas as pl
from jax.experimental.pallas import tpu as pltpu
from jax.sharding import PartitionSpec as P

HEADS = 12
WIN = 7
SHIFT = 3
BLK = 96


BETA_ONE = 0.5
BETA_TWO = 0.6
ADAM_EPSILON = 1e-08
RATE_BLOCKS = 0.04
RATE_SMALL = 0.2
MASK_FILL = -1e30
NORM_EPSILON = 1e-05
PRECISE = lax.Precision.HIGHEST


def passed_along(value, axis, steps):
    count = lax.axis_size(axis)
    pairs = [(source, (source + steps) % count) for source in range(count)]
    return lax.ppermute(value, axis, pairs)


def partner_of(value, axis, mask):
    count = lax.axis_size(axis)
    pairs = [(source, source ^ mask) for source in range(count)]
    return lax.ppermute(value, axis, pairs)


def bit_of(axis, mask):
    return ((lax.axis_index(axis) & mask) != 0).astype(jnp.int32)


LANES = 128
PARTS = 3
GROUP = 4
LANES = 128
MASK_FILL = -1e30
PAIR = 104


def _stacked(value, lane4):
    wide = jnp.broadcast_to(value.astype(jnp.float32)[None], (GROUP, PAIR, LANES))
    return jnp.where(lane4, wide, 0.0).reshape(GROUP * PAIR, LANES).astype(jnp.bfloat16)


def _gather_lanes(stack, lane4):
    return jnp.sum(jnp.where(lane4, stack.reshape(GROUP, PAIR, LANES), 0.0), 0)


def _scores(q4, k4, bias4, allowed, scale, lane4):
    raw = lax.dot_general(_stacked(q4, lane4), k4, (((1,), (1,)), ((), ())), preferred_element_type=jnp.float32)
    raw = raw.reshape(GROUP, PAIR, PAIR) * scale + bias4
    return jnp.where(allowed[None], raw, MASK_FILL)


def _lane_masks():
    lane4 = lax.broadcasted_iota(jnp.int32, (GROUP, 1, LANES), 2) // 32 == lax.broadcasted_iota(
        jnp.int32, (GROUP, 1, LANES), 0)
    return lane4, lax.broadcasted_iota(jnp.int32, (1, LANES), 1)


def _fwd_kernel(mix_ref, bias_ref, kc_ref, kr_ref, out_ref, lse_ref, *, scale):
    width = HEADS * 32
    lane4, head_lane = _lane_masks()
    allowed = kc_ref[0] == kr_ref[0]
    lse_all = jnp.zeros((PAIR, LANES), jnp.float32)
    for g in range(HEADS // GROUP):
        q4 = mix_ref[0, :, pl.ds(g * LANES, LANES)]
        k4 = mix_ref[0, :, pl.ds(width + g * LANES, LANES)]
        v4 = mix_ref[0, :, pl.ds(2 * width + g * LANES, LANES)]
        s = _scores(q4, k4, bias_ref[pl.ds(g * GROUP, GROUP)], allowed, scale, lane4)
        top = jnp.max(s, -1, keepdims=True)
        e = jnp.exp(s - top)
        total = jnp.sum(e, -1, keepdims=True)
        probs = (e / total).reshape(GROUP * PAIR, PAIR).astype(jnp.bfloat16)
        mixed_out = jnp.dot(probs, v4, preferred_element_type=jnp.float32)
        out_ref[0, :, pl.ds(g * LANES, LANES)] = _gather_lanes(mixed_out, lane4).astype(out_ref.dtype)
        lse = top + jnp.log(total)
        for j in range(GROUP):
            lse_all = jnp.where(head_lane == g * GROUP + j, lse[j], lse_all)
    lse_ref[0] = lse_all


def _bwd_kernel(mix_ref, grad_ref, lse_ref, bias_ref, kc_ref, kr_ref, gmix_ref, dbias_ref, *, scale):
    width = HEADS * 32
    lane4, head_lane = _lane_masks()
    step = pl.program_id(0)
    allowed = kc_ref[0] == kr_ref[0]
    lse_all = lse_ref[0]

    @pl.when(step == 0)
    def _():
        dbias_ref[...] = jnp.zeros_like(dbias_ref)

    for g in range(HEADS // GROUP):
        q4 = mix_ref[0, :, pl.ds(g * LANES, LANES)]
        k4 = mix_ref[0, :, pl.ds(width + g * LANES, LANES)]
        v4 = mix_ref[0, :, pl.ds(2 * width + g * LANES, LANES)]
        d4 = grad_ref[0, :, pl.ds(g * LANES, LANES)]
        heads = pl.ds(g * GROUP, GROUP)
        s = _scores(q4, k4, bias_ref[heads], allowed, scale, lane4)
        lse = jnp.stack([
            jnp.sum(jnp.where(head_lane == g * GROUP + j, lse_all, 0.0), -1, keepdims=True)
            for j in range(GROUP)
        ])
        probs = jnp.exp(s - lse)
        d_stack = _stacked(d4, lane4)
        dprobs = lax.dot_general(d_stack, v4, (((1,), (1,)), ((), ())), preferred_element_type=jnp.float32)
        dprobs = dprobs.reshape(GROUP, PAIR, PAIR)
        inner = jnp.sum(probs * dprobs, -1, keepdims=True)
        dscores = (probs * (dprobs - inner)).reshape(GROUP * PAIR, PAIR).astype(jnp.bfloat16)
        dbias_ref[heads] = dbias_ref[heads] + dscores.astype(jnp.float32).reshape(GROUP, PAIR, PAIR)
        gq = _gather_lanes(jnp.dot(dscores, k4, preferred_element_type=jnp.float32), lane4)
        gk = lax.dot_general(dscores, _stacked(q4, lane4), (((0,), (0,)), ((), ())), preferred_element_type=jnp.float32)
        gv = lax.dot_general(probs.reshape(GROUP * PAIR, PAIR).astype(jnp.bfloat16), d_stack,
                             (((0,), (0,)), ((), ())), preferred_element_type=jnp.float32)
        gmix_ref[0, :, pl.ds(g * LANES, LANES)] = (gq * scale).astype(gmix_ref.dtype)
        gmix_ref[0, :, pl.ds(width + g * LANES, LANES)] = (gk * scale).astype(gmix_ref.dtype)
        gmix_ref[0, :, pl.ds(2 * width + g * LANES, LANES)] = gv.astype(gmix_ref.dtype)


def _pair_spec(width):
    return pl.BlockSpec((1, PAIR, width), lambda p: (p, 0, 0))


def attention_fwd(mixed_pairs, bias, key_col, key_row, scale):
    pairs = mixed_pairs.shape[0]
    kernel = functools.partial(_fwd_kernel, scale=scale)
    return pl.pallas_call(
        kernel,
        grid=(pairs,),
        out_shape=(
            jax.ShapeDtypeStruct((pairs, PAIR, HEADS * 32), jnp.bfloat16),
            jax.ShapeDtypeStruct((pairs, PAIR, LANES), jnp.float32),
        ),
        in_specs=[_pair_spec(mixed_pairs.shape[2]), pl.BlockSpec(bias.shape, lambda p: (0, 0, 0)),
                  pl.BlockSpec((1, PAIR, 1), lambda p: (p, 0, 0)), pl.BlockSpec((1, 1, PAIR), lambda p: (p, 0, 0))],
        out_specs=(_pair_spec(HEADS * 32), _pair_spec(LANES)),
        compiler_params=pltpu.CompilerParams(dimension_semantics=("arbitrary",), vmem_limit_bytes=32 * 1024 * 1024),
    )(mixed_pairs, bias, key_col, key_row)


def attention_bwd(mixed_pairs, grad_pairs, lse, bias, key_col, key_row, scale):
    pairs = mixed_pairs.shape[0]
    kernel = functools.partial(_bwd_kernel, scale=scale)
    return pl.pallas_call(
        kernel,
        grid=(pairs,),
        out_shape=(
            jax.ShapeDtypeStruct(mixed_pairs.shape, jnp.bfloat16),
            jax.ShapeDtypeStruct(bias.shape, jnp.float32),
        ),
        in_specs=[_pair_spec(mixed_pairs.shape[2]), _pair_spec(HEADS * 32), _pair_spec(LANES),
                  pl.BlockSpec(bias.shape, lambda p: (0, 0, 0)),
                  pl.BlockSpec((1, PAIR, 1), lambda p: (p, 0, 0)), pl.BlockSpec((1, 1, PAIR), lambda p: (p, 0, 0))],
        out_specs=(_pair_spec(mixed_pairs.shape[2]), pl.BlockSpec(bias.shape, lambda p: (0, 0, 0))),
        compiler_params=pltpu.CompilerParams(dimension_semantics=("arbitrary",), vmem_limit_bytes=32 * 1024 * 1024),
    )(mixed_pairs, grad_pairs, lse, bias, key_col, key_row)


def lane_blocks(matrix):
    row_blocks, col_blocks = matrix.shape[0] // BLK, matrix.shape[1] // BLK
    shaped = matrix.reshape(row_blocks, BLK, col_blocks, BLK).transpose(0, 2, 1, 3)
    return shaped.reshape(row_blocks * col_blocks, BLK * BLK // LANES, LANES)


ROWS = 112
SQRT_HALF = float(np.sqrt(0.5))
INV_SQRT_TAU = float(1.0 / np.sqrt(2.0 * np.pi))


def _norm(tensor):
    center = tensor - jnp.mean(tensor, -1, keepdims=True)
    inverse = lax.rsqrt(jnp.mean(center * center, -1, keepdims=True) + NORM_EPSILON)
    return center * inverse, inverse


def _mlp_fwd_kernel(att_ref, res_ref, valid_ref, wp_ref, gain_ref, off_ref, w1_ref, w2_ref,
                    hid_ref, act_ref, gelu_ref, out_ref, stat_ref):
    step = pl.program_id(0)
    branch_one = jnp.dot(att_ref[...], wp_ref[...], preferred_element_type=jnp.float32)
    hidden = res_ref[...] + branch_one
    normed, _ = _norm(hidden)
    act = (normed * gain_ref[...] + off_ref[...]).astype(jnp.bfloat16)
    pre = jnp.dot(act, w1_ref[...], preferred_element_type=jnp.float32)
    gelu = ((0.5 * pre) * (1.0 + lax.erf(pre * SQRT_HALF))).astype(jnp.bfloat16)
    branch_two = jnp.dot(gelu, w2_ref[...], preferred_element_type=jnp.float32)
    output = hidden + branch_two
    valid = valid_ref[...]
    first = jnp.sum(valid * output * output)
    second = jnp.sum(valid * (branch_one * branch_one + branch_two * branch_two))
    lane = lax.broadcasted_iota(jnp.int32, (8, 128), 1)
    row = lax.broadcasted_iota(jnp.int32, (8, 128), 0)
    here = jnp.where((row == 0) & (lane == 0), first, 0.0) + jnp.where((row == 0) & (lane == 1), second, 0.0)

    @pl.when(step == 0)
    def _():
        stat_ref[...] = jnp.zeros_like(stat_ref)

    stat_ref[...] = stat_ref[...] + here
    hid_ref[...] = hidden
    act_ref[...] = act
    gelu_ref[...] = gelu
    out_ref[...] = output.astype(out_ref.dtype)


def _mlp_bwd_kernel(gout_ref, hid_ref, act_ref, gain_ref, w1_ref, w2_ref, wp_ref,
                    gpre_ref, ghid_ref, gbr_ref, gatt_ref, small_ref):
    step = pl.program_id(0)
    contract_last = (((1,), (1,)), ((), ()))
    pre = jnp.dot(act_ref[...], w1_ref[...], preferred_element_type=jnp.float32)
    grad_out = gout_ref[...]
    grad_gelu = lax.dot_general(grad_out, w2_ref[...], contract_last, preferred_element_type=jnp.float32)
    cdf = 0.5 * (1.0 + lax.erf(pre * SQRT_HALF))
    pdf = jnp.exp(-0.5 * pre * pre) * INV_SQRT_TAU
    grad_pre = (grad_gelu * (cdf + pre * pdf)).astype(jnp.bfloat16)
    grad_act = lax.dot_general(grad_pre, w1_ref[...], contract_last, preferred_element_type=jnp.float32)
    normed, inverse = _norm(hid_ref[...])
    scaled = grad_act * gain_ref[...]
    mean_one = jnp.mean(scaled, -1, keepdims=True)
    mean_two = jnp.mean(scaled * normed, -1, keepdims=True)
    grad_hidden = grad_out.astype(jnp.float32) + inverse * (scaled - mean_one - normed * mean_two)
    grad_branch = grad_hidden.astype(jnp.bfloat16)
    grad_att = lax.dot_general(grad_branch, wp_ref[...], contract_last, preferred_element_type=jnp.float32)
    sums = jnp.concatenate(
        [jnp.sum(grad_act * normed, 0, keepdims=True), jnp.sum(grad_act, 0, keepdims=True),
         jnp.zeros((6, grad_act.shape[1]), jnp.float32)], 0)

    @pl.when(step == 0)
    def _():
        small_ref[...] = jnp.zeros_like(small_ref)

    small_ref[...] = small_ref[...] + sums
    gpre_ref[...] = grad_pre
    ghid_ref[...] = grad_hidden
    gbr_ref[...] = grad_branch
    gatt_ref[...] = grad_att.astype(gatt_ref.dtype)


def _rows(width):
    return pl.BlockSpec((ROWS, width), lambda i: (i, 0))


def _whole(shape):
    return pl.BlockSpec(shape, lambda i: (0,) * len(shape))


def mlp_fwd(attended, residual, valid, w_proj, gain, offset, w_fc1, w_fc2):
    tokens, width = residual.shape
    hidden_width = w_fc1.shape[1]
    return pl.pallas_call(
        _mlp_fwd_kernel,
        grid=(tokens // ROWS,),
        out_shape=(
            jax.ShapeDtypeStruct((tokens, width), jnp.float32),
            jax.ShapeDtypeStruct((tokens, width), jnp.bfloat16),
            jax.ShapeDtypeStruct((tokens, hidden_width), jnp.bfloat16),
            jax.ShapeDtypeStruct((tokens, width), jnp.bfloat16),
            jax.ShapeDtypeStruct((8, 128), jnp.float32),
        ),
        in_specs=[_rows(width), _rows(width), _rows(1), _whole(w_proj.shape), _whole((1, width)),
                  _whole((1, width)), _whole(w_fc1.shape), _whole(w_fc2.shape)],
        out_specs=(_rows(width), _rows(width), _rows(hidden_width), _rows(width), _whole((8, 128))),
        compiler_params=pltpu.CompilerParams(dimension_semantics=("arbitrary",), vmem_limit_bytes=48 * 1024 * 1024),
    )(attended, residual, valid, w_proj, gain.reshape(1, -1), offset.reshape(1, -1), w_fc1, w_fc2)


def mlp_bwd(grad_out, hidden, act_two, gain, w_fc1, w_fc2, w_proj):
    tokens, width = hidden.shape
    hidden_width = w_fc1.shape[1]
    return pl.pallas_call(
        _mlp_bwd_kernel,
        grid=(tokens // ROWS,),
        out_shape=(
            jax.ShapeDtypeStruct((tokens, hidden_width), jnp.bfloat16),
            jax.ShapeDtypeStruct((tokens, width), jnp.float32),
            jax.ShapeDtypeStruct((tokens, width), jnp.bfloat16),
            jax.ShapeDtypeStruct((tokens, width), jnp.bfloat16),
            jax.ShapeDtypeStruct((8, width), jnp.float32),
        ),
        in_specs=[_rows(width), _rows(width), _rows(width), _whole((1, width)), _whole(w_fc1.shape),
                  _whole(w_fc2.shape), _whole(w_proj.shape)],
        out_specs=(_rows(hidden_width), _rows(width), _rows(width), _rows(width), _whole((8, width))),
        compiler_params=pltpu.CompilerParams(dimension_semantics=("arbitrary",), vmem_limit_bytes=48 * 1024 * 1024),
    )(grad_out, hidden, act_two, gain.reshape(1, -1), w_fc1, w_fc2, w_proj)


def reduce_to_owners(parted, small):
    groups = lax.axis_size("dp")
    dp_bits = groups.bit_length() - 1
    n_qy, n_qx = lax.axis_size("qy"), lax.axis_size("qx")
    count, depth = parted[0].shape[0], parted[0].shape[1]
    per_group = count // groups
    names = [("dp", 1 << power) for power in reversed(range(dp_bits))] + [("qy", 1), ("qx", 1)]
    cross = [("qy", 1)] + [("dp", 1 << power) for power in range(dp_bits)]
    pieces, piece_names, orders = [], [], []
    for index, part in enumerate(parted):
        pieces.append(
            part.reshape([2] * dp_bits + [n_qy, n_qx, per_group * depth // (n_qy * n_qx), LANES])
        )
        piece_names.append(list(names))
        turn = index % len(cross)
        orders.append([("qx", 1)] + cross[turn:] + cross[:turn])
    for stage in range(len(names)):
        for index in range(len(pieces)):
            bit = orders[index][stage]
            place = piece_names[index].index(bit)
            mine = bit_of(*bit)
            keep = lax.dynamic_index_in_dim(pieces[index], mine, place, keepdims=False)
            send = lax.dynamic_index_in_dim(pieces[index], 1 - mine, place, keepdims=False)
            piece_names[index].remove(bit)
            arrived = partner_of(send.astype(jnp.bfloat16), *bit)
            pieces[index] = keep + arrived.astype(jnp.float32)
            if index == 0:
                small = small + partner_of(small, *bit)
                pieces[0], small = lax.optimization_barrier((pieces[0], small))
    chunk = jnp.stack(pieces)
    other = partner_of(chunk, "qy", 1)
    pair = jnp.where(bit_of("qy", 1) == 1, jnp.stack([other, chunk], 1), jnp.stack([chunk, other], 1))
    other = partner_of(pair, "qx", 1)
    quad = jnp.where(bit_of("qx", 1) == 1, jnp.stack([other, pair], 2), jnp.stack([pair, other], 2))
    quad = quad.reshape(len(pieces), per_group, depth, LANES).transpose(1, 0, 2, 3)
    return quad.reshape(per_group, BLK, BLK), small


def cut_along(value, dim, devices):
    before, after = (value.shape[:dim], value.shape[dim + 1 :])
    return jnp.moveaxis(value.reshape(*before, devices, -1, *after), dim, 0)


def sent_and_summed(value, axis, dim):
    pieces = cut_along(value, dim, lax.axis_size(axis))
    arrived = lax.all_to_all(pieces, axis, split_axis=0, concat_axis=0, tiled=True)
    return arrived.astype(jnp.float32).sum(axis=0)


def norm_stats(tensor):
    center = tensor - jnp.mean(tensor, -1, keepdims=True)
    inverse = lax.rsqrt(jnp.mean(center * center, -1, keepdims=True) + NORM_EPSILON)
    return (center * inverse, inverse)


def norm_back(grad_act, normed, inverse, gain):
    scaled = grad_act * gain
    mean_one = jnp.mean(scaled, -1, keepdims=True)
    mean_two = jnp.mean(scaled * normed, -1, keepdims=True)
    return inverse * (scaled - mean_one - normed * mean_two)


def to_windows(tensor):
    canvases, rows_side, cols_side, channels = tensor.shape
    shaped = tensor.reshape(canvases, rows_side // WIN, WIN, cols_side // WIN, WIN, channels)
    return shaped.transpose(0, 1, 3, 2, 4, 5).reshape(
        canvases * (rows_side // WIN) * (cols_side // WIN), WIN * WIN, channels
    )


def from_windows(tensor, canvases, rows_side, cols_side):
    channels = tensor.shape[-1]
    shaped = tensor.reshape(canvases, rows_side // WIN, cols_side // WIN, WIN, WIN, channels)
    return shaped.transpose(0, 1, 3, 2, 4, 5).reshape(canvases, rows_side, cols_side, channels)


def relative_index():
    places = jnp.arange(WIN * WIN, dtype=jnp.int32)
    row_of = places // WIN
    col_of = places % WIN
    return (row_of[:, None] - row_of[None, :] + WIN - 1) * (2 * WIN - 1) + (
        col_of[:, None] - col_of[None, :] + WIN - 1
    )


def region_of(places, full):
    return jnp.where(places < full - WIN, 0, jnp.where(places < full - SHIFT, 1, 2)).astype(
        jnp.int32
    )


def advance(tensor):
    upper = passed_along(tensor[:, :SHIFT], "qy", -1)
    tensor = jnp.concatenate([tensor[:, SHIFT:], upper], 1)
    leftmost = passed_along(tensor[:, :, :SHIFT], "qx", -1)
    return jnp.concatenate([tensor[:, :, SHIFT:], leftmost], 2)


def retreat(tensor):
    lowest = passed_along(tensor[:, -SHIFT:], "qy", 1)
    tensor = jnp.concatenate([lowest, tensor[:, :-SHIFT]], 1)
    rightmost = passed_along(tensor[:, :, -SHIFT:], "qx", 1)
    return jnp.concatenate([rightmost, tensor[:, :, :-SHIFT]], 2)


def blocks_of(matrix):
    row_blocks = matrix.shape[0] // BLK
    col_blocks = matrix.shape[1] // BLK
    return (
        matrix.reshape(row_blocks, BLK, col_blocks, BLK)
        .transpose(0, 2, 1, 3)
        .reshape(row_blocks * col_blocks, BLK, BLK)
    )


def rotate_update(grads, master, first, second, left, right):
    turned = jnp.einsum("sji,sjk->sik", left, grads, precision=PRECISE)
    turned = jnp.einsum("sik,skl->sil", turned, right, precision=PRECISE)
    new_first = BETA_ONE * first + (1.0 - BETA_ONE) * turned
    new_second = BETA_TWO * second + (1.0 - BETA_TWO) * turned * turned
    direction = new_first / (jnp.sqrt(new_second) + ADAM_EPSILON)
    back = jnp.einsum("sij,sjk->sik", left, direction, precision=PRECISE)
    back = jnp.einsum("sik,slk->sil", back, right, precision=PRECISE)
    return (new_first, new_second, master - RATE_BLOCKS * back)


def small_update(grads, params, first, second):
    new_first = BETA_ONE * first + (1.0 - BETA_ONE) * grads
    new_second = BETA_TWO * second + (1.0 - BETA_TWO) * grads * grads
    direction = new_first / (jnp.sqrt(new_second) + ADAM_EPSILON)
    return (new_first, new_second, params - RATE_SMALL * direction)


def local(
    tokens,
    crop_ids,
    merge_order,
    owner_list,
    w_qkv,
    w_proj,
    w_fc1,
    w_fc2,
    small_params,
    small_first,
    small_second,
    master_blocks,
    first_moment,
    second_moment,
    basis_left,
    basis_right,
    merged_grad,
):
    canvases, quad_side, quad_cols, features = tokens.shape
    head_dim = features // HEADS
    score_scale = head_dim ** (-0.5)
    window_area = WIN * WIN
    quarters = lax.axis_size(("qy", "qx"))
    share_rows = quad_side * quad_cols // quarters
    row_base = lax.axis_index("qy") * quad_side
    col_base = lax.axis_index("qx") * quad_cols
    rolled = jnp.roll(crop_ids, (-SHIFT, -SHIFT), (1, 2))
    local_ids = lax.dynamic_slice(
        rolled, (jnp.int32(0), row_base, col_base), (canvases, quad_side, quad_cols)
    )
    region_row = region_of(
        row_base + jnp.arange(quad_side, dtype=jnp.int32), quad_side * lax.axis_size("qy")
    )
    region_col = region_of(
        col_base + jnp.arange(quad_cols, dtype=jnp.int32), quad_cols * lax.axis_size("qx")
    )
    labels = (local_ids + 1) * 9 + region_row[None, :, None] * 3 + region_col[None, None, :]
    win_labels = to_windows(labels[..., None])[..., 0]
    window_count = win_labels.shape[0]
    valid = (win_labels >= 9).reshape(-1).astype(jnp.float32)[:, None]
    gain_one = small_params[0:features]
    offset_one = small_params[features : 2 * features]
    gain_two = small_params[2 * features : 3 * features]
    offset_two = small_params[3 * features : 4 * features]
    table = small_params[4 * features :].reshape(HEADS, -1)
    onehot = (
        relative_index().reshape(-1)[:, None]
        == jnp.arange(table.shape[1], dtype=jnp.int32)[None, :]
    ).astype(jnp.float32)
    rel_bias = jnp.einsum("hr,pr->hp", table, onehot, precision=PRECISE).reshape(
        HEADS, window_area, window_area
    )

    residual = to_windows(advance(tokens)).reshape(-1, features).astype(jnp.float32)
    normed_one, inverse_one = norm_stats(residual)
    act_one = (normed_one * gain_one + offset_one).astype(jnp.bfloat16)
    mixed = jnp.dot(act_one, w_qkv, preferred_element_type=jnp.float32).astype(jnp.bfloat16)
    pair_area = 2 * window_area
    place = jnp.arange(PAIR, dtype=jnp.int32)
    pair_labels = jnp.pad(win_labels.reshape(-1, pair_area), ((0, 0), (0, PAIR - pair_area)))
    pair_keys = jnp.where(
        place[None] < pair_area,
        pair_labels * 2 + (place[None] >= window_area).astype(jnp.int32),
        -1 - place[None],
    )
    key_col, key_row = pair_keys[:, :, None], pair_keys[:, None, :]
    spread = (
        (place[:, None] % window_area == jnp.arange(window_area, dtype=jnp.int32)[None, :])
        & (place[:, None] < pair_area)
    ).astype(jnp.float32)
    dense_bias = jnp.einsum(
        "hti,ui->htu",
        jnp.einsum("ti,hij->htj", spread, rel_bias, precision=PRECISE),
        spread,
        precision=PRECISE,
    )

    def to_pairs(tensor):
        shaped = tensor.reshape(-1, pair_area, tensor.shape[-1])
        return jnp.pad(shaped, ((0, 0), (0, PAIR - pair_area), (0, 0)))

    def from_pairs(tensor):
        return tensor[:, :pair_area].reshape(-1, tensor.shape[-1])

    mixed_pairs = to_pairs(mixed)
    attended_pairs, log_total = attention_fwd(mixed_pairs, dense_bias, key_col, key_row, score_scale)
    attended = from_pairs(attended_pairs)
    hidden, act_two, gelu_low, output_flat, stat_block = mlp_fwd(
        attended, residual, valid, w_proj, gain_two, offset_two, w_fc1, w_fc2
    )
    stat_terms = jnp.stack([stat_block[0, 0], stat_block[0, 1], jnp.sum(valid) * features])
    output_low = output_flat.reshape(window_count, window_area, features)
    restored = retreat(from_windows(output_low, canvases, quad_side, quad_cols))
    flat_out = restored.reshape(canvases, quarters, share_rows, features)
    arrived = lax.all_to_all(flat_out, ("qy", "qx"), 1, 1, tiled=True)
    merged = jnp.take(arrived, merge_order, axis=1, mode="clip").transpose(0, 2, 1, 3).reshape(
        canvases, share_rows, quarters * features
    )
    quarter_ids = jnp.arange(quarters, dtype=jnp.int32)
    source_pick = jnp.sum(
        quarter_ids[:, None] * (merge_order[:, None] == quarter_ids[None, :]).astype(jnp.int32), 0
    )
    incoming = merged_grad.reshape(canvases, share_rows, quarters, features)
    unordered = jnp.take(incoming, source_pick, axis=2, mode="clip").transpose(0, 2, 1, 3)
    returned = lax.all_to_all(unordered, ("qy", "qx"), 1, 1, tiled=True)
    grad_orig = returned.reshape(canvases, quad_side, quad_cols, features)
    grad_out = to_windows(advance(grad_orig)).reshape(-1, features)
    grad_pre, grad_hidden, grad_branch, grad_attended, small_two = mlp_bwd(
        grad_out, hidden, act_two, gain_two, w_fc1, w_fc2, w_proj
    )
    grad_fc2 = jnp.einsum("rf,rc->fc", gelu_low, grad_out, preferred_element_type=jnp.float32)
    grad_fc1 = jnp.einsum("rc,rf->cf", act_two, grad_pre, preferred_element_type=jnp.float32)
    grad_proj = jnp.einsum("rc,rd->cd", attended, grad_branch, preferred_element_type=jnp.float32)
    grad_mixed_pairs, dense_grad_bias = attention_bwd(
        mixed_pairs, to_pairs(grad_attended), log_total, dense_bias, key_col, key_row, score_scale
    )
    grad_mixed = from_pairs(grad_mixed_pairs)
    grad_bias = jnp.einsum(
        "ti,htj->hij",
        spread,
        jnp.einsum("htu,uj->htj", dense_grad_bias, spread, precision=PRECISE),
        precision=PRECISE,
    )
    grad_table = jnp.dot(grad_bias.reshape(HEADS, -1), onehot, precision=PRECISE)
    grad_qkv = jnp.einsum("rc,rf->cf", act_one, grad_mixed, preferred_element_type=jnp.float32)
    grad_act_one = jnp.einsum("rf,cf->rc", grad_mixed, w_qkv, preferred_element_type=jnp.float32)
    grad_input = grad_hidden + norm_back(grad_act_one, normed_one, inverse_one, gain_one)
    grad_low = grad_input.astype(jnp.bfloat16).reshape(window_count, window_area, features)
    grad_tokens = retreat(from_windows(grad_low, canvases, quad_side, quad_cols))
    small_local = jnp.concatenate(
        [
            jnp.sum(grad_act_one * normed_one, 0),
            jnp.sum(grad_act_one, 0),
            small_two[0],
            small_two[1],
            grad_table.reshape(-1),
        ]
    )
    every_block = jnp.concatenate(
        [lane_blocks(grad_qkv), lane_blocks(grad_proj), lane_blocks(grad_fc1), lane_blocks(grad_fc2)],
        0,
    )
    depth = every_block.shape[1] // PARTS
    parted = [
        jnp.take(every_block[:, index * depth : (index + 1) * depth], owner_list, axis=0, mode="clip")
        for index in range(PARTS)
    ]
    owned_grads, small_all = reduce_to_owners(parted, jnp.concatenate([small_local, stat_terms]))
    small_total = small_all[: small_local.shape[0]]
    stat_total = small_all[small_local.shape[0] :]
    new_first, new_second, new_master = rotate_update(
        owned_grads, master_blocks, first_moment, second_moment, basis_left, basis_right
    )
    small_first_new, small_second_new, small_new = small_update(
        small_total, small_params, small_first, small_second
    )
    stats = jnp.stack(
        [jnp.sqrt(stat_total[0] / stat_total[2]), jnp.sqrt(stat_total[1] / (2.0 * stat_total[2]))]
    )
    return (
        merged,
        grad_tokens,
        owned_grads,
        new_master,
        new_first,
        new_second,
        new_master.astype(jnp.bfloat16),
        small_total,
        small_first_new,
        small_second_new,
        small_new,
        stats,
    )


def solution(mesh):
    placed = (
        P("dp", "qy", "qx", None),
        P("dp", None, None),
        P(),
        P(),
        P(),
        P(),
        P(),
        P(),
        P(),
        P(),
        P(),
        P("dp", None, None),
        P("dp", None, None),
        P("dp", None, None),
        P("dp", None, None),
        P("dp", None, None),
        P("dp", ("qy", "qx"), None),
    )
    return jax.shard_map(
        local,
        mesh=mesh,
        in_specs=placed,
        out_specs=(
            P("dp", ("qy", "qx"), None),
            P("dp", "qy", "qx", None),
            P("dp", None, None),
            P("dp", None, None),
            P("dp", None, None),
            P("dp", None, None),
            P("dp", None, None),
            P(),
            P(),
            P(),
            P(),
            P(),
        ),
        check_vma=False,
    )
```

```python
import functools
from functools import partial

import numpy as np

import jax
import jax.numpy as jnp
from jax import lax
from jax.experimental import pallas as pl
from jax.experimental.pallas import tpu as pltpu
from jax.sharding import PartitionSpec as P

HEADS = 12
WIN = 7
SHIFT = 3
BLK = 96


BETA_ONE = 0.5
BETA_TWO = 0.6
ADAM_EPSILON = 1e-08
RATE_BLOCKS = 0.04
RATE_SMALL = 0.2
MASK_FILL = -1e30
NORM_EPSILON = 1e-05
PRECISE = lax.Precision.HIGHEST


def passed_along(value, axis, steps):
    count = lax.axis_size(axis)
    pairs = [(source, (source + steps) % count) for source in range(count)]
    return lax.ppermute(value, axis, pairs)


def partner_of(value, axis, mask):
    count = lax.axis_size(axis)
    pairs = [(source, source ^ mask) for source in range(count)]
    return lax.ppermute(value, axis, pairs)


def bit_of(axis, mask):
    return ((lax.axis_index(axis) & mask) != 0).astype(jnp.int32)


LANES = 128
PARTS = 3
GROUP = 4
LANES = 128
MASK_FILL = -1e30
PAIR = 112


def _stacked(value, lane4):
    wide = jnp.broadcast_to(value.astype(jnp.float32)[None], (GROUP, PAIR, LANES))
    return jnp.where(lane4, wide, 0.0).reshape(GROUP * PAIR, LANES).astype(jnp.bfloat16)


def _gather_lanes(stack, lane4):
    return jnp.sum(jnp.where(lane4, stack.reshape(GROUP, PAIR, LANES), 0.0), 0)


def _scores(q4, k4, bias4, allowed, scale, lane4):
    raw = lax.dot_general(_stacked(q4, lane4), k4, (((1,), (1,)), ((), ())), preferred_element_type=jnp.float32)
    raw = raw.reshape(GROUP, PAIR, PAIR) * scale + bias4
    return jnp.where(allowed[None], raw, MASK_FILL)


def _lane_masks():
    lane4 = lax.broadcasted_iota(jnp.int32, (GROUP, 1, LANES), 2) // 32 == lax.broadcasted_iota(
        jnp.int32, (GROUP, 1, LANES), 0)
    return lane4, lax.broadcasted_iota(jnp.int32, (1, LANES), 1)


def _fwd_kernel(mix_ref, bias_ref, kc_ref, kr_ref, out_ref, lse_ref, *, scale):
    width = HEADS * 32
    lane4, head_lane = _lane_masks()
    allowed = kc_ref[0] == kr_ref[0]
    lse_all = jnp.zeros((PAIR, LANES), jnp.float32)
    for g in range(HEADS // GROUP):
        q4 = mix_ref[0, :, pl.ds(g * LANES, LANES)]
        k4 = mix_ref[0, :, pl.ds(width + g * LANES, LANES)]
        v4 = mix_ref[0, :, pl.ds(2 * width + g * LANES, LANES)]
        s = _scores(q4, k4, bias_ref[pl.ds(g * GROUP, GROUP)], allowed, scale, lane4)
        top = jnp.max(s, -1, keepdims=True)
        e = jnp.exp(s - top)
        total = jnp.sum(e, -1, keepdims=True)
        probs = (e / total).reshape(GROUP * PAIR, PAIR).astype(jnp.bfloat16)
        mixed_out = jnp.dot(probs, v4, preferred_element_type=jnp.float32)
        out_ref[0, :, pl.ds(g * LANES, LANES)] = _gather_lanes(mixed_out, lane4).astype(out_ref.dtype)
        lse = top + jnp.log(total)
        for j in range(GROUP):
            lse_all = jnp.where(head_lane == g * GROUP + j, lse[j], lse_all)
    lse_ref[0] = lse_all


def _bwd_kernel(mix_ref, grad_ref, lse_ref, bias_ref, kc_ref, kr_ref, gmix_ref, dbias_ref, *, scale):
    width = HEADS * 32
    lane4, head_lane = _lane_masks()
    step = pl.program_id(0)
    allowed = kc_ref[0] == kr_ref[0]
    lse_all = lse_ref[0]

    @pl.when(step == 0)
    def _():
        dbias_ref[...] = jnp.zeros_like(dbias_ref)

    for g in range(HEADS // GROUP):
        q4 = mix_ref[0, :, pl.ds(g * LANES, LANES)]
        k4 = mix_ref[0, :, pl.ds(width + g * LANES, LANES)]
        v4 = mix_ref[0, :, pl.ds(2 * width + g * LANES, LANES)]
        d4 = grad_ref[0, :, pl.ds(g * LANES, LANES)]
        heads = pl.ds(g * GROUP, GROUP)
        s = _scores(q4, k4, bias_ref[heads], allowed, scale, lane4)
        lse = jnp.stack([
            jnp.sum(jnp.where(head_lane == g * GROUP + j, lse_all, 0.0), -1, keepdims=True)
            for j in range(GROUP)
        ])
        probs = jnp.exp(s - lse)
        d_stack = _stacked(d4, lane4)
        dprobs = lax.dot_general(d_stack, v4, (((1,), (1,)), ((), ())), preferred_element_type=jnp.float32)
        dprobs = dprobs.reshape(GROUP, PAIR, PAIR)
        inner = jnp.sum(probs * dprobs, -1, keepdims=True)
        dscores = (probs * (dprobs - inner)).reshape(GROUP * PAIR, PAIR).astype(jnp.bfloat16)
        dbias_ref[heads] = dbias_ref[heads] + dscores.astype(jnp.float32).reshape(GROUP, PAIR, PAIR)
        gq = _gather_lanes(jnp.dot(dscores, k4, preferred_element_type=jnp.float32), lane4)
        gk = lax.dot_general(dscores, _stacked(q4, lane4), (((0,), (0,)), ((), ())), preferred_element_type=jnp.float32)
        gv = lax.dot_general(probs.reshape(GROUP * PAIR, PAIR).astype(jnp.bfloat16), d_stack,
                             (((0,), (0,)), ((), ())), preferred_element_type=jnp.float32)
        gmix_ref[0, :, pl.ds(g * LANES, LANES)] = (gq * scale).astype(gmix_ref.dtype)
        gmix_ref[0, :, pl.ds(width + g * LANES, LANES)] = (gk * scale).astype(gmix_ref.dtype)
        gmix_ref[0, :, pl.ds(2 * width + g * LANES, LANES)] = gv.astype(gmix_ref.dtype)


def _pair_spec(width):
    return pl.BlockSpec((1, PAIR, width), lambda p: (p, 0, 0))


def attention_fwd(mixed_pairs, bias, key_col, key_row, scale):
    pairs = mixed_pairs.shape[0]
    kernel = functools.partial(_fwd_kernel, scale=scale)
    return pl.pallas_call(
        kernel,
        grid=(pairs,),
        out_shape=(
            jax.ShapeDtypeStruct((pairs, PAIR, HEADS * 32), jnp.bfloat16),
            jax.ShapeDtypeStruct((pairs, PAIR, LANES), jnp.float32),
        ),
        in_specs=[_pair_spec(mixed_pairs.shape[2]), pl.BlockSpec(bias.shape, lambda p: (0, 0, 0)),
                  pl.BlockSpec((1, PAIR, 1), lambda p: (p, 0, 0)), pl.BlockSpec((1, 1, PAIR), lambda p: (p, 0, 0))],
        out_specs=(_pair_spec(HEADS * 32), _pair_spec(LANES)),
        compiler_params=pltpu.CompilerParams(dimension_semantics=("arbitrary",), vmem_limit_bytes=32 * 1024 * 1024),
    )(mixed_pairs, bias, key_col, key_row)


def attention_bwd(mixed_pairs, grad_pairs, lse, bias, key_col, key_row, scale):
    pairs = mixed_pairs.shape[0]
    kernel = functools.partial(_bwd_kernel, scale=scale)
    return pl.pallas_call(
        kernel,
        grid=(pairs,),
        out_shape=(
            jax.ShapeDtypeStruct(mixed_pairs.shape, jnp.bfloat16),
            jax.ShapeDtypeStruct(bias.shape, jnp.float32),
        ),
        in_specs=[_pair_spec(mixed_pairs.shape[2]), _pair_spec(HEADS * 32), _pair_spec(LANES),
                  pl.BlockSpec(bias.shape, lambda p: (0, 0, 0)),
                  pl.BlockSpec((1, PAIR, 1), lambda p: (p, 0, 0)), pl.BlockSpec((1, 1, PAIR), lambda p: (p, 0, 0))],
        out_specs=(_pair_spec(mixed_pairs.shape[2]), pl.BlockSpec(bias.shape, lambda p: (0, 0, 0))),
        compiler_params=pltpu.CompilerParams(dimension_semantics=("arbitrary",), vmem_limit_bytes=32 * 1024 * 1024),
    )(mixed_pairs, grad_pairs, lse, bias, key_col, key_row)


def lane_blocks(matrix):
    row_blocks, col_blocks = matrix.shape[0] // BLK, matrix.shape[1] // BLK
    shaped = matrix.reshape(row_blocks, BLK, col_blocks, BLK).transpose(0, 2, 1, 3)
    return shaped.reshape(row_blocks * col_blocks, BLK * BLK // LANES, LANES)


ROWS = 112
SQRT_HALF = float(np.sqrt(0.5))
INV_SQRT_TAU = float(1.0 / np.sqrt(2.0 * np.pi))


def _norm(tensor):
    center = tensor - jnp.mean(tensor, -1, keepdims=True)
    inverse = lax.rsqrt(jnp.mean(center * center, -1, keepdims=True) + NORM_EPSILON)
    return center * inverse, inverse


def _mlp_fwd_kernel(att_ref, res_ref, valid_ref, wp_ref, gain_ref, off_ref, w1_ref, w2_ref,
                    hid_ref, act_ref, gelu_ref, out_ref, stat_ref):
    step = pl.program_id(0)
    branch_one = jnp.dot(att_ref[...], wp_ref[...], preferred_element_type=jnp.float32)
    hidden = res_ref[...] + branch_one
    normed, _ = _norm(hidden)
    act = (normed * gain_ref[...] + off_ref[...]).astype(jnp.bfloat16)
    pre = jnp.dot(act, w1_ref[...], preferred_element_type=jnp.float32)
    gelu = ((0.5 * pre) * (1.0 + lax.erf(pre * SQRT_HALF))).astype(jnp.bfloat16)
    branch_two = jnp.dot(gelu, w2_ref[...], preferred_element_type=jnp.float32)
    output = hidden + branch_two
    valid = valid_ref[...]
    first = jnp.sum(valid * output * output)
    second = jnp.sum(valid * (branch_one * branch_one + branch_two * branch_two))
    lane = lax.broadcasted_iota(jnp.int32, (8, 128), 1)
    row = lax.broadcasted_iota(jnp.int32, (8, 128), 0)
    here = jnp.where((row == 0) & (lane == 0), first, 0.0) + jnp.where((row == 0) & (lane == 1), second, 0.0)

    @pl.when(step == 0)
    def _():
        stat_ref[...] = jnp.zeros_like(stat_ref)

    stat_ref[...] = stat_ref[...] + here
    hid_ref[...] = hidden
    act_ref[...] = act
    gelu_ref[...] = gelu
    out_ref[...] = output.astype(out_ref.dtype)


def _mlp_bwd_kernel(gout_ref, hid_ref, act_ref, gain_ref, w1_ref, w2_ref, wp_ref,
                    gpre_ref, ghid_ref, gbr_ref, gatt_ref, small_ref):
    step = pl.program_id(0)
    contract_last = (((1,), (1,)), ((), ()))
    pre = jnp.dot(act_ref[...], w1_ref[...], preferred_element_type=jnp.float32)
    grad_out = gout_ref[...]
    grad_gelu = lax.dot_general(grad_out, w2_ref[...], contract_last, preferred_element_type=jnp.float32)
    cdf = 0.5 * (1.0 + lax.erf(pre * SQRT_HALF))
    pdf = jnp.exp(-0.5 * pre * pre) * INV_SQRT_TAU
    grad_pre = (grad_gelu * (cdf + pre * pdf)).astype(jnp.bfloat16)
    grad_act = lax.dot_general(grad_pre, w1_ref[...], contract_last, preferred_element_type=jnp.float32)
    normed, inverse = _norm(hid_ref[...])
    scaled = grad_act * gain_ref[...]
    mean_one = jnp.mean(scaled, -1, keepdims=True)
    mean_two = jnp.mean(scaled * normed, -1, keepdims=True)
    grad_hidden = grad_out.astype(jnp.float32) + inverse * (scaled - mean_one - normed * mean_two)
    grad_branch = grad_hidden.astype(jnp.bfloat16)
    grad_att = lax.dot_general(grad_branch, wp_ref[...], contract_last, preferred_element_type=jnp.float32)
    sums = jnp.concatenate(
        [jnp.sum(grad_act * normed, 0, keepdims=True), jnp.sum(grad_act, 0, keepdims=True),
         jnp.zeros((6, grad_act.shape[1]), jnp.float32)], 0)

    @pl.when(step == 0)
    def _():
        small_ref[...] = jnp.zeros_like(small_ref)

    small_ref[...] = small_ref[...] + sums
    gpre_ref[...] = grad_pre
    ghid_ref[...] = grad_hidden
    gbr_ref[...] = grad_branch
    gatt_ref[...] = grad_att.astype(gatt_ref.dtype)


def _rows(width):
    return pl.BlockSpec((ROWS, width), lambda i: (i, 0))


def _whole(shape):
    return pl.BlockSpec(shape, lambda i: (0,) * len(shape))


def mlp_fwd(attended, residual, valid, w_proj, gain, offset, w_fc1, w_fc2):
    tokens, width = residual.shape
    hidden_width = w_fc1.shape[1]
    return pl.pallas_call(
        _mlp_fwd_kernel,
        grid=(tokens // ROWS,),
        out_shape=(
            jax.ShapeDtypeStruct((tokens, width), jnp.float32),
            jax.ShapeDtypeStruct((tokens, width), jnp.bfloat16),
            jax.ShapeDtypeStruct((tokens, hidden_width), jnp.bfloat16),
            jax.ShapeDtypeStruct((tokens, width), jnp.bfloat16),
            jax.ShapeDtypeStruct((8, 128), jnp.float32),
        ),
        in_specs=[_rows(width), _rows(width), _rows(1), _whole(w_proj.shape), _whole((1, width)),
                  _whole((1, width)), _whole(w_fc1.shape), _whole(w_fc2.shape)],
        out_specs=(_rows(width), _rows(width), _rows(hidden_width), _rows(width), _whole((8, 128))),
        compiler_params=pltpu.CompilerParams(dimension_semantics=("arbitrary",), vmem_limit_bytes=48 * 1024 * 1024),
    )(attended, residual, valid, w_proj, gain.reshape(1, -1), offset.reshape(1, -1), w_fc1, w_fc2)


def mlp_bwd(grad_out, hidden, act_two, gain, w_fc1, w_fc2, w_proj):
    tokens, width = hidden.shape
    hidden_width = w_fc1.shape[1]
    return pl.pallas_call(
        _mlp_bwd_kernel,
        grid=(tokens // ROWS,),
        out_shape=(
            jax.ShapeDtypeStruct((tokens, hidden_width), jnp.bfloat16),
            jax.ShapeDtypeStruct((tokens, width), jnp.float32),
            jax.ShapeDtypeStruct((tokens, width), jnp.bfloat16),
            jax.ShapeDtypeStruct((tokens, width), jnp.bfloat16),
            jax.ShapeDtypeStruct((8, width), jnp.float32),
        ),
        in_specs=[_rows(width), _rows(width), _rows(width), _whole((1, width)), _whole(w_fc1.shape),
                  _whole(w_fc2.shape), _whole(w_proj.shape)],
        out_specs=(_rows(hidden_width), _rows(width), _rows(width), _rows(width), _whole((8, width))),
        compiler_params=pltpu.CompilerParams(dimension_semantics=("arbitrary",), vmem_limit_bytes=48 * 1024 * 1024),
    )(grad_out, hidden, act_two, gain.reshape(1, -1), w_fc1, w_fc2, w_proj)


def reduce_to_owners(parted, small):
    groups = lax.axis_size("dp")
    dp_bits = groups.bit_length() - 1
    n_qy, n_qx = lax.axis_size("qy"), lax.axis_size("qx")
    count, depth = parted[0].shape[0], parted[0].shape[1]
    per_group = count // groups
    names = [("dp", 1 << power) for power in reversed(range(dp_bits))] + [("qy", 1), ("qx", 1)]
    cross = [("qy", 1)] + [("dp", 1 << power) for power in range(dp_bits)]
    pieces, piece_names, orders = [], [], []
    for index, part in enumerate(parted):
        pieces.append(
            part.reshape([2] * dp_bits + [n_qy, n_qx, per_group * depth // (n_qy * n_qx), LANES])
        )
        piece_names.append(list(names))
        turn = index % len(cross)
        orders.append([("qx", 1)] + cross[turn:] + cross[:turn])
    for stage in range(len(names)):
        for index in range(len(pieces)):
            bit = orders[index][stage]
            place = piece_names[index].index(bit)
            mine = bit_of(*bit)
            keep = lax.dynamic_index_in_dim(pieces[index], mine, place, keepdims=False)
            send = lax.dynamic_index_in_dim(pieces[index], 1 - mine, place, keepdims=False)
            piece_names[index].remove(bit)
            arrived = partner_of(send.astype(jnp.bfloat16), *bit)
            pieces[index] = keep + arrived.astype(jnp.float32)
            if index == 0:
                small = small + partner_of(small, *bit)
                pieces[0], small = lax.optimization_barrier((pieces[0], small))
    chunk = jnp.stack(pieces)
    other = partner_of(chunk, "qy", 1)
    pair = jnp.where(bit_of("qy", 1) == 1, jnp.stack([other, chunk], 1), jnp.stack([chunk, other], 1))
    other = partner_of(pair, "qx", 1)
    quad = jnp.where(bit_of("qx", 1) == 1, jnp.stack([other, pair], 2), jnp.stack([pair, other], 2))
    quad = quad.reshape(len(pieces), per_group, depth, LANES).transpose(1, 0, 2, 3)
    return quad.reshape(per_group, BLK, BLK), small


def cut_along(value, dim, devices):
    before, after = (value.shape[:dim], value.shape[dim + 1 :])
    return jnp.moveaxis(value.reshape(*before, devices, -1, *after), dim, 0)


def sent_and_summed(value, axis, dim):
    pieces = cut_along(value, dim, lax.axis_size(axis))
    arrived = lax.all_to_all(pieces, axis, split_axis=0, concat_axis=0, tiled=True)
    return arrived.astype(jnp.float32).sum(axis=0)


def norm_stats(tensor):
    center = tensor - jnp.mean(tensor, -1, keepdims=True)
    inverse = lax.rsqrt(jnp.mean(center * center, -1, keepdims=True) + NORM_EPSILON)
    return (center * inverse, inverse)


def norm_back(grad_act, normed, inverse, gain):
    scaled = grad_act * gain
    mean_one = jnp.mean(scaled, -1, keepdims=True)
    mean_two = jnp.mean(scaled * normed, -1, keepdims=True)
    return inverse * (scaled - mean_one - normed * mean_two)


def to_windows(tensor):
    canvases, rows_side, cols_side, channels = tensor.shape
    shaped = tensor.reshape(canvases, rows_side // WIN, WIN, cols_side // WIN, WIN, channels)
    return shaped.transpose(0, 1, 3, 2, 4, 5).reshape(
        canvases * (rows_side // WIN) * (cols_side // WIN), WIN * WIN, channels
    )


def from_windows(tensor, canvases, rows_side, cols_side):
    channels = tensor.shape[-1]
    shaped = tensor.reshape(canvases, rows_side // WIN, cols_side // WIN, WIN, WIN, channels)
    return shaped.transpose(0, 1, 3, 2, 4, 5).reshape(canvases, rows_side, cols_side, channels)


def relative_index():
    places = jnp.arange(WIN * WIN, dtype=jnp.int32)
    row_of = places // WIN
    col_of = places % WIN
    return (row_of[:, None] - row_of[None, :] + WIN - 1) * (2 * WIN - 1) + (
        col_of[:, None] - col_of[None, :] + WIN - 1
    )


def region_of(places, full):
    return jnp.where(places < full - WIN, 0, jnp.where(places < full - SHIFT, 1, 2)).astype(
        jnp.int32
    )


def advance(tensor):
    upper = passed_along(tensor[:, :SHIFT], "qy", -1)
    tensor = jnp.concatenate([tensor[:, SHIFT:], upper], 1)
    leftmost = passed_along(tensor[:, :, :SHIFT], "qx", -1)
    return jnp.concatenate([tensor[:, :, SHIFT:], leftmost], 2)


def retreat(tensor):
    lowest = passed_along(tensor[:, -SHIFT:], "qy", 1)
    tensor = jnp.concatenate([lowest, tensor[:, :-SHIFT]], 1)
    rightmost = passed_along(tensor[:, :, -SHIFT:], "qx", 1)
    return jnp.concatenate([rightmost, tensor[:, :, :-SHIFT]], 2)


def blocks_of(matrix):
    row_blocks = matrix.shape[0] // BLK
    col_blocks = matrix.shape[1] // BLK
    return (
        matrix.reshape(row_blocks, BLK, col_blocks, BLK)
        .transpose(0, 2, 1, 3)
        .reshape(row_blocks * col_blocks, BLK, BLK)
    )


def rotate_update(grads, master, first, second, left, right):
    turned = jnp.einsum("sji,sjk->sik", left, grads, precision=PRECISE)
    turned = jnp.einsum("sik,skl->sil", turned, right, precision=PRECISE)
    new_first = BETA_ONE * first + (1.0 - BETA_ONE) * turned
    new_second = BETA_TWO * second + (1.0 - BETA_TWO) * turned * turned
    direction = new_first / (jnp.sqrt(new_second) + ADAM_EPSILON)
    back = jnp.einsum("sij,sjk->sik", left, direction, precision=PRECISE)
    back = jnp.einsum("sik,slk->sil", back, right, precision=PRECISE)
    return (new_first, new_second, master - RATE_BLOCKS * back)


def small_update(grads, params, first, second):
    new_first = BETA_ONE * first + (1.0 - BETA_ONE) * grads
    new_second = BETA_TWO * second + (1.0 - BETA_TWO) * grads * grads
    direction = new_first / (jnp.sqrt(new_second) + ADAM_EPSILON)
    return (new_first, new_second, params - RATE_SMALL * direction)


def local(
    tokens,
    crop_ids,
    merge_order,
    owner_list,
    w_qkv,
    w_proj,
    w_fc1,
    w_fc2,
    small_params,
    small_first,
    small_second,
    master_blocks,
    first_moment,
    second_moment,
    basis_left,
    basis_right,
    merged_grad,
):
    canvases, quad_side, quad_cols, features = tokens.shape
    head_dim = features // HEADS
    score_scale = head_dim ** (-0.5)
    window_area = WIN * WIN
    quarters = lax.axis_size(("qy", "qx"))
    share_rows = quad_side * quad_cols // quarters
    row_base = lax.axis_index("qy") * quad_side
    col_base = lax.axis_index("qx") * quad_cols
    rolled = jnp.roll(crop_ids, (-SHIFT, -SHIFT), (1, 2))
    local_ids = lax.dynamic_slice(
        rolled, (jnp.int32(0), row_base, col_base), (canvases, quad_side, quad_cols)
    )
    region_row = region_of(
        row_base + jnp.arange(quad_side, dtype=jnp.int32), quad_side * lax.axis_size("qy")
    )
    region_col = region_of(
        col_base + jnp.arange(quad_cols, dtype=jnp.int32), quad_cols * lax.axis_size("qx")
    )
    labels = (local_ids + 1) * 9 + region_row[None, :, None] * 3 + region_col[None, None, :]
    win_labels = to_windows(labels[..., None])[..., 0]
    window_count = win_labels.shape[0]
    gain_one = small_params[0:features]
    offset_one = small_params[features : 2 * features]
    gain_two = small_params[2 * features : 3 * features]
    offset_two = small_params[3 * features : 4 * features]
    table = small_params[4 * features :].reshape(HEADS, -1)
    onehot = (
        relative_index().reshape(-1)[:, None]
        == jnp.arange(table.shape[1], dtype=jnp.int32)[None, :]
    ).astype(jnp.float32)
    rel_bias = jnp.einsum("hr,pr->hp", table, onehot, precision=PRECISE).reshape(
        HEADS, window_area, window_area
    )

    pair_area = 2 * window_area
    place = jnp.arange(PAIR, dtype=jnp.int32)
    pair_labels = jnp.pad(win_labels.reshape(-1, pair_area), ((0, 0), (0, PAIR - pair_area)))
    pair_keys = jnp.where(
        place[None] < pair_area,
        pair_labels * 2 + (place[None] >= window_area).astype(jnp.int32),
        -1 - place[None],
    )
    key_col, key_row = pair_keys[:, :, None], pair_keys[:, None, :]
    valid = (pair_labels >= 9).reshape(-1).astype(jnp.float32)[:, None]
    spread = (
        (place[:, None] % window_area == jnp.arange(window_area, dtype=jnp.int32)[None, :])
        & (place[:, None] < pair_area)
    ).astype(jnp.float32)
    dense_bias = jnp.einsum(
        "hti,ui->htu",
        jnp.einsum("ti,hij->htj", spread, rel_bias, precision=PRECISE),
        spread,
        precision=PRECISE,
    )

    def to_pairs(tensor):
        shaped = tensor.reshape(-1, pair_area, tensor.shape[-1])
        return jnp.pad(shaped, ((0, 0), (0, PAIR - pair_area), (0, 0))).reshape(-1, tensor.shape[-1])

    def from_pairs(tensor):
        shaped = tensor.reshape(-1, PAIR, tensor.shape[-1])
        return shaped[:, :pair_area].reshape(-1, window_area, tensor.shape[-1])

    residual = to_pairs(to_windows(advance(tokens)).astype(jnp.float32))
    normed_one, inverse_one = norm_stats(residual)
    act_one = (normed_one * gain_one + offset_one).astype(jnp.bfloat16)
    mixed = jnp.dot(act_one, w_qkv, preferred_element_type=jnp.float32).astype(jnp.bfloat16)
    mixed_pairs = mixed.reshape(-1, PAIR, mixed.shape[-1])
    attended_pairs, log_total = attention_fwd(mixed_pairs, dense_bias, key_col, key_row, score_scale)
    attended = attended_pairs.reshape(-1, features)
    hidden, act_two, gelu_low, output_flat, stat_block = mlp_fwd(
        attended, residual, valid, w_proj, gain_two, offset_two, w_fc1, w_fc2
    )
    stat_terms = jnp.stack([stat_block[0, 0], stat_block[0, 1], jnp.sum(valid) * features])
    output_low = from_pairs(output_flat)
    restored = retreat(from_windows(output_low, canvases, quad_side, quad_cols))
    flat_out = restored.reshape(canvases, quarters, share_rows, features)
    arrived = lax.all_to_all(flat_out, ("qy", "qx"), 1, 1, tiled=True)
    merged = jnp.take(arrived, merge_order, axis=1, mode="clip").transpose(0, 2, 1, 3).reshape(
        canvases, share_rows, quarters * features
    )
    quarter_ids = jnp.arange(quarters, dtype=jnp.int32)
    source_pick = jnp.sum(
        quarter_ids[:, None] * (merge_order[:, None] == quarter_ids[None, :]).astype(jnp.int32), 0
    )
    incoming = merged_grad.reshape(canvases, share_rows, quarters, features)
    unordered = jnp.take(incoming, source_pick, axis=2, mode="clip").transpose(0, 2, 1, 3)
    returned = lax.all_to_all(unordered, ("qy", "qx"), 1, 1, tiled=True)
    grad_orig = returned.reshape(canvases, quad_side, quad_cols, features)
    grad_out = to_pairs(to_windows(advance(grad_orig)))
    grad_pre, grad_hidden, grad_branch, grad_attended, small_two = mlp_bwd(
        grad_out, hidden, act_two, gain_two, w_fc1, w_fc2, w_proj
    )
    grad_fc2 = jnp.einsum("rf,rc->fc", gelu_low, grad_out, preferred_element_type=jnp.float32)
    grad_fc1 = jnp.einsum("rc,rf->cf", act_two, grad_pre, preferred_element_type=jnp.float32)
    grad_proj = jnp.einsum("rc,rd->cd", attended, grad_branch, preferred_element_type=jnp.float32)
    grad_mixed_pairs, dense_grad_bias = attention_bwd(
        mixed_pairs, grad_attended.reshape(-1, PAIR, features), log_total, dense_bias, key_col, key_row, score_scale
    )
    grad_mixed = grad_mixed_pairs.reshape(-1, 3 * features)
    grad_bias = jnp.einsum(
        "ti,htj->hij",
        spread,
        jnp.einsum("htu,uj->htj", dense_grad_bias, spread, precision=PRECISE),
        precision=PRECISE,
    )
    grad_table = jnp.dot(grad_bias.reshape(HEADS, -1), onehot, precision=PRECISE)
    grad_qkv = jnp.einsum("rc,rf->cf", act_one, grad_mixed, preferred_element_type=jnp.float32)
    grad_act_one = jnp.einsum("rf,cf->rc", grad_mixed, w_qkv, preferred_element_type=jnp.float32)
    grad_input = grad_hidden + norm_back(grad_act_one, normed_one, inverse_one, gain_one)
    grad_low = from_pairs(grad_input.astype(jnp.bfloat16))
    grad_tokens = retreat(from_windows(grad_low, canvases, quad_side, quad_cols))
    small_local = jnp.concatenate(
        [
            jnp.sum(grad_act_one * normed_one, 0),
            jnp.sum(grad_act_one, 0),
            small_two[0],
            small_two[1],
            grad_table.reshape(-1),
        ]
    )
    every_block = jnp.concatenate(
        [lane_blocks(grad_qkv), lane_blocks(grad_proj), lane_blocks(grad_fc1), lane_blocks(grad_fc2)],
        0,
    )
    depth = every_block.shape[1] // PARTS
    parted = [
        jnp.take(every_block[:, index * depth : (index + 1) * depth], owner_list, axis=0, mode="clip")
        for index in range(PARTS)
    ]
    owned_grads, small_all = reduce_to_owners(parted, jnp.concatenate([small_local, stat_terms]))
    small_total = small_all[: small_local.shape[0]]
    stat_total = small_all[small_local.shape[0] :]
    new_first, new_second, new_master = rotate_update(
        owned_grads, master_blocks, first_moment, second_moment, basis_left, basis_right
    )
    small_first_new, small_second_new, small_new = small_update(
        small_total, small_params, small_first, small_second
    )
    stats = jnp.stack(
        [jnp.sqrt(stat_total[0] / stat_total[2]), jnp.sqrt(stat_total[1] / (2.0 * stat_total[2]))]
    )
    return (
        merged,
        grad_tokens,
        owned_grads,
        new_master,
        new_first,
        new_second,
        new_master.astype(jnp.bfloat16),
        small_total,
        small_first_new,
        small_second_new,
        small_new,
        stats,
    )


def solution(mesh):
    placed = (
        P("dp", "qy", "qx", None),
        P("dp", None, None),
        P(),
        P(),
        P(),
        P(),
        P(),
        P(),
        P(),
        P(),
        P(),
        P("dp", None, None),
        P("dp", None, None),
        P("dp", None, None),
        P("dp", None, None),
        P("dp", None, None),
        P("dp", ("qy", "qx"), None),
    )
    return jax.shard_map(
        local,
        mesh=mesh,
        in_specs=placed,
        out_specs=(
            P("dp", ("qy", "qx"), None),
            P("dp", "qy", "qx", None),
            P("dp", None, None),
            P("dp", None, None),
            P("dp", None, None),
            P("dp", None, None),
            P("dp", None, None),
            P(),
            P(),
            P(),
            P(),
            P(),
        ),
        check_vma=False,
    )
```

```python
import functools
from functools import partial

import numpy as np

import jax
import jax.numpy as jnp
from jax import lax
from jax.experimental import pallas as pl
from jax.experimental.pallas import tpu as pltpu
from jax.sharding import PartitionSpec as P

HEADS = 12
WIN = 7
SHIFT = 3
BLK = 96


BETA_ONE = 0.5
BETA_TWO = 0.6
ADAM_EPSILON = 1e-08
RATE_BLOCKS = 0.04
RATE_SMALL = 0.2
MASK_FILL = -1e30
NORM_EPSILON = 1e-05
PRECISE = lax.Precision.HIGHEST


def passed_along(value, axis, steps):
    count = lax.axis_size(axis)
    pairs = [(source, (source + steps) % count) for source in range(count)]
    return lax.ppermute(value, axis, pairs)


def partner_of(value, axis, mask):
    count = lax.axis_size(axis)
    pairs = [(source, source ^ mask) for source in range(count)]
    return lax.ppermute(value, axis, pairs)


def bit_of(axis, mask):
    return ((lax.axis_index(axis) & mask) != 0).astype(jnp.int32)


LANES = 128
PARTS = 3
GROUP = 4
LANES = 128
MASK_FILL = -1e30
PAIR = 112


def _stacked(value, lane4):
    wide = jnp.broadcast_to(value.astype(jnp.float32)[None], (GROUP, PAIR, LANES))
    return jnp.where(lane4, wide, 0.0).reshape(GROUP * PAIR, LANES).astype(jnp.bfloat16)


def _gather_lanes(stack, lane4):
    return jnp.sum(jnp.where(lane4, stack.reshape(GROUP, PAIR, LANES), 0.0), 0)


def _scores(q4, k4, bias4, allowed, scale, lane4):
    raw = lax.dot_general(_stacked(q4, lane4), k4, (((1,), (1,)), ((), ())), preferred_element_type=jnp.float32)
    raw = raw.reshape(GROUP, PAIR, PAIR) * scale + bias4
    return jnp.where(allowed[None], raw, MASK_FILL)


def _lane_masks():
    lane4 = lax.broadcasted_iota(jnp.int32, (GROUP, 1, LANES), 2) // 32 == lax.broadcasted_iota(
        jnp.int32, (GROUP, 1, LANES), 0)
    return lane4, lax.broadcasted_iota(jnp.int32, (1, LANES), 1)


def _fwd_kernel(mix_ref, bias_ref, kc_ref, kr_ref, out_ref, lse_ref, *, scale):
    width = HEADS * 32
    lane4, head_lane = _lane_masks()
    allowed = kc_ref[0] == kr_ref[0]
    lse_all = jnp.zeros((PAIR, LANES), jnp.float32)
    for g in range(HEADS // GROUP):
        q4 = mix_ref[0, :, pl.ds(g * LANES, LANES)]
        k4 = mix_ref[0, :, pl.ds(width + g * LANES, LANES)]
        v4 = mix_ref[0, :, pl.ds(2 * width + g * LANES, LANES)]
        s = _scores(q4, k4, bias_ref[pl.ds(g * GROUP, GROUP)], allowed, scale, lane4)
        top = jnp.max(s, -1, keepdims=True)
        e = jnp.exp(s - top)
        total = jnp.sum(e, -1, keepdims=True)
        probs = (e / total).reshape(GROUP * PAIR, PAIR).astype(jnp.bfloat16)
        mixed_out = jnp.dot(probs, v4, preferred_element_type=jnp.float32)
        out_ref[0, :, pl.ds(g * LANES, LANES)] = _gather_lanes(mixed_out, lane4).astype(out_ref.dtype)
        lse = top + jnp.log(total)
        for j in range(GROUP):
            lse_all = jnp.where(head_lane == g * GROUP + j, lse[j], lse_all)
    lse_ref[0] = lse_all


def _bwd_kernel(mix_ref, grad_ref, lse_ref, bias_ref, kc_ref, kr_ref, gmix_ref, dbias_ref, *, scale):
    width = HEADS * 32
    lane4, head_lane = _lane_masks()
    step = pl.program_id(0)
    allowed = kc_ref[0] == kr_ref[0]
    lse_all = lse_ref[0]

    @pl.when(step == 0)
    def _():
        dbias_ref[...] = jnp.zeros_like(dbias_ref)

    for g in range(HEADS // GROUP):
        q4 = mix_ref[0, :, pl.ds(g * LANES, LANES)]
        k4 = mix_ref[0, :, pl.ds(width + g * LANES, LANES)]
        v4 = mix_ref[0, :, pl.ds(2 * width + g * LANES, LANES)]
        d4 = grad_ref[0, :, pl.ds(g * LANES, LANES)]
        heads = pl.ds(g * GROUP, GROUP)
        s = _scores(q4, k4, bias_ref[heads], allowed, scale, lane4)
        lse = jnp.stack([
            jnp.sum(jnp.where(head_lane == g * GROUP + j, lse_all, 0.0), -1, keepdims=True)
            for j in range(GROUP)
        ])
        probs = jnp.exp(s - lse)
        d_stack = _stacked(d4, lane4)
        dprobs = lax.dot_general(d_stack, v4, (((1,), (1,)), ((), ())), preferred_element_type=jnp.float32)
        dprobs = dprobs.reshape(GROUP, PAIR, PAIR)
        inner = jnp.sum(probs * dprobs, -1, keepdims=True)
        dscores = (probs * (dprobs - inner)).reshape(GROUP * PAIR, PAIR).astype(jnp.bfloat16)
        dbias_ref[heads] = dbias_ref[heads] + dscores.astype(jnp.float32).reshape(GROUP, PAIR, PAIR)
        gq = _gather_lanes(jnp.dot(dscores, k4, preferred_element_type=jnp.float32), lane4)
        gk = lax.dot_general(dscores, _stacked(q4, lane4), (((0,), (0,)), ((), ())), preferred_element_type=jnp.float32)
        gv = lax.dot_general(probs.reshape(GROUP * PAIR, PAIR).astype(jnp.bfloat16), d_stack,
                             (((0,), (0,)), ((), ())), preferred_element_type=jnp.float32)
        gmix_ref[0, :, pl.ds(g * LANES, LANES)] = (gq * scale).astype(gmix_ref.dtype)
        gmix_ref[0, :, pl.ds(width + g * LANES, LANES)] = (gk * scale).astype(gmix_ref.dtype)
        gmix_ref[0, :, pl.ds(2 * width + g * LANES, LANES)] = gv.astype(gmix_ref.dtype)


def _pair_spec(width):
    return pl.BlockSpec((1, PAIR, width), lambda p: (p, 0, 0))


def attention_fwd(mixed_pairs, bias, key_col, key_row, scale):
    pairs = mixed_pairs.shape[0]
    kernel = functools.partial(_fwd_kernel, scale=scale)
    return pl.pallas_call(
        kernel,
        grid=(pairs,),
        out_shape=(
            jax.ShapeDtypeStruct((pairs, PAIR, HEADS * 32), jnp.bfloat16),
            jax.ShapeDtypeStruct((pairs, PAIR, LANES), jnp.float32),
        ),
        in_specs=[_pair_spec(mixed_pairs.shape[2]), pl.BlockSpec(bias.shape, lambda p: (0, 0, 0)),
                  pl.BlockSpec((1, PAIR, 1), lambda p: (p, 0, 0)), pl.BlockSpec((1, 1, PAIR), lambda p: (p, 0, 0))],
        out_specs=(_pair_spec(HEADS * 32), _pair_spec(LANES)),
        compiler_params=pltpu.CompilerParams(dimension_semantics=("arbitrary",), vmem_limit_bytes=32 * 1024 * 1024),
    )(mixed_pairs, bias, key_col, key_row)


def attention_bwd(mixed_pairs, grad_pairs, lse, bias, key_col, key_row, scale):
    pairs = mixed_pairs.shape[0]
    kernel = functools.partial(_bwd_kernel, scale=scale)
    return pl.pallas_call(
        kernel,
        grid=(pairs,),
        out_shape=(
            jax.ShapeDtypeStruct(mixed_pairs.shape, jnp.bfloat16),
            jax.ShapeDtypeStruct(bias.shape, jnp.float32),
        ),
        in_specs=[_pair_spec(mixed_pairs.shape[2]), _pair_spec(HEADS * 32), _pair_spec(LANES),
                  pl.BlockSpec(bias.shape, lambda p: (0, 0, 0)),
                  pl.BlockSpec((1, PAIR, 1), lambda p: (p, 0, 0)), pl.BlockSpec((1, 1, PAIR), lambda p: (p, 0, 0))],
        out_specs=(_pair_spec(mixed_pairs.shape[2]), pl.BlockSpec(bias.shape, lambda p: (0, 0, 0))),
        compiler_params=pltpu.CompilerParams(dimension_semantics=("arbitrary",), vmem_limit_bytes=32 * 1024 * 1024),
    )(mixed_pairs, grad_pairs, lse, bias, key_col, key_row)


def pair_row(side_r, side_c, r, c):
    per_row = side_c // WIN
    window = (r // WIN) * per_row + (c // WIN)
    inside = (r % WIN) * WIN + (c % WIN)
    return (window // 2) * PAIR + (window % 2) * WIN * WIN + inside


def gather_rows(source, index):
    return jnp.take(source, jnp.asarray(index, jnp.int32), axis=1, mode="clip")


def into_pairs(tensor):
    canvases, side_r, side_c, features = tensor.shape
    flat = tensor.reshape(canvases, side_r * side_c, features)
    below = passed_along(tensor[:, :SHIFT].reshape(canvases, SHIFT * side_c, features), "qy", -1)
    source = jnp.concatenate([flat, below], 1)
    def t_index(r, c):
        return np.where(r < side_r - SHIFT, (r + SHIFT) * side_c + c, side_r * side_c + (r - (side_r - SHIFT)) * side_c + c)
    rr, cc = np.meshgrid(np.arange(side_r), np.arange(SHIFT), indexing="ij")
    right = passed_along(gather_rows(source, t_index(rr, cc).reshape(-1)), "qx", -1)
    zero = jnp.zeros((canvases, 1, features), tensor.dtype)
    source = jnp.concatenate([source, right, zero], 1)
    base_right = side_r * side_c + SHIFT * side_c
    rr, cc = np.meshgrid(np.arange(side_r), np.arange(side_c), indexing="ij")
    want = np.where(cc < side_c - SHIFT, t_index(rr, np.minimum(cc + SHIFT, side_c - 1)),
                    base_right + rr * SHIFT + (cc - (side_c - SHIFT)))
    windows = (side_r // WIN) * (side_c // WIN)
    index = np.full(windows // 2 * PAIR, base_right + side_r * SHIFT, np.int64)
    index[pair_row(side_r, side_c, rr, cc).reshape(-1)] = want.reshape(-1)
    return gather_rows(source, index)


def out_of_pairs(pairs, side_r, side_c):
    canvases, _, features = pairs.shape
    rr, cc = np.meshgrid(np.arange(SHIFT), np.arange(side_c), indexing="ij")
    lowest = passed_along(gather_rows(pairs, pair_row(side_r, side_c, rr + side_r - SHIFT, cc).reshape(-1)), "qy", 1)
    rows = pairs.shape[1]
    source = jnp.concatenate([pairs, lowest], 1)
    def t_index(r, c):
        return np.where(r < SHIFT, rows + r * side_c + c, pair_row(side_r, side_c, np.maximum(r - SHIFT, 0), c))
    rr, cc = np.meshgrid(np.arange(side_r), np.arange(SHIFT), indexing="ij")
    rightmost = passed_along(gather_rows(source, t_index(rr, cc + side_c - SHIFT).reshape(-1)), "qx", 1)
    source = jnp.concatenate([source, rightmost], 1)
    base = rows + SHIFT * side_c
    rr, cc = np.meshgrid(np.arange(side_r), np.arange(side_c), indexing="ij")
    want = np.where(cc < SHIFT, base + rr * SHIFT + cc, t_index(rr, np.maximum(cc - SHIFT, 0)))
    return gather_rows(source, want.reshape(-1)).reshape(canvases, side_r, side_c, features)


def lane_blocks(matrix):
    row_blocks, col_blocks = matrix.shape[0] // BLK, matrix.shape[1] // BLK
    shaped = matrix.reshape(row_blocks, BLK, col_blocks, BLK).transpose(0, 2, 1, 3)
    return shaped.reshape(row_blocks * col_blocks, BLK * BLK // LANES, LANES)


ROWS = 112
SQRT_HALF = float(np.sqrt(0.5))
INV_SQRT_TAU = float(1.0 / np.sqrt(2.0 * np.pi))


def _norm(tensor):
    center = tensor - jnp.mean(tensor, -1, keepdims=True)
    inverse = lax.rsqrt(jnp.mean(center * center, -1, keepdims=True) + NORM_EPSILON)
    return center * inverse, inverse


def _mlp_fwd_kernel(att_ref, res_ref, valid_ref, wp_ref, gain_ref, off_ref, w1_ref, w2_ref,
                    hid_ref, act_ref, gelu_ref, out_ref, stat_ref):
    step = pl.program_id(0)
    branch_one = jnp.dot(att_ref[...], wp_ref[...], preferred_element_type=jnp.float32)
    hidden = res_ref[...] + branch_one
    normed, _ = _norm(hidden)
    act = (normed * gain_ref[...] + off_ref[...]).astype(jnp.bfloat16)
    pre = jnp.dot(act, w1_ref[...], preferred_element_type=jnp.float32)
    gelu = ((0.5 * pre) * (1.0 + lax.erf(pre * SQRT_HALF))).astype(jnp.bfloat16)
    branch_two = jnp.dot(gelu, w2_ref[...], preferred_element_type=jnp.float32)
    output = hidden + branch_two
    valid = valid_ref[...]
    first = jnp.sum(valid * output * output)
    second = jnp.sum(valid * (branch_one * branch_one + branch_two * branch_two))
    lane = lax.broadcasted_iota(jnp.int32, (8, 128), 1)
    row = lax.broadcasted_iota(jnp.int32, (8, 128), 0)
    here = jnp.where((row == 0) & (lane == 0), first, 0.0) + jnp.where((row == 0) & (lane == 1), second, 0.0)

    @pl.when(step == 0)
    def _():
        stat_ref[...] = jnp.zeros_like(stat_ref)

    stat_ref[...] = stat_ref[...] + here
    hid_ref[...] = hidden
    act_ref[...] = act
    gelu_ref[...] = gelu
    out_ref[...] = output.astype(out_ref.dtype)


def _mlp_bwd_kernel(gout_ref, hid_ref, act_ref, gain_ref, w1_ref, w2_ref, wp_ref,
                    gpre_ref, ghid_ref, gbr_ref, gatt_ref, small_ref):
    step = pl.program_id(0)
    contract_last = (((1,), (1,)), ((), ()))
    pre = jnp.dot(act_ref[...], w1_ref[...], preferred_element_type=jnp.float32)
    grad_out = gout_ref[...]
    grad_gelu = lax.dot_general(grad_out, w2_ref[...], contract_last, preferred_element_type=jnp.float32)
    cdf = 0.5 * (1.0 + lax.erf(pre * SQRT_HALF))
    pdf = jnp.exp(-0.5 * pre * pre) * INV_SQRT_TAU
    grad_pre = (grad_gelu * (cdf + pre * pdf)).astype(jnp.bfloat16)
    grad_act = lax.dot_general(grad_pre, w1_ref[...], contract_last, preferred_element_type=jnp.float32)
    normed, inverse = _norm(hid_ref[...])
    scaled = grad_act * gain_ref[...]
    mean_one = jnp.mean(scaled, -1, keepdims=True)
    mean_two = jnp.mean(scaled * normed, -1, keepdims=True)
    grad_hidden = grad_out.astype(jnp.float32) + inverse * (scaled - mean_one - normed * mean_two)
    grad_branch = grad_hidden.astype(jnp.bfloat16)
    grad_att = lax.dot_general(grad_branch, wp_ref[...], contract_last, preferred_element_type=jnp.float32)
    sums = jnp.concatenate(
        [jnp.sum(grad_act * normed, 0, keepdims=True), jnp.sum(grad_act, 0, keepdims=True),
         jnp.zeros((6, grad_act.shape[1]), jnp.float32)], 0)

    @pl.when(step == 0)
    def _():
        small_ref[...] = jnp.zeros_like(small_ref)

    small_ref[...] = small_ref[...] + sums
    gpre_ref[...] = grad_pre
    ghid_ref[...] = grad_hidden
    gbr_ref[...] = grad_branch
    gatt_ref[...] = grad_att.astype(gatt_ref.dtype)


def _rows(width):
    return pl.BlockSpec((ROWS, width), lambda i: (i, 0))


def _whole(shape):
    return pl.BlockSpec(shape, lambda i: (0,) * len(shape))


def mlp_fwd(attended, residual, valid, w_proj, gain, offset, w_fc1, w_fc2):
    tokens, width = residual.shape
    hidden_width = w_fc1.shape[1]
    return pl.pallas_call(
        _mlp_fwd_kernel,
        grid=(tokens // ROWS,),
        out_shape=(
            jax.ShapeDtypeStruct((tokens, width), jnp.float32),
            jax.ShapeDtypeStruct((tokens, width), jnp.bfloat16),
            jax.ShapeDtypeStruct((tokens, hidden_width), jnp.bfloat16),
            jax.ShapeDtypeStruct((tokens, width), jnp.bfloat16),
            jax.ShapeDtypeStruct((8, 128), jnp.float32),
        ),
        in_specs=[_rows(width), _rows(width), _rows(1), _whole(w_proj.shape), _whole((1, width)),
                  _whole((1, width)), _whole(w_fc1.shape), _whole(w_fc2.shape)],
        out_specs=(_rows(width), _rows(width), _rows(hidden_width), _rows(width), _whole((8, 128))),
        compiler_params=pltpu.CompilerParams(dimension_semantics=("arbitrary",), vmem_limit_bytes=48 * 1024 * 1024),
    )(attended, residual, valid, w_proj, gain.reshape(1, -1), offset.reshape(1, -1), w_fc1, w_fc2)


def mlp_bwd(grad_out, hidden, act_two, gain, w_fc1, w_fc2, w_proj):
    tokens, width = hidden.shape
    hidden_width = w_fc1.shape[1]
    return pl.pallas_call(
        _mlp_bwd_kernel,
        grid=(tokens // ROWS,),
        out_shape=(
            jax.ShapeDtypeStruct((tokens, hidden_width), jnp.bfloat16),
            jax.ShapeDtypeStruct((tokens, width), jnp.float32),
            jax.ShapeDtypeStruct((tokens, width), jnp.bfloat16),
            jax.ShapeDtypeStruct((tokens, width), jnp.bfloat16),
            jax.ShapeDtypeStruct((8, width), jnp.float32),
        ),
        in_specs=[_rows(width), _rows(width), _rows(width), _whole((1, width)), _whole(w_fc1.shape),
                  _whole(w_fc2.shape), _whole(w_proj.shape)],
        out_specs=(_rows(hidden_width), _rows(width), _rows(width), _rows(width), _whole((8, width))),
        compiler_params=pltpu.CompilerParams(dimension_semantics=("arbitrary",), vmem_limit_bytes=48 * 1024 * 1024),
    )(grad_out, hidden, act_two, gain.reshape(1, -1), w_fc1, w_fc2, w_proj)


def reduce_to_owners(parted, small):
    groups = lax.axis_size("dp")
    dp_bits = groups.bit_length() - 1
    n_qy, n_qx = lax.axis_size("qy"), lax.axis_size("qx")
    count, depth = parted[0].shape[0], parted[0].shape[1]
    per_group = count // groups
    names = [("dp", 1 << power) for power in reversed(range(dp_bits))] + [("qy", 1), ("qx", 1)]
    cross = [("qy", 1)] + [("dp", 1 << power) for power in range(dp_bits)]
    pieces, piece_names, orders = [], [], []
    for index, part in enumerate(parted):
        pieces.append(
            part.reshape([2] * dp_bits + [n_qy, n_qx, per_group * depth // (n_qy * n_qx), LANES])
        )
        piece_names.append(list(names))
        turn = index % len(cross)
        orders.append([("qx", 1)] + cross[turn:] + cross[:turn])
    for stage in range(len(names)):
        for index in range(len(pieces)):
            bit = orders[index][stage]
            place = piece_names[index].index(bit)
            mine = bit_of(*bit)
            keep = lax.dynamic_index_in_dim(pieces[index], mine, place, keepdims=False)
            send = lax.dynamic_index_in_dim(pieces[index], 1 - mine, place, keepdims=False)
            piece_names[index].remove(bit)
            arrived = partner_of(send.astype(jnp.bfloat16), *bit)
            pieces[index] = keep + arrived.astype(jnp.float32)
            if index == 0:
                small = small + partner_of(small, *bit)
                pieces[0], small = lax.optimization_barrier((pieces[0], small))
    chunk = jnp.stack(pieces)
    other = partner_of(chunk, "qy", 1)
    pair = jnp.where(bit_of("qy", 1) == 1, jnp.stack([other, chunk], 1), jnp.stack([chunk, other], 1))
    other = partner_of(pair, "qx", 1)
    quad = jnp.where(bit_of("qx", 1) == 1, jnp.stack([other, pair], 2), jnp.stack([pair, other], 2))
    quad = quad.reshape(len(pieces), per_group, depth, LANES).transpose(1, 0, 2, 3)
    return quad.reshape(per_group, BLK, BLK), small


def cut_along(value, dim, devices):
    before, after = (value.shape[:dim], value.shape[dim + 1 :])
    return jnp.moveaxis(value.reshape(*before, devices, -1, *after), dim, 0)


def sent_and_summed(value, axis, dim):
    pieces = cut_along(value, dim, lax.axis_size(axis))
    arrived = lax.all_to_all(pieces, axis, split_axis=0, concat_axis=0, tiled=True)
    return arrived.astype(jnp.float32).sum(axis=0)


def norm_stats(tensor):
    center = tensor - jnp.mean(tensor, -1, keepdims=True)
    inverse = lax.rsqrt(jnp.mean(center * center, -1, keepdims=True) + NORM_EPSILON)
    return (center * inverse, inverse)


def norm_back(grad_act, normed, inverse, gain):
    scaled = grad_act * gain
    mean_one = jnp.mean(scaled, -1, keepdims=True)
    mean_two = jnp.mean(scaled * normed, -1, keepdims=True)
    return inverse * (scaled - mean_one - normed * mean_two)


def to_windows(tensor):
    canvases, rows_side, cols_side, channels = tensor.shape
    shaped = tensor.reshape(canvases, rows_side // WIN, WIN, cols_side // WIN, WIN, channels)
    return shaped.transpose(0, 1, 3, 2, 4, 5).reshape(
        canvases * (rows_side // WIN) * (cols_side // WIN), WIN * WIN, channels
    )


def from_windows(tensor, canvases, rows_side, cols_side):
    channels = tensor.shape[-1]
    shaped = tensor.reshape(canvases, rows_side // WIN, cols_side // WIN, WIN, WIN, channels)
    return shaped.transpose(0, 1, 3, 2, 4, 5).reshape(canvases, rows_side, cols_side, channels)


def relative_index():
    places = jnp.arange(WIN * WIN, dtype=jnp.int32)
    row_of = places // WIN
    col_of = places % WIN
    return (row_of[:, None] - row_of[None, :] + WIN - 1) * (2 * WIN - 1) + (
        col_of[:, None] - col_of[None, :] + WIN - 1
    )


def region_of(places, full):
    return jnp.where(places < full - WIN, 0, jnp.where(places < full - SHIFT, 1, 2)).astype(
        jnp.int32
    )


def advance(tensor):
    upper = passed_along(tensor[:, :SHIFT], "qy", -1)
    tensor = jnp.concatenate([tensor[:, SHIFT:], upper], 1)
    leftmost = passed_along(tensor[:, :, :SHIFT], "qx", -1)
    return jnp.concatenate([tensor[:, :, SHIFT:], leftmost], 2)


def retreat(tensor):
    lowest = passed_along(tensor[:, -SHIFT:], "qy", 1)
    tensor = jnp.concatenate([lowest, tensor[:, :-SHIFT]], 1)
    rightmost = passed_along(tensor[:, :, -SHIFT:], "qx", 1)
    return jnp.concatenate([rightmost, tensor[:, :, :-SHIFT]], 2)


def blocks_of(matrix):
    row_blocks = matrix.shape[0] // BLK
    col_blocks = matrix.shape[1] // BLK
    return (
        matrix.reshape(row_blocks, BLK, col_blocks, BLK)
        .transpose(0, 2, 1, 3)
        .reshape(row_blocks * col_blocks, BLK, BLK)
    )


def rotate_update(grads, master, first, second, left, right):
    turned = jnp.einsum("sji,sjk->sik", left, grads, precision=PRECISE)
    turned = jnp.einsum("sik,skl->sil", turned, right, precision=PRECISE)
    new_first = BETA_ONE * first + (1.0 - BETA_ONE) * turned
    new_second = BETA_TWO * second + (1.0 - BETA_TWO) * turned * turned
    direction = new_first / (jnp.sqrt(new_second) + ADAM_EPSILON)
    back = jnp.einsum("sij,sjk->sik", left, direction, precision=PRECISE)
    back = jnp.einsum("sik,slk->sil", back, right, precision=PRECISE)
    return (new_first, new_second, master - RATE_BLOCKS * back)


def small_update(grads, params, first, second):
    new_first = BETA_ONE * first + (1.0 - BETA_ONE) * grads
    new_second = BETA_TWO * second + (1.0 - BETA_TWO) * grads * grads
    direction = new_first / (jnp.sqrt(new_second) + ADAM_EPSILON)
    return (new_first, new_second, params - RATE_SMALL * direction)


def local(
    tokens,
    crop_ids,
    merge_order,
    owner_list,
    w_qkv,
    w_proj,
    w_fc1,
    w_fc2,
    small_params,
    small_first,
    small_second,
    master_blocks,
    first_moment,
    second_moment,
    basis_left,
    basis_right,
    merged_grad,
):
    canvases, quad_side, quad_cols, features = tokens.shape
    head_dim = features // HEADS
    score_scale = head_dim ** (-0.5)
    window_area = WIN * WIN
    quarters = lax.axis_size(("qy", "qx"))
    share_rows = quad_side * quad_cols // quarters
    row_base = lax.axis_index("qy") * quad_side
    col_base = lax.axis_index("qx") * quad_cols
    rolled = jnp.roll(crop_ids, (-SHIFT, -SHIFT), (1, 2))
    local_ids = lax.dynamic_slice(
        rolled, (jnp.int32(0), row_base, col_base), (canvases, quad_side, quad_cols)
    )
    region_row = region_of(
        row_base + jnp.arange(quad_side, dtype=jnp.int32), quad_side * lax.axis_size("qy")
    )
    region_col = region_of(
        col_base + jnp.arange(quad_cols, dtype=jnp.int32), quad_cols * lax.axis_size("qx")
    )
    labels = (local_ids + 1) * 9 + region_row[None, :, None] * 3 + region_col[None, None, :]
    win_labels = to_windows(labels[..., None])[..., 0]
    window_count = win_labels.shape[0]
    gain_one = small_params[0:features]
    offset_one = small_params[features : 2 * features]
    gain_two = small_params[2 * features : 3 * features]
    offset_two = small_params[3 * features : 4 * features]
    table = small_params[4 * features :].reshape(HEADS, -1)
    onehot = (
        relative_index().reshape(-1)[:, None]
        == jnp.arange(table.shape[1], dtype=jnp.int32)[None, :]
    ).astype(jnp.float32)
    rel_bias = jnp.einsum("hr,pr->hp", table, onehot, precision=PRECISE).reshape(
        HEADS, window_area, window_area
    )

    pair_area = 2 * window_area
    place = jnp.arange(PAIR, dtype=jnp.int32)
    pair_labels = jnp.pad(win_labels.reshape(-1, pair_area), ((0, 0), (0, PAIR - pair_area)))
    pair_keys = jnp.where(
        place[None] < pair_area,
        pair_labels * 2 + (place[None] >= window_area).astype(jnp.int32),
        -1 - place[None],
    )
    key_col, key_row = pair_keys[:, :, None], pair_keys[:, None, :]
    valid = (pair_labels >= 9).reshape(-1).astype(jnp.float32)[:, None]
    spread = (
        (place[:, None] % window_area == jnp.arange(window_area, dtype=jnp.int32)[None, :])
        & (place[:, None] < pair_area)
    ).astype(jnp.float32)
    dense_bias = jnp.einsum(
        "hti,ui->htu",
        jnp.einsum("ti,hij->htj", spread, rel_bias, precision=PRECISE),
        spread,
        precision=PRECISE,
    )

    def to_pairs(tensor):
        shaped = tensor.reshape(-1, pair_area, tensor.shape[-1])
        return jnp.pad(shaped, ((0, 0), (0, PAIR - pair_area), (0, 0))).reshape(-1, tensor.shape[-1])

    def from_pairs(tensor):
        shaped = tensor.reshape(-1, PAIR, tensor.shape[-1])
        return shaped[:, :pair_area].reshape(-1, window_area, tensor.shape[-1])

    residual = into_pairs(tokens).reshape(-1, features).astype(jnp.float32)
    normed_one, inverse_one = norm_stats(residual)
    act_one = (normed_one * gain_one + offset_one).astype(jnp.bfloat16)
    mixed = jnp.dot(act_one, w_qkv, preferred_element_type=jnp.float32).astype(jnp.bfloat16)
    mixed_pairs = mixed.reshape(-1, PAIR, mixed.shape[-1])
    attended_pairs, log_total = attention_fwd(mixed_pairs, dense_bias, key_col, key_row, score_scale)
    attended = attended_pairs.reshape(-1, features)
    hidden, act_two, gelu_low, output_flat, stat_block = mlp_fwd(
        attended, residual, valid, w_proj, gain_two, offset_two, w_fc1, w_fc2
    )
    stat_terms = jnp.stack([stat_block[0, 0], stat_block[0, 1], jnp.sum(valid) * features])
    restored = out_of_pairs(output_flat.reshape(canvases, -1, features), quad_side, quad_cols)
    flat_out = restored.reshape(canvases, quarters, share_rows, features)
    arrived = lax.all_to_all(flat_out, ("qy", "qx"), 1, 1, tiled=True)
    merged = jnp.take(arrived, merge_order, axis=1, mode="clip").transpose(0, 2, 1, 3).reshape(
        canvases, share_rows, quarters * features
    )
    quarter_ids = jnp.arange(quarters, dtype=jnp.int32)
    source_pick = jnp.sum(
        quarter_ids[:, None] * (merge_order[:, None] == quarter_ids[None, :]).astype(jnp.int32), 0
    )
    incoming = merged_grad.reshape(canvases, share_rows, quarters, features)
    unordered = jnp.take(incoming, source_pick, axis=2, mode="clip").transpose(0, 2, 1, 3)
    returned = lax.all_to_all(unordered, ("qy", "qx"), 1, 1, tiled=True)
    grad_orig = returned.reshape(canvases, quad_side, quad_cols, features)
    grad_out = into_pairs(grad_orig).reshape(-1, features)
    grad_pre, grad_hidden, grad_branch, grad_attended, small_two = mlp_bwd(
        grad_out, hidden, act_two, gain_two, w_fc1, w_fc2, w_proj
    )
    grad_fc2 = jnp.einsum("rf,rc->fc", gelu_low, grad_out, preferred_element_type=jnp.float32)
    grad_fc1 = jnp.einsum("rc,rf->cf", act_two, grad_pre, preferred_element_type=jnp.float32)
    grad_proj = jnp.einsum("rc,rd->cd", attended, grad_branch, preferred_element_type=jnp.float32)
    grad_mixed_pairs, dense_grad_bias = attention_bwd(
        mixed_pairs, grad_attended.reshape(-1, PAIR, features), log_total, dense_bias, key_col, key_row, score_scale
    )
    grad_mixed = grad_mixed_pairs.reshape(-1, 3 * features)
    grad_bias = jnp.einsum(
        "ti,htj->hij",
        spread,
        jnp.einsum("htu,uj->htj", dense_grad_bias, spread, precision=PRECISE),
        precision=PRECISE,
    )
    grad_table = jnp.dot(grad_bias.reshape(HEADS, -1), onehot, precision=PRECISE)
    grad_qkv = jnp.einsum("rc,rf->cf", act_one, grad_mixed, preferred_element_type=jnp.float32)
    grad_act_one = jnp.einsum("rf,cf->rc", grad_mixed, w_qkv, preferred_element_type=jnp.float32)
    grad_input = grad_hidden + norm_back(grad_act_one, normed_one, inverse_one, gain_one)
    grad_tokens = out_of_pairs(
        grad_input.astype(jnp.bfloat16).reshape(canvases, -1, features), quad_side, quad_cols
    )
    small_local = jnp.concatenate(
        [
            jnp.sum(grad_act_one * normed_one, 0),
            jnp.sum(grad_act_one, 0),
            small_two[0],
            small_two[1],
            grad_table.reshape(-1),
        ]
    )
    every_block = jnp.concatenate(
        [lane_blocks(grad_qkv), lane_blocks(grad_proj), lane_blocks(grad_fc1), lane_blocks(grad_fc2)],
        0,
    )
    depth = every_block.shape[1] // PARTS
    parted = [
        jnp.take(every_block[:, index * depth : (index + 1) * depth], owner_list, axis=0, mode="clip")
        for index in range(PARTS)
    ]
    owned_grads, small_all = reduce_to_owners(parted, jnp.concatenate([small_local, stat_terms]))
    small_total = small_all[: small_local.shape[0]]
    stat_total = small_all[small_local.shape[0] :]
    new_first, new_second, new_master = rotate_update(
        owned_grads, master_blocks, first_moment, second_moment, basis_left, basis_right
    )
    small_first_new, small_second_new, small_new = small_update(
        small_total, small_params, small_first, small_second
    )
    stats = jnp.stack(
        [jnp.sqrt(stat_total[0] / stat_total[2]), jnp.sqrt(stat_total[1] / (2.0 * stat_total[2]))]
    )
    return (
        merged,
        grad_tokens,
        owned_grads,
        new_master,
        new_first,
        new_second,
        new_master.astype(jnp.bfloat16),
        small_total,
        small_first_new,
        small_second_new,
        small_new,
        stats,
    )


def solution(mesh):
    placed = (
        P("dp", "qy", "qx", None),
        P("dp", None, None),
        P(),
        P(),
        P(),
        P(),
        P(),
        P(),
        P(),
        P(),
        P(),
        P("dp", None, None),
        P("dp", None, None),
        P("dp", None, None),
        P("dp", None, None),
        P("dp", None, None),
        P("dp", ("qy", "qx"), None),
    )
    return jax.shard_map(
        local,
        mesh=mesh,
        in_specs=placed,
        out_specs=(
            P("dp", ("qy", "qx"), None),
            P("dp", "qy", "qx", None),
            P("dp", None, None),
            P("dp", None, None),
            P("dp", None, None),
            P("dp", None, None),
            P("dp", None, None),
            P(),
            P(),
            P(),
            P(),
            P(),
        ),
        check_vma=False,
    )
```

```python
import functools
from functools import partial

import numpy as np

import jax
import jax.numpy as jnp
from jax import lax
from jax.experimental import pallas as pl
from jax.experimental.pallas import tpu as pltpu
from jax.sharding import PartitionSpec as P

HEADS = 12
WIN = 7
SHIFT = 3
BLK = 96


BETA_ONE = 0.5
BETA_TWO = 0.6
ADAM_EPSILON = 1e-08
RATE_BLOCKS = 0.04
RATE_SMALL = 0.2
MASK_FILL = -1e30
NORM_EPSILON = 1e-05
PRECISE = lax.Precision.HIGHEST


def passed_along(value, axis, steps):
    count = lax.axis_size(axis)
    pairs = [(source, (source + steps) % count) for source in range(count)]
    return lax.ppermute(value, axis, pairs)


def partner_of(value, axis, mask):
    count = lax.axis_size(axis)
    pairs = [(source, source ^ mask) for source in range(count)]
    return lax.ppermute(value, axis, pairs)


def bit_of(axis, mask):
    return ((lax.axis_index(axis) & mask) != 0).astype(jnp.int32)


LANES = 128
PARTS = 3
GROUP = 4
LANES = 128
MASK_FILL = -1e30
PAIR = 112


def _stacked(value, lane4):
    wide = jnp.broadcast_to(value.astype(jnp.float32)[None], (GROUP, PAIR, LANES))
    return jnp.where(lane4, wide, 0.0).reshape(GROUP * PAIR, LANES).astype(jnp.bfloat16)


def _gather_lanes(stack, lane4):
    return jnp.sum(jnp.where(lane4, stack.reshape(GROUP, PAIR, LANES), 0.0), 0)


def _scores(q4, k4, bias4, allowed, scale, lane4):
    raw = lax.dot_general(_stacked(q4, lane4), k4, (((1,), (1,)), ((), ())), preferred_element_type=jnp.float32)
    raw = raw.reshape(GROUP, PAIR, PAIR) * scale + bias4
    return jnp.where(allowed[None], raw, MASK_FILL)


def _lane_masks():
    lane4 = lax.broadcasted_iota(jnp.int32, (GROUP, 1, LANES), 2) // 32 == lax.broadcasted_iota(
        jnp.int32, (GROUP, 1, LANES), 0)
    return lane4, lax.broadcasted_iota(jnp.int32, (1, LANES), 1)


def _fwd_kernel(mix_ref, bias_ref, kc_ref, kr_ref, out_ref, lse_ref, *, scale):
    width = HEADS * 32
    lane4, head_lane = _lane_masks()
    allowed = kc_ref[0] == kr_ref[0]
    lse_all = jnp.zeros((PAIR, LANES), jnp.float32)
    for g in range(HEADS // GROUP):
        q4 = mix_ref[0, :, pl.ds(g * LANES, LANES)]
        k4 = mix_ref[0, :, pl.ds(width + g * LANES, LANES)]
        v4 = mix_ref[0, :, pl.ds(2 * width + g * LANES, LANES)]
        s = _scores(q4, k4, bias_ref[pl.ds(g * GROUP, GROUP)], allowed, scale, lane4)
        top = jnp.max(s, -1, keepdims=True)
        e = jnp.exp(s - top)
        total = jnp.sum(e, -1, keepdims=True)
        probs = (e / total).reshape(GROUP * PAIR, PAIR).astype(jnp.bfloat16)
        mixed_out = jnp.dot(probs, v4, preferred_element_type=jnp.float32)
        out_ref[0, :, pl.ds(g * LANES, LANES)] = _gather_lanes(mixed_out, lane4).astype(out_ref.dtype)
        lse = top + jnp.log(total)
        for j in range(GROUP):
            lse_all = jnp.where(head_lane == g * GROUP + j, lse[j], lse_all)
    lse_ref[0] = lse_all


def _bwd_kernel(mix_ref, grad_ref, lse_ref, bias_ref, kc_ref, kr_ref, gmix_ref, dbias_ref, *, scale):
    width = HEADS * 32
    lane4, head_lane = _lane_masks()
    step = pl.program_id(0)
    allowed = kc_ref[0] == kr_ref[0]
    lse_all = lse_ref[0]

    @pl.when(step == 0)
    def _():
        dbias_ref[...] = jnp.zeros_like(dbias_ref)

    for g in range(HEADS // GROUP):
        q4 = mix_ref[0, :, pl.ds(g * LANES, LANES)]
        k4 = mix_ref[0, :, pl.ds(width + g * LANES, LANES)]
        v4 = mix_ref[0, :, pl.ds(2 * width + g * LANES, LANES)]
        d4 = grad_ref[0, :, pl.ds(g * LANES, LANES)]
        heads = pl.ds(g * GROUP, GROUP)
        s = _scores(q4, k4, bias_ref[heads], allowed, scale, lane4)
        lse = jnp.stack([
            jnp.sum(jnp.where(head_lane == g * GROUP + j, lse_all, 0.0), -1, keepdims=True)
            for j in range(GROUP)
        ])
        probs = jnp.exp(s - lse)
        d_stack = _stacked(d4, lane4)
        dprobs = lax.dot_general(d_stack, v4, (((1,), (1,)), ((), ())), preferred_element_type=jnp.float32)
        dprobs = dprobs.reshape(GROUP, PAIR, PAIR)
        inner = jnp.sum(probs * dprobs, -1, keepdims=True)
        dscores = (probs * (dprobs - inner)).reshape(GROUP * PAIR, PAIR).astype(jnp.bfloat16)
        dbias_ref[heads] = dbias_ref[heads] + dscores.astype(jnp.float32).reshape(GROUP, PAIR, PAIR)
        gq = _gather_lanes(jnp.dot(dscores, k4, preferred_element_type=jnp.float32), lane4)
        gk = lax.dot_general(dscores, _stacked(q4, lane4), (((0,), (0,)), ((), ())), preferred_element_type=jnp.float32)
        gv = lax.dot_general(probs.reshape(GROUP * PAIR, PAIR).astype(jnp.bfloat16), d_stack,
                             (((0,), (0,)), ((), ())), preferred_element_type=jnp.float32)
        gmix_ref[0, :, pl.ds(g * LANES, LANES)] = (gq * scale).astype(gmix_ref.dtype)
        gmix_ref[0, :, pl.ds(width + g * LANES, LANES)] = (gk * scale).astype(gmix_ref.dtype)
        gmix_ref[0, :, pl.ds(2 * width + g * LANES, LANES)] = gv.astype(gmix_ref.dtype)


def _pair_spec(width):
    return pl.BlockSpec((1, PAIR, width), lambda p: (p, 0, 0))


def attention_fwd(mixed_pairs, bias, key_col, key_row, scale):
    pairs = mixed_pairs.shape[0]
    kernel = functools.partial(_fwd_kernel, scale=scale)
    return pl.pallas_call(
        kernel,
        grid=(pairs,),
        out_shape=(
            jax.ShapeDtypeStruct((pairs, PAIR, HEADS * 32), jnp.bfloat16),
            jax.ShapeDtypeStruct((pairs, PAIR, LANES), jnp.float32),
        ),
        in_specs=[_pair_spec(mixed_pairs.shape[2]), pl.BlockSpec(bias.shape, lambda p: (0, 0, 0)),
                  pl.BlockSpec((1, PAIR, 1), lambda p: (p, 0, 0)), pl.BlockSpec((1, 1, PAIR), lambda p: (p, 0, 0))],
        out_specs=(_pair_spec(HEADS * 32), _pair_spec(LANES)),
        compiler_params=pltpu.CompilerParams(dimension_semantics=("arbitrary",), vmem_limit_bytes=32 * 1024 * 1024),
    )(mixed_pairs, bias, key_col, key_row)


def attention_bwd(mixed_pairs, grad_pairs, lse, bias, key_col, key_row, scale):
    pairs = mixed_pairs.shape[0]
    kernel = functools.partial(_bwd_kernel, scale=scale)
    return pl.pallas_call(
        kernel,
        grid=(pairs,),
        out_shape=(
            jax.ShapeDtypeStruct(mixed_pairs.shape, jnp.bfloat16),
            jax.ShapeDtypeStruct(bias.shape, jnp.float32),
        ),
        in_specs=[_pair_spec(mixed_pairs.shape[2]), _pair_spec(HEADS * 32), _pair_spec(LANES),
                  pl.BlockSpec(bias.shape, lambda p: (0, 0, 0)),
                  pl.BlockSpec((1, PAIR, 1), lambda p: (p, 0, 0)), pl.BlockSpec((1, 1, PAIR), lambda p: (p, 0, 0))],
        out_specs=(_pair_spec(mixed_pairs.shape[2]), pl.BlockSpec(bias.shape, lambda p: (0, 0, 0))),
        compiler_params=pltpu.CompilerParams(dimension_semantics=("arbitrary",), vmem_limit_bytes=32 * 1024 * 1024),
    )(mixed_pairs, grad_pairs, lse, bias, key_col, key_row)


def pair_row(side_r, side_c, r, c):
    per_row = side_c // WIN
    window = (r // WIN) * per_row + (c // WIN)
    inside = (r % WIN) * WIN + (c % WIN)
    return (window // 2) * PAIR + (window % 2) * WIN * WIN + inside


def gather_rows(source, index):
    return jnp.take(source, jnp.asarray(index, jnp.int32), axis=1, mode="clip")


def into_pairs(tensor):
    canvases, side_r, side_c, features = tensor.shape
    flat = tensor.reshape(canvases, side_r * side_c, features)
    below = passed_along(tensor[:, :SHIFT].reshape(canvases, SHIFT * side_c, features), "qy", -1)
    source = jnp.concatenate([flat, below], 1)
    def t_index(r, c):
        return np.where(r < side_r - SHIFT, (r + SHIFT) * side_c + c, side_r * side_c + (r - (side_r - SHIFT)) * side_c + c)
    rr, cc = np.meshgrid(np.arange(side_r), np.arange(SHIFT), indexing="ij")
    right = passed_along(gather_rows(source, t_index(rr, cc).reshape(-1)), "qx", -1)
    zero = jnp.zeros((canvases, 1, features), tensor.dtype)
    source = jnp.concatenate([source, right, zero], 1)
    base_right = side_r * side_c + SHIFT * side_c
    rr, cc = np.meshgrid(np.arange(side_r), np.arange(side_c), indexing="ij")
    want = np.where(cc < side_c - SHIFT, t_index(rr, np.minimum(cc + SHIFT, side_c - 1)),
                    base_right + rr * SHIFT + (cc - (side_c - SHIFT)))
    windows = (side_r // WIN) * (side_c // WIN)
    index = np.full(windows // 2 * PAIR, base_right + side_r * SHIFT, np.int64)
    index[pair_row(side_r, side_c, rr, cc).reshape(-1)] = want.reshape(-1)
    return gather_rows(source, index)


def out_of_pairs(pairs, side_r, side_c):
    canvases, _, features = pairs.shape
    rr, cc = np.meshgrid(np.arange(SHIFT), np.arange(side_c), indexing="ij")
    lowest = passed_along(gather_rows(pairs, pair_row(side_r, side_c, rr + side_r - SHIFT, cc).reshape(-1)), "qy", 1)
    rows = pairs.shape[1]
    source = jnp.concatenate([pairs, lowest], 1)
    def t_index(r, c):
        return np.where(r < SHIFT, rows + r * side_c + c, pair_row(side_r, side_c, np.maximum(r - SHIFT, 0), c))
    rr, cc = np.meshgrid(np.arange(side_r), np.arange(SHIFT), indexing="ij")
    rightmost = passed_along(gather_rows(source, t_index(rr, cc + side_c - SHIFT).reshape(-1)), "qx", 1)
    source = jnp.concatenate([source, rightmost], 1)
    base = rows + SHIFT * side_c
    rr, cc = np.meshgrid(np.arange(side_r), np.arange(side_c), indexing="ij")
    want = np.where(cc < SHIFT, base + rr * SHIFT + cc, t_index(rr, np.maximum(cc - SHIFT, 0)))
    return gather_rows(source, want.reshape(-1)).reshape(canvases, side_r, side_c, features)


def lane_blocks(matrix):
    row_blocks, col_blocks = matrix.shape[0] // BLK, matrix.shape[1] // BLK
    shaped = matrix.reshape(row_blocks, BLK, col_blocks, BLK).transpose(0, 2, 1, 3)
    return shaped.reshape(row_blocks * col_blocks, BLK * BLK // LANES, LANES)


ROWS = 112
SQRT_HALF = float(np.sqrt(0.5))
INV_SQRT_TAU = float(1.0 / np.sqrt(2.0 * np.pi))


def _norm(tensor):
    center = tensor - jnp.mean(tensor, -1, keepdims=True)
    inverse = lax.rsqrt(jnp.mean(center * center, -1, keepdims=True) + NORM_EPSILON)
    return center * inverse, inverse


def _mlp_fwd_kernel(att_ref, res_ref, valid_ref, wp_ref, gain_ref, off_ref, w1_ref, w2_ref,
                    hid_ref, act_ref, gelu_ref, out_ref, stat_ref):
    step = pl.program_id(0)
    branch_one = jnp.dot(att_ref[...], wp_ref[...], preferred_element_type=jnp.float32)
    hidden = res_ref[...] + branch_one
    normed, _ = _norm(hidden)
    act = (normed * gain_ref[...] + off_ref[...]).astype(jnp.bfloat16)
    pre = jnp.dot(act, w1_ref[...], preferred_element_type=jnp.float32)
    gelu = ((0.5 * pre) * (1.0 + lax.erf(pre * SQRT_HALF))).astype(jnp.bfloat16)
    branch_two = jnp.dot(gelu, w2_ref[...], preferred_element_type=jnp.float32)
    output = hidden + branch_two
    valid = valid_ref[...]
    first = jnp.sum(valid * output * output)
    second = jnp.sum(valid * (branch_one * branch_one + branch_two * branch_two))
    lane = lax.broadcasted_iota(jnp.int32, (8, 128), 1)
    row = lax.broadcasted_iota(jnp.int32, (8, 128), 0)
    here = jnp.where((row == 0) & (lane == 0), first, 0.0) + jnp.where((row == 0) & (lane == 1), second, 0.0)

    @pl.when(step == 0)
    def _():
        stat_ref[...] = jnp.zeros_like(stat_ref)

    stat_ref[...] = stat_ref[...] + here
    hid_ref[...] = hidden
    act_ref[...] = act
    gelu_ref[...] = gelu
    out_ref[...] = output.astype(out_ref.dtype)


def _mlp_bwd_kernel(gout_ref, hid_ref, act_ref, gain_ref, w1_ref, w2_ref, wp_ref,
                    gpre_ref, ghid_ref, gbr_ref, gatt_ref, small_ref):
    step = pl.program_id(0)
    contract_last = (((1,), (1,)), ((), ()))
    pre = jnp.dot(act_ref[...], w1_ref[...], preferred_element_type=jnp.float32)
    grad_out = gout_ref[...]
    grad_gelu = lax.dot_general(grad_out, w2_ref[...], contract_last, preferred_element_type=jnp.float32)
    cdf = 0.5 * (1.0 + lax.erf(pre * SQRT_HALF))
    pdf = jnp.exp(-0.5 * pre * pre) * INV_SQRT_TAU
    grad_pre = (grad_gelu * (cdf + pre * pdf)).astype(jnp.bfloat16)
    grad_act = lax.dot_general(grad_pre, w1_ref[...], contract_last, preferred_element_type=jnp.float32)
    normed, inverse = _norm(hid_ref[...])
    scaled = grad_act * gain_ref[...]
    mean_one = jnp.mean(scaled, -1, keepdims=True)
    mean_two = jnp.mean(scaled * normed, -1, keepdims=True)
    grad_hidden = grad_out.astype(jnp.float32) + inverse * (scaled - mean_one - normed * mean_two)
    grad_branch = grad_hidden.astype(jnp.bfloat16)
    grad_att = lax.dot_general(grad_branch, wp_ref[...], contract_last, preferred_element_type=jnp.float32)
    sums = jnp.concatenate(
        [jnp.sum(grad_act * normed, 0, keepdims=True), jnp.sum(grad_act, 0, keepdims=True),
         jnp.zeros((6, grad_act.shape[1]), jnp.float32)], 0)

    @pl.when(step == 0)
    def _():
        small_ref[...] = jnp.zeros_like(small_ref)

    small_ref[...] = small_ref[...] + sums
    gpre_ref[...] = grad_pre
    ghid_ref[...] = grad_hidden
    gbr_ref[...] = grad_branch
    gatt_ref[...] = grad_att.astype(gatt_ref.dtype)


def _rows(width):
    return pl.BlockSpec((ROWS, width), lambda i: (i, 0))


def _whole(shape):
    return pl.BlockSpec(shape, lambda i: (0,) * len(shape))


def mlp_fwd(attended, residual, valid, w_proj, gain, offset, w_fc1, w_fc2):
    tokens, width = residual.shape
    hidden_width = w_fc1.shape[1]
    return pl.pallas_call(
        _mlp_fwd_kernel,
        grid=(tokens // ROWS,),
        out_shape=(
            jax.ShapeDtypeStruct((tokens, width), jnp.float32),
            jax.ShapeDtypeStruct((tokens, width), jnp.bfloat16),
            jax.ShapeDtypeStruct((tokens, hidden_width), jnp.bfloat16),
            jax.ShapeDtypeStruct((tokens, width), jnp.float32),
            jax.ShapeDtypeStruct((8, 128), jnp.float32),
        ),
        in_specs=[_rows(width), _rows(width), _rows(1), _whole(w_proj.shape), _whole((1, width)),
                  _whole((1, width)), _whole(w_fc1.shape), _whole(w_fc2.shape)],
        out_specs=(_rows(width), _rows(width), _rows(hidden_width), _rows(width), _whole((8, 128))),
        compiler_params=pltpu.CompilerParams(dimension_semantics=("arbitrary",), vmem_limit_bytes=48 * 1024 * 1024),
    )(attended, residual, valid, w_proj, gain.reshape(1, -1), offset.reshape(1, -1), w_fc1, w_fc2)


def mlp_bwd(grad_out, hidden, act_two, gain, w_fc1, w_fc2, w_proj):
    tokens, width = hidden.shape
    hidden_width = w_fc1.shape[1]
    return pl.pallas_call(
        _mlp_bwd_kernel,
        grid=(tokens // ROWS,),
        out_shape=(
            jax.ShapeDtypeStruct((tokens, hidden_width), jnp.bfloat16),
            jax.ShapeDtypeStruct((tokens, width), jnp.float32),
            jax.ShapeDtypeStruct((tokens, width), jnp.bfloat16),
            jax.ShapeDtypeStruct((tokens, width), jnp.bfloat16),
            jax.ShapeDtypeStruct((8, width), jnp.float32),
        ),
        in_specs=[_rows(width), _rows(width), _rows(width), _whole((1, width)), _whole(w_fc1.shape),
                  _whole(w_fc2.shape), _whole(w_proj.shape)],
        out_specs=(_rows(hidden_width), _rows(width), _rows(width), _rows(width), _whole((8, width))),
        compiler_params=pltpu.CompilerParams(dimension_semantics=("arbitrary",), vmem_limit_bytes=48 * 1024 * 1024),
    )(grad_out, hidden, act_two, gain.reshape(1, -1), w_fc1, w_fc2, w_proj)


def reduce_to_owners(parted, small):
    groups = lax.axis_size("dp")
    dp_bits = groups.bit_length() - 1
    n_qy, n_qx = lax.axis_size("qy"), lax.axis_size("qx")
    count, depth = parted[0].shape[0], parted[0].shape[1]
    per_group = count // groups
    names = [("dp", 1 << power) for power in reversed(range(dp_bits))] + [("qy", 1), ("qx", 1)]
    cross = [("qy", 1)] + [("dp", 1 << power) for power in range(dp_bits)]
    pieces, piece_names, orders = [], [], []
    for index, part in enumerate(parted):
        pieces.append(
            part.reshape([2] * dp_bits + [n_qy, n_qx, per_group * depth // (n_qy * n_qx), LANES])
        )
        piece_names.append(list(names))
        turn = index % len(cross)
        orders.append([("qx", 1)] + cross[turn:] + cross[:turn])
    for stage in range(len(names)):
        for index in range(len(pieces)):
            bit = orders[index][stage]
            place = piece_names[index].index(bit)
            mine = bit_of(*bit)
            keep = lax.dynamic_index_in_dim(pieces[index], mine, place, keepdims=False)
            send = lax.dynamic_index_in_dim(pieces[index], 1 - mine, place, keepdims=False)
            piece_names[index].remove(bit)
            arrived = partner_of(send.astype(jnp.bfloat16), *bit)
            pieces[index] = keep + arrived.astype(jnp.float32)
            if index == 0:
                small = small + partner_of(small, *bit)
                pieces[0], small = lax.optimization_barrier((pieces[0], small))
    chunk = jnp.stack(pieces)
    other = partner_of(chunk, "qy", 1)
    pair = jnp.where(bit_of("qy", 1) == 1, jnp.stack([other, chunk], 1), jnp.stack([chunk, other], 1))
    other = partner_of(pair, "qx", 1)
    quad = jnp.where(bit_of("qx", 1) == 1, jnp.stack([other, pair], 2), jnp.stack([pair, other], 2))
    quad = quad.reshape(len(pieces), per_group, depth, LANES).transpose(1, 0, 2, 3)
    return quad.reshape(per_group, BLK, BLK), small


def cut_along(value, dim, devices):
    before, after = (value.shape[:dim], value.shape[dim + 1 :])
    return jnp.moveaxis(value.reshape(*before, devices, -1, *after), dim, 0)


def sent_and_summed(value, axis, dim):
    pieces = cut_along(value, dim, lax.axis_size(axis))
    arrived = lax.all_to_all(pieces, axis, split_axis=0, concat_axis=0, tiled=True)
    return arrived.astype(jnp.float32).sum(axis=0)


def norm_stats(tensor):
    center = tensor - jnp.mean(tensor, -1, keepdims=True)
    inverse = lax.rsqrt(jnp.mean(center * center, -1, keepdims=True) + NORM_EPSILON)
    return (center * inverse, inverse)


def norm_back(grad_act, normed, inverse, gain):
    scaled = grad_act * gain
    mean_one = jnp.mean(scaled, -1, keepdims=True)
    mean_two = jnp.mean(scaled * normed, -1, keepdims=True)
    return inverse * (scaled - mean_one - normed * mean_two)


def to_windows(tensor):
    canvases, rows_side, cols_side, channels = tensor.shape
    shaped = tensor.reshape(canvases, rows_side // WIN, WIN, cols_side // WIN, WIN, channels)
    return shaped.transpose(0, 1, 3, 2, 4, 5).reshape(
        canvases * (rows_side // WIN) * (cols_side // WIN), WIN * WIN, channels
    )


def from_windows(tensor, canvases, rows_side, cols_side):
    channels = tensor.shape[-1]
    shaped = tensor.reshape(canvases, rows_side // WIN, cols_side // WIN, WIN, WIN, channels)
    return shaped.transpose(0, 1, 3, 2, 4, 5).reshape(canvases, rows_side, cols_side, channels)


def relative_index():
    places = jnp.arange(WIN * WIN, dtype=jnp.int32)
    row_of = places // WIN
    col_of = places % WIN
    return (row_of[:, None] - row_of[None, :] + WIN - 1) * (2 * WIN - 1) + (
        col_of[:, None] - col_of[None, :] + WIN - 1
    )


def region_of(places, full):
    return jnp.where(places < full - WIN, 0, jnp.where(places < full - SHIFT, 1, 2)).astype(
        jnp.int32
    )


def advance(tensor):
    upper = passed_along(tensor[:, :SHIFT], "qy", -1)
    tensor = jnp.concatenate([tensor[:, SHIFT:], upper], 1)
    leftmost = passed_along(tensor[:, :, :SHIFT], "qx", -1)
    return jnp.concatenate([tensor[:, :, SHIFT:], leftmost], 2)


def retreat(tensor):
    lowest = passed_along(tensor[:, -SHIFT:], "qy", 1)
    tensor = jnp.concatenate([lowest, tensor[:, :-SHIFT]], 1)
    rightmost = passed_along(tensor[:, :, -SHIFT:], "qx", 1)
    return jnp.concatenate([rightmost, tensor[:, :, :-SHIFT]], 2)


def blocks_of(matrix):
    row_blocks = matrix.shape[0] // BLK
    col_blocks = matrix.shape[1] // BLK
    return (
        matrix.reshape(row_blocks, BLK, col_blocks, BLK)
        .transpose(0, 2, 1, 3)
        .reshape(row_blocks * col_blocks, BLK, BLK)
    )


def rotate_update(grads, master, first, second, left, right):
    turned = jnp.einsum("sji,sjk->sik", left, grads, precision=PRECISE)
    turned = jnp.einsum("sik,skl->sil", turned, right, precision=PRECISE)
    new_first = BETA_ONE * first + (1.0 - BETA_ONE) * turned
    new_second = BETA_TWO * second + (1.0 - BETA_TWO) * turned * turned
    direction = new_first / (jnp.sqrt(new_second) + ADAM_EPSILON)
    back = jnp.einsum("sij,sjk->sik", left, direction, precision=PRECISE)
    back = jnp.einsum("sik,slk->sil", back, right, precision=PRECISE)
    return (new_first, new_second, master - RATE_BLOCKS * back)


def small_update(grads, params, first, second):
    new_first = BETA_ONE * first + (1.0 - BETA_ONE) * grads
    new_second = BETA_TWO * second + (1.0 - BETA_TWO) * grads * grads
    direction = new_first / (jnp.sqrt(new_second) + ADAM_EPSILON)
    return (new_first, new_second, params - RATE_SMALL * direction)


def local(
    tokens,
    crop_ids,
    merge_order,
    owner_list,
    w_qkv,
    w_proj,
    w_fc1,
    w_fc2,
    small_params,
    small_first,
    small_second,
    master_blocks,
    first_moment,
    second_moment,
    basis_left,
    basis_right,
    merged_grad,
):
    canvases, quad_side, quad_cols, features = tokens.shape
    head_dim = features // HEADS
    score_scale = head_dim ** (-0.5)
    window_area = WIN * WIN
    quarters = lax.axis_size(("qy", "qx"))
    share_rows = quad_side * quad_cols // quarters
    row_base = lax.axis_index("qy") * quad_side
    col_base = lax.axis_index("qx") * quad_cols
    rolled = jnp.roll(crop_ids, (-SHIFT, -SHIFT), (1, 2))
    local_ids = lax.dynamic_slice(
        rolled, (jnp.int32(0), row_base, col_base), (canvases, quad_side, quad_cols)
    )
    region_row = region_of(
        row_base + jnp.arange(quad_side, dtype=jnp.int32), quad_side * lax.axis_size("qy")
    )
    region_col = region_of(
        col_base + jnp.arange(quad_cols, dtype=jnp.int32), quad_cols * lax.axis_size("qx")
    )
    labels = (local_ids + 1) * 9 + region_row[None, :, None] * 3 + region_col[None, None, :]
    win_labels = to_windows(labels[..., None])[..., 0]
    window_count = win_labels.shape[0]
    gain_one = small_params[0:features]
    offset_one = small_params[features : 2 * features]
    gain_two = small_params[2 * features : 3 * features]
    offset_two = small_params[3 * features : 4 * features]
    table = small_params[4 * features :].reshape(HEADS, -1)
    onehot = (
        relative_index().reshape(-1)[:, None]
        == jnp.arange(table.shape[1], dtype=jnp.int32)[None, :]
    ).astype(jnp.float32)
    rel_bias = jnp.einsum("hr,pr->hp", table, onehot, precision=PRECISE).reshape(
        HEADS, window_area, window_area
    )

    pair_area = 2 * window_area
    place = jnp.arange(PAIR, dtype=jnp.int32)
    pair_labels = jnp.pad(win_labels.reshape(-1, pair_area), ((0, 0), (0, PAIR - pair_area)))
    pair_keys = jnp.where(
        place[None] < pair_area,
        pair_labels * 2 + (place[None] >= window_area).astype(jnp.int32),
        -1 - place[None],
    )
    key_col, key_row = pair_keys[:, :, None], pair_keys[:, None, :]
    valid = (pair_labels >= 9).reshape(-1).astype(jnp.float32)[:, None]
    spread = (
        (place[:, None] % window_area == jnp.arange(window_area, dtype=jnp.int32)[None, :])
        & (place[:, None] < pair_area)
    ).astype(jnp.float32)
    dense_bias = jnp.einsum(
        "hti,ui->htu",
        jnp.einsum("ti,hij->htj", spread, rel_bias, precision=PRECISE),
        spread,
        precision=PRECISE,
    )

    def to_pairs(tensor):
        shaped = tensor.reshape(-1, pair_area, tensor.shape[-1])
        return jnp.pad(shaped, ((0, 0), (0, PAIR - pair_area), (0, 0))).reshape(-1, tensor.shape[-1])

    def from_pairs(tensor):
        shaped = tensor.reshape(-1, PAIR, tensor.shape[-1])
        return shaped[:, :pair_area].reshape(-1, window_area, tensor.shape[-1])

    residual = into_pairs(tokens.astype(jnp.float32)).reshape(-1, features)
    normed_one, inverse_one = norm_stats(residual)
    act_one = (normed_one * gain_one + offset_one).astype(jnp.bfloat16)
    mixed = jnp.dot(act_one, w_qkv, preferred_element_type=jnp.float32).astype(jnp.bfloat16)
    mixed_pairs = mixed.reshape(-1, PAIR, mixed.shape[-1])
    attended_pairs, log_total = attention_fwd(mixed_pairs, dense_bias, key_col, key_row, score_scale)
    attended = attended_pairs.reshape(-1, features)
    hidden, act_two, gelu_low, output_flat, stat_block = mlp_fwd(
        attended, residual, valid, w_proj, gain_two, offset_two, w_fc1, w_fc2
    )
    stat_terms = jnp.stack([stat_block[0, 0], stat_block[0, 1], jnp.sum(valid) * features])
    restored = out_of_pairs(output_flat.reshape(canvases, -1, features), quad_side, quad_cols)
    restored = restored.astype(jnp.bfloat16)
    flat_out = restored.reshape(canvases, quarters, share_rows, features)
    arrived = lax.all_to_all(flat_out, ("qy", "qx"), 1, 1, tiled=True)
    merged = jnp.take(arrived, merge_order, axis=1, mode="clip").transpose(0, 2, 1, 3).reshape(
        canvases, share_rows, quarters * features
    )
    quarter_ids = jnp.arange(quarters, dtype=jnp.int32)
    source_pick = jnp.sum(
        quarter_ids[:, None] * (merge_order[:, None] == quarter_ids[None, :]).astype(jnp.int32), 0
    )
    incoming = merged_grad.reshape(canvases, share_rows, quarters, features)
    unordered = jnp.take(incoming, source_pick, axis=2, mode="clip").transpose(0, 2, 1, 3)
    returned = lax.all_to_all(unordered, ("qy", "qx"), 1, 1, tiled=True)
    grad_orig = returned.reshape(canvases, quad_side, quad_cols, features)
    grad_out = into_pairs(grad_orig.astype(jnp.float32)).reshape(-1, features).astype(jnp.bfloat16)
    grad_pre, grad_hidden, grad_branch, grad_attended, small_two = mlp_bwd(
        grad_out, hidden, act_two, gain_two, w_fc1, w_fc2, w_proj
    )
    grad_fc2 = jnp.einsum("rf,rc->fc", gelu_low, grad_out, preferred_element_type=jnp.float32)
    grad_fc1 = jnp.einsum("rc,rf->cf", act_two, grad_pre, preferred_element_type=jnp.float32)
    grad_proj = jnp.einsum("rc,rd->cd", attended, grad_branch, preferred_element_type=jnp.float32)
    grad_mixed_pairs, dense_grad_bias = attention_bwd(
        mixed_pairs, grad_attended.reshape(-1, PAIR, features), log_total, dense_bias, key_col, key_row, score_scale
    )
    grad_mixed = grad_mixed_pairs.reshape(-1, 3 * features)
    grad_bias = jnp.einsum(
        "ti,htj->hij",
        spread,
        jnp.einsum("htu,uj->htj", dense_grad_bias, spread, precision=PRECISE),
        precision=PRECISE,
    )
    grad_table = jnp.dot(grad_bias.reshape(HEADS, -1), onehot, precision=PRECISE)
    grad_qkv = jnp.einsum("rc,rf->cf", act_one, grad_mixed, preferred_element_type=jnp.float32)
    grad_act_one = jnp.einsum("rf,cf->rc", grad_mixed, w_qkv, preferred_element_type=jnp.float32)
    grad_input = grad_hidden + norm_back(grad_act_one, normed_one, inverse_one, gain_one)
    grad_tokens = out_of_pairs(
        grad_input.reshape(canvases, -1, features), quad_side, quad_cols
    ).astype(jnp.bfloat16)
    small_local = jnp.concatenate(
        [
            jnp.sum(grad_act_one * normed_one, 0),
            jnp.sum(grad_act_one, 0),
            small_two[0],
            small_two[1],
            grad_table.reshape(-1),
        ]
    )
    every_block = jnp.concatenate(
        [lane_blocks(grad_qkv), lane_blocks(grad_proj), lane_blocks(grad_fc1), lane_blocks(grad_fc2)],
        0,
    )
    depth = every_block.shape[1] // PARTS
    parted = [
        jnp.take(every_block[:, index * depth : (index + 1) * depth], owner_list, axis=0, mode="clip")
        for index in range(PARTS)
    ]
    owned_grads, small_all = reduce_to_owners(parted, jnp.concatenate([small_local, stat_terms]))
    small_total = small_all[: small_local.shape[0]]
    stat_total = small_all[small_local.shape[0] :]
    new_first, new_second, new_master = rotate_update(
        owned_grads, master_blocks, first_moment, second_moment, basis_left, basis_right
    )
    small_first_new, small_second_new, small_new = small_update(
        small_total, small_params, small_first, small_second
    )
    stats = jnp.stack(
        [jnp.sqrt(stat_total[0] / stat_total[2]), jnp.sqrt(stat_total[1] / (2.0 * stat_total[2]))]
    )
    return (
        merged,
        grad_tokens,
        owned_grads,
        new_master,
        new_first,
        new_second,
        new_master.astype(jnp.bfloat16),
        small_total,
        small_first_new,
        small_second_new,
        small_new,
        stats,
    )


def solution(mesh):
    placed = (
        P("dp", "qy", "qx", None),
        P("dp", None, None),
        P(),
        P(),
        P(),
        P(),
        P(),
        P(),
        P(),
        P(),
        P(),
        P("dp", None, None),
        P("dp", None, None),
        P("dp", None, None),
        P("dp", None, None),
        P("dp", None, None),
        P("dp", ("qy", "qx"), None),
    )
    return jax.shard_map(
        local,
        mesh=mesh,
        in_specs=placed,
        out_specs=(
            P("dp", ("qy", "qx"), None),
            P("dp", "qy", "qx", None),
            P("dp", None, None),
            P("dp", None, None),
            P("dp", None, None),
            P("dp", None, None),
            P("dp", None, None),
            P(),
            P(),
            P(),
            P(),
            P(),
        ),
        check_vma=False,
    )
```

```python
import functools
from functools import partial

import numpy as np

import jax
import jax.numpy as jnp
from jax import lax
from jax.experimental import pallas as pl
from jax.experimental.pallas import tpu as pltpu
from jax.sharding import PartitionSpec as P

HEADS = 12
WIN = 7
SHIFT = 3
BLK = 96


BETA_ONE = 0.5
BETA_TWO = 0.6
ADAM_EPSILON = 1e-08
RATE_BLOCKS = 0.04
RATE_SMALL = 0.2
MASK_FILL = -1e30
NORM_EPSILON = 1e-05
PRECISE = lax.Precision.HIGHEST
ROTATE = lax.Precision.HIGH


def passed_along(value, axis, steps):
    count = lax.axis_size(axis)
    pairs = [(source, (source + steps) % count) for source in range(count)]
    return lax.ppermute(value, axis, pairs)


def partner_of(value, axis, mask):
    count = lax.axis_size(axis)
    pairs = [(source, source ^ mask) for source in range(count)]
    return lax.ppermute(value, axis, pairs)


def bit_of(axis, mask):
    return ((lax.axis_index(axis) & mask) != 0).astype(jnp.int32)


LANES = 128
PARTS = 3
GROUP = 4
LANES = 128
MASK_FILL = -1e30
PAIR = 112


def _stacked(value, lane4):
    wide = jnp.broadcast_to(value.astype(jnp.float32)[None], (GROUP, PAIR, LANES))
    return jnp.where(lane4, wide, 0.0).reshape(GROUP * PAIR, LANES).astype(jnp.bfloat16)


def _gather_lanes(stack, lane4):
    return jnp.sum(jnp.where(lane4, stack.reshape(GROUP, PAIR, LANES), 0.0), 0)


def _scores(q4, k4, bias4, allowed, scale, lane4):
    raw = lax.dot_general(_stacked(q4, lane4), k4, (((1,), (1,)), ((), ())), preferred_element_type=jnp.float32)
    raw = raw.reshape(GROUP, PAIR, PAIR) * scale + bias4
    return jnp.where(allowed[None], raw, MASK_FILL)


def _lane_masks():
    lane4 = lax.broadcasted_iota(jnp.int32, (GROUP, 1, LANES), 2) // 32 == lax.broadcasted_iota(
        jnp.int32, (GROUP, 1, LANES), 0)
    return lane4, lax.broadcasted_iota(jnp.int32, (1, LANES), 1)


def _fwd_kernel(mix_ref, bias_ref, kc_ref, kr_ref, out_ref, lse_ref, *, scale):
    width = HEADS * 32
    lane4, head_lane = _lane_masks()
    allowed = kc_ref[0] == kr_ref[0]
    lse_all = jnp.zeros((PAIR, LANES), jnp.float32)
    for g in range(HEADS // GROUP):
        q4 = mix_ref[0, :, pl.ds(g * LANES, LANES)]
        k4 = mix_ref[0, :, pl.ds(width + g * LANES, LANES)]
        v4 = mix_ref[0, :, pl.ds(2 * width + g * LANES, LANES)]
        s = _scores(q4, k4, bias_ref[pl.ds(g * GROUP, GROUP)], allowed, scale, lane4)
        top = jnp.max(s, -1, keepdims=True)
        e = jnp.exp(s - top)
        total = jnp.sum(e, -1, keepdims=True)
        probs = (e / total).reshape(GROUP * PAIR, PAIR).astype(jnp.bfloat16)
        mixed_out = jnp.dot(probs, v4, preferred_element_type=jnp.float32)
        out_ref[0, :, pl.ds(g * LANES, LANES)] = _gather_lanes(mixed_out, lane4).astype(out_ref.dtype)
        lse = top + jnp.log(total)
        for j in range(GROUP):
            lse_all = jnp.where(head_lane == g * GROUP + j, lse[j], lse_all)
    lse_ref[0] = lse_all


def _bwd_kernel(mix_ref, grad_ref, lse_ref, bias_ref, kc_ref, kr_ref, gmix_ref, dbias_ref, *, scale):
    width = HEADS * 32
    lane4, head_lane = _lane_masks()
    step = pl.program_id(0)
    allowed = kc_ref[0] == kr_ref[0]
    lse_all = lse_ref[0]

    @pl.when(step == 0)
    def _():
        dbias_ref[...] = jnp.zeros_like(dbias_ref)

    for g in range(HEADS // GROUP):
        q4 = mix_ref[0, :, pl.ds(g * LANES, LANES)]
        k4 = mix_ref[0, :, pl.ds(width + g * LANES, LANES)]
        v4 = mix_ref[0, :, pl.ds(2 * width + g * LANES, LANES)]
        d4 = grad_ref[0, :, pl.ds(g * LANES, LANES)]
        heads = pl.ds(g * GROUP, GROUP)
        s = _scores(q4, k4, bias_ref[heads], allowed, scale, lane4)
        lse = jnp.stack([
            jnp.sum(jnp.where(head_lane == g * GROUP + j, lse_all, 0.0), -1, keepdims=True)
            for j in range(GROUP)
        ])
        probs = jnp.exp(s - lse)
        d_stack = _stacked(d4, lane4)
        dprobs = lax.dot_general(d_stack, v4, (((1,), (1,)), ((), ())), preferred_element_type=jnp.float32)
        dprobs = dprobs.reshape(GROUP, PAIR, PAIR)
        inner = jnp.sum(probs * dprobs, -1, keepdims=True)
        dscores = (probs * (dprobs - inner)).reshape(GROUP * PAIR, PAIR).astype(jnp.bfloat16)
        dbias_ref[heads] = dbias_ref[heads] + dscores.astype(jnp.float32).reshape(GROUP, PAIR, PAIR)
        gq = _gather_lanes(jnp.dot(dscores, k4, preferred_element_type=jnp.float32), lane4)
        gk = lax.dot_general(dscores, _stacked(q4, lane4), (((0,), (0,)), ((), ())), preferred_element_type=jnp.float32)
        gv = lax.dot_general(probs.reshape(GROUP * PAIR, PAIR).astype(jnp.bfloat16), d_stack,
                             (((0,), (0,)), ((), ())), preferred_element_type=jnp.float32)
        gmix_ref[0, :, pl.ds(g * LANES, LANES)] = (gq * scale).astype(gmix_ref.dtype)
        gmix_ref[0, :, pl.ds(width + g * LANES, LANES)] = (gk * scale).astype(gmix_ref.dtype)
        gmix_ref[0, :, pl.ds(2 * width + g * LANES, LANES)] = gv.astype(gmix_ref.dtype)


def _pair_spec(width):
    return pl.BlockSpec((1, PAIR, width), lambda p: (p, 0, 0))


def attention_fwd(mixed_pairs, bias, key_col, key_row, scale):
    pairs = mixed_pairs.shape[0]
    kernel = functools.partial(_fwd_kernel, scale=scale)
    return pl.pallas_call(
        kernel,
        grid=(pairs,),
        out_shape=(
            jax.ShapeDtypeStruct((pairs, PAIR, HEADS * 32), jnp.bfloat16),
            jax.ShapeDtypeStruct((pairs, PAIR, LANES), jnp.float32),
        ),
        in_specs=[_pair_spec(mixed_pairs.shape[2]), pl.BlockSpec(bias.shape, lambda p: (0, 0, 0)),
                  pl.BlockSpec((1, PAIR, 1), lambda p: (p, 0, 0)), pl.BlockSpec((1, 1, PAIR), lambda p: (p, 0, 0))],
        out_specs=(_pair_spec(HEADS * 32), _pair_spec(LANES)),
        compiler_params=pltpu.CompilerParams(dimension_semantics=("arbitrary",), vmem_limit_bytes=32 * 1024 * 1024),
    )(mixed_pairs, bias, key_col, key_row)


def attention_bwd(mixed_pairs, grad_pairs, lse, bias, key_col, key_row, scale):
    pairs = mixed_pairs.shape[0]
    kernel = functools.partial(_bwd_kernel, scale=scale)
    return pl.pallas_call(
        kernel,
        grid=(pairs,),
        out_shape=(
            jax.ShapeDtypeStruct(mixed_pairs.shape, jnp.bfloat16),
            jax.ShapeDtypeStruct(bias.shape, jnp.float32),
        ),
        in_specs=[_pair_spec(mixed_pairs.shape[2]), _pair_spec(HEADS * 32), _pair_spec(LANES),
                  pl.BlockSpec(bias.shape, lambda p: (0, 0, 0)),
                  pl.BlockSpec((1, PAIR, 1), lambda p: (p, 0, 0)), pl.BlockSpec((1, 1, PAIR), lambda p: (p, 0, 0))],
        out_specs=(_pair_spec(mixed_pairs.shape[2]), pl.BlockSpec(bias.shape, lambda p: (0, 0, 0))),
        compiler_params=pltpu.CompilerParams(dimension_semantics=("arbitrary",), vmem_limit_bytes=32 * 1024 * 1024),
    )(mixed_pairs, grad_pairs, lse, bias, key_col, key_row)


def lane_blocks(matrix):
    row_blocks, col_blocks = matrix.shape[0] // BLK, matrix.shape[1] // BLK
    shaped = matrix.reshape(row_blocks, BLK, col_blocks, BLK).transpose(0, 2, 1, 3)
    return shaped.reshape(row_blocks * col_blocks, BLK * BLK // LANES, LANES)


ROWS = 112
SQRT_HALF = float(np.sqrt(0.5))
INV_SQRT_TAU = float(1.0 / np.sqrt(2.0 * np.pi))


def _norm(tensor):
    center = tensor - jnp.mean(tensor, -1, keepdims=True)
    inverse = lax.rsqrt(jnp.mean(center * center, -1, keepdims=True) + NORM_EPSILON)
    return center * inverse, inverse


def _mlp_fwd_kernel(att_ref, res_ref, valid_ref, wp_ref, gain_ref, off_ref, w1_ref, w2_ref,
                    hid_ref, act_ref, gelu_ref, out_ref, stat_ref):
    step = pl.program_id(0)
    branch_one = jnp.dot(att_ref[...], wp_ref[...], preferred_element_type=jnp.float32)
    hidden = res_ref[...] + branch_one
    normed, _ = _norm(hidden)
    act = (normed * gain_ref[...] + off_ref[...]).astype(jnp.bfloat16)
    pre = jnp.dot(act, w1_ref[...], preferred_element_type=jnp.float32)
    gelu = ((0.5 * pre) * (1.0 + lax.erf(pre * SQRT_HALF))).astype(jnp.bfloat16)
    branch_two = jnp.dot(gelu, w2_ref[...], preferred_element_type=jnp.float32)
    output = hidden + branch_two
    valid = valid_ref[...]
    first = jnp.sum(valid * output * output)
    second = jnp.sum(valid * (branch_one * branch_one + branch_two * branch_two))
    lane = lax.broadcasted_iota(jnp.int32, (8, 128), 1)
    row = lax.broadcasted_iota(jnp.int32, (8, 128), 0)
    here = jnp.where((row == 0) & (lane == 0), first, 0.0) + jnp.where((row == 0) & (lane == 1), second, 0.0)

    @pl.when(step == 0)
    def _():
        stat_ref[...] = jnp.zeros_like(stat_ref)

    stat_ref[...] = stat_ref[...] + here
    hid_ref[...] = hidden
    act_ref[...] = act
    gelu_ref[...] = gelu
    out_ref[...] = output.astype(out_ref.dtype)


def _mlp_bwd_kernel(gout_ref, hid_ref, act_ref, gain_ref, w1_ref, w2_ref, wp_ref,
                    gpre_ref, ghid_ref, gbr_ref, gatt_ref, small_ref):
    step = pl.program_id(0)
    contract_last = (((1,), (1,)), ((), ()))
    pre = jnp.dot(act_ref[...], w1_ref[...], preferred_element_type=jnp.float32)
    grad_out = gout_ref[...]
    grad_gelu = lax.dot_general(grad_out, w2_ref[...], contract_last, preferred_element_type=jnp.float32)
    cdf = 0.5 * (1.0 + lax.erf(pre * SQRT_HALF))
    pdf = jnp.exp(-0.5 * pre * pre) * INV_SQRT_TAU
    grad_pre = (grad_gelu * (cdf + pre * pdf)).astype(jnp.bfloat16)
    grad_act = lax.dot_general(grad_pre, w1_ref[...], contract_last, preferred_element_type=jnp.float32)
    normed, inverse = _norm(hid_ref[...])
    scaled = grad_act * gain_ref[...]
    mean_one = jnp.mean(scaled, -1, keepdims=True)
    mean_two = jnp.mean(scaled * normed, -1, keepdims=True)
    grad_hidden = grad_out.astype(jnp.float32) + inverse * (scaled - mean_one - normed * mean_two)
    grad_branch = grad_hidden.astype(jnp.bfloat16)
    grad_att = lax.dot_general(grad_branch, wp_ref[...], contract_last, preferred_element_type=jnp.float32)
    sums = jnp.concatenate(
        [jnp.sum(grad_act * normed, 0, keepdims=True), jnp.sum(grad_act, 0, keepdims=True),
         jnp.zeros((6, grad_act.shape[1]), jnp.float32)], 0)

    @pl.when(step == 0)
    def _():
        small_ref[...] = jnp.zeros_like(small_ref)

    small_ref[...] = small_ref[...] + sums
    gpre_ref[...] = grad_pre
    ghid_ref[...] = grad_hidden
    gbr_ref[...] = grad_branch
    gatt_ref[...] = grad_att.astype(gatt_ref.dtype)


def _rows(width):
    return pl.BlockSpec((ROWS, width), lambda i: (i, 0))


def _whole(shape):
    return pl.BlockSpec(shape, lambda i: (0,) * len(shape))


def mlp_fwd(attended, residual, valid, w_proj, gain, offset, w_fc1, w_fc2):
    tokens, width = residual.shape
    hidden_width = w_fc1.shape[1]
    return pl.pallas_call(
        _mlp_fwd_kernel,
        grid=(tokens // ROWS,),
        out_shape=(
            jax.ShapeDtypeStruct((tokens, width), jnp.float32),
            jax.ShapeDtypeStruct((tokens, width), jnp.bfloat16),
            jax.ShapeDtypeStruct((tokens, hidden_width), jnp.bfloat16),
            jax.ShapeDtypeStruct((tokens, width), jnp.bfloat16),
            jax.ShapeDtypeStruct((8, 128), jnp.float32),
        ),
        in_specs=[_rows(width), _rows(width), _rows(1), _whole(w_proj.shape), _whole((1, width)),
                  _whole((1, width)), _whole(w_fc1.shape), _whole(w_fc2.shape)],
        out_specs=(_rows(width), _rows(width), _rows(hidden_width), _rows(width), _whole((8, 128))),
        compiler_params=pltpu.CompilerParams(dimension_semantics=("arbitrary",), vmem_limit_bytes=48 * 1024 * 1024),
    )(attended, residual, valid, w_proj, gain.reshape(1, -1), offset.reshape(1, -1), w_fc1, w_fc2)


def mlp_bwd(grad_out, hidden, act_two, gain, w_fc1, w_fc2, w_proj):
    tokens, width = hidden.shape
    hidden_width = w_fc1.shape[1]
    return pl.pallas_call(
        _mlp_bwd_kernel,
        grid=(tokens // ROWS,),
        out_shape=(
            jax.ShapeDtypeStruct((tokens, hidden_width), jnp.bfloat16),
            jax.ShapeDtypeStruct((tokens, width), jnp.float32),
            jax.ShapeDtypeStruct((tokens, width), jnp.bfloat16),
            jax.ShapeDtypeStruct((tokens, width), jnp.bfloat16),
            jax.ShapeDtypeStruct((8, width), jnp.float32),
        ),
        in_specs=[_rows(width), _rows(width), _rows(width), _whole((1, width)), _whole(w_fc1.shape),
                  _whole(w_fc2.shape), _whole(w_proj.shape)],
        out_specs=(_rows(hidden_width), _rows(width), _rows(width), _rows(width), _whole((8, width))),
        compiler_params=pltpu.CompilerParams(dimension_semantics=("arbitrary",), vmem_limit_bytes=48 * 1024 * 1024),
    )(grad_out, hidden, act_two, gain.reshape(1, -1), w_fc1, w_fc2, w_proj)


def reduce_to_owners(parted, small):
    groups = lax.axis_size("dp")
    dp_bits = groups.bit_length() - 1
    n_qy, n_qx = lax.axis_size("qy"), lax.axis_size("qx")
    count, depth = parted[0].shape[0], parted[0].shape[1]
    per_group = count // groups
    names = [("dp", 1 << power) for power in reversed(range(dp_bits))] + [("qy", 1), ("qx", 1)]
    cross = [("qy", 1)] + [("dp", 1 << power) for power in range(dp_bits)]
    pieces, piece_names, orders = [], [], []
    for index, part in enumerate(parted):
        pieces.append(
            part.reshape([2] * dp_bits + [n_qy, n_qx, per_group * depth // (n_qy * n_qx), LANES])
        )
        piece_names.append(list(names))
        turn = index % len(cross)
        orders.append([("qx", 1)] + cross[turn:] + cross[:turn])
    for stage in range(len(names)):
        for index in range(len(pieces)):
            bit = orders[index][stage]
            place = piece_names[index].index(bit)
            mine = bit_of(*bit)
            keep = lax.dynamic_index_in_dim(pieces[index], mine, place, keepdims=False)
            send = lax.dynamic_index_in_dim(pieces[index], 1 - mine, place, keepdims=False)
            piece_names[index].remove(bit)
            arrived = partner_of(send.astype(jnp.bfloat16), *bit)
            pieces[index] = keep + arrived.astype(jnp.float32)
            if index == 0:
                small = small + partner_of(small, *bit)
                pieces[0], small = lax.optimization_barrier((pieces[0], small))
    chunk = jnp.stack(pieces)
    other = partner_of(chunk, "qy", 1)
    pair = jnp.where(bit_of("qy", 1) == 1, jnp.stack([other, chunk], 1), jnp.stack([chunk, other], 1))
    other = partner_of(pair, "qx", 1)
    quad = jnp.where(bit_of("qx", 1) == 1, jnp.stack([other, pair], 2), jnp.stack([pair, other], 2))
    quad = quad.reshape(len(pieces), per_group, depth, LANES).transpose(1, 0, 2, 3)
    return quad.reshape(per_group, BLK, BLK), small


def cut_along(value, dim, devices):
    before, after = (value.shape[:dim], value.shape[dim + 1 :])
    return jnp.moveaxis(value.reshape(*before, devices, -1, *after), dim, 0)


def sent_and_summed(value, axis, dim):
    pieces = cut_along(value, dim, lax.axis_size(axis))
    arrived = lax.all_to_all(pieces, axis, split_axis=0, concat_axis=0, tiled=True)
    return arrived.astype(jnp.float32).sum(axis=0)


def norm_stats(tensor):
    center = tensor - jnp.mean(tensor, -1, keepdims=True)
    inverse = lax.rsqrt(jnp.mean(center * center, -1, keepdims=True) + NORM_EPSILON)
    return (center * inverse, inverse)


def norm_back(grad_act, normed, inverse, gain):
    scaled = grad_act * gain
    mean_one = jnp.mean(scaled, -1, keepdims=True)
    mean_two = jnp.mean(scaled * normed, -1, keepdims=True)
    return inverse * (scaled - mean_one - normed * mean_two)


def to_windows(tensor):
    canvases, rows_side, cols_side, channels = tensor.shape
    shaped = tensor.reshape(canvases, rows_side // WIN, WIN, cols_side // WIN, WIN, channels)
    return shaped.transpose(0, 1, 3, 2, 4, 5).reshape(
        canvases * (rows_side // WIN) * (cols_side // WIN), WIN * WIN, channels
    )


def from_windows(tensor, canvases, rows_side, cols_side):
    channels = tensor.shape[-1]
    shaped = tensor.reshape(canvases, rows_side // WIN, cols_side // WIN, WIN, WIN, channels)
    return shaped.transpose(0, 1, 3, 2, 4, 5).reshape(canvases, rows_side, cols_side, channels)


def relative_index():
    places = jnp.arange(WIN * WIN, dtype=jnp.int32)
    row_of = places // WIN
    col_of = places % WIN
    return (row_of[:, None] - row_of[None, :] + WIN - 1) * (2 * WIN - 1) + (
        col_of[:, None] - col_of[None, :] + WIN - 1
    )


def region_of(places, full):
    return jnp.where(places < full - WIN, 0, jnp.where(places < full - SHIFT, 1, 2)).astype(
        jnp.int32
    )


def advance(tensor):
    upper = passed_along(tensor[:, :SHIFT], "qy", -1)
    tensor = jnp.concatenate([tensor[:, SHIFT:], upper], 1)
    leftmost = passed_along(tensor[:, :, :SHIFT], "qx", -1)
    return jnp.concatenate([tensor[:, :, SHIFT:], leftmost], 2)


def retreat(tensor):
    lowest = passed_along(tensor[:, -SHIFT:], "qy", 1)
    tensor = jnp.concatenate([lowest, tensor[:, :-SHIFT]], 1)
    rightmost = passed_along(tensor[:, :, -SHIFT:], "qx", 1)
    return jnp.concatenate([rightmost, tensor[:, :, :-SHIFT]], 2)


def blocks_of(matrix):
    row_blocks = matrix.shape[0] // BLK
    col_blocks = matrix.shape[1] // BLK
    return (
        matrix.reshape(row_blocks, BLK, col_blocks, BLK)
        .transpose(0, 2, 1, 3)
        .reshape(row_blocks * col_blocks, BLK, BLK)
    )


def rotate_update(grads, master, first, second, left, right):
    turned = jnp.einsum("sji,sjk->sik", left, grads, precision=ROTATE)
    turned = jnp.einsum("sik,skl->sil", turned, right, precision=ROTATE)
    new_first = BETA_ONE * first + (1.0 - BETA_ONE) * turned
    new_second = BETA_TWO * second + (1.0 - BETA_TWO) * turned * turned
    direction = new_first / (jnp.sqrt(new_second) + ADAM_EPSILON)
    back = jnp.einsum("sij,sjk->sik", left, direction, precision=ROTATE)
    back = jnp.einsum("sik,slk->sil", back, right, precision=ROTATE)
    return (new_first, new_second, master - RATE_BLOCKS * back)


def small_update(grads, params, first, second):
    new_first = BETA_ONE * first + (1.0 - BETA_ONE) * grads
    new_second = BETA_TWO * second + (1.0 - BETA_TWO) * grads * grads
    direction = new_first / (jnp.sqrt(new_second) + ADAM_EPSILON)
    return (new_first, new_second, params - RATE_SMALL * direction)


def local(
    tokens,
    crop_ids,
    merge_order,
    owner_list,
    w_qkv,
    w_proj,
    w_fc1,
    w_fc2,
    small_params,
    small_first,
    small_second,
    master_blocks,
    first_moment,
    second_moment,
    basis_left,
    basis_right,
    merged_grad,
):
    canvases, quad_side, quad_cols, features = tokens.shape
    head_dim = features // HEADS
    score_scale = head_dim ** (-0.5)
    window_area = WIN * WIN
    quarters = lax.axis_size(("qy", "qx"))
    share_rows = quad_side * quad_cols // quarters
    row_base = lax.axis_index("qy") * quad_side
    col_base = lax.axis_index("qx") * quad_cols
    rolled = jnp.roll(crop_ids, (-SHIFT, -SHIFT), (1, 2))
    local_ids = lax.dynamic_slice(
        rolled, (jnp.int32(0), row_base, col_base), (canvases, quad_side, quad_cols)
    )
    region_row = region_of(
        row_base + jnp.arange(quad_side, dtype=jnp.int32), quad_side * lax.axis_size("qy")
    )
    region_col = region_of(
        col_base + jnp.arange(quad_cols, dtype=jnp.int32), quad_cols * lax.axis_size("qx")
    )
    labels = (local_ids + 1) * 9 + region_row[None, :, None] * 3 + region_col[None, None, :]
    win_labels = to_windows(labels[..., None])[..., 0]
    window_count = win_labels.shape[0]
    gain_one = small_params[0:features]
    offset_one = small_params[features : 2 * features]
    gain_two = small_params[2 * features : 3 * features]
    offset_two = small_params[3 * features : 4 * features]
    table = small_params[4 * features :].reshape(HEADS, -1)
    onehot = (
        relative_index().reshape(-1)[:, None]
        == jnp.arange(table.shape[1], dtype=jnp.int32)[None, :]
    ).astype(jnp.float32)
    rel_bias = jnp.einsum("hr,pr->hp", table, onehot, precision=PRECISE).reshape(
        HEADS, window_area, window_area
    )

    pair_area = 2 * window_area
    place = jnp.arange(PAIR, dtype=jnp.int32)
    pair_labels = jnp.pad(win_labels.reshape(-1, pair_area), ((0, 0), (0, PAIR - pair_area)))
    pair_keys = jnp.where(
        place[None] < pair_area,
        pair_labels * 2 + (place[None] >= window_area).astype(jnp.int32),
        -1 - place[None],
    )
    key_col, key_row = pair_keys[:, :, None], pair_keys[:, None, :]
    valid = (pair_labels >= 9).reshape(-1).astype(jnp.float32)[:, None]
    spread = (
        (place[:, None] % window_area == jnp.arange(window_area, dtype=jnp.int32)[None, :])
        & (place[:, None] < pair_area)
    ).astype(jnp.float32)
    dense_bias = jnp.einsum(
        "hti,ui->htu",
        jnp.einsum("ti,hij->htj", spread, rel_bias, precision=PRECISE),
        spread,
        precision=PRECISE,
    )

    def to_pairs(tensor):
        shaped = tensor.reshape(-1, pair_area, tensor.shape[-1])
        return jnp.pad(shaped, ((0, 0), (0, PAIR - pair_area), (0, 0))).reshape(-1, tensor.shape[-1])

    def from_pairs(tensor):
        shaped = tensor.reshape(-1, PAIR, tensor.shape[-1])
        return shaped[:, :pair_area].reshape(-1, window_area, tensor.shape[-1])

    residual = to_pairs(to_windows(advance(tokens)).astype(jnp.float32))
    normed_one, inverse_one = norm_stats(residual)
    act_one = (normed_one * gain_one + offset_one).astype(jnp.bfloat16)
    mixed = jnp.dot(act_one, w_qkv, preferred_element_type=jnp.float32).astype(jnp.bfloat16)
    mixed_pairs = mixed.reshape(-1, PAIR, mixed.shape[-1])
    attended_pairs, log_total = attention_fwd(mixed_pairs, dense_bias, key_col, key_row, score_scale)
    attended = attended_pairs.reshape(-1, features)
    hidden, act_two, gelu_low, output_flat, stat_block = mlp_fwd(
        attended, residual, valid, w_proj, gain_two, offset_two, w_fc1, w_fc2
    )
    stat_terms = jnp.stack([stat_block[0, 0], stat_block[0, 1], jnp.sum(valid) * features])
    output_low = from_pairs(output_flat)
    restored = retreat(from_windows(output_low, canvases, quad_side, quad_cols))
    flat_out = restored.reshape(canvases, quarters, share_rows, features)
    arrived = lax.all_to_all(flat_out, ("qy", "qx"), 1, 1, tiled=True)
    merged = jnp.take(arrived, merge_order, axis=1, mode="clip").transpose(0, 2, 1, 3).reshape(
        canvases, share_rows, quarters * features
    )
    quarter_ids = jnp.arange(quarters, dtype=jnp.int32)
    source_pick = jnp.sum(
        quarter_ids[:, None] * (merge_order[:, None] == quarter_ids[None, :]).astype(jnp.int32), 0
    )
    incoming = merged_grad.reshape(canvases, share_rows, quarters, features)
    unordered = jnp.take(incoming, source_pick, axis=2, mode="clip").transpose(0, 2, 1, 3)
    returned = lax.all_to_all(unordered, ("qy", "qx"), 1, 1, tiled=True)
    grad_orig = returned.reshape(canvases, quad_side, quad_cols, features)
    grad_out = to_pairs(to_windows(advance(grad_orig)))
    grad_pre, grad_hidden, grad_branch, grad_attended, small_two = mlp_bwd(
        grad_out, hidden, act_two, gain_two, w_fc1, w_fc2, w_proj
    )
    grad_fc2 = jnp.einsum("rf,rc->fc", gelu_low, grad_out, preferred_element_type=jnp.float32)
    grad_fc1 = jnp.einsum("rc,rf->cf", act_two, grad_pre, preferred_element_type=jnp.float32)
    grad_proj = jnp.einsum("rc,rd->cd", attended, grad_branch, preferred_element_type=jnp.float32)
    grad_mixed_pairs, dense_grad_bias = attention_bwd(
        mixed_pairs, grad_attended.reshape(-1, PAIR, features), log_total, dense_bias, key_col, key_row, score_scale
    )
    grad_mixed = grad_mixed_pairs.reshape(-1, 3 * features)
    grad_bias = jnp.einsum(
        "ti,htj->hij",
        spread,
        jnp.einsum("htu,uj->htj", dense_grad_bias, spread, precision=PRECISE),
        precision=PRECISE,
    )
    grad_table = jnp.dot(grad_bias.reshape(HEADS, -1), onehot, precision=PRECISE)
    grad_qkv = jnp.einsum("rc,rf->cf", act_one, grad_mixed, preferred_element_type=jnp.float32)
    grad_act_one = jnp.einsum("rf,cf->rc", grad_mixed, w_qkv, preferred_element_type=jnp.float32)
    grad_input = grad_hidden + norm_back(grad_act_one, normed_one, inverse_one, gain_one)
    grad_low = from_pairs(grad_input.astype(jnp.bfloat16))
    grad_tokens = retreat(from_windows(grad_low, canvases, quad_side, quad_cols))
    small_local = jnp.concatenate(
        [
            jnp.sum(grad_act_one * normed_one, 0),
            jnp.sum(grad_act_one, 0),
            small_two[0],
            small_two[1],
            grad_table.reshape(-1),
        ]
    )
    every_block = jnp.concatenate(
        [lane_blocks(grad_qkv), lane_blocks(grad_proj), lane_blocks(grad_fc1), lane_blocks(grad_fc2)],
        0,
    )
    depth = every_block.shape[1] // PARTS
    parted = [
        jnp.take(every_block[:, index * depth : (index + 1) * depth], owner_list, axis=0, mode="clip")
        for index in range(PARTS)
    ]
    owned_grads, small_all = reduce_to_owners(parted, jnp.concatenate([small_local, stat_terms]))
    small_total = small_all[: small_local.shape[0]]
    stat_total = small_all[small_local.shape[0] :]
    new_first, new_second, new_master = rotate_update(
        owned_grads, master_blocks, first_moment, second_moment, basis_left, basis_right
    )
    small_first_new, small_second_new, small_new = small_update(
        small_total, small_params, small_first, small_second
    )
    stats = jnp.stack(
        [jnp.sqrt(stat_total[0] / stat_total[2]), jnp.sqrt(stat_total[1] / (2.0 * stat_total[2]))]
    )
    return (
        merged,
        grad_tokens,
        owned_grads,
        new_master,
        new_first,
        new_second,
        new_master.astype(jnp.bfloat16),
        small_total,
        small_first_new,
        small_second_new,
        small_new,
        stats,
    )


def solution(mesh):
    placed = (
        P("dp", "qy", "qx", None),
        P("dp", None, None),
        P(),
        P(),
        P(),
        P(),
        P(),
        P(),
        P(),
        P(),
        P(),
        P("dp", None, None),
        P("dp", None, None),
        P("dp", None, None),
        P("dp", None, None),
        P("dp", None, None),
        P("dp", ("qy", "qx"), None),
    )
    return jax.shard_map(
        local,
        mesh=mesh,
        in_specs=placed,
        out_specs=(
            P("dp", ("qy", "qx"), None),
            P("dp", "qy", "qx", None),
            P("dp", None, None),
            P("dp", None, None),
            P("dp", None, None),
            P("dp", None, None),
            P("dp", None, None),
            P(),
            P(),
            P(),
            P(),
            P(),
        ),
        check_vma=False,
    )
```

```python
import functools
from functools import partial

import numpy as np

import jax
import jax.numpy as jnp
from jax import lax
from jax.experimental import pallas as pl
from jax.experimental.pallas import tpu as pltpu
from jax.sharding import PartitionSpec as P

HEADS = 12
WIN = 7
SHIFT = 3
BLK = 96


BETA_ONE = 0.5
BETA_TWO = 0.6
ADAM_EPSILON = 1e-08
RATE_BLOCKS = 0.04
RATE_SMALL = 0.2
MASK_FILL = -1e30
NORM_EPSILON = 1e-05
PRECISE = lax.Precision.HIGHEST
ROTATE = lax.Precision.HIGH


def passed_along(value, axis, steps):
    count = lax.axis_size(axis)
    pairs = [(source, (source + steps) % count) for source in range(count)]
    return lax.ppermute(value, axis, pairs)


def partner_of(value, axis, mask):
    count = lax.axis_size(axis)
    pairs = [(source, source ^ mask) for source in range(count)]
    return lax.ppermute(value, axis, pairs)


def bit_of(axis, mask):
    return ((lax.axis_index(axis) & mask) != 0).astype(jnp.int32)


LANES = 128
PARTS = 3
GROUP = 4
LANES = 128
MASK_FILL = -1e30
PAIR = 112
STEP_PAIRS = 2


def _stacked(value, lane4):
    wide = jnp.broadcast_to(value.astype(jnp.float32)[None], (GROUP, PAIR, LANES))
    return jnp.where(lane4, wide, 0.0).reshape(GROUP * PAIR, LANES).astype(jnp.bfloat16)


def _gather_lanes(stack, lane4):
    return jnp.sum(jnp.where(lane4, stack.reshape(GROUP, PAIR, LANES), 0.0), 0)


def _scores(q4, k4, bias4, allowed, scale, lane4):
    raw = lax.dot_general(_stacked(q4, lane4), k4, (((1,), (1,)), ((), ())), preferred_element_type=jnp.float32)
    raw = raw.reshape(GROUP, PAIR, PAIR) * scale + bias4
    return jnp.where(allowed[None], raw, MASK_FILL)


def _lane_masks():
    lane4 = lax.broadcasted_iota(jnp.int32, (GROUP, 1, LANES), 2) // 32 == lax.broadcasted_iota(
        jnp.int32, (GROUP, 1, LANES), 0)
    return lane4, lax.broadcasted_iota(jnp.int32, (1, LANES), 1)


def _fwd_kernel(mix_ref, bias_ref, kc_ref, kr_ref, out_ref, lse_ref, *, scale):
    width = HEADS * 32
    lane4, head_lane = _lane_masks()
    for sub in range(STEP_PAIRS):
        allowed = kc_ref[sub] == kr_ref[sub]
        lse_all = jnp.zeros((PAIR, LANES), jnp.float32)
        for g in range(HEADS // GROUP):
            q4 = mix_ref[sub, :, pl.ds(g * LANES, LANES)]
            k4 = mix_ref[sub, :, pl.ds(width + g * LANES, LANES)]
            v4 = mix_ref[sub, :, pl.ds(2 * width + g * LANES, LANES)]
            s = _scores(q4, k4, bias_ref[pl.ds(g * GROUP, GROUP)], allowed, scale, lane4)
            top = jnp.max(s, -1, keepdims=True)
            e = jnp.exp(s - top)
            total = jnp.sum(e, -1, keepdims=True)
            probs = (e / total).reshape(GROUP * PAIR, PAIR).astype(jnp.bfloat16)
            mixed_out = jnp.dot(probs, v4, preferred_element_type=jnp.float32)
            out_ref[sub, :, pl.ds(g * LANES, LANES)] = _gather_lanes(mixed_out, lane4).astype(out_ref.dtype)
            lse = top + jnp.log(total)
            for j in range(GROUP):
                lse_all = jnp.where(head_lane == g * GROUP + j, lse[j], lse_all)
        lse_ref[sub] = lse_all


def _bwd_kernel(mix_ref, grad_ref, lse_ref, bias_ref, kc_ref, kr_ref, gmix_ref, dbias_ref, *, scale):
    width = HEADS * 32
    lane4, head_lane = _lane_masks()
    step = pl.program_id(0)

    @pl.when(step == 0)
    def _():
        dbias_ref[...] = jnp.zeros_like(dbias_ref)

    for sub in range(STEP_PAIRS):
        allowed = kc_ref[sub] == kr_ref[sub]
        lse_all = lse_ref[sub]
        for g in range(HEADS // GROUP):
            q4 = mix_ref[sub, :, pl.ds(g * LANES, LANES)]
            k4 = mix_ref[sub, :, pl.ds(width + g * LANES, LANES)]
            v4 = mix_ref[sub, :, pl.ds(2 * width + g * LANES, LANES)]
            d4 = grad_ref[sub, :, pl.ds(g * LANES, LANES)]
            heads = pl.ds(g * GROUP, GROUP)
            s = _scores(q4, k4, bias_ref[heads], allowed, scale, lane4)
            lse = jnp.stack([
                jnp.sum(jnp.where(head_lane == g * GROUP + j, lse_all, 0.0), -1, keepdims=True)
                for j in range(GROUP)
            ])
            probs = jnp.exp(s - lse)
            d_stack = _stacked(d4, lane4)
            dprobs = lax.dot_general(d_stack, v4, (((1,), (1,)), ((), ())), preferred_element_type=jnp.float32)
            dprobs = dprobs.reshape(GROUP, PAIR, PAIR)
            inner = jnp.sum(probs * dprobs, -1, keepdims=True)
            dscores = (probs * (dprobs - inner)).reshape(GROUP * PAIR, PAIR).astype(jnp.bfloat16)
            dbias_ref[heads] = dbias_ref[heads] + dscores.astype(jnp.float32).reshape(GROUP, PAIR, PAIR)
            gq = _gather_lanes(jnp.dot(dscores, k4, preferred_element_type=jnp.float32), lane4)
            gk = lax.dot_general(dscores, _stacked(q4, lane4), (((0,), (0,)), ((), ())), preferred_element_type=jnp.float32)
            gv = lax.dot_general(probs.reshape(GROUP * PAIR, PAIR).astype(jnp.bfloat16), d_stack,
                                 (((0,), (0,)), ((), ())), preferred_element_type=jnp.float32)
            gmix_ref[sub, :, pl.ds(g * LANES, LANES)] = (gq * scale).astype(gmix_ref.dtype)
            gmix_ref[sub, :, pl.ds(width + g * LANES, LANES)] = (gk * scale).astype(gmix_ref.dtype)
            gmix_ref[sub, :, pl.ds(2 * width + g * LANES, LANES)] = gv.astype(gmix_ref.dtype)


def _pair_spec(width):
    return pl.BlockSpec((STEP_PAIRS, PAIR, width), lambda p: (p, 0, 0))


def attention_fwd(mixed_pairs, bias, key_col, key_row, scale):
    pairs = mixed_pairs.shape[0]
    kernel = functools.partial(_fwd_kernel, scale=scale)
    return pl.pallas_call(
        kernel,
        grid=(pairs // STEP_PAIRS,),
        out_shape=(
            jax.ShapeDtypeStruct((pairs, PAIR, HEADS * 32), jnp.bfloat16),
            jax.ShapeDtypeStruct((pairs, PAIR, LANES), jnp.float32),
        ),
        in_specs=[_pair_spec(mixed_pairs.shape[2]), pl.BlockSpec(bias.shape, lambda p: (0, 0, 0)),
                  pl.BlockSpec((STEP_PAIRS, PAIR, 1), lambda p: (p, 0, 0)), pl.BlockSpec((STEP_PAIRS, 1, PAIR), lambda p: (p, 0, 0))],
        out_specs=(_pair_spec(HEADS * 32), _pair_spec(LANES)),
        compiler_params=pltpu.CompilerParams(dimension_semantics=("arbitrary",), vmem_limit_bytes=32 * 1024 * 1024),
    )(mixed_pairs, bias, key_col, key_row)


def attention_bwd(mixed_pairs, grad_pairs, lse, bias, key_col, key_row, scale):
    pairs = mixed_pairs.shape[0]
    kernel = functools.partial(_bwd_kernel, scale=scale)
    return pl.pallas_call(
        kernel,
        grid=(pairs // STEP_PAIRS,),
        out_shape=(
            jax.ShapeDtypeStruct(mixed_pairs.shape, jnp.bfloat16),
            jax.ShapeDtypeStruct(bias.shape, jnp.float32),
        ),
        in_specs=[_pair_spec(mixed_pairs.shape[2]), _pair_spec(HEADS * 32), _pair_spec(LANES),
                  pl.BlockSpec(bias.shape, lambda p: (0, 0, 0)),
                  pl.BlockSpec((STEP_PAIRS, PAIR, 1), lambda p: (p, 0, 0)), pl.BlockSpec((STEP_PAIRS, 1, PAIR), lambda p: (p, 0, 0))],
        out_specs=(_pair_spec(mixed_pairs.shape[2]), pl.BlockSpec(bias.shape, lambda p: (0, 0, 0))),
        compiler_params=pltpu.CompilerParams(dimension_semantics=("arbitrary",), vmem_limit_bytes=32 * 1024 * 1024),
    )(mixed_pairs, grad_pairs, lse, bias, key_col, key_row)


def lane_blocks(matrix):
    row_blocks, col_blocks = matrix.shape[0] // BLK, matrix.shape[1] // BLK
    shaped = matrix.reshape(row_blocks, BLK, col_blocks, BLK).transpose(0, 2, 1, 3)
    return shaped.reshape(row_blocks * col_blocks, BLK * BLK // LANES, LANES)


ROWS = 224
SQRT_HALF = float(np.sqrt(0.5))
INV_SQRT_TAU = float(1.0 / np.sqrt(2.0 * np.pi))


def _norm(tensor):
    center = tensor - jnp.mean(tensor, -1, keepdims=True)
    inverse = lax.rsqrt(jnp.mean(center * center, -1, keepdims=True) + NORM_EPSILON)
    return center * inverse, inverse


def _mlp_fwd_kernel(att_ref, res_ref, valid_ref, wp_ref, gain_ref, off_ref, w1_ref, w2_ref,
                    hid_ref, act_ref, gelu_ref, out_ref, stat_ref):
    step = pl.program_id(0)
    branch_one = jnp.dot(att_ref[...], wp_ref[...], preferred_element_type=jnp.float32)
    hidden = res_ref[...] + branch_one
    normed, _ = _norm(hidden)
    act = (normed * gain_ref[...] + off_ref[...]).astype(jnp.bfloat16)
    pre = jnp.dot(act, w1_ref[...], preferred_element_type=jnp.float32)
    gelu = ((0.5 * pre) * (1.0 + lax.erf(pre * SQRT_HALF))).astype(jnp.bfloat16)
    branch_two = jnp.dot(gelu, w2_ref[...], preferred_element_type=jnp.float32)
    output = hidden + branch_two
    valid = valid_ref[...]
    first = jnp.sum(valid * output * output)
    second = jnp.sum(valid * (branch_one * branch_one + branch_two * branch_two))
    lane = lax.broadcasted_iota(jnp.int32, (8, 128), 1)
    row = lax.broadcasted_iota(jnp.int32, (8, 128), 0)
    here = jnp.where((row == 0) & (lane == 0), first, 0.0) + jnp.where((row == 0) & (lane == 1), second, 0.0)

    @pl.when(step == 0)
    def _():
        stat_ref[...] = jnp.zeros_like(stat_ref)

    stat_ref[...] = stat_ref[...] + here
    hid_ref[...] = hidden
    act_ref[...] = act
    gelu_ref[...] = gelu
    out_ref[...] = output.astype(out_ref.dtype)


def _mlp_bwd_kernel(gout_ref, hid_ref, act_ref, gain_ref, w1_ref, w2_ref, wp_ref,
                    gpre_ref, ghid_ref, gbr_ref, gatt_ref, small_ref):
    step = pl.program_id(0)
    contract_last = (((1,), (1,)), ((), ()))
    pre = jnp.dot(act_ref[...], w1_ref[...], preferred_element_type=jnp.float32)
    grad_out = gout_ref[...]
    grad_gelu = lax.dot_general(grad_out, w2_ref[...], contract_last, preferred_element_type=jnp.float32)
    cdf = 0.5 * (1.0 + lax.erf(pre * SQRT_HALF))
    pdf = jnp.exp(-0.5 * pre * pre) * INV_SQRT_TAU
    grad_pre = (grad_gelu * (cdf + pre * pdf)).astype(jnp.bfloat16)
    grad_act = lax.dot_general(grad_pre, w1_ref[...], contract_last, preferred_element_type=jnp.float32)
    normed, inverse = _norm(hid_ref[...])
    scaled = grad_act * gain_ref[...]
    mean_one = jnp.mean(scaled, -1, keepdims=True)
    mean_two = jnp.mean(scaled * normed, -1, keepdims=True)
    grad_hidden = grad_out.astype(jnp.float32) + inverse * (scaled - mean_one - normed * mean_two)
    grad_branch = grad_hidden.astype(jnp.bfloat16)
    grad_att = lax.dot_general(grad_branch, wp_ref[...], contract_last, preferred_element_type=jnp.float32)
    sums = jnp.concatenate(
        [jnp.sum(grad_act * normed, 0, keepdims=True), jnp.sum(grad_act, 0, keepdims=True),
         jnp.zeros((6, grad_act.shape[1]), jnp.float32)], 0)

    @pl.when(step == 0)
    def _():
        small_ref[...] = jnp.zeros_like(small_ref)

    small_ref[...] = small_ref[...] + sums
    gpre_ref[...] = grad_pre
    ghid_ref[...] = grad_hidden
    gbr_ref[...] = grad_branch
    gatt_ref[...] = grad_att.astype(gatt_ref.dtype)


def _rows(width):
    return pl.BlockSpec((ROWS, width), lambda i: (i, 0))


def _whole(shape):
    return pl.BlockSpec(shape, lambda i: (0,) * len(shape))


def mlp_fwd(attended, residual, valid, w_proj, gain, offset, w_fc1, w_fc2):
    tokens, width = residual.shape
    hidden_width = w_fc1.shape[1]
    return pl.pallas_call(
        _mlp_fwd_kernel,
        grid=(tokens // ROWS,),
        out_shape=(
            jax.ShapeDtypeStruct((tokens, width), jnp.float32),
            jax.ShapeDtypeStruct((tokens, width), jnp.bfloat16),
            jax.ShapeDtypeStruct((tokens, hidden_width), jnp.bfloat16),
            jax.ShapeDtypeStruct((tokens, width), jnp.bfloat16),
            jax.ShapeDtypeStruct((8, 128), jnp.float32),
        ),
        in_specs=[_rows(width), _rows(width), _rows(1), _whole(w_proj.shape), _whole((1, width)),
                  _whole((1, width)), _whole(w_fc1.shape), _whole(w_fc2.shape)],
        out_specs=(_rows(width), _rows(width), _rows(hidden_width), _rows(width), _whole((8, 128))),
        compiler_params=pltpu.CompilerParams(dimension_semantics=("arbitrary",), vmem_limit_bytes=48 * 1024 * 1024),
    )(attended, residual, valid, w_proj, gain.reshape(1, -1), offset.reshape(1, -1), w_fc1, w_fc2)


def mlp_bwd(grad_out, hidden, act_two, gain, w_fc1, w_fc2, w_proj):
    tokens, width = hidden.shape
    hidden_width = w_fc1.shape[1]
    return pl.pallas_call(
        _mlp_bwd_kernel,
        grid=(tokens // ROWS,),
        out_shape=(
            jax.ShapeDtypeStruct((tokens, hidden_width), jnp.bfloat16),
            jax.ShapeDtypeStruct((tokens, width), jnp.float32),
            jax.ShapeDtypeStruct((tokens, width), jnp.bfloat16),
            jax.ShapeDtypeStruct((tokens, width), jnp.bfloat16),
            jax.ShapeDtypeStruct((8, width), jnp.float32),
        ),
        in_specs=[_rows(width), _rows(width), _rows(width), _whole((1, width)), _whole(w_fc1.shape),
                  _whole(w_fc2.shape), _whole(w_proj.shape)],
        out_specs=(_rows(hidden_width), _rows(width), _rows(width), _rows(width), _whole((8, width))),
        compiler_params=pltpu.CompilerParams(dimension_semantics=("arbitrary",), vmem_limit_bytes=48 * 1024 * 1024),
    )(grad_out, hidden, act_two, gain.reshape(1, -1), w_fc1, w_fc2, w_proj)


def reduce_to_owners(parted, small):
    groups = lax.axis_size("dp")
    dp_bits = groups.bit_length() - 1
    n_qy, n_qx = lax.axis_size("qy"), lax.axis_size("qx")
    count, depth = parted[0].shape[0], parted[0].shape[1]
    per_group = count // groups
    names = [("dp", 1 << power) for power in reversed(range(dp_bits))] + [("qy", 1), ("qx", 1)]
    cross = [("qy", 1)] + [("dp", 1 << power) for power in range(dp_bits)]
    pieces, piece_names, orders = [], [], []
    for index, part in enumerate(parted):
        pieces.append(
            part.reshape([2] * dp_bits + [n_qy, n_qx, per_group * depth // (n_qy * n_qx), LANES])
        )
        piece_names.append(list(names))
        turn = index % len(cross)
        orders.append([("qx", 1)] + cross[turn:] + cross[:turn])
    for stage in range(len(names)):
        for index in range(len(pieces)):
            bit = orders[index][stage]
            place = piece_names[index].index(bit)
            mine = bit_of(*bit)
            keep = lax.dynamic_index_in_dim(pieces[index], mine, place, keepdims=False)
            send = lax.dynamic_index_in_dim(pieces[index], 1 - mine, place, keepdims=False)
            piece_names[index].remove(bit)
            arrived = partner_of(send.astype(jnp.bfloat16), *bit)
            pieces[index] = keep + arrived.astype(jnp.float32)
            if index == 0:
                small = small + partner_of(small, *bit)
                pieces[0], small = lax.optimization_barrier((pieces[0], small))
    chunk = jnp.stack(pieces)
    other = partner_of(chunk, "qy", 1)
    pair = jnp.where(bit_of("qy", 1) == 1, jnp.stack([other, chunk], 1), jnp.stack([chunk, other], 1))
    other = partner_of(pair, "qx", 1)
    quad = jnp.where(bit_of("qx", 1) == 1, jnp.stack([other, pair], 2), jnp.stack([pair, other], 2))
    quad = quad.reshape(len(pieces), per_group, depth, LANES).transpose(1, 0, 2, 3)
    return quad.reshape(per_group, BLK, BLK), small


def cut_along(value, dim, devices):
    before, after = (value.shape[:dim], value.shape[dim + 1 :])
    return jnp.moveaxis(value.reshape(*before, devices, -1, *after), dim, 0)


def sent_and_summed(value, axis, dim):
    pieces = cut_along(value, dim, lax.axis_size(axis))
    arrived = lax.all_to_all(pieces, axis, split_axis=0, concat_axis=0, tiled=True)
    return arrived.astype(jnp.float32).sum(axis=0)


def norm_stats(tensor):
    center = tensor - jnp.mean(tensor, -1, keepdims=True)
    inverse = lax.rsqrt(jnp.mean(center * center, -1, keepdims=True) + NORM_EPSILON)
    return (center * inverse, inverse)


def norm_back(grad_act, normed, inverse, gain):
    scaled = grad_act * gain
    mean_one = jnp.mean(scaled, -1, keepdims=True)
    mean_two = jnp.mean(scaled * normed, -1, keepdims=True)
    return inverse * (scaled - mean_one - normed * mean_two)


def to_windows(tensor):
    canvases, rows_side, cols_side, channels = tensor.shape
    shaped = tensor.reshape(canvases, rows_side // WIN, WIN, cols_side // WIN, WIN, channels)
    return shaped.transpose(0, 1, 3, 2, 4, 5).reshape(
        canvases * (rows_side // WIN) * (cols_side // WIN), WIN * WIN, channels
    )


def from_windows(tensor, canvases, rows_side, cols_side):
    channels = tensor.shape[-1]
    shaped = tensor.reshape(canvases, rows_side // WIN, cols_side // WIN, WIN, WIN, channels)
    return shaped.transpose(0, 1, 3, 2, 4, 5).reshape(canvases, rows_side, cols_side, channels)


def relative_index():
    places = jnp.arange(WIN * WIN, dtype=jnp.int32)
    row_of = places // WIN
    col_of = places % WIN
    return (row_of[:, None] - row_of[None, :] + WIN - 1) * (2 * WIN - 1) + (
        col_of[:, None] - col_of[None, :] + WIN - 1
    )


def region_of(places, full):
    return jnp.where(places < full - WIN, 0, jnp.where(places < full - SHIFT, 1, 2)).astype(
        jnp.int32
    )


def advance(tensor):
    upper = passed_along(tensor[:, :SHIFT], "qy", -1)
    tensor = jnp.concatenate([tensor[:, SHIFT:], upper], 1)
    leftmost = passed_along(tensor[:, :, :SHIFT], "qx", -1)
    return jnp.concatenate([tensor[:, :, SHIFT:], leftmost], 2)


def retreat(tensor):
    lowest = passed_along(tensor[:, -SHIFT:], "qy", 1)
    tensor = jnp.concatenate([lowest, tensor[:, :-SHIFT]], 1)
    rightmost = passed_along(tensor[:, :, -SHIFT:], "qx", 1)
    return jnp.concatenate([rightmost, tensor[:, :, :-SHIFT]], 2)


def blocks_of(matrix):
    row_blocks = matrix.shape[0] // BLK
    col_blocks = matrix.shape[1] // BLK
    return (
        matrix.reshape(row_blocks, BLK, col_blocks, BLK)
        .transpose(0, 2, 1, 3)
        .reshape(row_blocks * col_blocks, BLK, BLK)
    )


def rotate_update(grads, master, first, second, left, right):
    turned = jnp.einsum("sji,sjk->sik", left, grads, precision=ROTATE)
    turned = jnp.einsum("sik,skl->sil", turned, right, precision=ROTATE)
    new_first = BETA_ONE * first + (1.0 - BETA_ONE) * turned
    new_second = BETA_TWO * second + (1.0 - BETA_TWO) * turned * turned
    direction = new_first / (jnp.sqrt(new_second) + ADAM_EPSILON)
    back = jnp.einsum("sij,sjk->sik", left, direction, precision=ROTATE)
    back = jnp.einsum("sik,slk->sil", back, right, precision=ROTATE)
    return (new_first, new_second, master - RATE_BLOCKS * back)


def small_update(grads, params, first, second):
    new_first = BETA_ONE * first + (1.0 - BETA_ONE) * grads
    new_second = BETA_TWO * second + (1.0 - BETA_TWO) * grads * grads
    direction = new_first / (jnp.sqrt(new_second) + ADAM_EPSILON)
    return (new_first, new_second, params - RATE_SMALL * direction)


def local(
    tokens,
    crop_ids,
    merge_order,
    owner_list,
    w_qkv,
    w_proj,
    w_fc1,
    w_fc2,
    small_params,
    small_first,
    small_second,
    master_blocks,
    first_moment,
    second_moment,
    basis_left,
    basis_right,
    merged_grad,
):
    canvases, quad_side, quad_cols, features = tokens.shape
    head_dim = features // HEADS
    score_scale = head_dim ** (-0.5)
    window_area = WIN * WIN
    quarters = lax.axis_size(("qy", "qx"))
    share_rows = quad_side * quad_cols // quarters
    row_base = lax.axis_index("qy") * quad_side
    col_base = lax.axis_index("qx") * quad_cols
    rolled = jnp.roll(crop_ids, (-SHIFT, -SHIFT), (1, 2))
    local_ids = lax.dynamic_slice(
        rolled, (jnp.int32(0), row_base, col_base), (canvases, quad_side, quad_cols)
    )
    region_row = region_of(
        row_base + jnp.arange(quad_side, dtype=jnp.int32), quad_side * lax.axis_size("qy")
    )
    region_col = region_of(
        col_base + jnp.arange(quad_cols, dtype=jnp.int32), quad_cols * lax.axis_size("qx")
    )
    labels = (local_ids + 1) * 9 + region_row[None, :, None] * 3 + region_col[None, None, :]
    win_labels = to_windows(labels[..., None])[..., 0]
    window_count = win_labels.shape[0]
    gain_one = small_params[0:features]
    offset_one = small_params[features : 2 * features]
    gain_two = small_params[2 * features : 3 * features]
    offset_two = small_params[3 * features : 4 * features]
    table = small_params[4 * features :].reshape(HEADS, -1)
    onehot = (
        relative_index().reshape(-1)[:, None]
        == jnp.arange(table.shape[1], dtype=jnp.int32)[None, :]
    ).astype(jnp.float32)
    rel_bias = jnp.einsum("hr,pr->hp", table, onehot, precision=PRECISE).reshape(
        HEADS, window_area, window_area
    )

    pair_area = 2 * window_area
    place = jnp.arange(PAIR, dtype=jnp.int32)
    pair_labels = jnp.pad(win_labels.reshape(-1, pair_area), ((0, 0), (0, PAIR - pair_area)))
    pair_keys = jnp.where(
        place[None] < pair_area,
        pair_labels * 2 + (place[None] >= window_area).astype(jnp.int32),
        -1 - place[None],
    )
    key_col, key_row = pair_keys[:, :, None], pair_keys[:, None, :]
    valid = (pair_labels >= 9).reshape(-1).astype(jnp.float32)[:, None]
    spread = (
        (place[:, None] % window_area == jnp.arange(window_area, dtype=jnp.int32)[None, :])
        & (place[:, None] < pair_area)
    ).astype(jnp.float32)
    dense_bias = jnp.einsum(
        "hti,ui->htu",
        jnp.einsum("ti,hij->htj", spread, rel_bias, precision=PRECISE),
        spread,
        precision=PRECISE,
    )

    def to_pairs(tensor):
        shaped = tensor.reshape(-1, pair_area, tensor.shape[-1])
        return jnp.pad(shaped, ((0, 0), (0, PAIR - pair_area), (0, 0))).reshape(-1, tensor.shape[-1])

    def from_pairs(tensor):
        shaped = tensor.reshape(-1, PAIR, tensor.shape[-1])
        return shaped[:, :pair_area].reshape(-1, window_area, tensor.shape[-1])

    residual = to_pairs(to_windows(advance(tokens)).astype(jnp.float32))
    normed_one, inverse_one = norm_stats(residual)
    act_one = (normed_one * gain_one + offset_one).astype(jnp.bfloat16)
    mixed = jnp.dot(act_one, w_qkv, preferred_element_type=jnp.float32).astype(jnp.bfloat16)
    mixed_pairs = mixed.reshape(-1, PAIR, mixed.shape[-1])
    attended_pairs, log_total = attention_fwd(mixed_pairs, dense_bias, key_col, key_row, score_scale)
    attended = attended_pairs.reshape(-1, features)
    hidden, act_two, gelu_low, output_flat, stat_block = mlp_fwd(
        attended, residual, valid, w_proj, gain_two, offset_two, w_fc1, w_fc2
    )
    stat_terms = jnp.stack([stat_block[0, 0], stat_block[0, 1], jnp.sum(valid) * features])
    output_low = from_pairs(output_flat)
    restored = retreat(from_windows(output_low, canvases, quad_side, quad_cols))
    flat_out = restored.reshape(canvases, quarters, share_rows, features)
    arrived = lax.all_to_all(flat_out, ("qy", "qx"), 1, 1, tiled=True)
    merged = jnp.take(arrived, merge_order, axis=1, mode="clip").transpose(0, 2, 1, 3).reshape(
        canvases, share_rows, quarters * features
    )
    quarter_ids = jnp.arange(quarters, dtype=jnp.int32)
    source_pick = jnp.sum(
        quarter_ids[:, None] * (merge_order[:, None] == quarter_ids[None, :]).astype(jnp.int32), 0
    )
    incoming = merged_grad.reshape(canvases, share_rows, quarters, features)
    unordered = jnp.take(incoming, source_pick, axis=2, mode="clip").transpose(0, 2, 1, 3)
    returned = lax.all_to_all(unordered, ("qy", "qx"), 1, 1, tiled=True)
    grad_orig = returned.reshape(canvases, quad_side, quad_cols, features)
    grad_out = to_pairs(to_windows(advance(grad_orig)))
    grad_pre, grad_hidden, grad_branch, grad_attended, small_two = mlp_bwd(
        grad_out, hidden, act_two, gain_two, w_fc1, w_fc2, w_proj
    )
    grad_fc2 = jnp.einsum("rf,rc->fc", gelu_low, grad_out, preferred_element_type=jnp.float32)
    grad_fc1 = jnp.einsum("rc,rf->cf", act_two, grad_pre, preferred_element_type=jnp.float32)
    grad_proj = jnp.einsum("rc,rd->cd", attended, grad_branch, preferred_element_type=jnp.float32)
    grad_mixed_pairs, dense_grad_bias = attention_bwd(
        mixed_pairs, grad_attended.reshape(-1, PAIR, features), log_total, dense_bias, key_col, key_row, score_scale
    )
    grad_mixed = grad_mixed_pairs.reshape(-1, 3 * features)
    grad_bias = jnp.einsum(
        "ti,htj->hij",
        spread,
        jnp.einsum("htu,uj->htj", dense_grad_bias, spread, precision=PRECISE),
        precision=PRECISE,
    )
    grad_table = jnp.dot(grad_bias.reshape(HEADS, -1), onehot, precision=PRECISE)
    grad_qkv = jnp.einsum("rc,rf->cf", act_one, grad_mixed, preferred_element_type=jnp.float32)
    grad_act_one = jnp.einsum("rf,cf->rc", grad_mixed, w_qkv, preferred_element_type=jnp.float32)
    grad_input = grad_hidden + norm_back(grad_act_one, normed_one, inverse_one, gain_one)
    grad_low = from_pairs(grad_input.astype(jnp.bfloat16))
    grad_tokens = retreat(from_windows(grad_low, canvases, quad_side, quad_cols))
    small_local = jnp.concatenate(
        [
            jnp.sum(grad_act_one * normed_one, 0),
            jnp.sum(grad_act_one, 0),
            small_two[0],
            small_two[1],
            grad_table.reshape(-1),
        ]
    )
    every_block = jnp.concatenate(
        [lane_blocks(grad_qkv), lane_blocks(grad_proj), lane_blocks(grad_fc1), lane_blocks(grad_fc2)],
        0,
    )
    depth = every_block.shape[1] // PARTS
    parted = [
        jnp.take(every_block[:, index * depth : (index + 1) * depth], owner_list, axis=0, mode="clip")
        for index in range(PARTS)
    ]
    owned_grads, small_all = reduce_to_owners(parted, jnp.concatenate([small_local, stat_terms]))
    small_total = small_all[: small_local.shape[0]]
    stat_total = small_all[small_local.shape[0] :]
    new_first, new_second, new_master = rotate_update(
        owned_grads, master_blocks, first_moment, second_moment, basis_left, basis_right
    )
    small_first_new, small_second_new, small_new = small_update(
        small_total, small_params, small_first, small_second
    )
    stats = jnp.stack(
        [jnp.sqrt(stat_total[0] / stat_total[2]), jnp.sqrt(stat_total[1] / (2.0 * stat_total[2]))]
    )
    return (
        merged,
        grad_tokens,
        owned_grads,
        new_master,
        new_first,
        new_second,
        new_master.astype(jnp.bfloat16),
        small_total,
        small_first_new,
        small_second_new,
        small_new,
        stats,
    )


def solution(mesh):
    placed = (
        P("dp", "qy", "qx", None),
        P("dp", None, None),
        P(),
        P(),
        P(),
        P(),
        P(),
        P(),
        P(),
        P(),
        P(),
        P("dp", None, None),
        P("dp", None, None),
        P("dp", None, None),
        P("dp", None, None),
        P("dp", None, None),
        P("dp", ("qy", "qx"), None),
    )
    return jax.shard_map(
        local,
        mesh=mesh,
        in_specs=placed,
        out_specs=(
            P("dp", ("qy", "qx"), None),
            P("dp", "qy", "qx", None),
            P("dp", None, None),
            P("dp", None, None),
            P("dp", None, None),
            P("dp", None, None),
            P("dp", None, None),
            P(),
            P(),
            P(),
            P(),
            P(),
        ),
        check_vma=False,
    )
```

```python
import functools
from functools import partial

import numpy as np

import jax
import jax.numpy as jnp
from jax import lax
from jax.experimental import pallas as pl
from jax.experimental.pallas import tpu as pltpu
from jax.sharding import PartitionSpec as P

HEADS = 12
WIN = 7
SHIFT = 3
BLK = 96


BETA_ONE = 0.5
BETA_TWO = 0.6
ADAM_EPSILON = 1e-08
RATE_BLOCKS = 0.04
RATE_SMALL = 0.2
MASK_FILL = -1e30
NORM_EPSILON = 1e-05
PRECISE = lax.Precision.HIGHEST
ROTATE = lax.Precision.HIGH


def passed_along(value, axis, steps):
    count = lax.axis_size(axis)
    pairs = [(source, (source + steps) % count) for source in range(count)]
    return lax.ppermute(value, axis, pairs)


def partner_of(value, axis, mask):
    count = lax.axis_size(axis)
    pairs = [(source, source ^ mask) for source in range(count)]
    return lax.ppermute(value, axis, pairs)


def bit_of(axis, mask):
    return ((lax.axis_index(axis) & mask) != 0).astype(jnp.int32)


LANES = 128
PARTS = 3
GROUP = 4
LANES = 128
MASK_FILL = -1e30
PAIR = 112
STEP_PAIRS = 4


def _stacked(value, lane4):
    wide = jnp.broadcast_to(value.astype(jnp.float32)[None], (GROUP, PAIR, LANES))
    return jnp.where(lane4, wide, 0.0).reshape(GROUP * PAIR, LANES).astype(jnp.bfloat16)


def _gather_lanes(stack, lane4):
    return jnp.sum(jnp.where(lane4, stack.reshape(GROUP, PAIR, LANES), 0.0), 0)


def _scores(q4, k4, bias4, allowed, scale, lane4):
    raw = lax.dot_general(_stacked(q4, lane4), k4, (((1,), (1,)), ((), ())), preferred_element_type=jnp.float32)
    raw = raw.reshape(GROUP, PAIR, PAIR) * scale + bias4
    return jnp.where(allowed[None], raw, MASK_FILL)


def _lane_masks():
    lane4 = lax.broadcasted_iota(jnp.int32, (GROUP, 1, LANES), 2) // 32 == lax.broadcasted_iota(
        jnp.int32, (GROUP, 1, LANES), 0)
    return lane4, lax.broadcasted_iota(jnp.int32, (1, LANES), 1)


def _fwd_kernel(mix_ref, bias_ref, kc_ref, kr_ref, out_ref, lse_ref, *, scale):
    width = HEADS * 32
    lane4, head_lane = _lane_masks()
    for sub in range(STEP_PAIRS):
        allowed = kc_ref[sub] == kr_ref[sub]
        lse_all = jnp.zeros((PAIR, LANES), jnp.float32)
        for g in range(HEADS // GROUP):
            q4 = mix_ref[sub, :, pl.ds(g * LANES, LANES)]
            k4 = mix_ref[sub, :, pl.ds(width + g * LANES, LANES)]
            v4 = mix_ref[sub, :, pl.ds(2 * width + g * LANES, LANES)]
            s = _scores(q4, k4, bias_ref[pl.ds(g * GROUP, GROUP)], allowed, scale, lane4)
            top = jnp.max(s, -1, keepdims=True)
            e = jnp.exp(s - top)
            total = jnp.sum(e, -1, keepdims=True)
            probs = (e / total).reshape(GROUP * PAIR, PAIR).astype(jnp.bfloat16)
            mixed_out = jnp.dot(probs, v4, preferred_element_type=jnp.float32)
            out_ref[sub, :, pl.ds(g * LANES, LANES)] = _gather_lanes(mixed_out, lane4).astype(out_ref.dtype)
            lse = top + jnp.log(total)
            for j in range(GROUP):
                lse_all = jnp.where(head_lane == g * GROUP + j, lse[j], lse_all)
        lse_ref[sub] = lse_all


def _bwd_kernel(mix_ref, grad_ref, lse_ref, bias_ref, kc_ref, kr_ref, gmix_ref, dbias_ref, *, scale):
    width = HEADS * 32
    lane4, head_lane = _lane_masks()
    step = pl.program_id(0)

    @pl.when(step == 0)
    def _():
        dbias_ref[...] = jnp.zeros_like(dbias_ref)

    for sub in range(STEP_PAIRS):
        allowed = kc_ref[sub] == kr_ref[sub]
        lse_all = lse_ref[sub]
        for g in range(HEADS // GROUP):
            q4 = mix_ref[sub, :, pl.ds(g * LANES, LANES)]
            k4 = mix_ref[sub, :, pl.ds(width + g * LANES, LANES)]
            v4 = mix_ref[sub, :, pl.ds(2 * width + g * LANES, LANES)]
            d4 = grad_ref[sub, :, pl.ds(g * LANES, LANES)]
            heads = pl.ds(g * GROUP, GROUP)
            s = _scores(q4, k4, bias_ref[heads], allowed, scale, lane4)
            lse = jnp.stack([
                jnp.sum(jnp.where(head_lane == g * GROUP + j, lse_all, 0.0), -1, keepdims=True)
                for j in range(GROUP)
            ])
            probs = jnp.exp(s - lse)
            d_stack = _stacked(d4, lane4)
            dprobs = lax.dot_general(d_stack, v4, (((1,), (1,)), ((), ())), preferred_element_type=jnp.float32)
            dprobs = dprobs.reshape(GROUP, PAIR, PAIR)
            inner = jnp.sum(probs * dprobs, -1, keepdims=True)
            dscores = (probs * (dprobs - inner)).reshape(GROUP * PAIR, PAIR).astype(jnp.bfloat16)
            dbias_ref[heads] = dbias_ref[heads] + dscores.astype(jnp.float32).reshape(GROUP, PAIR, PAIR)
            gq = _gather_lanes(jnp.dot(dscores, k4, preferred_element_type=jnp.float32), lane4)
            gk = lax.dot_general(dscores, _stacked(q4, lane4), (((0,), (0,)), ((), ())), preferred_element_type=jnp.float32)
            gv = lax.dot_general(probs.reshape(GROUP * PAIR, PAIR).astype(jnp.bfloat16), d_stack,
                                 (((0,), (0,)), ((), ())), preferred_element_type=jnp.float32)
            gmix_ref[sub, :, pl.ds(g * LANES, LANES)] = (gq * scale).astype(gmix_ref.dtype)
            gmix_ref[sub, :, pl.ds(width + g * LANES, LANES)] = (gk * scale).astype(gmix_ref.dtype)
            gmix_ref[sub, :, pl.ds(2 * width + g * LANES, LANES)] = gv.astype(gmix_ref.dtype)


def _pair_spec(width):
    return pl.BlockSpec((STEP_PAIRS, PAIR, width), lambda p: (p, 0, 0))


def attention_fwd(mixed_pairs, bias, key_col, key_row, scale):
    pairs = mixed_pairs.shape[0]
    kernel = functools.partial(_fwd_kernel, scale=scale)
    return pl.pallas_call(
        kernel,
        grid=(pairs // STEP_PAIRS,),
        out_shape=(
            jax.ShapeDtypeStruct((pairs, PAIR, HEADS * 32), jnp.bfloat16),
            jax.ShapeDtypeStruct((pairs, PAIR, LANES), jnp.float32),
        ),
        in_specs=[_pair_spec(mixed_pairs.shape[2]), pl.BlockSpec(bias.shape, lambda p: (0, 0, 0)),
                  pl.BlockSpec((STEP_PAIRS, PAIR, 1), lambda p: (p, 0, 0)), pl.BlockSpec((STEP_PAIRS, 1, PAIR), lambda p: (p, 0, 0))],
        out_specs=(_pair_spec(HEADS * 32), _pair_spec(LANES)),
        compiler_params=pltpu.CompilerParams(dimension_semantics=("arbitrary",), vmem_limit_bytes=32 * 1024 * 1024),
    )(mixed_pairs, bias, key_col, key_row)


def attention_bwd(mixed_pairs, grad_pairs, lse, bias, key_col, key_row, scale):
    pairs = mixed_pairs.shape[0]
    kernel = functools.partial(_bwd_kernel, scale=scale)
    return pl.pallas_call(
        kernel,
        grid=(pairs // STEP_PAIRS,),
        out_shape=(
            jax.ShapeDtypeStruct(mixed_pairs.shape, jnp.bfloat16),
            jax.ShapeDtypeStruct(bias.shape, jnp.float32),
        ),
        in_specs=[_pair_spec(mixed_pairs.shape[2]), _pair_spec(HEADS * 32), _pair_spec(LANES),
                  pl.BlockSpec(bias.shape, lambda p: (0, 0, 0)),
                  pl.BlockSpec((STEP_PAIRS, PAIR, 1), lambda p: (p, 0, 0)), pl.BlockSpec((STEP_PAIRS, 1, PAIR), lambda p: (p, 0, 0))],
        out_specs=(_pair_spec(mixed_pairs.shape[2]), pl.BlockSpec(bias.shape, lambda p: (0, 0, 0))),
        compiler_params=pltpu.CompilerParams(dimension_semantics=("arbitrary",), vmem_limit_bytes=32 * 1024 * 1024),
    )(mixed_pairs, grad_pairs, lse, bias, key_col, key_row)


def lane_blocks(matrix):
    row_blocks, col_blocks = matrix.shape[0] // BLK, matrix.shape[1] // BLK
    shaped = matrix.reshape(row_blocks, BLK, col_blocks, BLK).transpose(0, 2, 1, 3)
    return shaped.reshape(row_blocks * col_blocks, BLK * BLK // LANES, LANES)


ROWS = 448
SQRT_HALF = float(np.sqrt(0.5))
INV_SQRT_TAU = float(1.0 / np.sqrt(2.0 * np.pi))


def _norm(tensor):
    center = tensor - jnp.mean(tensor, -1, keepdims=True)
    inverse = lax.rsqrt(jnp.mean(center * center, -1, keepdims=True) + NORM_EPSILON)
    return center * inverse, inverse


def _mlp_fwd_kernel(att_ref, res_ref, valid_ref, wp_ref, gain_ref, off_ref, w1_ref, w2_ref,
                    hid_ref, act_ref, gelu_ref, out_ref, stat_ref):
    step = pl.program_id(0)
    branch_one = jnp.dot(att_ref[...], wp_ref[...], preferred_element_type=jnp.float32)
    hidden = res_ref[...] + branch_one
    normed, _ = _norm(hidden)
    act = (normed * gain_ref[...] + off_ref[...]).astype(jnp.bfloat16)
    pre = jnp.dot(act, w1_ref[...], preferred_element_type=jnp.float32)
    gelu = ((0.5 * pre) * (1.0 + lax.erf(pre * SQRT_HALF))).astype(jnp.bfloat16)
    branch_two = jnp.dot(gelu, w2_ref[...], preferred_element_type=jnp.float32)
    output = hidden + branch_two
    valid = valid_ref[...]
    first = jnp.sum(valid * output * output)
    second = jnp.sum(valid * (branch_one * branch_one + branch_two * branch_two))
    lane = lax.broadcasted_iota(jnp.int32, (8, 128), 1)
    row = lax.broadcasted_iota(jnp.int32, (8, 128), 0)
    here = jnp.where((row == 0) & (lane == 0), first, 0.0) + jnp.where((row == 0) & (lane == 1), second, 0.0)

    @pl.when(step == 0)
    def _():
        stat_ref[...] = jnp.zeros_like(stat_ref)

    stat_ref[...] = stat_ref[...] + here
    hid_ref[...] = hidden
    act_ref[...] = act
    gelu_ref[...] = gelu
    out_ref[...] = output.astype(out_ref.dtype)


def _mlp_bwd_kernel(gout_ref, hid_ref, act_ref, gain_ref, w1_ref, w2_ref, wp_ref,
                    gpre_ref, ghid_ref, gbr_ref, gatt_ref, small_ref):
    step = pl.program_id(0)
    contract_last = (((1,), (1,)), ((), ()))
    pre = jnp.dot(act_ref[...], w1_ref[...], preferred_element_type=jnp.float32)
    grad_out = gout_ref[...]
    grad_gelu = lax.dot_general(grad_out, w2_ref[...], contract_last, preferred_element_type=jnp.float32)
    cdf = 0.5 * (1.0 + lax.erf(pre * SQRT_HALF))
    pdf = jnp.exp(-0.5 * pre * pre) * INV_SQRT_TAU
    grad_pre = (grad_gelu * (cdf + pre * pdf)).astype(jnp.bfloat16)
    grad_act = lax.dot_general(grad_pre, w1_ref[...], contract_last, preferred_element_type=jnp.float32)
    normed, inverse = _norm(hid_ref[...])
    scaled = grad_act * gain_ref[...]
    mean_one = jnp.mean(scaled, -1, keepdims=True)
    mean_two = jnp.mean(scaled * normed, -1, keepdims=True)
    grad_hidden = grad_out.astype(jnp.float32) + inverse * (scaled - mean_one - normed * mean_two)
    grad_branch = grad_hidden.astype(jnp.bfloat16)
    grad_att = lax.dot_general(grad_branch, wp_ref[...], contract_last, preferred_element_type=jnp.float32)
    sums = jnp.concatenate(
        [jnp.sum(grad_act * normed, 0, keepdims=True), jnp.sum(grad_act, 0, keepdims=True),
         jnp.zeros((6, grad_act.shape[1]), jnp.float32)], 0)

    @pl.when(step == 0)
    def _():
        small_ref[...] = jnp.zeros_like(small_ref)

    small_ref[...] = small_ref[...] + sums
    gpre_ref[...] = grad_pre
    ghid_ref[...] = grad_hidden
    gbr_ref[...] = grad_branch
    gatt_ref[...] = grad_att.astype(gatt_ref.dtype)


def _rows(width):
    return pl.BlockSpec((ROWS, width), lambda i: (i, 0))


def _whole(shape):
    return pl.BlockSpec(shape, lambda i: (0,) * len(shape))


def mlp_fwd(attended, residual, valid, w_proj, gain, offset, w_fc1, w_fc2):
    tokens, width = residual.shape
    hidden_width = w_fc1.shape[1]
    return pl.pallas_call(
        _mlp_fwd_kernel,
        grid=(tokens // ROWS,),
        out_shape=(
            jax.ShapeDtypeStruct((tokens, width), jnp.float32),
            jax.ShapeDtypeStruct((tokens, width), jnp.bfloat16),
            jax.ShapeDtypeStruct((tokens, hidden_width), jnp.bfloat16),
            jax.ShapeDtypeStruct((tokens, width), jnp.bfloat16),
            jax.ShapeDtypeStruct((8, 128), jnp.float32),
        ),
        in_specs=[_rows(width), _rows(width), _rows(1), _whole(w_proj.shape), _whole((1, width)),
                  _whole((1, width)), _whole(w_fc1.shape), _whole(w_fc2.shape)],
        out_specs=(_rows(width), _rows(width), _rows(hidden_width), _rows(width), _whole((8, 128))),
        compiler_params=pltpu.CompilerParams(dimension_semantics=("arbitrary",), vmem_limit_bytes=48 * 1024 * 1024),
    )(attended, residual, valid, w_proj, gain.reshape(1, -1), offset.reshape(1, -1), w_fc1, w_fc2)


def mlp_bwd(grad_out, hidden, act_two, gain, w_fc1, w_fc2, w_proj):
    tokens, width = hidden.shape
    hidden_width = w_fc1.shape[1]
    return pl.pallas_call(
        _mlp_bwd_kernel,
        grid=(tokens // ROWS,),
        out_shape=(
            jax.ShapeDtypeStruct((tokens, hidden_width), jnp.bfloat16),
            jax.ShapeDtypeStruct((tokens, width), jnp.float32),
            jax.ShapeDtypeStruct((tokens, width), jnp.bfloat16),
            jax.ShapeDtypeStruct((tokens, width), jnp.bfloat16),
            jax.ShapeDtypeStruct((8, width), jnp.float32),
        ),
        in_specs=[_rows(width), _rows(width), _rows(width), _whole((1, width)), _whole(w_fc1.shape),
                  _whole(w_fc2.shape), _whole(w_proj.shape)],
        out_specs=(_rows(hidden_width), _rows(width), _rows(width), _rows(width), _whole((8, width))),
        compiler_params=pltpu.CompilerParams(dimension_semantics=("arbitrary",), vmem_limit_bytes=48 * 1024 * 1024),
    )(grad_out, hidden, act_two, gain.reshape(1, -1), w_fc1, w_fc2, w_proj)


def reduce_to_owners(parted, small):
    groups = lax.axis_size("dp")
    dp_bits = groups.bit_length() - 1
    n_qy, n_qx = lax.axis_size("qy"), lax.axis_size("qx")
    count, depth = parted[0].shape[0], parted[0].shape[1]
    per_group = count // groups
    names = [("dp", 1 << power) for power in reversed(range(dp_bits))] + [("qy", 1), ("qx", 1)]
    cross = [("qy", 1)] + [("dp", 1 << power) for power in range(dp_bits)]
    pieces, piece_names, orders = [], [], []
    for index, part in enumerate(parted):
        pieces.append(
            part.reshape([2] * dp_bits + [n_qy, n_qx, per_group * depth // (n_qy * n_qx), LANES])
        )
        piece_names.append(list(names))
        turn = index % len(cross)
        orders.append([("qx", 1)] + cross[turn:] + cross[:turn])
    for stage in range(len(names)):
        for index in range(len(pieces)):
            bit = orders[index][stage]
            place = piece_names[index].index(bit)
            mine = bit_of(*bit)
            keep = lax.dynamic_index_in_dim(pieces[index], mine, place, keepdims=False)
            send = lax.dynamic_index_in_dim(pieces[index], 1 - mine, place, keepdims=False)
            piece_names[index].remove(bit)
            arrived = partner_of(send.astype(jnp.bfloat16), *bit)
            pieces[index] = keep + arrived.astype(jnp.float32)
            if index == 0:
                small = small + partner_of(small, *bit)
                pieces[0], small = lax.optimization_barrier((pieces[0], small))
    chunk = jnp.stack(pieces)
    other = partner_of(chunk, "qy", 1)
    pair = jnp.where(bit_of("qy", 1) == 1, jnp.stack([other, chunk], 1), jnp.stack([chunk, other], 1))
    other = partner_of(pair, "qx", 1)
    quad = jnp.where(bit_of("qx", 1) == 1, jnp.stack([other, pair], 2), jnp.stack([pair, other], 2))
    quad = quad.reshape(len(pieces), per_group, depth, LANES).transpose(1, 0, 2, 3)
    return quad.reshape(per_group, BLK, BLK), small


def cut_along(value, dim, devices):
    before, after = (value.shape[:dim], value.shape[dim + 1 :])
    return jnp.moveaxis(value.reshape(*before, devices, -1, *after), dim, 0)


def sent_and_summed(value, axis, dim):
    pieces = cut_along(value, dim, lax.axis_size(axis))
    arrived = lax.all_to_all(pieces, axis, split_axis=0, concat_axis=0, tiled=True)
    return arrived.astype(jnp.float32).sum(axis=0)


def norm_stats(tensor):
    center = tensor - jnp.mean(tensor, -1, keepdims=True)
    inverse = lax.rsqrt(jnp.mean(center * center, -1, keepdims=True) + NORM_EPSILON)
    return (center * inverse, inverse)


def norm_back(grad_act, normed, inverse, gain):
    scaled = grad_act * gain
    mean_one = jnp.mean(scaled, -1, keepdims=True)
    mean_two = jnp.mean(scaled * normed, -1, keepdims=True)
    return inverse * (scaled - mean_one - normed * mean_two)


def to_windows(tensor):
    canvases, rows_side, cols_side, channels = tensor.shape
    shaped = tensor.reshape(canvases, rows_side // WIN, WIN, cols_side // WIN, WIN, channels)
    return shaped.transpose(0, 1, 3, 2, 4, 5).reshape(
        canvases * (rows_side // WIN) * (cols_side // WIN), WIN * WIN, channels
    )


def from_windows(tensor, canvases, rows_side, cols_side):
    channels = tensor.shape[-1]
    shaped = tensor.reshape(canvases, rows_side // WIN, cols_side // WIN, WIN, WIN, channels)
    return shaped.transpose(0, 1, 3, 2, 4, 5).reshape(canvases, rows_side, cols_side, channels)


def relative_index():
    places = jnp.arange(WIN * WIN, dtype=jnp.int32)
    row_of = places // WIN
    col_of = places % WIN
    return (row_of[:, None] - row_of[None, :] + WIN - 1) * (2 * WIN - 1) + (
        col_of[:, None] - col_of[None, :] + WIN - 1
    )


def region_of(places, full):
    return jnp.where(places < full - WIN, 0, jnp.where(places < full - SHIFT, 1, 2)).astype(
        jnp.int32
    )


def advance(tensor):
    upper = passed_along(tensor[:, :SHIFT], "qy", -1)
    tensor = jnp.concatenate([tensor[:, SHIFT:], upper], 1)
    leftmost = passed_along(tensor[:, :, :SHIFT], "qx", -1)
    return jnp.concatenate([tensor[:, :, SHIFT:], leftmost], 2)


def retreat(tensor):
    lowest = passed_along(tensor[:, -SHIFT:], "qy", 1)
    tensor = jnp.concatenate([lowest, tensor[:, :-SHIFT]], 1)
    rightmost = passed_along(tensor[:, :, -SHIFT:], "qx", 1)
    return jnp.concatenate([rightmost, tensor[:, :, :-SHIFT]], 2)


def blocks_of(matrix):
    row_blocks = matrix.shape[0] // BLK
    col_blocks = matrix.shape[1] // BLK
    return (
        matrix.reshape(row_blocks, BLK, col_blocks, BLK)
        .transpose(0, 2, 1, 3)
        .reshape(row_blocks * col_blocks, BLK, BLK)
    )


def rotate_update(grads, master, first, second, left, right):
    turned = jnp.einsum("sji,sjk->sik", left, grads, precision=ROTATE)
    turned = jnp.einsum("sik,skl->sil", turned, right, precision=ROTATE)
    new_first = BETA_ONE * first + (1.0 - BETA_ONE) * turned
    new_second = BETA_TWO * second + (1.0 - BETA_TWO) * turned * turned
    direction = new_first / (jnp.sqrt(new_second) + ADAM_EPSILON)
    back = jnp.einsum("sij,sjk->sik", left, direction, precision=ROTATE)
    back = jnp.einsum("sik,slk->sil", back, right, precision=ROTATE)
    return (new_first, new_second, master - RATE_BLOCKS * back)


def small_update(grads, params, first, second):
    new_first = BETA_ONE * first + (1.0 - BETA_ONE) * grads
    new_second = BETA_TWO * second + (1.0 - BETA_TWO) * grads * grads
    direction = new_first / (jnp.sqrt(new_second) + ADAM_EPSILON)
    return (new_first, new_second, params - RATE_SMALL * direction)


def local(
    tokens,
    crop_ids,
    merge_order,
    owner_list,
    w_qkv,
    w_proj,
    w_fc1,
    w_fc2,
    small_params,
    small_first,
    small_second,
    master_blocks,
    first_moment,
    second_moment,
    basis_left,
    basis_right,
    merged_grad,
):
    canvases, quad_side, quad_cols, features = tokens.shape
    head_dim = features // HEADS
    score_scale = head_dim ** (-0.5)
    window_area = WIN * WIN
    quarters = lax.axis_size(("qy", "qx"))
    share_rows = quad_side * quad_cols // quarters
    row_base = lax.axis_index("qy") * quad_side
    col_base = lax.axis_index("qx") * quad_cols
    rolled = jnp.roll(crop_ids, (-SHIFT, -SHIFT), (1, 2))
    local_ids = lax.dynamic_slice(
        rolled, (jnp.int32(0), row_base, col_base), (canvases, quad_side, quad_cols)
    )
    region_row = region_of(
        row_base + jnp.arange(quad_side, dtype=jnp.int32), quad_side * lax.axis_size("qy")
    )
    region_col = region_of(
        col_base + jnp.arange(quad_cols, dtype=jnp.int32), quad_cols * lax.axis_size("qx")
    )
    labels = (local_ids + 1) * 9 + region_row[None, :, None] * 3 + region_col[None, None, :]
    win_labels = to_windows(labels[..., None])[..., 0]
    window_count = win_labels.shape[0]
    gain_one = small_params[0:features]
    offset_one = small_params[features : 2 * features]
    gain_two = small_params[2 * features : 3 * features]
    offset_two = small_params[3 * features : 4 * features]
    table = small_params[4 * features :].reshape(HEADS, -1)
    onehot = (
        relative_index().reshape(-1)[:, None]
        == jnp.arange(table.shape[1], dtype=jnp.int32)[None, :]
    ).astype(jnp.float32)
    rel_bias = jnp.einsum("hr,pr->hp", table, onehot, precision=PRECISE).reshape(
        HEADS, window_area, window_area
    )

    pair_area = 2 * window_area
    place = jnp.arange(PAIR, dtype=jnp.int32)
    pair_labels = jnp.pad(win_labels.reshape(-1, pair_area), ((0, 0), (0, PAIR - pair_area)))
    pair_keys = jnp.where(
        place[None] < pair_area,
        pair_labels * 2 + (place[None] >= window_area).astype(jnp.int32),
        -1 - place[None],
    )
    key_col, key_row = pair_keys[:, :, None], pair_keys[:, None, :]
    valid = (pair_labels >= 9).reshape(-1).astype(jnp.float32)[:, None]
    spread = (
        (place[:, None] % window_area == jnp.arange(window_area, dtype=jnp.int32)[None, :])
        & (place[:, None] < pair_area)
    ).astype(jnp.float32)
    dense_bias = jnp.einsum(
        "hti,ui->htu",
        jnp.einsum("ti,hij->htj", spread, rel_bias, precision=PRECISE),
        spread,
        precision=PRECISE,
    )

    def to_pairs(tensor):
        shaped = tensor.reshape(-1, pair_area, tensor.shape[-1])
        return jnp.pad(shaped, ((0, 0), (0, PAIR - pair_area), (0, 0))).reshape(-1, tensor.shape[-1])

    def from_pairs(tensor):
        shaped = tensor.reshape(-1, PAIR, tensor.shape[-1])
        return shaped[:, :pair_area].reshape(-1, window_area, tensor.shape[-1])

    residual = to_pairs(to_windows(advance(tokens)).astype(jnp.float32))
    normed_one, inverse_one = norm_stats(residual)
    act_one = (normed_one * gain_one + offset_one).astype(jnp.bfloat16)
    mixed = jnp.dot(act_one, w_qkv, preferred_element_type=jnp.float32).astype(jnp.bfloat16)
    mixed_pairs = mixed.reshape(-1, PAIR, mixed.shape[-1])
    attended_pairs, log_total = attention_fwd(mixed_pairs, dense_bias, key_col, key_row, score_scale)
    attended = attended_pairs.reshape(-1, features)
    hidden, act_two, gelu_low, output_flat, stat_block = mlp_fwd(
        attended, residual, valid, w_proj, gain_two, offset_two, w_fc1, w_fc2
    )
    stat_terms = jnp.stack([stat_block[0, 0], stat_block[0, 1], jnp.sum(valid) * features])
    output_low = from_pairs(output_flat)
    restored = retreat(from_windows(output_low, canvases, quad_side, quad_cols))
    flat_out = restored.reshape(canvases, quarters, share_rows, features)
    arrived = lax.all_to_all(flat_out, ("qy", "qx"), 1, 1, tiled=True)
    merged = jnp.take(arrived, merge_order, axis=1, mode="clip").transpose(0, 2, 1, 3).reshape(
        canvases, share_rows, quarters * features
    )
    quarter_ids = jnp.arange(quarters, dtype=jnp.int32)
    source_pick = jnp.sum(
        quarter_ids[:, None] * (merge_order[:, None] == quarter_ids[None, :]).astype(jnp.int32), 0
    )
    incoming = merged_grad.reshape(canvases, share_rows, quarters, features)
    unordered = jnp.take(incoming, source_pick, axis=2, mode="clip").transpose(0, 2, 1, 3)
    returned = lax.all_to_all(unordered, ("qy", "qx"), 1, 1, tiled=True)
    grad_orig = returned.reshape(canvases, quad_side, quad_cols, features)
    grad_out = to_pairs(to_windows(advance(grad_orig)))
    grad_pre, grad_hidden, grad_branch, grad_attended, small_two = mlp_bwd(
        grad_out, hidden, act_two, gain_two, w_fc1, w_fc2, w_proj
    )
    grad_fc2 = jnp.einsum("rf,rc->fc", gelu_low, grad_out, preferred_element_type=jnp.float32)
    grad_fc1 = jnp.einsum("rc,rf->cf", act_two, grad_pre, preferred_element_type=jnp.float32)
    grad_proj = jnp.einsum("rc,rd->cd", attended, grad_branch, preferred_element_type=jnp.float32)
    grad_mixed_pairs, dense_grad_bias = attention_bwd(
        mixed_pairs, grad_attended.reshape(-1, PAIR, features), log_total, dense_bias, key_col, key_row, score_scale
    )
    grad_mixed = grad_mixed_pairs.reshape(-1, 3 * features)
    grad_bias = jnp.einsum(
        "ti,htj->hij",
        spread,
        jnp.einsum("htu,uj->htj", dense_grad_bias, spread, precision=PRECISE),
        precision=PRECISE,
    )
    grad_table = jnp.dot(grad_bias.reshape(HEADS, -1), onehot, precision=PRECISE)
    grad_qkv = jnp.einsum("rc,rf->cf", act_one, grad_mixed, preferred_element_type=jnp.float32)
    grad_act_one = jnp.einsum("rf,cf->rc", grad_mixed, w_qkv, preferred_element_type=jnp.float32)
    grad_input = grad_hidden + norm_back(grad_act_one, normed_one, inverse_one, gain_one)
    grad_low = from_pairs(grad_input.astype(jnp.bfloat16))
    grad_tokens = retreat(from_windows(grad_low, canvases, quad_side, quad_cols))
    small_local = jnp.concatenate(
        [
            jnp.sum(grad_act_one * normed_one, 0),
            jnp.sum(grad_act_one, 0),
            small_two[0],
            small_two[1],
            grad_table.reshape(-1),
        ]
    )
    every_block = jnp.concatenate(
        [lane_blocks(grad_qkv), lane_blocks(grad_proj), lane_blocks(grad_fc1), lane_blocks(grad_fc2)],
        0,
    )
    depth = every_block.shape[1] // PARTS
    parted = [
        jnp.take(every_block[:, index * depth : (index + 1) * depth], owner_list, axis=0, mode="clip")
        for index in range(PARTS)
    ]
    owned_grads, small_all = reduce_to_owners(parted, jnp.concatenate([small_local, stat_terms]))
    small_total = small_all[: small_local.shape[0]]
    stat_total = small_all[small_local.shape[0] :]
    new_first, new_second, new_master = rotate_update(
        owned_grads, master_blocks, first_moment, second_moment, basis_left, basis_right
    )
    small_first_new, small_second_new, small_new = small_update(
        small_total, small_params, small_first, small_second
    )
    stats = jnp.stack(
        [jnp.sqrt(stat_total[0] / stat_total[2]), jnp.sqrt(stat_total[1] / (2.0 * stat_total[2]))]
    )
    return (
        merged,
        grad_tokens,
        owned_grads,
        new_master,
        new_first,
        new_second,
        new_master.astype(jnp.bfloat16),
        small_total,
        small_first_new,
        small_second_new,
        small_new,
        stats,
    )


def solution(mesh):
    placed = (
        P("dp", "qy", "qx", None),
        P("dp", None, None),
        P(),
        P(),
        P(),
        P(),
        P(),
        P(),
        P(),
        P(),
        P(),
        P("dp", None, None),
        P("dp", None, None),
        P("dp", None, None),
        P("dp", None, None),
        P("dp", None, None),
        P("dp", ("qy", "qx"), None),
    )
    return jax.shard_map(
        local,
        mesh=mesh,
        in_specs=placed,
        out_specs=(
            P("dp", ("qy", "qx"), None),
            P("dp", "qy", "qx", None),
            P("dp", None, None),
            P("dp", None, None),
            P("dp", None, None),
            P("dp", None, None),
            P("dp", None, None),
            P(),
            P(),
            P(),
            P(),
            P(),
        ),
        check_vma=False,
    )
```

```python
import functools
from functools import partial

import numpy as np

import jax
import jax.numpy as jnp
from jax import lax
from jax.experimental import pallas as pl
from jax.experimental.pallas import tpu as pltpu
from jax.sharding import PartitionSpec as P

HEADS = 12
WIN = 7
SHIFT = 3
BLK = 96


BETA_ONE = 0.5
BETA_TWO = 0.6
ADAM_EPSILON = 1e-08
RATE_BLOCKS = 0.04
RATE_SMALL = 0.2
MASK_FILL = -1e30
NORM_EPSILON = 1e-05
PRECISE = lax.Precision.HIGHEST
ROTATE = lax.Precision.HIGH


def passed_along(value, axis, steps):
    count = lax.axis_size(axis)
    pairs = [(source, (source + steps) % count) for source in range(count)]
    return lax.ppermute(value, axis, pairs)


def partner_of(value, axis, mask):
    count = lax.axis_size(axis)
    pairs = [(source, source ^ mask) for source in range(count)]
    return lax.ppermute(value, axis, pairs)


def bit_of(axis, mask):
    return ((lax.axis_index(axis) & mask) != 0).astype(jnp.int32)


LANES = 128
PARTS = 3
GROUP = 4
LANES = 128
MASK_FILL = -1e30
PAIR = 112
STEP_PAIRS = 4


def _stacked(value, lane4):
    wide = jnp.broadcast_to(value.astype(jnp.float32)[None], (GROUP, PAIR, LANES))
    return jnp.where(lane4, wide, 0.0).reshape(GROUP * PAIR, LANES).astype(jnp.bfloat16)


def _gather_lanes(stack, lane4):
    return jnp.sum(jnp.where(lane4, stack.reshape(GROUP, PAIR, LANES), 0.0), 0)


def _scores(q4, k4, bias4, allowed, scale, lane4):
    raw = lax.dot_general(_stacked(q4, lane4), k4, (((1,), (1,)), ((), ())), preferred_element_type=jnp.float32)
    raw = raw.reshape(GROUP, PAIR, PAIR) * scale + bias4
    return jnp.where(allowed[None], raw, MASK_FILL)


def _lane_masks():
    lane4 = lax.broadcasted_iota(jnp.int32, (GROUP, 1, LANES), 2) // 32 == lax.broadcasted_iota(
        jnp.int32, (GROUP, 1, LANES), 0)
    return lane4, lax.broadcasted_iota(jnp.int32, (1, LANES), 1)


def _fwd_kernel(mix_ref, bias_ref, kc_ref, kr_ref, out_ref, lse_ref, *, scale):
    width = HEADS * 32
    lane4, head_lane = _lane_masks()
    for sub in range(STEP_PAIRS):
        allowed = kc_ref[sub] == kr_ref[sub]
        lse_all = jnp.zeros((PAIR, LANES), jnp.float32)
        for g in range(HEADS // GROUP):
            q4 = mix_ref[sub, :, pl.ds(g * LANES, LANES)]
            k4 = mix_ref[sub, :, pl.ds(width + g * LANES, LANES)]
            v4 = mix_ref[sub, :, pl.ds(2 * width + g * LANES, LANES)]
            s = _scores(q4, k4, bias_ref[pl.ds(g * GROUP, GROUP)], allowed, scale, lane4)
            top = jnp.max(s, -1, keepdims=True)
            e = jnp.exp(s - top)
            total = jnp.sum(e, -1, keepdims=True)
            probs = (e / total).reshape(GROUP * PAIR, PAIR).astype(jnp.bfloat16)
            mixed_out = jnp.dot(probs, v4, preferred_element_type=jnp.float32)
            out_ref[sub, :, pl.ds(g * LANES, LANES)] = _gather_lanes(mixed_out, lane4).astype(out_ref.dtype)
            lse = top + jnp.log(total)
            for j in range(GROUP):
                lse_all = jnp.where(head_lane == g * GROUP + j, lse[j], lse_all)
        lse_ref[sub] = lse_all


def _bwd_kernel(mix_ref, grad_ref, lse_ref, bias_ref, kc_ref, kr_ref, gmix_ref, dbias_ref, *, scale):
    width = HEADS * 32
    lane4, head_lane = _lane_masks()
    step = pl.program_id(0)

    @pl.when(step == 0)
    def _():
        dbias_ref[...] = jnp.zeros_like(dbias_ref)

    for sub in range(STEP_PAIRS):
        allowed = kc_ref[sub] == kr_ref[sub]
        lse_all = lse_ref[sub]
        for g in range(HEADS // GROUP):
            q4 = mix_ref[sub, :, pl.ds(g * LANES, LANES)]
            k4 = mix_ref[sub, :, pl.ds(width + g * LANES, LANES)]
            v4 = mix_ref[sub, :, pl.ds(2 * width + g * LANES, LANES)]
            d4 = grad_ref[sub, :, pl.ds(g * LANES, LANES)]
            heads = pl.ds(g * GROUP, GROUP)
            s = _scores(q4, k4, bias_ref[heads], allowed, scale, lane4)
            lse = jnp.stack([
                jnp.sum(jnp.where(head_lane == g * GROUP + j, lse_all, 0.0), -1, keepdims=True)
                for j in range(GROUP)
            ])
            probs = jnp.exp(s - lse)
            d_stack = _stacked(d4, lane4)
            dprobs = lax.dot_general(d_stack, v4, (((1,), (1,)), ((), ())), preferred_element_type=jnp.float32)
            dprobs = dprobs.reshape(GROUP, PAIR, PAIR)
            inner = jnp.sum(probs * dprobs, -1, keepdims=True)
            dscores = (probs * (dprobs - inner)).reshape(GROUP * PAIR, PAIR).astype(jnp.bfloat16)
            dbias_ref[heads] = dbias_ref[heads] + dscores.astype(jnp.float32).reshape(GROUP, PAIR, PAIR)
            gq = _gather_lanes(jnp.dot(dscores, k4, preferred_element_type=jnp.float32), lane4)
            gk = lax.dot_general(dscores, _stacked(q4, lane4), (((0,), (0,)), ((), ())), preferred_element_type=jnp.float32)
            gv = lax.dot_general(probs.reshape(GROUP * PAIR, PAIR).astype(jnp.bfloat16), d_stack,
                                 (((0,), (0,)), ((), ())), preferred_element_type=jnp.float32)
            gmix_ref[sub, :, pl.ds(g * LANES, LANES)] = (gq * scale).astype(gmix_ref.dtype)
            gmix_ref[sub, :, pl.ds(width + g * LANES, LANES)] = (gk * scale).astype(gmix_ref.dtype)
            gmix_ref[sub, :, pl.ds(2 * width + g * LANES, LANES)] = gv.astype(gmix_ref.dtype)


def _pair_spec(width):
    return pl.BlockSpec((STEP_PAIRS, PAIR, width), lambda p: (p, 0, 0))


def attention_fwd(mixed_pairs, bias, key_col, key_row, scale):
    pairs = mixed_pairs.shape[0]
    kernel = functools.partial(_fwd_kernel, scale=scale)
    return pl.pallas_call(
        kernel,
        grid=(pairs // STEP_PAIRS,),
        out_shape=(
            jax.ShapeDtypeStruct((pairs, PAIR, HEADS * 32), jnp.bfloat16),
            jax.ShapeDtypeStruct((pairs, PAIR, LANES), jnp.float32),
        ),
        in_specs=[_pair_spec(mixed_pairs.shape[2]), pl.BlockSpec(bias.shape, lambda p: (0, 0, 0)),
                  pl.BlockSpec((STEP_PAIRS, PAIR, 1), lambda p: (p, 0, 0)), pl.BlockSpec((STEP_PAIRS, 1, PAIR), lambda p: (p, 0, 0))],
        out_specs=(_pair_spec(HEADS * 32), _pair_spec(LANES)),
        compiler_params=pltpu.CompilerParams(dimension_semantics=("arbitrary",), vmem_limit_bytes=32 * 1024 * 1024),
    )(mixed_pairs, bias, key_col, key_row)


def attention_bwd(mixed_pairs, grad_pairs, lse, bias, key_col, key_row, scale):
    pairs = mixed_pairs.shape[0]
    kernel = functools.partial(_bwd_kernel, scale=scale)
    return pl.pallas_call(
        kernel,
        grid=(pairs // STEP_PAIRS,),
        out_shape=(
            jax.ShapeDtypeStruct(mixed_pairs.shape, jnp.bfloat16),
            jax.ShapeDtypeStruct(bias.shape, jnp.float32),
        ),
        in_specs=[_pair_spec(mixed_pairs.shape[2]), _pair_spec(HEADS * 32), _pair_spec(LANES),
                  pl.BlockSpec(bias.shape, lambda p: (0, 0, 0)),
                  pl.BlockSpec((STEP_PAIRS, PAIR, 1), lambda p: (p, 0, 0)), pl.BlockSpec((STEP_PAIRS, 1, PAIR), lambda p: (p, 0, 0))],
        out_specs=(_pair_spec(mixed_pairs.shape[2]), pl.BlockSpec(bias.shape, lambda p: (0, 0, 0))),
        compiler_params=pltpu.CompilerParams(dimension_semantics=("arbitrary",), vmem_limit_bytes=32 * 1024 * 1024),
    )(mixed_pairs, grad_pairs, lse, bias, key_col, key_row)


def grad_blocks(left, right):
    tokens = left.shape[0]
    shaped = jnp.einsum(
        "tai,tbj->abij",
        left.reshape(tokens, -1, BLK),
        right.reshape(tokens, -1, BLK),
        preferred_element_type=jnp.float32,
    )
    return shaped.reshape(-1, BLK * BLK // LANES, LANES)


def lane_blocks(matrix):
    row_blocks, col_blocks = matrix.shape[0] // BLK, matrix.shape[1] // BLK
    shaped = matrix.reshape(row_blocks, BLK, col_blocks, BLK).transpose(0, 2, 1, 3)
    return shaped.reshape(row_blocks * col_blocks, BLK * BLK // LANES, LANES)


ROWS = 448
SQRT_HALF = float(np.sqrt(0.5))
INV_SQRT_TAU = float(1.0 / np.sqrt(2.0 * np.pi))


def _norm(tensor):
    center = tensor - jnp.mean(tensor, -1, keepdims=True)
    inverse = lax.rsqrt(jnp.mean(center * center, -1, keepdims=True) + NORM_EPSILON)
    return center * inverse, inverse


def _mlp_fwd_kernel(att_ref, res_ref, valid_ref, wp_ref, gain_ref, off_ref, w1_ref, w2_ref,
                    hid_ref, act_ref, gelu_ref, out_ref, stat_ref):
    step = pl.program_id(0)
    branch_one = jnp.dot(att_ref[...], wp_ref[...], preferred_element_type=jnp.float32)
    hidden = res_ref[...] + branch_one
    normed, _ = _norm(hidden)
    act = (normed * gain_ref[...] + off_ref[...]).astype(jnp.bfloat16)
    pre = jnp.dot(act, w1_ref[...], preferred_element_type=jnp.float32)
    gelu = ((0.5 * pre) * (1.0 + lax.erf(pre * SQRT_HALF))).astype(jnp.bfloat16)
    branch_two = jnp.dot(gelu, w2_ref[...], preferred_element_type=jnp.float32)
    output = hidden + branch_two
    valid = valid_ref[...]
    first = jnp.sum(valid * output * output)
    second = jnp.sum(valid * (branch_one * branch_one + branch_two * branch_two))
    lane = lax.broadcasted_iota(jnp.int32, (8, 128), 1)
    row = lax.broadcasted_iota(jnp.int32, (8, 128), 0)
    here = jnp.where((row == 0) & (lane == 0), first, 0.0) + jnp.where((row == 0) & (lane == 1), second, 0.0)

    @pl.when(step == 0)
    def _():
        stat_ref[...] = jnp.zeros_like(stat_ref)

    stat_ref[...] = stat_ref[...] + here
    hid_ref[...] = hidden
    act_ref[...] = act
    gelu_ref[...] = gelu
    out_ref[...] = output.astype(out_ref.dtype)


def _mlp_bwd_kernel(gout_ref, hid_ref, act_ref, gain_ref, w1_ref, w2_ref, wp_ref,
                    gpre_ref, ghid_ref, gbr_ref, gatt_ref, small_ref):
    step = pl.program_id(0)
    contract_last = (((1,), (1,)), ((), ()))
    pre = jnp.dot(act_ref[...], w1_ref[...], preferred_element_type=jnp.float32)
    grad_out = gout_ref[...]
    grad_gelu = lax.dot_general(grad_out, w2_ref[...], contract_last, preferred_element_type=jnp.float32)
    cdf = 0.5 * (1.0 + lax.erf(pre * SQRT_HALF))
    pdf = jnp.exp(-0.5 * pre * pre) * INV_SQRT_TAU
    grad_pre = (grad_gelu * (cdf + pre * pdf)).astype(jnp.bfloat16)
    grad_act = lax.dot_general(grad_pre, w1_ref[...], contract_last, preferred_element_type=jnp.float32)
    normed, inverse = _norm(hid_ref[...])
    scaled = grad_act * gain_ref[...]
    mean_one = jnp.mean(scaled, -1, keepdims=True)
    mean_two = jnp.mean(scaled * normed, -1, keepdims=True)
    grad_hidden = grad_out.astype(jnp.float32) + inverse * (scaled - mean_one - normed * mean_two)
    grad_branch = grad_hidden.astype(jnp.bfloat16)
    grad_att = lax.dot_general(grad_branch, wp_ref[...], contract_last, preferred_element_type=jnp.float32)
    sums = jnp.concatenate(
        [jnp.sum(grad_act * normed, 0, keepdims=True), jnp.sum(grad_act, 0, keepdims=True),
         jnp.zeros((6, grad_act.shape[1]), jnp.float32)], 0)

    @pl.when(step == 0)
    def _():
        small_ref[...] = jnp.zeros_like(small_ref)

    small_ref[...] = small_ref[...] + sums
    gpre_ref[...] = grad_pre
    ghid_ref[...] = grad_hidden
    gbr_ref[...] = grad_branch
    gatt_ref[...] = grad_att.astype(gatt_ref.dtype)


def _rows(width):
    return pl.BlockSpec((ROWS, width), lambda i: (i, 0))


def _whole(shape):
    return pl.BlockSpec(shape, lambda i: (0,) * len(shape))


def mlp_fwd(attended, residual, valid, w_proj, gain, offset, w_fc1, w_fc2):
    tokens, width = residual.shape
    hidden_width = w_fc1.shape[1]
    return pl.pallas_call(
        _mlp_fwd_kernel,
        grid=(tokens // ROWS,),
        out_shape=(
            jax.ShapeDtypeStruct((tokens, width), jnp.float32),
            jax.ShapeDtypeStruct((tokens, width), jnp.bfloat16),
            jax.ShapeDtypeStruct((tokens, hidden_width), jnp.bfloat16),
            jax.ShapeDtypeStruct((tokens, width), jnp.bfloat16),
            jax.ShapeDtypeStruct((8, 128), jnp.float32),
        ),
        in_specs=[_rows(width), _rows(width), _rows(1), _whole(w_proj.shape), _whole((1, width)),
                  _whole((1, width)), _whole(w_fc1.shape), _whole(w_fc2.shape)],
        out_specs=(_rows(width), _rows(width), _rows(hidden_width), _rows(width), _whole((8, 128))),
        compiler_params=pltpu.CompilerParams(dimension_semantics=("arbitrary",), vmem_limit_bytes=48 * 1024 * 1024),
    )(attended, residual, valid, w_proj, gain.reshape(1, -1), offset.reshape(1, -1), w_fc1, w_fc2)


def mlp_bwd(grad_out, hidden, act_two, gain, w_fc1, w_fc2, w_proj):
    tokens, width = hidden.shape
    hidden_width = w_fc1.shape[1]
    return pl.pallas_call(
        _mlp_bwd_kernel,
        grid=(tokens // ROWS,),
        out_shape=(
            jax.ShapeDtypeStruct((tokens, hidden_width), jnp.bfloat16),
            jax.ShapeDtypeStruct((tokens, width), jnp.float32),
            jax.ShapeDtypeStruct((tokens, width), jnp.bfloat16),
            jax.ShapeDtypeStruct((tokens, width), jnp.bfloat16),
            jax.ShapeDtypeStruct((8, width), jnp.float32),
        ),
        in_specs=[_rows(width), _rows(width), _rows(width), _whole((1, width)), _whole(w_fc1.shape),
                  _whole(w_fc2.shape), _whole(w_proj.shape)],
        out_specs=(_rows(hidden_width), _rows(width), _rows(width), _rows(width), _whole((8, width))),
        compiler_params=pltpu.CompilerParams(dimension_semantics=("arbitrary",), vmem_limit_bytes=48 * 1024 * 1024),
    )(grad_out, hidden, act_two, gain.reshape(1, -1), w_fc1, w_fc2, w_proj)


def reduce_to_owners(parted, small):
    groups = lax.axis_size("dp")
    dp_bits = groups.bit_length() - 1
    n_qy, n_qx = lax.axis_size("qy"), lax.axis_size("qx")
    count, depth = parted[0].shape[0], parted[0].shape[1]
    per_group = count // groups
    names = [("dp", 1 << power) for power in reversed(range(dp_bits))] + [("qy", 1), ("qx", 1)]
    cross = [("qy", 1)] + [("dp", 1 << power) for power in range(dp_bits)]
    pieces, piece_names, orders = [], [], []
    for index, part in enumerate(parted):
        pieces.append(
            part.reshape([2] * dp_bits + [n_qy, n_qx, per_group * depth // (n_qy * n_qx), LANES])
        )
        piece_names.append(list(names))
        turn = index % len(cross)
        orders.append([("qx", 1)] + cross[turn:] + cross[:turn])
    for stage in range(len(names)):
        for index in range(len(pieces)):
            bit = orders[index][stage]
            place = piece_names[index].index(bit)
            mine = bit_of(*bit)
            keep = lax.dynamic_index_in_dim(pieces[index], mine, place, keepdims=False)
            send = lax.dynamic_index_in_dim(pieces[index], 1 - mine, place, keepdims=False)
            piece_names[index].remove(bit)
            arrived = partner_of(send.astype(jnp.bfloat16), *bit)
            pieces[index] = keep + arrived.astype(jnp.float32)
            if index == 0:
                small = small + partner_of(small, *bit)
                pieces[0], small = lax.optimization_barrier((pieces[0], small))
    chunk = jnp.stack(pieces)
    other = partner_of(chunk, "qy", 1)
    pair = jnp.where(bit_of("qy", 1) == 1, jnp.stack([other, chunk], 1), jnp.stack([chunk, other], 1))
    other = partner_of(pair, "qx", 1)
    quad = jnp.where(bit_of("qx", 1) == 1, jnp.stack([other, pair], 2), jnp.stack([pair, other], 2))
    quad = quad.reshape(len(pieces), per_group, depth, LANES).transpose(1, 0, 2, 3)
    return quad.reshape(per_group, BLK, BLK), small


def cut_along(value, dim, devices):
    before, after = (value.shape[:dim], value.shape[dim + 1 :])
    return jnp.moveaxis(value.reshape(*before, devices, -1, *after), dim, 0)


def sent_and_summed(value, axis, dim):
    pieces = cut_along(value, dim, lax.axis_size(axis))
    arrived = lax.all_to_all(pieces, axis, split_axis=0, concat_axis=0, tiled=True)
    return arrived.astype(jnp.float32).sum(axis=0)


def norm_stats(tensor):
    center = tensor - jnp.mean(tensor, -1, keepdims=True)
    inverse = lax.rsqrt(jnp.mean(center * center, -1, keepdims=True) + NORM_EPSILON)
    return (center * inverse, inverse)


def norm_back(grad_act, normed, inverse, gain):
    scaled = grad_act * gain
    mean_one = jnp.mean(scaled, -1, keepdims=True)
    mean_two = jnp.mean(scaled * normed, -1, keepdims=True)
    return inverse * (scaled - mean_one - normed * mean_two)


def to_windows(tensor):
    canvases, rows_side, cols_side, channels = tensor.shape
    shaped = tensor.reshape(canvases, rows_side // WIN, WIN, cols_side // WIN, WIN, channels)
    return shaped.transpose(0, 1, 3, 2, 4, 5).reshape(
        canvases * (rows_side // WIN) * (cols_side // WIN), WIN * WIN, channels
    )


def from_windows(tensor, canvases, rows_side, cols_side):
    channels = tensor.shape[-1]
    shaped = tensor.reshape(canvases, rows_side // WIN, cols_side // WIN, WIN, WIN, channels)
    return shaped.transpose(0, 1, 3, 2, 4, 5).reshape(canvases, rows_side, cols_side, channels)


def relative_index():
    places = jnp.arange(WIN * WIN, dtype=jnp.int32)
    row_of = places // WIN
    col_of = places % WIN
    return (row_of[:, None] - row_of[None, :] + WIN - 1) * (2 * WIN - 1) + (
        col_of[:, None] - col_of[None, :] + WIN - 1
    )


def region_of(places, full):
    return jnp.where(places < full - WIN, 0, jnp.where(places < full - SHIFT, 1, 2)).astype(
        jnp.int32
    )


def advance(tensor):
    upper = passed_along(tensor[:, :SHIFT], "qy", -1)
    tensor = jnp.concatenate([tensor[:, SHIFT:], upper], 1)
    leftmost = passed_along(tensor[:, :, :SHIFT], "qx", -1)
    return jnp.concatenate([tensor[:, :, SHIFT:], leftmost], 2)


def retreat(tensor):
    lowest = passed_along(tensor[:, -SHIFT:], "qy", 1)
    tensor = jnp.concatenate([lowest, tensor[:, :-SHIFT]], 1)
    rightmost = passed_along(tensor[:, :, -SHIFT:], "qx", 1)
    return jnp.concatenate([rightmost, tensor[:, :, :-SHIFT]], 2)


def blocks_of(matrix):
    row_blocks = matrix.shape[0] // BLK
    col_blocks = matrix.shape[1] // BLK
    return (
        matrix.reshape(row_blocks, BLK, col_blocks, BLK)
        .transpose(0, 2, 1, 3)
        .reshape(row_blocks * col_blocks, BLK, BLK)
    )


def rotate_update(grads, master, first, second, left, right):
    turned = jnp.einsum("sji,sjk->sik", left, grads, precision=ROTATE)
    turned = jnp.einsum("sik,skl->sil", turned, right, precision=ROTATE)
    new_first = BETA_ONE * first + (1.0 - BETA_ONE) * turned
    new_second = BETA_TWO * second + (1.0 - BETA_TWO) * turned * turned
    direction = new_first / (jnp.sqrt(new_second) + ADAM_EPSILON)
    back = jnp.einsum("sij,sjk->sik", left, direction, precision=ROTATE)
    back = jnp.einsum("sik,slk->sil", back, right, precision=ROTATE)
    return (new_first, new_second, master - RATE_BLOCKS * back)


def small_update(grads, params, first, second):
    new_first = BETA_ONE * first + (1.0 - BETA_ONE) * grads
    new_second = BETA_TWO * second + (1.0 - BETA_TWO) * grads * grads
    direction = new_first / (jnp.sqrt(new_second) + ADAM_EPSILON)
    return (new_first, new_second, params - RATE_SMALL * direction)


def local(
    tokens,
    crop_ids,
    merge_order,
    owner_list,
    w_qkv,
    w_proj,
    w_fc1,
    w_fc2,
    small_params,
    small_first,
    small_second,
    master_blocks,
    first_moment,
    second_moment,
    basis_left,
    basis_right,
    merged_grad,
):
    canvases, quad_side, quad_cols, features = tokens.shape
    head_dim = features // HEADS
    score_scale = head_dim ** (-0.5)
    window_area = WIN * WIN
    quarters = lax.axis_size(("qy", "qx"))
    share_rows = quad_side * quad_cols // quarters
    row_base = lax.axis_index("qy") * quad_side
    col_base = lax.axis_index("qx") * quad_cols
    rolled = jnp.roll(crop_ids, (-SHIFT, -SHIFT), (1, 2))
    local_ids = lax.dynamic_slice(
        rolled, (jnp.int32(0), row_base, col_base), (canvases, quad_side, quad_cols)
    )
    region_row = region_of(
        row_base + jnp.arange(quad_side, dtype=jnp.int32), quad_side * lax.axis_size("qy")
    )
    region_col = region_of(
        col_base + jnp.arange(quad_cols, dtype=jnp.int32), quad_cols * lax.axis_size("qx")
    )
    labels = (local_ids + 1) * 9 + region_row[None, :, None] * 3 + region_col[None, None, :]
    win_labels = to_windows(labels[..., None])[..., 0]
    window_count = win_labels.shape[0]
    gain_one = small_params[0:features]
    offset_one = small_params[features : 2 * features]
    gain_two = small_params[2 * features : 3 * features]
    offset_two = small_params[3 * features : 4 * features]
    table = small_params[4 * features :].reshape(HEADS, -1)
    onehot = (
        relative_index().reshape(-1)[:, None]
        == jnp.arange(table.shape[1], dtype=jnp.int32)[None, :]
    ).astype(jnp.float32)
    rel_bias = jnp.einsum("hr,pr->hp", table, onehot, precision=PRECISE).reshape(
        HEADS, window_area, window_area
    )

    pair_area = 2 * window_area
    place = jnp.arange(PAIR, dtype=jnp.int32)
    pair_labels = jnp.pad(win_labels.reshape(-1, pair_area), ((0, 0), (0, PAIR - pair_area)))
    pair_keys = jnp.where(
        place[None] < pair_area,
        pair_labels * 2 + (place[None] >= window_area).astype(jnp.int32),
        -1 - place[None],
    )
    key_col, key_row = pair_keys[:, :, None], pair_keys[:, None, :]
    valid = (pair_labels >= 9).reshape(-1).astype(jnp.float32)[:, None]
    spread = (
        (place[:, None] % window_area == jnp.arange(window_area, dtype=jnp.int32)[None, :])
        & (place[:, None] < pair_area)
    ).astype(jnp.float32)
    dense_bias = jnp.einsum(
        "hti,ui->htu",
        jnp.einsum("ti,hij->htj", spread, rel_bias, precision=PRECISE),
        spread,
        precision=PRECISE,
    )

    def to_pairs(tensor):
        shaped = tensor.reshape(-1, pair_area, tensor.shape[-1])
        return jnp.pad(shaped, ((0, 0), (0, PAIR - pair_area), (0, 0))).reshape(-1, tensor.shape[-1])

    def from_pairs(tensor):
        shaped = tensor.reshape(-1, PAIR, tensor.shape[-1])
        return shaped[:, :pair_area].reshape(-1, window_area, tensor.shape[-1])

    residual = to_pairs(to_windows(advance(tokens)).astype(jnp.float32))
    normed_one, inverse_one = norm_stats(residual)
    act_one = (normed_one * gain_one + offset_one).astype(jnp.bfloat16)
    mixed = jnp.dot(act_one, w_qkv, preferred_element_type=jnp.float32).astype(jnp.bfloat16)
    mixed_pairs = mixed.reshape(-1, PAIR, mixed.shape[-1])
    attended_pairs, log_total = attention_fwd(mixed_pairs, dense_bias, key_col, key_row, score_scale)
    attended = attended_pairs.reshape(-1, features)
    hidden, act_two, gelu_low, output_flat, stat_block = mlp_fwd(
        attended, residual, valid, w_proj, gain_two, offset_two, w_fc1, w_fc2
    )
    stat_terms = jnp.stack([stat_block[0, 0], stat_block[0, 1], jnp.sum(valid) * features])
    output_low = from_pairs(output_flat)
    restored = retreat(from_windows(output_low, canvases, quad_side, quad_cols))
    flat_out = restored.reshape(canvases, quarters, share_rows, features)
    arrived = lax.all_to_all(flat_out, ("qy", "qx"), 1, 1, tiled=True)
    merged = jnp.take(arrived, merge_order, axis=1, mode="clip").transpose(0, 2, 1, 3).reshape(
        canvases, share_rows, quarters * features
    )
    quarter_ids = jnp.arange(quarters, dtype=jnp.int32)
    source_pick = jnp.sum(
        quarter_ids[:, None] * (merge_order[:, None] == quarter_ids[None, :]).astype(jnp.int32), 0
    )
    incoming = merged_grad.reshape(canvases, share_rows, quarters, features)
    unordered = jnp.take(incoming, source_pick, axis=2, mode="clip").transpose(0, 2, 1, 3)
    returned = lax.all_to_all(unordered, ("qy", "qx"), 1, 1, tiled=True)
    grad_orig = returned.reshape(canvases, quad_side, quad_cols, features)
    grad_out = to_pairs(to_windows(advance(grad_orig)))
    grad_pre, grad_hidden, grad_branch, grad_attended, small_two = mlp_bwd(
        grad_out, hidden, act_two, gain_two, w_fc1, w_fc2, w_proj
    )
    blocks_fc2 = grad_blocks(gelu_low, grad_out)
    blocks_fc1 = grad_blocks(act_two, grad_pre)
    blocks_proj = grad_blocks(attended, grad_branch)
    grad_mixed_pairs, dense_grad_bias = attention_bwd(
        mixed_pairs, grad_attended.reshape(-1, PAIR, features), log_total, dense_bias, key_col, key_row, score_scale
    )
    grad_mixed = grad_mixed_pairs.reshape(-1, 3 * features)
    grad_bias = jnp.einsum(
        "ti,htj->hij",
        spread,
        jnp.einsum("htu,uj->htj", dense_grad_bias, spread, precision=PRECISE),
        precision=PRECISE,
    )
    grad_table = jnp.dot(grad_bias.reshape(HEADS, -1), onehot, precision=PRECISE)
    blocks_qkv = grad_blocks(act_one, grad_mixed)
    grad_act_one = jnp.einsum("rf,cf->rc", grad_mixed, w_qkv, preferred_element_type=jnp.float32)
    grad_input = grad_hidden + norm_back(grad_act_one, normed_one, inverse_one, gain_one)
    grad_low = from_pairs(grad_input.astype(jnp.bfloat16))
    grad_tokens = retreat(from_windows(grad_low, canvases, quad_side, quad_cols))
    small_local = jnp.concatenate(
        [
            jnp.sum(grad_act_one * normed_one, 0),
            jnp.sum(grad_act_one, 0),
            small_two[0],
            small_two[1],
            grad_table.reshape(-1),
        ]
    )
    every_block = jnp.concatenate(
        [blocks_qkv, blocks_proj, blocks_fc1, blocks_fc2],
        0,
    )
    depth = every_block.shape[1] // PARTS
    parted = [
        jnp.take(every_block[:, index * depth : (index + 1) * depth], owner_list, axis=0, mode="clip")
        for index in range(PARTS)
    ]
    owned_grads, small_all = reduce_to_owners(parted, jnp.concatenate([small_local, stat_terms]))
    small_total = small_all[: small_local.shape[0]]
    stat_total = small_all[small_local.shape[0] :]
    new_first, new_second, new_master = rotate_update(
        owned_grads, master_blocks, first_moment, second_moment, basis_left, basis_right
    )
    small_first_new, small_second_new, small_new = small_update(
        small_total, small_params, small_first, small_second
    )
    stats = jnp.stack(
        [jnp.sqrt(stat_total[0] / stat_total[2]), jnp.sqrt(stat_total[1] / (2.0 * stat_total[2]))]
    )
    return (
        merged,
        grad_tokens,
        owned_grads,
        new_master,
        new_first,
        new_second,
        new_master.astype(jnp.bfloat16),
        small_total,
        small_first_new,
        small_second_new,
        small_new,
        stats,
    )


def solution(mesh):
    placed = (
        P("dp", "qy", "qx", None),
        P("dp", None, None),
        P(),
        P(),
        P(),
        P(),
        P(),
        P(),
        P(),
        P(),
        P(),
        P("dp", None, None),
        P("dp", None, None),
        P("dp", None, None),
        P("dp", None, None),
        P("dp", None, None),
        P("dp", ("qy", "qx"), None),
    )
    return jax.shard_map(
        local,
        mesh=mesh,
        in_specs=placed,
        out_specs=(
            P("dp", ("qy", "qx"), None),
            P("dp", "qy", "qx", None),
            P("dp", None, None),
            P("dp", None, None),
            P("dp", None, None),
            P("dp", None, None),
            P("dp", None, None),
            P(),
            P(),
            P(),
            P(),
            P(),
        ),
        check_vma=False,
    )
```

```python
import functools
from functools import partial

import numpy as np

import jax
import jax.numpy as jnp
from jax import lax
from jax.experimental import pallas as pl
from jax.experimental.pallas import tpu as pltpu
from jax.sharding import PartitionSpec as P

HEADS = 12
WIN = 7
SHIFT = 3
BLK = 96


BETA_ONE = 0.5
BETA_TWO = 0.6
ADAM_EPSILON = 1e-08
RATE_BLOCKS = 0.04
RATE_SMALL = 0.2
MASK_FILL = -1e30
NORM_EPSILON = 1e-05
PRECISE = lax.Precision.HIGHEST
ROTATE = lax.Precision.HIGH


def passed_along(value, axis, steps):
    count = lax.axis_size(axis)
    pairs = [(source, (source + steps) % count) for source in range(count)]
    return lax.ppermute(value, axis, pairs)


def partner_of(value, axis, mask):
    count = lax.axis_size(axis)
    pairs = [(source, source ^ mask) for source in range(count)]
    return lax.ppermute(value, axis, pairs)


def bit_of(axis, mask):
    return ((lax.axis_index(axis) & mask) != 0).astype(jnp.int32)


LANES = 128
PARTS = 3
GROUP = 4
LANES = 128
MASK_FILL = -1e30
PAIR = 112
STEP_PAIRS = 8


def _stacked(value, lane4):
    wide = jnp.broadcast_to(value.astype(jnp.float32)[None], (GROUP, PAIR, LANES))
    return jnp.where(lane4, wide, 0.0).reshape(GROUP * PAIR, LANES).astype(jnp.bfloat16)


def _gather_lanes(stack, lane4):
    return jnp.sum(jnp.where(lane4, stack.reshape(GROUP, PAIR, LANES), 0.0), 0)


def _scores(q4, k4, bias4, allowed, scale, lane4):
    raw = lax.dot_general(_stacked(q4, lane4), k4, (((1,), (1,)), ((), ())), preferred_element_type=jnp.float32)
    raw = raw.reshape(GROUP, PAIR, PAIR) * scale + bias4
    return jnp.where(allowed[None], raw, MASK_FILL)


def _lane_masks():
    lane4 = lax.broadcasted_iota(jnp.int32, (GROUP, 1, LANES), 2) // 32 == lax.broadcasted_iota(
        jnp.int32, (GROUP, 1, LANES), 0)
    return lane4, lax.broadcasted_iota(jnp.int32, (1, LANES), 1)


def _fwd_kernel(mix_ref, bias_ref, kc_ref, kr_ref, out_ref, lse_ref, *, scale):
    width = HEADS * 32
    lane4, head_lane = _lane_masks()
    for sub in range(STEP_PAIRS):
        allowed = kc_ref[sub] == kr_ref[sub]
        lse_all = jnp.zeros((PAIR, LANES), jnp.float32)
        for g in range(HEADS // GROUP):
            q4 = mix_ref[sub, :, pl.ds(g * LANES, LANES)]
            k4 = mix_ref[sub, :, pl.ds(width + g * LANES, LANES)]
            v4 = mix_ref[sub, :, pl.ds(2 * width + g * LANES, LANES)]
            s = _scores(q4, k4, bias_ref[pl.ds(g * GROUP, GROUP)], allowed, scale, lane4)
            top = jnp.max(s, -1, keepdims=True)
            e = jnp.exp(s - top)
            total = jnp.sum(e, -1, keepdims=True)
            probs = (e / total).reshape(GROUP * PAIR, PAIR).astype(jnp.bfloat16)
            mixed_out = jnp.dot(probs, v4, preferred_element_type=jnp.float32)
            out_ref[sub, :, pl.ds(g * LANES, LANES)] = _gather_lanes(mixed_out, lane4).astype(out_ref.dtype)
            lse = top + jnp.log(total)
            for j in range(GROUP):
                lse_all = jnp.where(head_lane == g * GROUP + j, lse[j], lse_all)
        lse_ref[sub] = lse_all


def _bwd_kernel(mix_ref, grad_ref, lse_ref, bias_ref, kc_ref, kr_ref, gmix_ref, dbias_ref, *, scale):
    width = HEADS * 32
    lane4, head_lane = _lane_masks()
    step = pl.program_id(0)

    @pl.when(step == 0)
    def _():
        dbias_ref[...] = jnp.zeros_like(dbias_ref)

    for sub in range(STEP_PAIRS):
        allowed = kc_ref[sub] == kr_ref[sub]
        lse_all = lse_ref[sub]
        for g in range(HEADS // GROUP):
            q4 = mix_ref[sub, :, pl.ds(g * LANES, LANES)]
            k4 = mix_ref[sub, :, pl.ds(width + g * LANES, LANES)]
            v4 = mix_ref[sub, :, pl.ds(2 * width + g * LANES, LANES)]
            d4 = grad_ref[sub, :, pl.ds(g * LANES, LANES)]
            heads = pl.ds(g * GROUP, GROUP)
            s = _scores(q4, k4, bias_ref[heads], allowed, scale, lane4)
            lse = jnp.stack([
                jnp.sum(jnp.where(head_lane == g * GROUP + j, lse_all, 0.0), -1, keepdims=True)
                for j in range(GROUP)
            ])
            probs = jnp.exp(s - lse)
            d_stack = _stacked(d4, lane4)
            dprobs = lax.dot_general(d_stack, v4, (((1,), (1,)), ((), ())), preferred_element_type=jnp.float32)
            dprobs = dprobs.reshape(GROUP, PAIR, PAIR)
            inner = jnp.sum(probs * dprobs, -1, keepdims=True)
            dscores = (probs * (dprobs - inner)).reshape(GROUP * PAIR, PAIR).astype(jnp.bfloat16)
            dbias_ref[heads] = dbias_ref[heads] + dscores.astype(jnp.float32).reshape(GROUP, PAIR, PAIR)
            gq = _gather_lanes(jnp.dot(dscores, k4, preferred_element_type=jnp.float32), lane4)
            gk = lax.dot_general(dscores, _stacked(q4, lane4), (((0,), (0,)), ((), ())), preferred_element_type=jnp.float32)
            gv = lax.dot_general(probs.reshape(GROUP * PAIR, PAIR).astype(jnp.bfloat16), d_stack,
                                 (((0,), (0,)), ((), ())), preferred_element_type=jnp.float32)
            gmix_ref[sub, :, pl.ds(g * LANES, LANES)] = (gq * scale).astype(gmix_ref.dtype)
            gmix_ref[sub, :, pl.ds(width + g * LANES, LANES)] = (gk * scale).astype(gmix_ref.dtype)
            gmix_ref[sub, :, pl.ds(2 * width + g * LANES, LANES)] = gv.astype(gmix_ref.dtype)


def _pair_spec(width):
    return pl.BlockSpec((STEP_PAIRS, PAIR, width), lambda p: (p, 0, 0))


def attention_fwd(mixed_pairs, bias, key_col, key_row, scale):
    pairs = mixed_pairs.shape[0]
    kernel = functools.partial(_fwd_kernel, scale=scale)
    return pl.pallas_call(
        kernel,
        grid=(pairs // STEP_PAIRS,),
        out_shape=(
            jax.ShapeDtypeStruct((pairs, PAIR, HEADS * 32), jnp.bfloat16),
            jax.ShapeDtypeStruct((pairs, PAIR, LANES), jnp.float32),
        ),
        in_specs=[_pair_spec(mixed_pairs.shape[2]), pl.BlockSpec(bias.shape, lambda p: (0, 0, 0)),
                  pl.BlockSpec((STEP_PAIRS, PAIR, 1), lambda p: (p, 0, 0)), pl.BlockSpec((STEP_PAIRS, 1, PAIR), lambda p: (p, 0, 0))],
        out_specs=(_pair_spec(HEADS * 32), _pair_spec(LANES)),
        compiler_params=pltpu.CompilerParams(dimension_semantics=("arbitrary",), vmem_limit_bytes=32 * 1024 * 1024),
    )(mixed_pairs, bias, key_col, key_row)


def attention_bwd(mixed_pairs, grad_pairs, lse, bias, key_col, key_row, scale):
    pairs = mixed_pairs.shape[0]
    kernel = functools.partial(_bwd_kernel, scale=scale)
    return pl.pallas_call(
        kernel,
        grid=(pairs // STEP_PAIRS,),
        out_shape=(
            jax.ShapeDtypeStruct(mixed_pairs.shape, jnp.bfloat16),
            jax.ShapeDtypeStruct(bias.shape, jnp.float32),
        ),
        in_specs=[_pair_spec(mixed_pairs.shape[2]), _pair_spec(HEADS * 32), _pair_spec(LANES),
                  pl.BlockSpec(bias.shape, lambda p: (0, 0, 0)),
                  pl.BlockSpec((STEP_PAIRS, PAIR, 1), lambda p: (p, 0, 0)), pl.BlockSpec((STEP_PAIRS, 1, PAIR), lambda p: (p, 0, 0))],
        out_specs=(_pair_spec(mixed_pairs.shape[2]), pl.BlockSpec(bias.shape, lambda p: (0, 0, 0))),
        compiler_params=pltpu.CompilerParams(dimension_semantics=("arbitrary",), vmem_limit_bytes=32 * 1024 * 1024),
    )(mixed_pairs, grad_pairs, lse, bias, key_col, key_row)


def lane_blocks(matrix):
    row_blocks, col_blocks = matrix.shape[0] // BLK, matrix.shape[1] // BLK
    shaped = matrix.reshape(row_blocks, BLK, col_blocks, BLK).transpose(0, 2, 1, 3)
    return shaped.reshape(row_blocks * col_blocks, BLK * BLK // LANES, LANES)


ROWS = 896
SQRT_HALF = float(np.sqrt(0.5))
INV_SQRT_TAU = float(1.0 / np.sqrt(2.0 * np.pi))


def _norm(tensor):
    center = tensor - jnp.mean(tensor, -1, keepdims=True)
    inverse = lax.rsqrt(jnp.mean(center * center, -1, keepdims=True) + NORM_EPSILON)
    return center * inverse, inverse


def _mlp_fwd_kernel(att_ref, res_ref, valid_ref, wp_ref, gain_ref, off_ref, w1_ref, w2_ref,
                    hid_ref, act_ref, gelu_ref, out_ref, stat_ref):
    step = pl.program_id(0)
    branch_one = jnp.dot(att_ref[...], wp_ref[...], preferred_element_type=jnp.float32)
    hidden = res_ref[...] + branch_one
    normed, _ = _norm(hidden)
    act = (normed * gain_ref[...] + off_ref[...]).astype(jnp.bfloat16)
    pre = jnp.dot(act, w1_ref[...], preferred_element_type=jnp.float32)
    gelu = ((0.5 * pre) * (1.0 + lax.erf(pre * SQRT_HALF))).astype(jnp.bfloat16)
    branch_two = jnp.dot(gelu, w2_ref[...], preferred_element_type=jnp.float32)
    output = hidden + branch_two
    valid = valid_ref[...]
    first = jnp.sum(valid * output * output)
    second = jnp.sum(valid * (branch_one * branch_one + branch_two * branch_two))
    lane = lax.broadcasted_iota(jnp.int32, (8, 128), 1)
    row = lax.broadcasted_iota(jnp.int32, (8, 128), 0)
    here = jnp.where((row == 0) & (lane == 0), first, 0.0) + jnp.where((row == 0) & (lane == 1), second, 0.0)

    @pl.when(step == 0)
    def _():
        stat_ref[...] = jnp.zeros_like(stat_ref)

    stat_ref[...] = stat_ref[...] + here
    hid_ref[...] = hidden
    act_ref[...] = act
    gelu_ref[...] = gelu
    out_ref[...] = output.astype(out_ref.dtype)


def _mlp_bwd_kernel(gout_ref, hid_ref, act_ref, gain_ref, w1_ref, w2_ref, wp_ref,
                    gpre_ref, ghid_ref, gbr_ref, gatt_ref, small_ref):
    step = pl.program_id(0)
    contract_last = (((1,), (1,)), ((), ()))
    pre = jnp.dot(act_ref[...], w1_ref[...], preferred_element_type=jnp.float32)
    grad_out = gout_ref[...]
    grad_gelu = lax.dot_general(grad_out, w2_ref[...], contract_last, preferred_element_type=jnp.float32)
    cdf = 0.5 * (1.0 + lax.erf(pre * SQRT_HALF))
    pdf = jnp.exp(-0.5 * pre * pre) * INV_SQRT_TAU
    grad_pre = (grad_gelu * (cdf + pre * pdf)).astype(jnp.bfloat16)
    grad_act = lax.dot_general(grad_pre, w1_ref[...], contract_last, preferred_element_type=jnp.float32)
    normed, inverse = _norm(hid_ref[...])
    scaled = grad_act * gain_ref[...]
    mean_one = jnp.mean(scaled, -1, keepdims=True)
    mean_two = jnp.mean(scaled * normed, -1, keepdims=True)
    grad_hidden = grad_out.astype(jnp.float32) + inverse * (scaled - mean_one - normed * mean_two)
    grad_branch = grad_hidden.astype(jnp.bfloat16)
    grad_att = lax.dot_general(grad_branch, wp_ref[...], contract_last, preferred_element_type=jnp.float32)
    sums = jnp.concatenate(
        [jnp.sum(grad_act * normed, 0, keepdims=True), jnp.sum(grad_act, 0, keepdims=True),
         jnp.zeros((6, grad_act.shape[1]), jnp.float32)], 0)

    @pl.when(step == 0)
    def _():
        small_ref[...] = jnp.zeros_like(small_ref)

    small_ref[...] = small_ref[...] + sums
    gpre_ref[...] = grad_pre
    ghid_ref[...] = grad_hidden
    gbr_ref[...] = grad_branch
    gatt_ref[...] = grad_att.astype(gatt_ref.dtype)


def _rows(width):
    return pl.BlockSpec((ROWS, width), lambda i: (i, 0))


def _whole(shape):
    return pl.BlockSpec(shape, lambda i: (0,) * len(shape))


def mlp_fwd(attended, residual, valid, w_proj, gain, offset, w_fc1, w_fc2):
    tokens, width = residual.shape
    hidden_width = w_fc1.shape[1]
    return pl.pallas_call(
        _mlp_fwd_kernel,
        grid=(tokens // ROWS,),
        out_shape=(
            jax.ShapeDtypeStruct((tokens, width), jnp.float32),
            jax.ShapeDtypeStruct((tokens, width), jnp.bfloat16),
            jax.ShapeDtypeStruct((tokens, hidden_width), jnp.bfloat16),
            jax.ShapeDtypeStruct((tokens, width), jnp.bfloat16),
            jax.ShapeDtypeStruct((8, 128), jnp.float32),
        ),
        in_specs=[_rows(width), _rows(width), _rows(1), _whole(w_proj.shape), _whole((1, width)),
                  _whole((1, width)), _whole(w_fc1.shape), _whole(w_fc2.shape)],
        out_specs=(_rows(width), _rows(width), _rows(hidden_width), _rows(width), _whole((8, 128))),
        compiler_params=pltpu.CompilerParams(dimension_semantics=("arbitrary",), vmem_limit_bytes=48 * 1024 * 1024),
    )(attended, residual, valid, w_proj, gain.reshape(1, -1), offset.reshape(1, -1), w_fc1, w_fc2)


def mlp_bwd(grad_out, hidden, act_two, gain, w_fc1, w_fc2, w_proj):
    tokens, width = hidden.shape
    hidden_width = w_fc1.shape[1]
    return pl.pallas_call(
        _mlp_bwd_kernel,
        grid=(tokens // ROWS,),
        out_shape=(
            jax.ShapeDtypeStruct((tokens, hidden_width), jnp.bfloat16),
            jax.ShapeDtypeStruct((tokens, width), jnp.float32),
            jax.ShapeDtypeStruct((tokens, width), jnp.bfloat16),
            jax.ShapeDtypeStruct((tokens, width), jnp.bfloat16),
            jax.ShapeDtypeStruct((8, width), jnp.float32),
        ),
        in_specs=[_rows(width), _rows(width), _rows(width), _whole((1, width)), _whole(w_fc1.shape),
                  _whole(w_fc2.shape), _whole(w_proj.shape)],
        out_specs=(_rows(hidden_width), _rows(width), _rows(width), _rows(width), _whole((8, width))),
        compiler_params=pltpu.CompilerParams(dimension_semantics=("arbitrary",), vmem_limit_bytes=48 * 1024 * 1024),
    )(grad_out, hidden, act_two, gain.reshape(1, -1), w_fc1, w_fc2, w_proj)


def reduce_to_owners(parted, small):
    groups = lax.axis_size("dp")
    dp_bits = groups.bit_length() - 1
    n_qy, n_qx = lax.axis_size("qy"), lax.axis_size("qx")
    count, depth = parted[0].shape[0], parted[0].shape[1]
    per_group = count // groups
    names = [("dp", 1 << power) for power in reversed(range(dp_bits))] + [("qy", 1), ("qx", 1)]
    cross = [("qy", 1)] + [("dp", 1 << power) for power in range(dp_bits)]
    pieces, piece_names, orders = [], [], []
    for index, part in enumerate(parted):
        pieces.append(
            part.reshape([2] * dp_bits + [n_qy, n_qx, per_group * depth // (n_qy * n_qx), LANES])
        )
        piece_names.append(list(names))
        turn = index % len(cross)
        orders.append([("qx", 1)] + cross[turn:] + cross[:turn])
    for stage in range(len(names)):
        for index in range(len(pieces)):
            bit = orders[index][stage]
            place = piece_names[index].index(bit)
            mine = bit_of(*bit)
            keep = lax.dynamic_index_in_dim(pieces[index], mine, place, keepdims=False)
            send = lax.dynamic_index_in_dim(pieces[index], 1 - mine, place, keepdims=False)
            piece_names[index].remove(bit)
            arrived = partner_of(send.astype(jnp.bfloat16), *bit)
            pieces[index] = keep + arrived.astype(jnp.float32)
            if index == 0:
                small = small + partner_of(small, *bit)
                pieces[0], small = lax.optimization_barrier((pieces[0], small))
    chunk = jnp.stack(pieces)
    other = partner_of(chunk, "qy", 1)
    pair = jnp.where(bit_of("qy", 1) == 1, jnp.stack([other, chunk], 1), jnp.stack([chunk, other], 1))
    other = partner_of(pair, "qx", 1)
    quad = jnp.where(bit_of("qx", 1) == 1, jnp.stack([other, pair], 2), jnp.stack([pair, other], 2))
    quad = quad.reshape(len(pieces), per_group, depth, LANES).transpose(1, 0, 2, 3)
    return quad.reshape(per_group, BLK, BLK), small


def cut_along(value, dim, devices):
    before, after = (value.shape[:dim], value.shape[dim + 1 :])
    return jnp.moveaxis(value.reshape(*before, devices, -1, *after), dim, 0)


def sent_and_summed(value, axis, dim):
    pieces = cut_along(value, dim, lax.axis_size(axis))
    arrived = lax.all_to_all(pieces, axis, split_axis=0, concat_axis=0, tiled=True)
    return arrived.astype(jnp.float32).sum(axis=0)


def norm_stats(tensor):
    center = tensor - jnp.mean(tensor, -1, keepdims=True)
    inverse = lax.rsqrt(jnp.mean(center * center, -1, keepdims=True) + NORM_EPSILON)
    return (center * inverse, inverse)


def norm_back(grad_act, normed, inverse, gain):
    scaled = grad_act * gain
    mean_one = jnp.mean(scaled, -1, keepdims=True)
    mean_two = jnp.mean(scaled * normed, -1, keepdims=True)
    return inverse * (scaled - mean_one - normed * mean_two)


def to_windows(tensor):
    canvases, rows_side, cols_side, channels = tensor.shape
    shaped = tensor.reshape(canvases, rows_side // WIN, WIN, cols_side // WIN, WIN, channels)
    return shaped.transpose(0, 1, 3, 2, 4, 5).reshape(
        canvases * (rows_side // WIN) * (cols_side // WIN), WIN * WIN, channels
    )


def from_windows(tensor, canvases, rows_side, cols_side):
    channels = tensor.shape[-1]
    shaped = tensor.reshape(canvases, rows_side // WIN, cols_side // WIN, WIN, WIN, channels)
    return shaped.transpose(0, 1, 3, 2, 4, 5).reshape(canvases, rows_side, cols_side, channels)


def relative_index():
    places = jnp.arange(WIN * WIN, dtype=jnp.int32)
    row_of = places // WIN
    col_of = places % WIN
    return (row_of[:, None] - row_of[None, :] + WIN - 1) * (2 * WIN - 1) + (
        col_of[:, None] - col_of[None, :] + WIN - 1
    )


def region_of(places, full):
    return jnp.where(places < full - WIN, 0, jnp.where(places < full - SHIFT, 1, 2)).astype(
        jnp.int32
    )


def advance(tensor):
    upper = passed_along(tensor[:, :SHIFT], "qy", -1)
    tensor = jnp.concatenate([tensor[:, SHIFT:], upper], 1)
    leftmost = passed_along(tensor[:, :, :SHIFT], "qx", -1)
    return jnp.concatenate([tensor[:, :, SHIFT:], leftmost], 2)


def retreat(tensor):
    lowest = passed_along(tensor[:, -SHIFT:], "qy", 1)
    tensor = jnp.concatenate([lowest, tensor[:, :-SHIFT]], 1)
    rightmost = passed_along(tensor[:, :, -SHIFT:], "qx", 1)
    return jnp.concatenate([rightmost, tensor[:, :, :-SHIFT]], 2)


def blocks_of(matrix):
    row_blocks = matrix.shape[0] // BLK
    col_blocks = matrix.shape[1] // BLK
    return (
        matrix.reshape(row_blocks, BLK, col_blocks, BLK)
        .transpose(0, 2, 1, 3)
        .reshape(row_blocks * col_blocks, BLK, BLK)
    )


def rotate_update(grads, master, first, second, left, right):
    turned = jnp.einsum("sji,sjk->sik", left, grads, precision=ROTATE)
    turned = jnp.einsum("sik,skl->sil", turned, right, precision=ROTATE)
    new_first = BETA_ONE * first + (1.0 - BETA_ONE) * turned
    new_second = BETA_TWO * second + (1.0 - BETA_TWO) * turned * turned
    direction = new_first / (jnp.sqrt(new_second) + ADAM_EPSILON)
    back = jnp.einsum("sij,sjk->sik", left, direction, precision=ROTATE)
    back = jnp.einsum("sik,slk->sil", back, right, precision=ROTATE)
    return (new_first, new_second, master - RATE_BLOCKS * back)


def small_update(grads, params, first, second):
    new_first = BETA_ONE * first + (1.0 - BETA_ONE) * grads
    new_second = BETA_TWO * second + (1.0 - BETA_TWO) * grads * grads
    direction = new_first / (jnp.sqrt(new_second) + ADAM_EPSILON)
    return (new_first, new_second, params - RATE_SMALL * direction)


def local(
    tokens,
    crop_ids,
    merge_order,
    owner_list,
    w_qkv,
    w_proj,
    w_fc1,
    w_fc2,
    small_params,
    small_first,
    small_second,
    master_blocks,
    first_moment,
    second_moment,
    basis_left,
    basis_right,
    merged_grad,
):
    canvases, quad_side, quad_cols, features = tokens.shape
    head_dim = features // HEADS
    score_scale = head_dim ** (-0.5)
    window_area = WIN * WIN
    quarters = lax.axis_size(("qy", "qx"))
    share_rows = quad_side * quad_cols // quarters
    row_base = lax.axis_index("qy") * quad_side
    col_base = lax.axis_index("qx") * quad_cols
    rolled = jnp.roll(crop_ids, (-SHIFT, -SHIFT), (1, 2))
    local_ids = lax.dynamic_slice(
        rolled, (jnp.int32(0), row_base, col_base), (canvases, quad_side, quad_cols)
    )
    region_row = region_of(
        row_base + jnp.arange(quad_side, dtype=jnp.int32), quad_side * lax.axis_size("qy")
    )
    region_col = region_of(
        col_base + jnp.arange(quad_cols, dtype=jnp.int32), quad_cols * lax.axis_size("qx")
    )
    labels = (local_ids + 1) * 9 + region_row[None, :, None] * 3 + region_col[None, None, :]
    win_labels = to_windows(labels[..., None])[..., 0]
    window_count = win_labels.shape[0]
    gain_one = small_params[0:features]
    offset_one = small_params[features : 2 * features]
    gain_two = small_params[2 * features : 3 * features]
    offset_two = small_params[3 * features : 4 * features]
    table = small_params[4 * features :].reshape(HEADS, -1)
    onehot = (
        relative_index().reshape(-1)[:, None]
        == jnp.arange(table.shape[1], dtype=jnp.int32)[None, :]
    ).astype(jnp.float32)
    rel_bias = jnp.einsum("hr,pr->hp", table, onehot, precision=PRECISE).reshape(
        HEADS, window_area, window_area
    )

    pair_area = 2 * window_area
    place = jnp.arange(PAIR, dtype=jnp.int32)
    pair_labels = jnp.pad(win_labels.reshape(-1, pair_area), ((0, 0), (0, PAIR - pair_area)))
    pair_keys = jnp.where(
        place[None] < pair_area,
        pair_labels * 2 + (place[None] >= window_area).astype(jnp.int32),
        -1 - place[None],
    )
    key_col, key_row = pair_keys[:, :, None], pair_keys[:, None, :]
    valid = (pair_labels >= 9).reshape(-1).astype(jnp.float32)[:, None]
    spread = (
        (place[:, None] % window_area == jnp.arange(window_area, dtype=jnp.int32)[None, :])
        & (place[:, None] < pair_area)
    ).astype(jnp.float32)
    dense_bias = jnp.einsum(
        "hti,ui->htu",
        jnp.einsum("ti,hij->htj", spread, rel_bias, precision=PRECISE),
        spread,
        precision=PRECISE,
    )

    def to_pairs(tensor):
        shaped = tensor.reshape(-1, pair_area, tensor.shape[-1])
        return jnp.pad(shaped, ((0, 0), (0, PAIR - pair_area), (0, 0))).reshape(-1, tensor.shape[-1])

    def from_pairs(tensor):
        shaped = tensor.reshape(-1, PAIR, tensor.shape[-1])
        return shaped[:, :pair_area].reshape(-1, window_area, tensor.shape[-1])

    residual = to_pairs(to_windows(advance(tokens)).astype(jnp.float32))
    normed_one, inverse_one = norm_stats(residual)
    act_one = (normed_one * gain_one + offset_one).astype(jnp.bfloat16)
    mixed = jnp.dot(act_one, w_qkv, preferred_element_type=jnp.float32).astype(jnp.bfloat16)
    mixed_pairs = mixed.reshape(-1, PAIR, mixed.shape[-1])
    attended_pairs, log_total = attention_fwd(mixed_pairs, dense_bias, key_col, key_row, score_scale)
    attended = attended_pairs.reshape(-1, features)
    hidden, act_two, gelu_low, output_flat, stat_block = mlp_fwd(
        attended, residual, valid, w_proj, gain_two, offset_two, w_fc1, w_fc2
    )
    stat_terms = jnp.stack([stat_block[0, 0], stat_block[0, 1], jnp.sum(valid) * features])
    output_low = from_pairs(output_flat)
    restored = retreat(from_windows(output_low, canvases, quad_side, quad_cols))
    flat_out = restored.reshape(canvases, quarters, share_rows, features)
    arrived = lax.all_to_all(flat_out, ("qy", "qx"), 1, 1, tiled=True)
    merged = jnp.take(arrived, merge_order, axis=1, mode="clip").transpose(0, 2, 1, 3).reshape(
        canvases, share_rows, quarters * features
    )
    quarter_ids = jnp.arange(quarters, dtype=jnp.int32)
    source_pick = jnp.sum(
        quarter_ids[:, None] * (merge_order[:, None] == quarter_ids[None, :]).astype(jnp.int32), 0
    )
    incoming = merged_grad.reshape(canvases, share_rows, quarters, features)
    unordered = jnp.take(incoming, source_pick, axis=2, mode="clip").transpose(0, 2, 1, 3)
    returned = lax.all_to_all(unordered, ("qy", "qx"), 1, 1, tiled=True)
    grad_orig = returned.reshape(canvases, quad_side, quad_cols, features)
    grad_out = to_pairs(to_windows(advance(grad_orig)))
    grad_pre, grad_hidden, grad_branch, grad_attended, small_two = mlp_bwd(
        grad_out, hidden, act_two, gain_two, w_fc1, w_fc2, w_proj
    )
    grad_fc2 = jnp.einsum("rf,rc->fc", gelu_low, grad_out, preferred_element_type=jnp.float32)
    grad_fc1 = jnp.einsum("rc,rf->cf", act_two, grad_pre, preferred_element_type=jnp.float32)
    grad_proj = jnp.einsum("rc,rd->cd", attended, grad_branch, preferred_element_type=jnp.float32)
    grad_mixed_pairs, dense_grad_bias = attention_bwd(
        mixed_pairs, grad_attended.reshape(-1, PAIR, features), log_total, dense_bias, key_col, key_row, score_scale
    )
    grad_mixed = grad_mixed_pairs.reshape(-1, 3 * features)
    grad_bias = jnp.einsum(
        "ti,htj->hij",
        spread,
        jnp.einsum("htu,uj->htj", dense_grad_bias, spread, precision=PRECISE),
        precision=PRECISE,
    )
    grad_table = jnp.dot(grad_bias.reshape(HEADS, -1), onehot, precision=PRECISE)
    grad_qkv = jnp.einsum("rc,rf->cf", act_one, grad_mixed, preferred_element_type=jnp.float32)
    grad_act_one = jnp.einsum("rf,cf->rc", grad_mixed, w_qkv, preferred_element_type=jnp.float32)
    grad_input = grad_hidden + norm_back(grad_act_one, normed_one, inverse_one, gain_one)
    grad_low = from_pairs(grad_input.astype(jnp.bfloat16))
    grad_tokens = retreat(from_windows(grad_low, canvases, quad_side, quad_cols))
    small_local = jnp.concatenate(
        [
            jnp.sum(grad_act_one * normed_one, 0),
            jnp.sum(grad_act_one, 0),
            small_two[0],
            small_two[1],
            grad_table.reshape(-1),
        ]
    )
    every_block = jnp.concatenate(
        [lane_blocks(grad_qkv), lane_blocks(grad_proj), lane_blocks(grad_fc1), lane_blocks(grad_fc2)],
        0,
    )
    depth = every_block.shape[1] // PARTS
    parted = [
        jnp.take(every_block[:, index * depth : (index + 1) * depth], owner_list, axis=0, mode="clip")
        for index in range(PARTS)
    ]
    owned_grads, small_all = reduce_to_owners(parted, jnp.concatenate([small_local, stat_terms]))
    small_total = small_all[: small_local.shape[0]]
    stat_total = small_all[small_local.shape[0] :]
    new_first, new_second, new_master = rotate_update(
        owned_grads, master_blocks, first_moment, second_moment, basis_left, basis_right
    )
    small_first_new, small_second_new, small_new = small_update(
        small_total, small_params, small_first, small_second
    )
    stats = jnp.stack(
        [jnp.sqrt(stat_total[0] / stat_total[2]), jnp.sqrt(stat_total[1] / (2.0 * stat_total[2]))]
    )
    return (
        merged,
        grad_tokens,
        owned_grads,
        new_master,
        new_first,
        new_second,
        new_master.astype(jnp.bfloat16),
        small_total,
        small_first_new,
        small_second_new,
        small_new,
        stats,
    )


def solution(mesh):
    placed = (
        P("dp", "qy", "qx", None),
        P("dp", None, None),
        P(),
        P(),
        P(),
        P(),
        P(),
        P(),
        P(),
        P(),
        P(),
        P("dp", None, None),
        P("dp", None, None),
        P("dp", None, None),
        P("dp", None, None),
        P("dp", None, None),
        P("dp", ("qy", "qx"), None),
    )
    return jax.shard_map(
        local,
        mesh=mesh,
        in_specs=placed,
        out_specs=(
            P("dp", ("qy", "qx"), None),
            P("dp", "qy", "qx", None),
            P("dp", None, None),
            P("dp", None, None),
            P("dp", None, None),
            P("dp", None, None),
            P("dp", None, None),
            P(),
            P(),
            P(),
            P(),
            P(),
        ),
        check_vma=False,
    )
```

```python
import functools
from functools import partial

import numpy as np

import jax
import jax.numpy as jnp
from jax import lax
from jax.experimental import pallas as pl
from jax.experimental.pallas import tpu as pltpu
from jax.sharding import PartitionSpec as P

HEADS = 12
WIN = 7
SHIFT = 3
BLK = 96


BETA_ONE = 0.5
BETA_TWO = 0.6
ADAM_EPSILON = 1e-08
RATE_BLOCKS = 0.04
RATE_SMALL = 0.2
MASK_FILL = -1e30
NORM_EPSILON = 1e-05
PRECISE = lax.Precision.HIGHEST
ROTATE = lax.Precision.HIGH


def passed_along(value, axis, steps):
    count = lax.axis_size(axis)
    pairs = [(source, (source + steps) % count) for source in range(count)]
    return lax.ppermute(value, axis, pairs)


def partner_of(value, axis, mask):
    count = lax.axis_size(axis)
    pairs = [(source, source ^ mask) for source in range(count)]
    return lax.ppermute(value, axis, pairs)


def bit_of(axis, mask):
    return ((lax.axis_index(axis) & mask) != 0).astype(jnp.int32)


LANES = 128
PARTS = 3
GROUP = 4
LANES = 128
MASK_FILL = -1e30
PAIR = 112
STEP_PAIRS = 8


def _stacked(value, lane4):
    wide = jnp.broadcast_to(value.astype(jnp.float32)[None], (GROUP, PAIR, LANES))
    return jnp.where(lane4, wide, 0.0).reshape(GROUP * PAIR, LANES).astype(jnp.bfloat16)


def _gather_lanes(stack, lane4):
    return jnp.sum(jnp.where(lane4, stack.reshape(GROUP, PAIR, LANES), 0.0), 0)


def _scores(q4, k4, bias4, allowed, scale, lane4):
    raw = lax.dot_general(_stacked(q4, lane4), k4, (((1,), (1,)), ((), ())), preferred_element_type=jnp.float32)
    raw = raw.reshape(GROUP, PAIR, PAIR) * scale + bias4
    return jnp.where(allowed[None], raw, MASK_FILL)


def _lane_masks():
    lane4 = lax.broadcasted_iota(jnp.int32, (GROUP, 1, LANES), 2) // 32 == lax.broadcasted_iota(
        jnp.int32, (GROUP, 1, LANES), 0)
    return lane4, lax.broadcasted_iota(jnp.int32, (1, LANES), 1)


def _fwd_kernel(mix_ref, bias_ref, kc_ref, kr_ref, out_ref, lse_ref, *, scale):
    width = HEADS * 32
    lane4, head_lane = _lane_masks()
    for sub in range(STEP_PAIRS):
        allowed = kc_ref[sub] == kr_ref[sub]
        lse_all = jnp.zeros((PAIR, LANES), jnp.float32)
        for g in range(HEADS // GROUP):
            q4 = mix_ref[sub, :, pl.ds(g * LANES, LANES)]
            k4 = mix_ref[sub, :, pl.ds(width + g * LANES, LANES)]
            v4 = mix_ref[sub, :, pl.ds(2 * width + g * LANES, LANES)]
            s = _scores(q4, k4, bias_ref[pl.ds(g * GROUP, GROUP)], allowed, scale, lane4)
            top = jnp.max(s, -1, keepdims=True)
            e = jnp.exp(s - top)
            total = jnp.sum(e, -1, keepdims=True)
            probs = (e / total).reshape(GROUP * PAIR, PAIR).astype(jnp.bfloat16)
            mixed_out = jnp.dot(probs, v4, preferred_element_type=jnp.float32)
            out_ref[sub, :, pl.ds(g * LANES, LANES)] = _gather_lanes(mixed_out, lane4).astype(out_ref.dtype)
            lse = top + jnp.log(total)
            for j in range(GROUP):
                lse_all = jnp.where(head_lane == g * GROUP + j, lse[j], lse_all)
        lse_ref[sub] = lse_all


def _bwd_kernel(mix_ref, grad_ref, lse_ref, bias_ref, kc_ref, kr_ref, gmix_ref, dbias_ref, *, scale):
    width = HEADS * 32
    lane4, head_lane = _lane_masks()
    step = pl.program_id(0)

    @pl.when(step == 0)
    def _():
        dbias_ref[...] = jnp.zeros_like(dbias_ref)

    for sub in range(STEP_PAIRS):
        allowed = kc_ref[sub] == kr_ref[sub]
        lse_all = lse_ref[sub]
        for g in range(HEADS // GROUP):
            q4 = mix_ref[sub, :, pl.ds(g * LANES, LANES)]
            k4 = mix_ref[sub, :, pl.ds(width + g * LANES, LANES)]
            v4 = mix_ref[sub, :, pl.ds(2 * width + g * LANES, LANES)]
            d4 = grad_ref[sub, :, pl.ds(g * LANES, LANES)]
            heads = pl.ds(g * GROUP, GROUP)
            s = _scores(q4, k4, bias_ref[heads], allowed, scale, lane4)
            lse = jnp.stack([
                jnp.sum(jnp.where(head_lane == g * GROUP + j, lse_all, 0.0), -1, keepdims=True)
                for j in range(GROUP)
            ])
            probs = jnp.exp(s - lse)
            d_stack = _stacked(d4, lane4)
            dprobs = lax.dot_general(d_stack, v4, (((1,), (1,)), ((), ())), preferred_element_type=jnp.float32)
            dprobs = dprobs.reshape(GROUP, PAIR, PAIR)
            inner = jnp.sum(probs * dprobs, -1, keepdims=True)
            dscores = (probs * (dprobs - inner)).reshape(GROUP * PAIR, PAIR).astype(jnp.bfloat16)
            dbias_ref[heads] = dbias_ref[heads] + dscores.astype(jnp.float32).reshape(GROUP, PAIR, PAIR)
            gq = _gather_lanes(jnp.dot(dscores, k4, preferred_element_type=jnp.float32), lane4)
            gk = lax.dot_general(dscores, _stacked(q4, lane4), (((0,), (0,)), ((), ())), preferred_element_type=jnp.float32)
            gv = lax.dot_general(probs.reshape(GROUP * PAIR, PAIR).astype(jnp.bfloat16), d_stack,
                                 (((0,), (0,)), ((), ())), preferred_element_type=jnp.float32)
            gmix_ref[sub, :, pl.ds(g * LANES, LANES)] = (gq * scale).astype(gmix_ref.dtype)
            gmix_ref[sub, :, pl.ds(width + g * LANES, LANES)] = (gk * scale).astype(gmix_ref.dtype)
            gmix_ref[sub, :, pl.ds(2 * width + g * LANES, LANES)] = gv.astype(gmix_ref.dtype)


def _pair_spec(width):
    return pl.BlockSpec((STEP_PAIRS, PAIR, width), lambda p: (p, 0, 0))


def attention_fwd(mixed_pairs, bias, key_col, key_row, scale):
    pairs = mixed_pairs.shape[0]
    kernel = functools.partial(_fwd_kernel, scale=scale)
    return pl.pallas_call(
        kernel,
        grid=(pairs // STEP_PAIRS,),
        out_shape=(
            jax.ShapeDtypeStruct((pairs, PAIR, HEADS * 32), jnp.bfloat16),
            jax.ShapeDtypeStruct((pairs, PAIR, LANES), jnp.float32),
        ),
        in_specs=[_pair_spec(mixed_pairs.shape[2]), pl.BlockSpec(bias.shape, lambda p: (0, 0, 0)),
                  pl.BlockSpec((STEP_PAIRS, PAIR, 1), lambda p: (p, 0, 0)), pl.BlockSpec((STEP_PAIRS, 1, PAIR), lambda p: (p, 0, 0))],
        out_specs=(_pair_spec(HEADS * 32), _pair_spec(LANES)),
        compiler_params=pltpu.CompilerParams(dimension_semantics=("arbitrary",), vmem_limit_bytes=32 * 1024 * 1024),
    )(mixed_pairs, bias, key_col, key_row)


def attention_bwd(mixed_pairs, grad_pairs, lse, bias, key_col, key_row, scale):
    pairs = mixed_pairs.shape[0]
    kernel = functools.partial(_bwd_kernel, scale=scale)
    return pl.pallas_call(
        kernel,
        grid=(pairs // STEP_PAIRS,),
        out_shape=(
            jax.ShapeDtypeStruct(mixed_pairs.shape, jnp.bfloat16),
            jax.ShapeDtypeStruct(bias.shape, jnp.float32),
        ),
        in_specs=[_pair_spec(mixed_pairs.shape[2]), _pair_spec(HEADS * 32), _pair_spec(LANES),
                  pl.BlockSpec(bias.shape, lambda p: (0, 0, 0)),
                  pl.BlockSpec((STEP_PAIRS, PAIR, 1), lambda p: (p, 0, 0)), pl.BlockSpec((STEP_PAIRS, 1, PAIR), lambda p: (p, 0, 0))],
        out_specs=(_pair_spec(mixed_pairs.shape[2]), pl.BlockSpec(bias.shape, lambda p: (0, 0, 0))),
        compiler_params=pltpu.CompilerParams(dimension_semantics=("arbitrary",), vmem_limit_bytes=32 * 1024 * 1024),
    )(mixed_pairs, grad_pairs, lse, bias, key_col, key_row)


def lane_blocks(matrix):
    row_blocks, col_blocks = matrix.shape[0] // BLK, matrix.shape[1] // BLK
    shaped = matrix.reshape(row_blocks, BLK, col_blocks, BLK).transpose(0, 2, 1, 3)
    return shaped.reshape(row_blocks * col_blocks, BLK * BLK // LANES, LANES)


ROWS = 896
SQRT_HALF = float(np.sqrt(0.5))
INV_SQRT_TAU = float(1.0 / np.sqrt(2.0 * np.pi))


def _norm(tensor):
    center = tensor - jnp.mean(tensor, -1, keepdims=True)
    inverse = lax.rsqrt(jnp.mean(center * center, -1, keepdims=True) + NORM_EPSILON)
    return center * inverse, inverse


def _mlp_fwd_kernel(att_ref, res_ref, valid_ref, wp_ref, gain_ref, off_ref, w1_ref, w2_ref,
                    hid_ref, act_ref, gelu_ref, out_ref, stat_ref):
    step = pl.program_id(0)
    branch_one = jnp.dot(att_ref[...], wp_ref[...], preferred_element_type=jnp.float32)
    hidden = res_ref[...] + branch_one
    normed, _ = _norm(hidden)
    act = (normed * gain_ref[...] + off_ref[...]).astype(jnp.bfloat16)
    pre = jnp.dot(act, w1_ref[...], preferred_element_type=jnp.float32)
    gelu = ((0.5 * pre) * (1.0 + lax.erf(pre * SQRT_HALF))).astype(jnp.bfloat16)
    branch_two = jnp.dot(gelu, w2_ref[...], preferred_element_type=jnp.float32)
    output = hidden + branch_two
    valid = valid_ref[...]
    first = jnp.sum(valid * output * output)
    second = jnp.sum(valid * (branch_one * branch_one + branch_two * branch_two))
    lane = lax.broadcasted_iota(jnp.int32, (8, 128), 1)
    row = lax.broadcasted_iota(jnp.int32, (8, 128), 0)
    here = jnp.where((row == 0) & (lane == 0), first, 0.0) + jnp.where((row == 0) & (lane == 1), second, 0.0)

    @pl.when(step == 0)
    def _():
        stat_ref[...] = jnp.zeros_like(stat_ref)

    stat_ref[...] = stat_ref[...] + here
    hid_ref[...] = hidden
    act_ref[...] = act
    gelu_ref[...] = gelu
    out_ref[...] = output.astype(out_ref.dtype)


def _mlp_bwd_kernel(gout_ref, hid_ref, act_ref, gain_ref, w1_ref, w2_ref, wp_ref,
                    gpre_ref, ghid_ref, gbr_ref, gatt_ref, small_ref):
    step = pl.program_id(0)
    contract_last = (((1,), (1,)), ((), ()))
    pre = jnp.dot(act_ref[...], w1_ref[...], preferred_element_type=jnp.float32)
    grad_out = gout_ref[...]
    grad_gelu = lax.dot_general(grad_out, w2_ref[...], contract_last, preferred_element_type=jnp.float32)
    cdf = 0.5 * (1.0 + lax.erf(pre * SQRT_HALF))
    pdf = jnp.exp(-0.5 * pre * pre) * INV_SQRT_TAU
    grad_pre = (grad_gelu * (cdf + pre * pdf)).astype(jnp.bfloat16)
    grad_act = lax.dot_general(grad_pre, w1_ref[...], contract_last, preferred_element_type=jnp.float32)
    normed, inverse = _norm(hid_ref[...])
    scaled = grad_act * gain_ref[...]
    mean_one = jnp.mean(scaled, -1, keepdims=True)
    mean_two = jnp.mean(scaled * normed, -1, keepdims=True)
    grad_hidden = grad_out.astype(jnp.float32) + inverse * (scaled - mean_one - normed * mean_two)
    grad_branch = grad_hidden.astype(jnp.bfloat16)
    grad_att = lax.dot_general(grad_branch, wp_ref[...], contract_last, preferred_element_type=jnp.float32)
    sums = jnp.concatenate(
        [jnp.sum(grad_act * normed, 0, keepdims=True), jnp.sum(grad_act, 0, keepdims=True),
         jnp.zeros((6, grad_act.shape[1]), jnp.float32)], 0)

    @pl.when(step == 0)
    def _():
        small_ref[...] = jnp.zeros_like(small_ref)

    small_ref[...] = small_ref[...] + sums
    gpre_ref[...] = grad_pre
    ghid_ref[...] = grad_hidden
    gbr_ref[...] = grad_branch
    gatt_ref[...] = grad_att.astype(gatt_ref.dtype)


def _rows(width):
    return pl.BlockSpec((ROWS, width), lambda i: (i, 0))


def _whole(shape):
    return pl.BlockSpec(shape, lambda i: (0,) * len(shape))


def mlp_fwd(attended, residual, valid, w_proj, gain, offset, w_fc1, w_fc2):
    tokens, width = residual.shape
    hidden_width = w_fc1.shape[1]
    return pl.pallas_call(
        _mlp_fwd_kernel,
        grid=(tokens // ROWS,),
        out_shape=(
            jax.ShapeDtypeStruct((tokens, width), jnp.float32),
            jax.ShapeDtypeStruct((tokens, width), jnp.bfloat16),
            jax.ShapeDtypeStruct((tokens, hidden_width), jnp.bfloat16),
            jax.ShapeDtypeStruct((tokens, width), jnp.bfloat16),
            jax.ShapeDtypeStruct((8, 128), jnp.float32),
        ),
        in_specs=[_rows(width), _rows(width), _rows(1), _whole(w_proj.shape), _whole((1, width)),
                  _whole((1, width)), _whole(w_fc1.shape), _whole(w_fc2.shape)],
        out_specs=(_rows(width), _rows(width), _rows(hidden_width), _rows(width), _whole((8, 128))),
        compiler_params=pltpu.CompilerParams(dimension_semantics=("arbitrary",), vmem_limit_bytes=48 * 1024 * 1024),
    )(attended, residual, valid, w_proj, gain.reshape(1, -1), offset.reshape(1, -1), w_fc1, w_fc2)


def mlp_bwd(grad_out, hidden, act_two, gain, w_fc1, w_fc2, w_proj):
    tokens, width = hidden.shape
    hidden_width = w_fc1.shape[1]
    return pl.pallas_call(
        _mlp_bwd_kernel,
        grid=(tokens // ROWS,),
        out_shape=(
            jax.ShapeDtypeStruct((tokens, hidden_width), jnp.bfloat16),
            jax.ShapeDtypeStruct((tokens, width), jnp.float32),
            jax.ShapeDtypeStruct((tokens, width), jnp.bfloat16),
            jax.ShapeDtypeStruct((tokens, width), jnp.bfloat16),
            jax.ShapeDtypeStruct((8, width), jnp.float32),
        ),
        in_specs=[_rows(width), _rows(width), _rows(width), _whole((1, width)), _whole(w_fc1.shape),
                  _whole(w_fc2.shape), _whole(w_proj.shape)],
        out_specs=(_rows(hidden_width), _rows(width), _rows(width), _rows(width), _whole((8, width))),
        compiler_params=pltpu.CompilerParams(dimension_semantics=("arbitrary",), vmem_limit_bytes=48 * 1024 * 1024),
    )(grad_out, hidden, act_two, gain.reshape(1, -1), w_fc1, w_fc2, w_proj)


def split_by_core(owner_list, count):
    groups = lax.axis_size("dp")
    n_qy, n_qx = lax.axis_size("qy"), lax.axis_size("qx")
    if count % (groups * n_qy * n_qx) or n_qx != 2:
        return None
    places = np.arange(count).reshape(groups, n_qy, n_qx, -1)
    first = jnp.take(owner_list, jnp.asarray(places[:, :, 0].reshape(-1)), mode="clip")
    second = jnp.take(owner_list, jnp.asarray(places[:, :, 1].reshape(-1)), mode="clip")
    mine = bit_of("qx", 1) == 1
    return jnp.where(mine, second, first), jnp.where(mine, first, second)


def reduce_to_owners(parted, small, split=False):
    groups = lax.axis_size("dp")
    dp_bits = groups.bit_length() - 1
    n_qy, n_qx = lax.axis_size("qy"), lax.axis_size("qx")
    count = parted[0][0].shape[0] * 2 if split else parted[0].shape[0]
    depth = parted[0][0].shape[1] if split else parted[0].shape[1]
    per_group = count // groups
    names = [("dp", 1 << power) for power in reversed(range(dp_bits))] + [("qy", 1), ("qx", 1)]
    cross = [("qy", 1)] + [("dp", 1 << power) for power in range(dp_bits)]
    pieces, piece_names, orders = [], [], []
    rows_each = per_group * depth // (n_qy * n_qx)
    for index, part in enumerate(parted):
        turn = index % len(cross)
        orders.append([("qx", 1)] + cross[turn:] + cross[:turn])
        if split:
            keep, send = part
            arrived = partner_of(send, "qx", 1)
            shape = [2] * dp_bits + [n_qy, rows_each, LANES]
            pieces.append(keep.reshape(shape) + arrived.reshape(shape).astype(jnp.float32))
            piece_names.append(list(names[:-1]))
            if index == 0:
                small = small + partner_of(small, "qx", 1)
                pieces[0], small = lax.optimization_barrier((pieces[0], small))
        else:
            pieces.append(part.reshape([2] * dp_bits + [n_qy, n_qx, rows_each, LANES]))
            piece_names.append(list(names))
    for stage in range(1 if split else 0, len(names)):
        for index in range(len(pieces)):
            bit = orders[index][stage]
            place = piece_names[index].index(bit)
            mine = bit_of(*bit)
            keep = lax.dynamic_index_in_dim(pieces[index], mine, place, keepdims=False)
            send = lax.dynamic_index_in_dim(pieces[index], 1 - mine, place, keepdims=False)
            piece_names[index].remove(bit)
            arrived = partner_of(send.astype(jnp.bfloat16), *bit)
            pieces[index] = keep + arrived.astype(jnp.float32)
            if index == 0:
                small = small + partner_of(small, *bit)
                pieces[0], small = lax.optimization_barrier((pieces[0], small))
    chunk = jnp.stack(pieces)
    other = partner_of(chunk, "qy", 1)
    pair = jnp.where(bit_of("qy", 1) == 1, jnp.stack([other, chunk], 1), jnp.stack([chunk, other], 1))
    other = partner_of(pair, "qx", 1)
    quad = jnp.where(bit_of("qx", 1) == 1, jnp.stack([other, pair], 2), jnp.stack([pair, other], 2))
    quad = quad.reshape(len(pieces), per_group, depth, LANES).transpose(1, 0, 2, 3)
    return quad.reshape(per_group, BLK, BLK), small


def cut_along(value, dim, devices):
    before, after = (value.shape[:dim], value.shape[dim + 1 :])
    return jnp.moveaxis(value.reshape(*before, devices, -1, *after), dim, 0)


def sent_and_summed(value, axis, dim):
    pieces = cut_along(value, dim, lax.axis_size(axis))
    arrived = lax.all_to_all(pieces, axis, split_axis=0, concat_axis=0, tiled=True)
    return arrived.astype(jnp.float32).sum(axis=0)


def norm_stats(tensor):
    center = tensor - jnp.mean(tensor, -1, keepdims=True)
    inverse = lax.rsqrt(jnp.mean(center * center, -1, keepdims=True) + NORM_EPSILON)
    return (center * inverse, inverse)


def norm_back(grad_act, normed, inverse, gain):
    scaled = grad_act * gain
    mean_one = jnp.mean(scaled, -1, keepdims=True)
    mean_two = jnp.mean(scaled * normed, -1, keepdims=True)
    return inverse * (scaled - mean_one - normed * mean_two)


def to_windows(tensor):
    canvases, rows_side, cols_side, channels = tensor.shape
    shaped = tensor.reshape(canvases, rows_side // WIN, WIN, cols_side // WIN, WIN, channels)
    return shaped.transpose(0, 1, 3, 2, 4, 5).reshape(
        canvases * (rows_side // WIN) * (cols_side // WIN), WIN * WIN, channels
    )


def from_windows(tensor, canvases, rows_side, cols_side):
    channels = tensor.shape[-1]
    shaped = tensor.reshape(canvases, rows_side // WIN, cols_side // WIN, WIN, WIN, channels)
    return shaped.transpose(0, 1, 3, 2, 4, 5).reshape(canvases, rows_side, cols_side, channels)


def relative_index():
    places = jnp.arange(WIN * WIN, dtype=jnp.int32)
    row_of = places // WIN
    col_of = places % WIN
    return (row_of[:, None] - row_of[None, :] + WIN - 1) * (2 * WIN - 1) + (
        col_of[:, None] - col_of[None, :] + WIN - 1
    )


def region_of(places, full):
    return jnp.where(places < full - WIN, 0, jnp.where(places < full - SHIFT, 1, 2)).astype(
        jnp.int32
    )


def advance(tensor):
    upper = passed_along(tensor[:, :SHIFT], "qy", -1)
    tensor = jnp.concatenate([tensor[:, SHIFT:], upper], 1)
    leftmost = passed_along(tensor[:, :, :SHIFT], "qx", -1)
    return jnp.concatenate([tensor[:, :, SHIFT:], leftmost], 2)


def retreat(tensor):
    lowest = passed_along(tensor[:, -SHIFT:], "qy", 1)
    tensor = jnp.concatenate([lowest, tensor[:, :-SHIFT]], 1)
    rightmost = passed_along(tensor[:, :, -SHIFT:], "qx", 1)
    return jnp.concatenate([rightmost, tensor[:, :, :-SHIFT]], 2)


def blocks_of(matrix):
    row_blocks = matrix.shape[0] // BLK
    col_blocks = matrix.shape[1] // BLK
    return (
        matrix.reshape(row_blocks, BLK, col_blocks, BLK)
        .transpose(0, 2, 1, 3)
        .reshape(row_blocks * col_blocks, BLK, BLK)
    )


def rotate_update(grads, master, first, second, left, right):
    turned = jnp.einsum("sji,sjk->sik", left, grads, precision=ROTATE)
    turned = jnp.einsum("sik,skl->sil", turned, right, precision=ROTATE)
    new_first = BETA_ONE * first + (1.0 - BETA_ONE) * turned
    new_second = BETA_TWO * second + (1.0 - BETA_TWO) * turned * turned
    direction = new_first / (jnp.sqrt(new_second) + ADAM_EPSILON)
    back = jnp.einsum("sij,sjk->sik", left, direction, precision=ROTATE)
    back = jnp.einsum("sik,slk->sil", back, right, precision=ROTATE)
    return (new_first, new_second, master - RATE_BLOCKS * back)


def small_update(grads, params, first, second):
    new_first = BETA_ONE * first + (1.0 - BETA_ONE) * grads
    new_second = BETA_TWO * second + (1.0 - BETA_TWO) * grads * grads
    direction = new_first / (jnp.sqrt(new_second) + ADAM_EPSILON)
    return (new_first, new_second, params - RATE_SMALL * direction)


def local(
    tokens,
    crop_ids,
    merge_order,
    owner_list,
    w_qkv,
    w_proj,
    w_fc1,
    w_fc2,
    small_params,
    small_first,
    small_second,
    master_blocks,
    first_moment,
    second_moment,
    basis_left,
    basis_right,
    merged_grad,
):
    canvases, quad_side, quad_cols, features = tokens.shape
    head_dim = features // HEADS
    score_scale = head_dim ** (-0.5)
    window_area = WIN * WIN
    quarters = lax.axis_size(("qy", "qx"))
    share_rows = quad_side * quad_cols // quarters
    row_base = lax.axis_index("qy") * quad_side
    col_base = lax.axis_index("qx") * quad_cols
    rolled = jnp.roll(crop_ids, (-SHIFT, -SHIFT), (1, 2))
    local_ids = lax.dynamic_slice(
        rolled, (jnp.int32(0), row_base, col_base), (canvases, quad_side, quad_cols)
    )
    region_row = region_of(
        row_base + jnp.arange(quad_side, dtype=jnp.int32), quad_side * lax.axis_size("qy")
    )
    region_col = region_of(
        col_base + jnp.arange(quad_cols, dtype=jnp.int32), quad_cols * lax.axis_size("qx")
    )
    labels = (local_ids + 1) * 9 + region_row[None, :, None] * 3 + region_col[None, None, :]
    win_labels = to_windows(labels[..., None])[..., 0]
    window_count = win_labels.shape[0]
    gain_one = small_params[0:features]
    offset_one = small_params[features : 2 * features]
    gain_two = small_params[2 * features : 3 * features]
    offset_two = small_params[3 * features : 4 * features]
    table = small_params[4 * features :].reshape(HEADS, -1)
    onehot = (
        relative_index().reshape(-1)[:, None]
        == jnp.arange(table.shape[1], dtype=jnp.int32)[None, :]
    ).astype(jnp.float32)
    rel_bias = jnp.einsum("hr,pr->hp", table, onehot, precision=PRECISE).reshape(
        HEADS, window_area, window_area
    )

    pair_area = 2 * window_area
    place = jnp.arange(PAIR, dtype=jnp.int32)
    pair_labels = jnp.pad(win_labels.reshape(-1, pair_area), ((0, 0), (0, PAIR - pair_area)))
    pair_keys = jnp.where(
        place[None] < pair_area,
        pair_labels * 2 + (place[None] >= window_area).astype(jnp.int32),
        -1 - place[None],
    )
    key_col, key_row = pair_keys[:, :, None], pair_keys[:, None, :]
    valid = (pair_labels >= 9).reshape(-1).astype(jnp.float32)[:, None]
    spread = (
        (place[:, None] % window_area == jnp.arange(window_area, dtype=jnp.int32)[None, :])
        & (place[:, None] < pair_area)
    ).astype(jnp.float32)
    dense_bias = jnp.einsum(
        "hti,ui->htu",
        jnp.einsum("ti,hij->htj", spread, rel_bias, precision=PRECISE),
        spread,
        precision=PRECISE,
    )

    def to_pairs(tensor):
        shaped = tensor.reshape(-1, pair_area, tensor.shape[-1])
        return jnp.pad(shaped, ((0, 0), (0, PAIR - pair_area), (0, 0))).reshape(-1, tensor.shape[-1])

    def from_pairs(tensor):
        shaped = tensor.reshape(-1, PAIR, tensor.shape[-1])
        return shaped[:, :pair_area].reshape(-1, window_area, tensor.shape[-1])

    residual = to_pairs(to_windows(advance(tokens)).astype(jnp.float32))
    normed_one, inverse_one = norm_stats(residual)
    act_one = (normed_one * gain_one + offset_one).astype(jnp.bfloat16)
    mixed = jnp.dot(act_one, w_qkv, preferred_element_type=jnp.float32).astype(jnp.bfloat16)
    mixed_pairs = mixed.reshape(-1, PAIR, mixed.shape[-1])
    attended_pairs, log_total = attention_fwd(mixed_pairs, dense_bias, key_col, key_row, score_scale)
    attended = attended_pairs.reshape(-1, features)
    hidden, act_two, gelu_low, output_flat, stat_block = mlp_fwd(
        attended, residual, valid, w_proj, gain_two, offset_two, w_fc1, w_fc2
    )
    stat_terms = jnp.stack([stat_block[0, 0], stat_block[0, 1], jnp.sum(valid) * features])
    output_low = from_pairs(output_flat)
    restored = retreat(from_windows(output_low, canvases, quad_side, quad_cols))
    flat_out = restored.reshape(canvases, quarters, share_rows, features)
    arrived = lax.all_to_all(flat_out, ("qy", "qx"), 1, 1, tiled=True)
    merged = jnp.take(arrived, merge_order, axis=1, mode="clip").transpose(0, 2, 1, 3).reshape(
        canvases, share_rows, quarters * features
    )
    quarter_ids = jnp.arange(quarters, dtype=jnp.int32)
    source_pick = jnp.sum(
        quarter_ids[:, None] * (merge_order[:, None] == quarter_ids[None, :]).astype(jnp.int32), 0
    )
    incoming = merged_grad.reshape(canvases, share_rows, quarters, features)
    unordered = jnp.take(incoming, source_pick, axis=2, mode="clip").transpose(0, 2, 1, 3)
    returned = lax.all_to_all(unordered, ("qy", "qx"), 1, 1, tiled=True)
    grad_orig = returned.reshape(canvases, quad_side, quad_cols, features)
    grad_out = to_pairs(to_windows(advance(grad_orig)))
    grad_pre, grad_hidden, grad_branch, grad_attended, small_two = mlp_bwd(
        grad_out, hidden, act_two, gain_two, w_fc1, w_fc2, w_proj
    )
    grad_fc2 = jnp.einsum("rf,rc->fc", gelu_low, grad_out, preferred_element_type=jnp.float32)
    grad_fc1 = jnp.einsum("rc,rf->cf", act_two, grad_pre, preferred_element_type=jnp.float32)
    grad_proj = jnp.einsum("rc,rd->cd", attended, grad_branch, preferred_element_type=jnp.float32)
    grad_mixed_pairs, dense_grad_bias = attention_bwd(
        mixed_pairs, grad_attended.reshape(-1, PAIR, features), log_total, dense_bias, key_col, key_row, score_scale
    )
    grad_mixed = grad_mixed_pairs.reshape(-1, 3 * features)
    grad_bias = jnp.einsum(
        "ti,htj->hij",
        spread,
        jnp.einsum("htu,uj->htj", dense_grad_bias, spread, precision=PRECISE),
        precision=PRECISE,
    )
    grad_table = jnp.dot(grad_bias.reshape(HEADS, -1), onehot, precision=PRECISE)
    grad_qkv = jnp.einsum("rc,rf->cf", act_one, grad_mixed, preferred_element_type=jnp.float32)
    grad_act_one = jnp.einsum("rf,cf->rc", grad_mixed, w_qkv, preferred_element_type=jnp.float32)
    grad_input = grad_hidden + norm_back(grad_act_one, normed_one, inverse_one, gain_one)
    grad_low = from_pairs(grad_input.astype(jnp.bfloat16))
    grad_tokens = retreat(from_windows(grad_low, canvases, quad_side, quad_cols))
    small_local = jnp.concatenate(
        [
            jnp.sum(grad_act_one * normed_one, 0),
            jnp.sum(grad_act_one, 0),
            small_two[0],
            small_two[1],
            grad_table.reshape(-1),
        ]
    )
    every_block = jnp.concatenate(
        [lane_blocks(grad_qkv), lane_blocks(grad_proj), lane_blocks(grad_fc1), lane_blocks(grad_fc2)],
        0,
    )
    depth = every_block.shape[1] // PARTS
    halves = split_by_core(owner_list, every_block.shape[0])
    if halves is None:
        parted = [
            jnp.take(every_block[:, index * depth : (index + 1) * depth], owner_list, axis=0, mode="clip")
            for index in range(PARTS)
        ]
    else:
        parted = [
            (
                jnp.take(every_block[:, index * depth : (index + 1) * depth], halves[0], axis=0, mode="clip"),
                jnp.take(
                    every_block[:, index * depth : (index + 1) * depth], halves[1], axis=0, mode="clip"
                ).astype(jnp.bfloat16),
            )
            for index in range(PARTS)
        ]
    owned_grads, small_all = reduce_to_owners(
        parted, jnp.concatenate([small_local, stat_terms]), split=halves is not None
    )
    small_total = small_all[: small_local.shape[0]]
    stat_total = small_all[small_local.shape[0] :]
    new_first, new_second, new_master = rotate_update(
        owned_grads, master_blocks, first_moment, second_moment, basis_left, basis_right
    )
    small_first_new, small_second_new, small_new = small_update(
        small_total, small_params, small_first, small_second
    )
    stats = jnp.stack(
        [jnp.sqrt(stat_total[0] / stat_total[2]), jnp.sqrt(stat_total[1] / (2.0 * stat_total[2]))]
    )
    return (
        merged,
        grad_tokens,
        owned_grads,
        new_master,
        new_first,
        new_second,
        new_master.astype(jnp.bfloat16),
        small_total,
        small_first_new,
        small_second_new,
        small_new,
        stats,
    )


def solution(mesh):
    placed = (
        P("dp", "qy", "qx", None),
        P("dp", None, None),
        P(),
        P(),
        P(),
        P(),
        P(),
        P(),
        P(),
        P(),
        P(),
        P("dp", None, None),
        P("dp", None, None),
        P("dp", None, None),
        P("dp", None, None),
        P("dp", None, None),
        P("dp", ("qy", "qx"), None),
    )
    return jax.shard_map(
        local,
        mesh=mesh,
        in_specs=placed,
        out_specs=(
            P("dp", ("qy", "qx"), None),
            P("dp", "qy", "qx", None),
            P("dp", None, None),
            P("dp", None, None),
            P("dp", None, None),
            P("dp", None, None),
            P("dp", None, None),
            P(),
            P(),
            P(),
            P(),
            P(),
        ),
        check_vma=False,
    )
```

```python
import functools
from functools import partial

import numpy as np

import jax
import jax.numpy as jnp
from jax import lax
from jax.experimental import pallas as pl
from jax.experimental.pallas import tpu as pltpu
from jax.sharding import PartitionSpec as P

HEADS = 12
WIN = 7
SHIFT = 3
BLK = 96


BETA_ONE = 0.5
BETA_TWO = 0.6
ADAM_EPSILON = 1e-08
RATE_BLOCKS = 0.04
RATE_SMALL = 0.2
MASK_FILL = -1e30
NORM_EPSILON = 1e-05
PRECISE = lax.Precision.HIGHEST
ROTATE = lax.Precision.HIGH


def passed_along(value, axis, steps):
    count = lax.axis_size(axis)
    pairs = [(source, (source + steps) % count) for source in range(count)]
    return lax.ppermute(value, axis, pairs)


def partner_of(value, axis, mask):
    count = lax.axis_size(axis)
    pairs = [(source, source ^ mask) for source in range(count)]
    return lax.ppermute(value, axis, pairs)


def bit_of(axis, mask):
    return ((lax.axis_index(axis) & mask) != 0).astype(jnp.int32)


LANES = 128
PARTS = 3
GROUP = 4
LANES = 128
MASK_FILL = -1e30
PAIR = 112
STEP_PAIRS = 8


def _stacked(value, lane4):
    wide = jnp.broadcast_to(value.astype(jnp.float32)[None], (GROUP, PAIR, LANES))
    return jnp.where(lane4, wide, 0.0).reshape(GROUP * PAIR, LANES).astype(jnp.bfloat16)


def _gather_lanes(stack, lane4):
    return jnp.sum(jnp.where(lane4, stack.reshape(GROUP, PAIR, LANES), 0.0), 0)


def _scores(q4, k4, bias4, allowed, scale, lane4):
    raw = lax.dot_general(_stacked(q4, lane4), k4, (((1,), (1,)), ((), ())), preferred_element_type=jnp.float32)
    raw = raw.reshape(GROUP, PAIR, PAIR) * scale + bias4
    return jnp.where(allowed[None], raw, MASK_FILL)


def _lane_masks():
    lane4 = lax.broadcasted_iota(jnp.int32, (GROUP, 1, LANES), 2) // 32 == lax.broadcasted_iota(
        jnp.int32, (GROUP, 1, LANES), 0)
    return lane4, lax.broadcasted_iota(jnp.int32, (1, LANES), 1)


def _fwd_kernel(mix_ref, bias_ref, kc_ref, kr_ref, out_ref, lse_ref, *, scale):
    width = HEADS * 32
    lane4, head_lane = _lane_masks()
    for sub in range(STEP_PAIRS):
        allowed = kc_ref[sub] == kr_ref[sub]
        lse_all = jnp.zeros((PAIR, LANES), jnp.float32)
        for g in range(HEADS // GROUP):
            q4 = mix_ref[sub, :, pl.ds(g * LANES, LANES)]
            k4 = mix_ref[sub, :, pl.ds(width + g * LANES, LANES)]
            v4 = mix_ref[sub, :, pl.ds(2 * width + g * LANES, LANES)]
            s = _scores(q4, k4, bias_ref[pl.ds(g * GROUP, GROUP)], allowed, scale, lane4)
            top = jnp.max(s, -1, keepdims=True)
            e = jnp.exp(s - top)
            total = jnp.sum(e, -1, keepdims=True)
            probs = (e / total).reshape(GROUP * PAIR, PAIR).astype(jnp.bfloat16)
            mixed_out = jnp.dot(probs, v4, preferred_element_type=jnp.float32)
            out_ref[sub, :, pl.ds(g * LANES, LANES)] = _gather_lanes(mixed_out, lane4).astype(out_ref.dtype)
            lse = top + jnp.log(total)
            for j in range(GROUP):
                lse_all = jnp.where(head_lane == g * GROUP + j, lse[j], lse_all)
        lse_ref[sub] = lse_all


def _bwd_kernel(mix_ref, grad_ref, lse_ref, bias_ref, kc_ref, kr_ref, gmix_ref, dbias_ref, *, scale):
    width = HEADS * 32
    lane4, head_lane = _lane_masks()
    step = pl.program_id(0)

    @pl.when(step == 0)
    def _():
        dbias_ref[...] = jnp.zeros_like(dbias_ref)

    for sub in range(STEP_PAIRS):
        allowed = kc_ref[sub] == kr_ref[sub]
        lse_all = lse_ref[sub]
        for g in range(HEADS // GROUP):
            q4 = mix_ref[sub, :, pl.ds(g * LANES, LANES)]
            k4 = mix_ref[sub, :, pl.ds(width + g * LANES, LANES)]
            v4 = mix_ref[sub, :, pl.ds(2 * width + g * LANES, LANES)]
            d4 = grad_ref[sub, :, pl.ds(g * LANES, LANES)]
            heads = pl.ds(g * GROUP, GROUP)
            s = _scores(q4, k4, bias_ref[heads], allowed, scale, lane4)
            lse = jnp.stack([
                jnp.sum(jnp.where(head_lane == g * GROUP + j, lse_all, 0.0), -1, keepdims=True)
                for j in range(GROUP)
            ])
            probs = jnp.exp(s - lse)
            d_stack = _stacked(d4, lane4)
            dprobs = lax.dot_general(d_stack, v4, (((1,), (1,)), ((), ())), preferred_element_type=jnp.float32)
            dprobs = dprobs.reshape(GROUP, PAIR, PAIR)
            inner = jnp.sum(probs * dprobs, -1, keepdims=True)
            dscores = (probs * (dprobs - inner)).reshape(GROUP * PAIR, PAIR).astype(jnp.bfloat16)
            dbias_ref[heads] = dbias_ref[heads] + dscores.astype(jnp.float32).reshape(GROUP, PAIR, PAIR)
            gq = _gather_lanes(jnp.dot(dscores, k4, preferred_element_type=jnp.float32), lane4)
            gk = lax.dot_general(dscores, _stacked(q4, lane4), (((0,), (0,)), ((), ())), preferred_element_type=jnp.float32)
            gv = lax.dot_general(probs.reshape(GROUP * PAIR, PAIR).astype(jnp.bfloat16), d_stack,
                                 (((0,), (0,)), ((), ())), preferred_element_type=jnp.float32)
            gmix_ref[sub, :, pl.ds(g * LANES, LANES)] = (gq * scale).astype(gmix_ref.dtype)
            gmix_ref[sub, :, pl.ds(width + g * LANES, LANES)] = (gk * scale).astype(gmix_ref.dtype)
            gmix_ref[sub, :, pl.ds(2 * width + g * LANES, LANES)] = gv.astype(gmix_ref.dtype)


def _pair_spec(width):
    return pl.BlockSpec((STEP_PAIRS, PAIR, width), lambda p: (p, 0, 0))


def attention_fwd(mixed_pairs, bias, key_col, key_row, scale):
    pairs = mixed_pairs.shape[0]
    kernel = functools.partial(_fwd_kernel, scale=scale)
    return pl.pallas_call(
        kernel,
        grid=(pairs // STEP_PAIRS,),
        out_shape=(
            jax.ShapeDtypeStruct((pairs, PAIR, HEADS * 32), jnp.bfloat16),
            jax.ShapeDtypeStruct((pairs, PAIR, LANES), jnp.float32),
        ),
        in_specs=[_pair_spec(mixed_pairs.shape[2]), pl.BlockSpec(bias.shape, lambda p: (0, 0, 0)),
                  pl.BlockSpec((STEP_PAIRS, PAIR, 1), lambda p: (p, 0, 0)), pl.BlockSpec((STEP_PAIRS, 1, PAIR), lambda p: (p, 0, 0))],
        out_specs=(_pair_spec(HEADS * 32), _pair_spec(LANES)),
        compiler_params=pltpu.CompilerParams(dimension_semantics=("arbitrary",), vmem_limit_bytes=32 * 1024 * 1024),
    )(mixed_pairs, bias, key_col, key_row)


def attention_bwd(mixed_pairs, grad_pairs, lse, bias, key_col, key_row, scale):
    pairs = mixed_pairs.shape[0]
    kernel = functools.partial(_bwd_kernel, scale=scale)
    return pl.pallas_call(
        kernel,
        grid=(pairs // STEP_PAIRS,),
        out_shape=(
            jax.ShapeDtypeStruct(mixed_pairs.shape, jnp.bfloat16),
            jax.ShapeDtypeStruct(bias.shape, jnp.float32),
        ),
        in_specs=[_pair_spec(mixed_pairs.shape[2]), _pair_spec(HEADS * 32), _pair_spec(LANES),
                  pl.BlockSpec(bias.shape, lambda p: (0, 0, 0)),
                  pl.BlockSpec((STEP_PAIRS, PAIR, 1), lambda p: (p, 0, 0)), pl.BlockSpec((STEP_PAIRS, 1, PAIR), lambda p: (p, 0, 0))],
        out_specs=(_pair_spec(mixed_pairs.shape[2]), pl.BlockSpec(bias.shape, lambda p: (0, 0, 0))),
        compiler_params=pltpu.CompilerParams(dimension_semantics=("arbitrary",), vmem_limit_bytes=32 * 1024 * 1024),
    )(mixed_pairs, grad_pairs, lse, bias, key_col, key_row)


def lane_blocks(matrix):
    row_blocks, col_blocks = matrix.shape[0] // BLK, matrix.shape[1] // BLK
    shaped = matrix.reshape(row_blocks, BLK, col_blocks, BLK).transpose(0, 2, 1, 3)
    return shaped.reshape(row_blocks * col_blocks, BLK * BLK // LANES, LANES)


ROWS = 896
SQRT_HALF = float(np.sqrt(0.5))
INV_SQRT_TAU = float(1.0 / np.sqrt(2.0 * np.pi))


def _norm(tensor):
    center = tensor - jnp.mean(tensor, -1, keepdims=True)
    inverse = lax.rsqrt(jnp.mean(center * center, -1, keepdims=True) + NORM_EPSILON)
    return center * inverse, inverse


def _mlp_fwd_kernel(att_ref, res_ref, valid_ref, wp_ref, gain_ref, off_ref, w1_ref, w2_ref,
                    hid_ref, act_ref, gelu_ref, out_ref, stat_ref):
    step = pl.program_id(0)
    branch_one = jnp.dot(att_ref[...], wp_ref[...], preferred_element_type=jnp.float32)
    hidden = res_ref[...] + branch_one
    normed, _ = _norm(hidden)
    act = (normed * gain_ref[...] + off_ref[...]).astype(jnp.bfloat16)
    pre = jnp.dot(act, w1_ref[...], preferred_element_type=jnp.float32)
    gelu = ((0.5 * pre) * (1.0 + lax.erf(pre * SQRT_HALF))).astype(jnp.bfloat16)
    branch_two = jnp.dot(gelu, w2_ref[...], preferred_element_type=jnp.float32)
    output = hidden + branch_two
    valid = valid_ref[...]
    first = jnp.sum(valid * output * output)
    second = jnp.sum(valid * (branch_one * branch_one + branch_two * branch_two))
    lane = lax.broadcasted_iota(jnp.int32, (8, 128), 1)
    row = lax.broadcasted_iota(jnp.int32, (8, 128), 0)
    here = jnp.where((row == 0) & (lane == 0), first, 0.0) + jnp.where((row == 0) & (lane == 1), second, 0.0)

    @pl.when(step == 0)
    def _():
        stat_ref[...] = jnp.zeros_like(stat_ref)

    stat_ref[...] = stat_ref[...] + here
    hid_ref[...] = hidden
    act_ref[...] = act
    gelu_ref[...] = gelu
    out_ref[...] = output.astype(out_ref.dtype)


def _mlp_bwd_kernel(gout_ref, hid_ref, act_ref, gain_ref, w1_ref, w2_ref, wp_ref,
                    gpre_ref, ghid_ref, gbr_ref, gatt_ref, small_ref):
    step = pl.program_id(0)
    contract_last = (((1,), (1,)), ((), ()))
    pre = jnp.dot(act_ref[...], w1_ref[...], preferred_element_type=jnp.float32)
    grad_out = gout_ref[...]
    grad_gelu = lax.dot_general(grad_out, w2_ref[...], contract_last, preferred_element_type=jnp.float32)
    cdf = 0.5 * (1.0 + lax.erf(pre * SQRT_HALF))
    pdf = jnp.exp(-0.5 * pre * pre) * INV_SQRT_TAU
    grad_pre = (grad_gelu * (cdf + pre * pdf)).astype(jnp.bfloat16)
    grad_act = lax.dot_general(grad_pre, w1_ref[...], contract_last, preferred_element_type=jnp.float32)
    normed, inverse = _norm(hid_ref[...])
    scaled = grad_act * gain_ref[...]
    mean_one = jnp.mean(scaled, -1, keepdims=True)
    mean_two = jnp.mean(scaled * normed, -1, keepdims=True)
    grad_hidden = grad_out.astype(jnp.float32) + inverse * (scaled - mean_one - normed * mean_two)
    grad_branch = grad_hidden.astype(jnp.bfloat16)
    grad_att = lax.dot_general(grad_branch, wp_ref[...], contract_last, preferred_element_type=jnp.float32)
    sums = jnp.concatenate(
        [jnp.sum(grad_act * normed, 0, keepdims=True), jnp.sum(grad_act, 0, keepdims=True),
         jnp.zeros((6, grad_act.shape[1]), jnp.float32)], 0)

    @pl.when(step == 0)
    def _():
        small_ref[...] = jnp.zeros_like(small_ref)

    small_ref[...] = small_ref[...] + sums
    gpre_ref[...] = grad_pre
    ghid_ref[...] = grad_hidden
    gbr_ref[...] = grad_branch
    gatt_ref[...] = grad_att.astype(gatt_ref.dtype)


def _rows(width):
    return pl.BlockSpec((ROWS, width), lambda i: (i, 0))


def _whole(shape):
    return pl.BlockSpec(shape, lambda i: (0,) * len(shape))


def mlp_fwd(attended, residual, valid, w_proj, gain, offset, w_fc1, w_fc2):
    tokens, width = residual.shape
    hidden_width = w_fc1.shape[1]
    return pl.pallas_call(
        _mlp_fwd_kernel,
        grid=(tokens // ROWS,),
        out_shape=(
            jax.ShapeDtypeStruct((tokens, width), jnp.float32),
            jax.ShapeDtypeStruct((tokens, width), jnp.bfloat16),
            jax.ShapeDtypeStruct((tokens, hidden_width), jnp.bfloat16),
            jax.ShapeDtypeStruct((tokens, width), jnp.bfloat16),
            jax.ShapeDtypeStruct((8, 128), jnp.float32),
        ),
        in_specs=[_rows(width), _rows(width), _rows(1), _whole(w_proj.shape), _whole((1, width)),
                  _whole((1, width)), _whole(w_fc1.shape), _whole(w_fc2.shape)],
        out_specs=(_rows(width), _rows(width), _rows(hidden_width), _rows(width), _whole((8, 128))),
        compiler_params=pltpu.CompilerParams(dimension_semantics=("arbitrary",), vmem_limit_bytes=48 * 1024 * 1024),
    )(attended, residual, valid, w_proj, gain.reshape(1, -1), offset.reshape(1, -1), w_fc1, w_fc2)


def mlp_bwd(grad_out, hidden, act_two, gain, w_fc1, w_fc2, w_proj):
    tokens, width = hidden.shape
    hidden_width = w_fc1.shape[1]
    return pl.pallas_call(
        _mlp_bwd_kernel,
        grid=(tokens // ROWS,),
        out_shape=(
            jax.ShapeDtypeStruct((tokens, hidden_width), jnp.bfloat16),
            jax.ShapeDtypeStruct((tokens, width), jnp.float32),
            jax.ShapeDtypeStruct((tokens, width), jnp.bfloat16),
            jax.ShapeDtypeStruct((tokens, width), jnp.bfloat16),
            jax.ShapeDtypeStruct((8, width), jnp.float32),
        ),
        in_specs=[_rows(width), _rows(width), _rows(width), _whole((1, width)), _whole(w_fc1.shape),
                  _whole(w_fc2.shape), _whole(w_proj.shape)],
        out_specs=(_rows(hidden_width), _rows(width), _rows(width), _rows(width), _whole((8, width))),
        compiler_params=pltpu.CompilerParams(dimension_semantics=("arbitrary",), vmem_limit_bytes=48 * 1024 * 1024),
    )(grad_out, hidden, act_two, gain.reshape(1, -1), w_fc1, w_fc2, w_proj)


def reduce_to_owners(parted, small):
    groups = lax.axis_size("dp")
    dp_bits = groups.bit_length() - 1
    n_qy, n_qx = lax.axis_size("qy"), lax.axis_size("qx")
    count, depth = parted[0].shape[0], parted[0].shape[1]
    per_group = count // groups
    names = [("dp", 1 << power) for power in reversed(range(dp_bits))] + [("qy", 1), ("qx", 1)]
    cross = [("qy", 1)] + [("dp", 1 << power) for power in range(dp_bits)]
    pieces, piece_names, orders = [], [], []
    for index, part in enumerate(parted):
        pieces.append(
            part.reshape([2] * dp_bits + [n_qy, n_qx, per_group * depth // (n_qy * n_qx), LANES])
        )
        piece_names.append(list(names))
        turn = index % len(cross)
        orders.append([("qx", 1)] + cross[turn:] + cross[:turn])
    for stage in range(len(names)):
        for index in range(len(pieces)):
            bit = orders[index][stage]
            place = piece_names[index].index(bit)
            mine = bit_of(*bit)
            keep = lax.dynamic_index_in_dim(pieces[index], mine, place, keepdims=False)
            send = lax.dynamic_index_in_dim(pieces[index], 1 - mine, place, keepdims=False)
            piece_names[index].remove(bit)
            arrived = partner_of(send.astype(jnp.bfloat16), *bit)
            pieces[index] = keep + arrived.astype(jnp.float32)
            if index == 0 and small is not None:
                small = small + partner_of(small, *bit)
                pieces[0], small = lax.optimization_barrier((pieces[0], small))
    chunk = jnp.stack(pieces)
    other = partner_of(chunk, "qy", 1)
    pair = jnp.where(bit_of("qy", 1) == 1, jnp.stack([other, chunk], 1), jnp.stack([chunk, other], 1))
    other = partner_of(pair, "qx", 1)
    quad = jnp.where(bit_of("qx", 1) == 1, jnp.stack([other, pair], 2), jnp.stack([pair, other], 2))
    quad = quad.reshape(len(pieces), per_group, depth, LANES).transpose(1, 0, 2, 3)
    return quad.reshape(per_group, BLK, BLK), small


def cut_along(value, dim, devices):
    before, after = (value.shape[:dim], value.shape[dim + 1 :])
    return jnp.moveaxis(value.reshape(*before, devices, -1, *after), dim, 0)


def sent_and_summed(value, axis, dim):
    pieces = cut_along(value, dim, lax.axis_size(axis))
    arrived = lax.all_to_all(pieces, axis, split_axis=0, concat_axis=0, tiled=True)
    return arrived.astype(jnp.float32).sum(axis=0)


def norm_stats(tensor):
    center = tensor - jnp.mean(tensor, -1, keepdims=True)
    inverse = lax.rsqrt(jnp.mean(center * center, -1, keepdims=True) + NORM_EPSILON)
    return (center * inverse, inverse)


def norm_back(grad_act, normed, inverse, gain):
    scaled = grad_act * gain
    mean_one = jnp.mean(scaled, -1, keepdims=True)
    mean_two = jnp.mean(scaled * normed, -1, keepdims=True)
    return inverse * (scaled - mean_one - normed * mean_two)


def to_windows(tensor):
    canvases, rows_side, cols_side, channels = tensor.shape
    shaped = tensor.reshape(canvases, rows_side // WIN, WIN, cols_side // WIN, WIN, channels)
    return shaped.transpose(0, 1, 3, 2, 4, 5).reshape(
        canvases * (rows_side // WIN) * (cols_side // WIN), WIN * WIN, channels
    )


def from_windows(tensor, canvases, rows_side, cols_side):
    channels = tensor.shape[-1]
    shaped = tensor.reshape(canvases, rows_side // WIN, cols_side // WIN, WIN, WIN, channels)
    return shaped.transpose(0, 1, 3, 2, 4, 5).reshape(canvases, rows_side, cols_side, channels)


def relative_index():
    places = jnp.arange(WIN * WIN, dtype=jnp.int32)
    row_of = places // WIN
    col_of = places % WIN
    return (row_of[:, None] - row_of[None, :] + WIN - 1) * (2 * WIN - 1) + (
        col_of[:, None] - col_of[None, :] + WIN - 1
    )


def region_of(places, full):
    return jnp.where(places < full - WIN, 0, jnp.where(places < full - SHIFT, 1, 2)).astype(
        jnp.int32
    )


def advance(tensor):
    upper = passed_along(tensor[:, :SHIFT], "qy", -1)
    tensor = jnp.concatenate([tensor[:, SHIFT:], upper], 1)
    leftmost = passed_along(tensor[:, :, :SHIFT], "qx", -1)
    return jnp.concatenate([tensor[:, :, SHIFT:], leftmost], 2)


def retreat(tensor):
    lowest = passed_along(tensor[:, -SHIFT:], "qy", 1)
    tensor = jnp.concatenate([lowest, tensor[:, :-SHIFT]], 1)
    rightmost = passed_along(tensor[:, :, -SHIFT:], "qx", 1)
    return jnp.concatenate([rightmost, tensor[:, :, :-SHIFT]], 2)


def blocks_of(matrix):
    row_blocks = matrix.shape[0] // BLK
    col_blocks = matrix.shape[1] // BLK
    return (
        matrix.reshape(row_blocks, BLK, col_blocks, BLK)
        .transpose(0, 2, 1, 3)
        .reshape(row_blocks * col_blocks, BLK, BLK)
    )


def rotate_update(grads, master, first, second, left, right):
    turned = jnp.einsum("sji,sjk->sik", left, grads, precision=ROTATE)
    turned = jnp.einsum("sik,skl->sil", turned, right, precision=ROTATE)
    new_first = BETA_ONE * first + (1.0 - BETA_ONE) * turned
    new_second = BETA_TWO * second + (1.0 - BETA_TWO) * turned * turned
    direction = new_first / (jnp.sqrt(new_second) + ADAM_EPSILON)
    back = jnp.einsum("sij,sjk->sik", left, direction, precision=ROTATE)
    back = jnp.einsum("sik,slk->sil", back, right, precision=ROTATE)
    return (new_first, new_second, master - RATE_BLOCKS * back)


def small_update(grads, params, first, second):
    new_first = BETA_ONE * first + (1.0 - BETA_ONE) * grads
    new_second = BETA_TWO * second + (1.0 - BETA_TWO) * grads * grads
    direction = new_first / (jnp.sqrt(new_second) + ADAM_EPSILON)
    return (new_first, new_second, params - RATE_SMALL * direction)


def local(
    tokens,
    crop_ids,
    merge_order,
    owner_list,
    w_qkv,
    w_proj,
    w_fc1,
    w_fc2,
    small_params,
    small_first,
    small_second,
    master_blocks,
    first_moment,
    second_moment,
    basis_left,
    basis_right,
    merged_grad,
):
    canvases, quad_side, quad_cols, features = tokens.shape
    head_dim = features // HEADS
    score_scale = head_dim ** (-0.5)
    window_area = WIN * WIN
    quarters = lax.axis_size(("qy", "qx"))
    share_rows = quad_side * quad_cols // quarters
    row_base = lax.axis_index("qy") * quad_side
    col_base = lax.axis_index("qx") * quad_cols
    rolled = jnp.roll(crop_ids, (-SHIFT, -SHIFT), (1, 2))
    local_ids = lax.dynamic_slice(
        rolled, (jnp.int32(0), row_base, col_base), (canvases, quad_side, quad_cols)
    )
    region_row = region_of(
        row_base + jnp.arange(quad_side, dtype=jnp.int32), quad_side * lax.axis_size("qy")
    )
    region_col = region_of(
        col_base + jnp.arange(quad_cols, dtype=jnp.int32), quad_cols * lax.axis_size("qx")
    )
    labels = (local_ids + 1) * 9 + region_row[None, :, None] * 3 + region_col[None, None, :]
    win_labels = to_windows(labels[..., None])[..., 0]
    window_count = win_labels.shape[0]
    gain_one = small_params[0:features]
    offset_one = small_params[features : 2 * features]
    gain_two = small_params[2 * features : 3 * features]
    offset_two = small_params[3 * features : 4 * features]
    table = small_params[4 * features :].reshape(HEADS, -1)
    onehot = (
        relative_index().reshape(-1)[:, None]
        == jnp.arange(table.shape[1], dtype=jnp.int32)[None, :]
    ).astype(jnp.float32)
    rel_bias = jnp.einsum("hr,pr->hp", table, onehot, precision=PRECISE).reshape(
        HEADS, window_area, window_area
    )

    pair_area = 2 * window_area
    place = jnp.arange(PAIR, dtype=jnp.int32)
    pair_labels = jnp.pad(win_labels.reshape(-1, pair_area), ((0, 0), (0, PAIR - pair_area)))
    pair_keys = jnp.where(
        place[None] < pair_area,
        pair_labels * 2 + (place[None] >= window_area).astype(jnp.int32),
        -1 - place[None],
    )
    key_col, key_row = pair_keys[:, :, None], pair_keys[:, None, :]
    valid = (pair_labels >= 9).reshape(-1).astype(jnp.float32)[:, None]
    spread = (
        (place[:, None] % window_area == jnp.arange(window_area, dtype=jnp.int32)[None, :])
        & (place[:, None] < pair_area)
    ).astype(jnp.float32)
    dense_bias = jnp.einsum(
        "hti,ui->htu",
        jnp.einsum("ti,hij->htj", spread, rel_bias, precision=PRECISE),
        spread,
        precision=PRECISE,
    )

    def to_pairs(tensor):
        shaped = tensor.reshape(-1, pair_area, tensor.shape[-1])
        return jnp.pad(shaped, ((0, 0), (0, PAIR - pair_area), (0, 0))).reshape(-1, tensor.shape[-1])

    def from_pairs(tensor):
        shaped = tensor.reshape(-1, PAIR, tensor.shape[-1])
        return shaped[:, :pair_area].reshape(-1, window_area, tensor.shape[-1])

    residual = to_pairs(to_windows(advance(tokens)).astype(jnp.float32))
    normed_one, inverse_one = norm_stats(residual)
    act_one = (normed_one * gain_one + offset_one).astype(jnp.bfloat16)
    mixed = jnp.dot(act_one, w_qkv, preferred_element_type=jnp.float32).astype(jnp.bfloat16)
    mixed_pairs = mixed.reshape(-1, PAIR, mixed.shape[-1])
    attended_pairs, log_total = attention_fwd(mixed_pairs, dense_bias, key_col, key_row, score_scale)
    attended = attended_pairs.reshape(-1, features)
    hidden, act_two, gelu_low, output_flat, stat_block = mlp_fwd(
        attended, residual, valid, w_proj, gain_two, offset_two, w_fc1, w_fc2
    )
    stat_terms = jnp.stack([stat_block[0, 0], stat_block[0, 1], jnp.sum(valid) * features])
    output_low = from_pairs(output_flat)
    restored = retreat(from_windows(output_low, canvases, quad_side, quad_cols))
    flat_out = restored.reshape(canvases, quarters, share_rows, features)
    arrived = lax.all_to_all(flat_out, ("qy", "qx"), 1, 1, tiled=True)
    merged = jnp.take(arrived, merge_order, axis=1, mode="clip").transpose(0, 2, 1, 3).reshape(
        canvases, share_rows, quarters * features
    )
    quarter_ids = jnp.arange(quarters, dtype=jnp.int32)
    source_pick = jnp.sum(
        quarter_ids[:, None] * (merge_order[:, None] == quarter_ids[None, :]).astype(jnp.int32), 0
    )
    incoming = merged_grad.reshape(canvases, share_rows, quarters, features)
    unordered = jnp.take(incoming, source_pick, axis=2, mode="clip").transpose(0, 2, 1, 3)
    returned = lax.all_to_all(unordered, ("qy", "qx"), 1, 1, tiled=True)
    grad_orig = returned.reshape(canvases, quad_side, quad_cols, features)
    grad_out = to_pairs(to_windows(advance(grad_orig)))
    grad_pre, grad_hidden, grad_branch, grad_attended, small_two = mlp_bwd(
        grad_out, hidden, act_two, gain_two, w_fc1, w_fc2, w_proj
    )
    grad_fc2 = jnp.einsum("rf,rc->fc", gelu_low, grad_out, preferred_element_type=jnp.float32)
    grad_fc1 = jnp.einsum("rc,rf->cf", act_two, grad_pre, preferred_element_type=jnp.float32)
    grad_proj = jnp.einsum("rc,rd->cd", attended, grad_branch, preferred_element_type=jnp.float32)
    grad_mixed_pairs, dense_grad_bias = attention_bwd(
        mixed_pairs, grad_attended.reshape(-1, PAIR, features), log_total, dense_bias, key_col, key_row, score_scale
    )
    grad_mixed = grad_mixed_pairs.reshape(-1, 3 * features)
    grad_bias = jnp.einsum(
        "ti,htj->hij",
        spread,
        jnp.einsum("htu,uj->htj", dense_grad_bias, spread, precision=PRECISE),
        precision=PRECISE,
    )
    grad_table = jnp.dot(grad_bias.reshape(HEADS, -1), onehot, precision=PRECISE)
    grad_qkv = jnp.einsum("rc,rf->cf", act_one, grad_mixed, preferred_element_type=jnp.float32)
    grad_act_one = jnp.einsum("rf,cf->rc", grad_mixed, w_qkv, preferred_element_type=jnp.float32)
    grad_input = grad_hidden + norm_back(grad_act_one, normed_one, inverse_one, gain_one)
    grad_low = from_pairs(grad_input.astype(jnp.bfloat16))
    grad_tokens = retreat(from_windows(grad_low, canvases, quad_side, quad_cols))
    small_local = jnp.concatenate(
        [
            jnp.sum(grad_act_one * normed_one, 0),
            jnp.sum(grad_act_one, 0),
            small_two[0],
            small_two[1],
            grad_table.reshape(-1),
        ]
    )
    every_block = jnp.concatenate(
        [lane_blocks(grad_qkv), lane_blocks(grad_proj), lane_blocks(grad_fc1), lane_blocks(grad_fc2)],
        0,
    )
    depth = every_block.shape[1] // PARTS
    parted = [
        jnp.take(every_block[:, index * depth : (index + 1) * depth], owner_list, axis=0, mode="clip")
        for index in range(PARTS)
    ]
    small_every = lax.all_gather(
        jnp.concatenate([small_local, stat_terms]), ("dp", "qy", "qx"), axis=0, tiled=False
    )
    owned_grads, _ = reduce_to_owners(parted, None)
    small_all = jnp.sum(small_every, 0)
    small_total = small_all[: small_local.shape[0]]
    stat_total = small_all[small_local.shape[0] :]
    new_first, new_second, new_master = rotate_update(
        owned_grads, master_blocks, first_moment, second_moment, basis_left, basis_right
    )
    small_first_new, small_second_new, small_new = small_update(
        small_total, small_params, small_first, small_second
    )
    stats = jnp.stack(
        [jnp.sqrt(stat_total[0] / stat_total[2]), jnp.sqrt(stat_total[1] / (2.0 * stat_total[2]))]
    )
    return (
        merged,
        grad_tokens,
        owned_grads,
        new_master,
        new_first,
        new_second,
        new_master.astype(jnp.bfloat16),
        small_total,
        small_first_new,
        small_second_new,
        small_new,
        stats,
    )


def solution(mesh):
    placed = (
        P("dp", "qy", "qx", None),
        P("dp", None, None),
        P(),
        P(),
        P(),
        P(),
        P(),
        P(),
        P(),
        P(),
        P(),
        P("dp", None, None),
        P("dp", None, None),
        P("dp", None, None),
        P("dp", None, None),
        P("dp", None, None),
        P("dp", ("qy", "qx"), None),
    )
    return jax.shard_map(
        local,
        mesh=mesh,
        in_specs=placed,
        out_specs=(
            P("dp", ("qy", "qx"), None),
            P("dp", "qy", "qx", None),
            P("dp", None, None),
            P("dp", None, None),
            P("dp", None, None),
            P("dp", None, None),
            P("dp", None, None),
            P(),
            P(),
            P(),
            P(),
            P(),
        ),
        check_vma=False,
    )
```

```python
import functools
from functools import partial

import numpy as np

import jax
import jax.numpy as jnp
from jax import lax
from jax.experimental import pallas as pl
from jax.experimental.pallas import tpu as pltpu
from jax.sharding import PartitionSpec as P

HEADS = 12
WIN = 7
SHIFT = 3
BLK = 96


BETA_ONE = 0.5
BETA_TWO = 0.6
ADAM_EPSILON = 1e-08
RATE_BLOCKS = 0.04
RATE_SMALL = 0.2
MASK_FILL = -1e30
NORM_EPSILON = 1e-05
PRECISE = lax.Precision.HIGHEST
ROTATE = lax.Precision.HIGH


def passed_along(value, axis, steps):
    count = lax.axis_size(axis)
    pairs = [(source, (source + steps) % count) for source in range(count)]
    return lax.ppermute(value, axis, pairs)


def partner_of(value, axis, mask):
    count = lax.axis_size(axis)
    pairs = [(source, source ^ mask) for source in range(count)]
    return lax.ppermute(value, axis, pairs)


def bit_of(axis, mask):
    return ((lax.axis_index(axis) & mask) != 0).astype(jnp.int32)


LANES = 128
PARTS = 3
GROUP = 4
LANES = 128
MASK_FILL = -1e30
PAIR = 112
STEP_PAIRS = 8


def _stacked(value, lane4):
    wide = jnp.broadcast_to(value.astype(jnp.float32)[None], (GROUP, PAIR, LANES))
    return jnp.where(lane4, wide, 0.0).reshape(GROUP * PAIR, LANES).astype(jnp.bfloat16)


def _gather_lanes(stack, lane4):
    return jnp.sum(jnp.where(lane4, stack.reshape(GROUP, PAIR, LANES), 0.0), 0)


def _scores(q4, k4, bias4, allowed, scale, lane4):
    raw = lax.dot_general(_stacked(q4, lane4), k4, (((1,), (1,)), ((), ())), preferred_element_type=jnp.float32)
    raw = raw.reshape(GROUP, PAIR, PAIR) * scale + bias4
    return jnp.where(allowed[None], raw, MASK_FILL)


def _lane_masks():
    lane4 = lax.broadcasted_iota(jnp.int32, (GROUP, 1, LANES), 2) // 32 == lax.broadcasted_iota(
        jnp.int32, (GROUP, 1, LANES), 0)
    return lane4, lax.broadcasted_iota(jnp.int32, (1, LANES), 1)


def _fwd_kernel(mix_ref, bias_ref, kc_ref, kr_ref, out_ref, lse_ref, *, scale):
    width = HEADS * 32
    lane4, head_lane = _lane_masks()
    for sub in range(STEP_PAIRS):
        allowed = kc_ref[sub] == kr_ref[sub]
        lse_all = jnp.zeros((PAIR, LANES), jnp.float32)
        for g in range(HEADS // GROUP):
            q4 = mix_ref[sub, :, pl.ds(g * LANES, LANES)]
            k4 = mix_ref[sub, :, pl.ds(width + g * LANES, LANES)]
            v4 = mix_ref[sub, :, pl.ds(2 * width + g * LANES, LANES)]
            s = _scores(q4, k4, bias_ref[pl.ds(g * GROUP, GROUP)], allowed, scale, lane4)
            top = jnp.max(s, -1, keepdims=True)
            e = jnp.exp(s - top)
            total = jnp.sum(e, -1, keepdims=True)
            probs = (e / total).reshape(GROUP * PAIR, PAIR).astype(jnp.bfloat16)
            mixed_out = jnp.dot(probs, v4, preferred_element_type=jnp.float32)
            out_ref[sub, :, pl.ds(g * LANES, LANES)] = _gather_lanes(mixed_out, lane4).astype(out_ref.dtype)
            lse = top + jnp.log(total)
            for j in range(GROUP):
                lse_all = jnp.where(head_lane == g * GROUP + j, lse[j], lse_all)
        lse_ref[sub] = lse_all


def _bwd_kernel(mix_ref, grad_ref, lse_ref, bias_ref, kc_ref, kr_ref, gmix_ref, dbias_ref, *, scale):
    width = HEADS * 32
    lane4, head_lane = _lane_masks()
    step = pl.program_id(0)

    @pl.when(step == 0)
    def _():
        dbias_ref[...] = jnp.zeros_like(dbias_ref)

    for sub in range(STEP_PAIRS):
        allowed = kc_ref[sub] == kr_ref[sub]
        lse_all = lse_ref[sub]
        for g in range(HEADS // GROUP):
            q4 = mix_ref[sub, :, pl.ds(g * LANES, LANES)]
            k4 = mix_ref[sub, :, pl.ds(width + g * LANES, LANES)]
            v4 = mix_ref[sub, :, pl.ds(2 * width + g * LANES, LANES)]
            d4 = grad_ref[sub, :, pl.ds(g * LANES, LANES)]
            heads = pl.ds(g * GROUP, GROUP)
            s = _scores(q4, k4, bias_ref[heads], allowed, scale, lane4)
            lse = jnp.stack([
                jnp.sum(jnp.where(head_lane == g * GROUP + j, lse_all, 0.0), -1, keepdims=True)
                for j in range(GROUP)
            ])
            probs = jnp.exp(s - lse)
            d_stack = _stacked(d4, lane4)
            dprobs = lax.dot_general(d_stack, v4, (((1,), (1,)), ((), ())), preferred_element_type=jnp.float32)
            dprobs = dprobs.reshape(GROUP, PAIR, PAIR)
            inner = jnp.sum(probs * dprobs, -1, keepdims=True)
            dscores = (probs * (dprobs - inner)).reshape(GROUP * PAIR, PAIR).astype(jnp.bfloat16)
            dbias_ref[heads] = dbias_ref[heads] + dscores.astype(jnp.float32).reshape(GROUP, PAIR, PAIR)
            gq = _gather_lanes(jnp.dot(dscores, k4, preferred_element_type=jnp.float32), lane4)
            gk = lax.dot_general(dscores, _stacked(q4, lane4), (((0,), (0,)), ((), ())), preferred_element_type=jnp.float32)
            gv = lax.dot_general(probs.reshape(GROUP * PAIR, PAIR).astype(jnp.bfloat16), d_stack,
                                 (((0,), (0,)), ((), ())), preferred_element_type=jnp.float32)
            gmix_ref[sub, :, pl.ds(g * LANES, LANES)] = (gq * scale).astype(gmix_ref.dtype)
            gmix_ref[sub, :, pl.ds(width + g * LANES, LANES)] = (gk * scale).astype(gmix_ref.dtype)
            gmix_ref[sub, :, pl.ds(2 * width + g * LANES, LANES)] = gv.astype(gmix_ref.dtype)


def _pair_spec(width):
    return pl.BlockSpec((STEP_PAIRS, PAIR, width), lambda p: (p, 0, 0))


def attention_fwd(mixed_pairs, bias, key_col, key_row, scale):
    pairs = mixed_pairs.shape[0]
    kernel = functools.partial(_fwd_kernel, scale=scale)
    return pl.pallas_call(
        kernel,
        grid=(pairs // STEP_PAIRS,),
        out_shape=(
            jax.ShapeDtypeStruct((pairs, PAIR, HEADS * 32), jnp.bfloat16),
            jax.ShapeDtypeStruct((pairs, PAIR, LANES), jnp.float32),
        ),
        in_specs=[_pair_spec(mixed_pairs.shape[2]), pl.BlockSpec(bias.shape, lambda p: (0, 0, 0)),
                  pl.BlockSpec((STEP_PAIRS, PAIR, 1), lambda p: (p, 0, 0)), pl.BlockSpec((STEP_PAIRS, 1, PAIR), lambda p: (p, 0, 0))],
        out_specs=(_pair_spec(HEADS * 32), _pair_spec(LANES)),
        compiler_params=pltpu.CompilerParams(dimension_semantics=("arbitrary",), vmem_limit_bytes=32 * 1024 * 1024),
    )(mixed_pairs, bias, key_col, key_row)


def attention_bwd(mixed_pairs, grad_pairs, lse, bias, key_col, key_row, scale):
    pairs = mixed_pairs.shape[0]
    kernel = functools.partial(_bwd_kernel, scale=scale)
    return pl.pallas_call(
        kernel,
        grid=(pairs // STEP_PAIRS,),
        out_shape=(
            jax.ShapeDtypeStruct(mixed_pairs.shape, jnp.bfloat16),
            jax.ShapeDtypeStruct(bias.shape, jnp.float32),
        ),
        in_specs=[_pair_spec(mixed_pairs.shape[2]), _pair_spec(HEADS * 32), _pair_spec(LANES),
                  pl.BlockSpec(bias.shape, lambda p: (0, 0, 0)),
                  pl.BlockSpec((STEP_PAIRS, PAIR, 1), lambda p: (p, 0, 0)), pl.BlockSpec((STEP_PAIRS, 1, PAIR), lambda p: (p, 0, 0))],
        out_specs=(_pair_spec(mixed_pairs.shape[2]), pl.BlockSpec(bias.shape, lambda p: (0, 0, 0))),
        compiler_params=pltpu.CompilerParams(dimension_semantics=("arbitrary",), vmem_limit_bytes=32 * 1024 * 1024),
    )(mixed_pairs, grad_pairs, lse, bias, key_col, key_row)


def lane_blocks(matrix):
    row_blocks, col_blocks = matrix.shape[0] // BLK, matrix.shape[1] // BLK
    shaped = matrix.reshape(row_blocks, BLK, col_blocks, BLK).transpose(0, 2, 1, 3)
    return shaped.reshape(row_blocks * col_blocks, BLK * BLK // LANES, LANES)


ROWS = 896
SQRT_HALF = float(np.sqrt(0.5))
INV_SQRT_TAU = float(1.0 / np.sqrt(2.0 * np.pi))


def _norm(tensor):
    center = tensor - jnp.mean(tensor, -1, keepdims=True)
    inverse = lax.rsqrt(jnp.mean(center * center, -1, keepdims=True) + NORM_EPSILON)
    return center * inverse, inverse


def _mlp_fwd_kernel(att_ref, res_ref, valid_ref, wp_ref, gain_ref, off_ref, w1_ref, w2_ref,
                    hid_ref, act_ref, gelu_ref, out_ref, stat_ref):
    step = pl.program_id(0)
    branch_one = jnp.dot(att_ref[...], wp_ref[...], preferred_element_type=jnp.float32)
    hidden = res_ref[...] + branch_one
    normed, _ = _norm(hidden)
    act = (normed * gain_ref[...] + off_ref[...]).astype(jnp.bfloat16)
    pre = jnp.dot(act, w1_ref[...], preferred_element_type=jnp.float32)
    gelu = ((0.5 * pre) * (1.0 + lax.erf(pre * SQRT_HALF))).astype(jnp.bfloat16)
    branch_two = jnp.dot(gelu, w2_ref[...], preferred_element_type=jnp.float32)
    output = hidden + branch_two
    valid = valid_ref[...]
    first = jnp.sum(valid * output * output)
    second = jnp.sum(valid * (branch_one * branch_one + branch_two * branch_two))
    lane = lax.broadcasted_iota(jnp.int32, (8, 128), 1)
    row = lax.broadcasted_iota(jnp.int32, (8, 128), 0)
    here = jnp.where((row == 0) & (lane == 0), first, 0.0) + jnp.where((row == 0) & (lane == 1), second, 0.0)

    @pl.when(step == 0)
    def _():
        stat_ref[...] = jnp.zeros_like(stat_ref)

    stat_ref[...] = stat_ref[...] + here
    hid_ref[...] = hidden
    act_ref[...] = act
    gelu_ref[...] = gelu
    out_ref[...] = output.astype(out_ref.dtype)


def _mlp_bwd_kernel(gout_ref, hid_ref, act_ref, gain_ref, w1_ref, w2_ref, wp_ref, att_ref, gelu_ref,
                    gpre_ref, ghid_ref, gbr_ref, gatt_ref, small_ref, gfc1_ref, gfc2_ref, gproj_ref):
    step = pl.program_id(0)
    contract_last = (((1,), (1,)), ((), ()))
    pre = jnp.dot(act_ref[...], w1_ref[...], preferred_element_type=jnp.float32)
    grad_out = gout_ref[...]
    grad_gelu = lax.dot_general(grad_out, w2_ref[...], contract_last, preferred_element_type=jnp.float32)
    cdf = 0.5 * (1.0 + lax.erf(pre * SQRT_HALF))
    pdf = jnp.exp(-0.5 * pre * pre) * INV_SQRT_TAU
    grad_pre = (grad_gelu * (cdf + pre * pdf)).astype(jnp.bfloat16)
    grad_act = lax.dot_general(grad_pre, w1_ref[...], contract_last, preferred_element_type=jnp.float32)
    normed, inverse = _norm(hid_ref[...])
    scaled = grad_act * gain_ref[...]
    mean_one = jnp.mean(scaled, -1, keepdims=True)
    mean_two = jnp.mean(scaled * normed, -1, keepdims=True)
    grad_hidden = grad_out.astype(jnp.float32) + inverse * (scaled - mean_one - normed * mean_two)
    grad_branch = grad_hidden.astype(jnp.bfloat16)
    grad_att = lax.dot_general(grad_branch, wp_ref[...], contract_last, preferred_element_type=jnp.float32)
    sums = jnp.concatenate(
        [jnp.sum(grad_act * normed, 0, keepdims=True), jnp.sum(grad_act, 0, keepdims=True),
         jnp.zeros((6, grad_act.shape[1]), jnp.float32)], 0)

    contract_rows = (((0,), (0,)), ((), ()))
    fc1 = lax.dot_general(act_ref[...], grad_pre, contract_rows, preferred_element_type=jnp.float32)
    fc2 = lax.dot_general(gelu_ref[...], grad_out, contract_rows, preferred_element_type=jnp.float32)
    proj = lax.dot_general(att_ref[...], grad_branch, contract_rows, preferred_element_type=jnp.float32)

    @pl.when(step == 0)
    def _():
        small_ref[...] = jnp.zeros_like(small_ref)
        gfc1_ref[...] = jnp.zeros_like(gfc1_ref)
        gfc2_ref[...] = jnp.zeros_like(gfc2_ref)
        gproj_ref[...] = jnp.zeros_like(gproj_ref)

    small_ref[...] = small_ref[...] + sums
    gfc1_ref[...] = gfc1_ref[...] + fc1
    gfc2_ref[...] = gfc2_ref[...] + fc2
    gproj_ref[...] = gproj_ref[...] + proj
    gpre_ref[...] = grad_pre
    ghid_ref[...] = grad_hidden
    gbr_ref[...] = grad_branch
    gatt_ref[...] = grad_att.astype(gatt_ref.dtype)


def _rows(width):
    return pl.BlockSpec((ROWS, width), lambda i: (i, 0))


def _whole(shape):
    return pl.BlockSpec(shape, lambda i: (0,) * len(shape))


def mlp_fwd(attended, residual, valid, w_proj, gain, offset, w_fc1, w_fc2):
    tokens, width = residual.shape
    hidden_width = w_fc1.shape[1]
    return pl.pallas_call(
        _mlp_fwd_kernel,
        grid=(tokens // ROWS,),
        out_shape=(
            jax.ShapeDtypeStruct((tokens, width), jnp.float32),
            jax.ShapeDtypeStruct((tokens, width), jnp.bfloat16),
            jax.ShapeDtypeStruct((tokens, hidden_width), jnp.bfloat16),
            jax.ShapeDtypeStruct((tokens, width), jnp.bfloat16),
            jax.ShapeDtypeStruct((8, 128), jnp.float32),
        ),
        in_specs=[_rows(width), _rows(width), _rows(1), _whole(w_proj.shape), _whole((1, width)),
                  _whole((1, width)), _whole(w_fc1.shape), _whole(w_fc2.shape)],
        out_specs=(_rows(width), _rows(width), _rows(hidden_width), _rows(width), _whole((8, 128))),
        compiler_params=pltpu.CompilerParams(dimension_semantics=("arbitrary",), vmem_limit_bytes=48 * 1024 * 1024),
    )(attended, residual, valid, w_proj, gain.reshape(1, -1), offset.reshape(1, -1), w_fc1, w_fc2)


def mlp_bwd(grad_out, hidden, act_two, gain, w_fc1, w_fc2, w_proj, attended, gelu_low):
    tokens, width = hidden.shape
    hidden_width = w_fc1.shape[1]
    return pl.pallas_call(
        _mlp_bwd_kernel,
        grid=(tokens // ROWS,),
        out_shape=(
            jax.ShapeDtypeStruct((tokens, hidden_width), jnp.bfloat16),
            jax.ShapeDtypeStruct((tokens, width), jnp.float32),
            jax.ShapeDtypeStruct((tokens, width), jnp.bfloat16),
            jax.ShapeDtypeStruct((tokens, width), jnp.bfloat16),
            jax.ShapeDtypeStruct((8, width), jnp.float32),
            jax.ShapeDtypeStruct(w_fc1.shape, jnp.float32),
            jax.ShapeDtypeStruct(w_fc2.shape, jnp.float32),
            jax.ShapeDtypeStruct(w_proj.shape, jnp.float32),
        ),
        in_specs=[_rows(width), _rows(width), _rows(width), _whole((1, width)), _whole(w_fc1.shape),
                  _whole(w_fc2.shape), _whole(w_proj.shape), _rows(width), _rows(hidden_width)],
        out_specs=(_rows(hidden_width), _rows(width), _rows(width), _rows(width), _whole((8, width)),
                   _whole(w_fc1.shape), _whole(w_fc2.shape), _whole(w_proj.shape)),
        compiler_params=pltpu.CompilerParams(dimension_semantics=("arbitrary",), vmem_limit_bytes=48 * 1024 * 1024),
    )(grad_out, hidden, act_two, gain.reshape(1, -1), w_fc1, w_fc2, w_proj, attended, gelu_low)


def reduce_to_owners(parted, small):
    groups = lax.axis_size("dp")
    dp_bits = groups.bit_length() - 1
    n_qy, n_qx = lax.axis_size("qy"), lax.axis_size("qx")
    count, depth = parted[0].shape[0], parted[0].shape[1]
    per_group = count // groups
    names = [("dp", 1 << power) for power in reversed(range(dp_bits))] + [("qy", 1), ("qx", 1)]
    cross = [("qy", 1)] + [("dp", 1 << power) for power in range(dp_bits)]
    pieces, piece_names, orders = [], [], []
    for index, part in enumerate(parted):
        pieces.append(
            part.reshape([2] * dp_bits + [n_qy, n_qx, per_group * depth // (n_qy * n_qx), LANES])
        )
        piece_names.append(list(names))
        turn = index % len(cross)
        orders.append([("qx", 1)] + cross[turn:] + cross[:turn])
    for stage in range(len(names)):
        for index in range(len(pieces)):
            bit = orders[index][stage]
            place = piece_names[index].index(bit)
            mine = bit_of(*bit)
            keep = lax.dynamic_index_in_dim(pieces[index], mine, place, keepdims=False)
            send = lax.dynamic_index_in_dim(pieces[index], 1 - mine, place, keepdims=False)
            piece_names[index].remove(bit)
            arrived = partner_of(send.astype(jnp.bfloat16), *bit)
            pieces[index] = keep + arrived.astype(jnp.float32)
            if index == 0:
                small = small + partner_of(small, *bit)
                pieces[0], small = lax.optimization_barrier((pieces[0], small))
    chunk = jnp.stack(pieces)
    other = partner_of(chunk, "qy", 1)
    pair = jnp.where(bit_of("qy", 1) == 1, jnp.stack([other, chunk], 1), jnp.stack([chunk, other], 1))
    other = partner_of(pair, "qx", 1)
    quad = jnp.where(bit_of("qx", 1) == 1, jnp.stack([other, pair], 2), jnp.stack([pair, other], 2))
    quad = quad.reshape(len(pieces), per_group, depth, LANES).transpose(1, 0, 2, 3)
    return quad.reshape(per_group, BLK, BLK), small


def cut_along(value, dim, devices):
    before, after = (value.shape[:dim], value.shape[dim + 1 :])
    return jnp.moveaxis(value.reshape(*before, devices, -1, *after), dim, 0)


def sent_and_summed(value, axis, dim):
    pieces = cut_along(value, dim, lax.axis_size(axis))
    arrived = lax.all_to_all(pieces, axis, split_axis=0, concat_axis=0, tiled=True)
    return arrived.astype(jnp.float32).sum(axis=0)


def norm_stats(tensor):
    center = tensor - jnp.mean(tensor, -1, keepdims=True)
    inverse = lax.rsqrt(jnp.mean(center * center, -1, keepdims=True) + NORM_EPSILON)
    return (center * inverse, inverse)


def norm_back(grad_act, normed, inverse, gain):
    scaled = grad_act * gain
    mean_one = jnp.mean(scaled, -1, keepdims=True)
    mean_two = jnp.mean(scaled * normed, -1, keepdims=True)
    return inverse * (scaled - mean_one - normed * mean_two)


def to_windows(tensor):
    canvases, rows_side, cols_side, channels = tensor.shape
    shaped = tensor.reshape(canvases, rows_side // WIN, WIN, cols_side // WIN, WIN, channels)
    return shaped.transpose(0, 1, 3, 2, 4, 5).reshape(
        canvases * (rows_side // WIN) * (cols_side // WIN), WIN * WIN, channels
    )


def from_windows(tensor, canvases, rows_side, cols_side):
    channels = tensor.shape[-1]
    shaped = tensor.reshape(canvases, rows_side // WIN, cols_side // WIN, WIN, WIN, channels)
    return shaped.transpose(0, 1, 3, 2, 4, 5).reshape(canvases, rows_side, cols_side, channels)


def relative_index():
    places = jnp.arange(WIN * WIN, dtype=jnp.int32)
    row_of = places // WIN
    col_of = places % WIN
    return (row_of[:, None] - row_of[None, :] + WIN - 1) * (2 * WIN - 1) + (
        col_of[:, None] - col_of[None, :] + WIN - 1
    )


def region_of(places, full):
    return jnp.where(places < full - WIN, 0, jnp.where(places < full - SHIFT, 1, 2)).astype(
        jnp.int32
    )


def advance(tensor):
    upper = passed_along(tensor[:, :SHIFT], "qy", -1)
    tensor = jnp.concatenate([tensor[:, SHIFT:], upper], 1)
    leftmost = passed_along(tensor[:, :, :SHIFT], "qx", -1)
    return jnp.concatenate([tensor[:, :, SHIFT:], leftmost], 2)


def retreat(tensor):
    lowest = passed_along(tensor[:, -SHIFT:], "qy", 1)
    tensor = jnp.concatenate([lowest, tensor[:, :-SHIFT]], 1)
    rightmost = passed_along(tensor[:, :, -SHIFT:], "qx", 1)
    return jnp.concatenate([rightmost, tensor[:, :, :-SHIFT]], 2)


def blocks_of(matrix):
    row_blocks = matrix.shape[0] // BLK
    col_blocks = matrix.shape[1] // BLK
    return (
        matrix.reshape(row_blocks, BLK, col_blocks, BLK)
        .transpose(0, 2, 1, 3)
        .reshape(row_blocks * col_blocks, BLK, BLK)
    )


def rotate_update(grads, master, first, second, left, right):
    turned = jnp.einsum("sji,sjk->sik", left, grads, precision=ROTATE)
    turned = jnp.einsum("sik,skl->sil", turned, right, precision=ROTATE)
    new_first = BETA_ONE * first + (1.0 - BETA_ONE) * turned
    new_second = BETA_TWO * second + (1.0 - BETA_TWO) * turned * turned
    direction = new_first / (jnp.sqrt(new_second) + ADAM_EPSILON)
    back = jnp.einsum("sij,sjk->sik", left, direction, precision=ROTATE)
    back = jnp.einsum("sik,slk->sil", back, right, precision=ROTATE)
    return (new_first, new_second, master - RATE_BLOCKS * back)


def small_update(grads, params, first, second):
    new_first = BETA_ONE * first + (1.0 - BETA_ONE) * grads
    new_second = BETA_TWO * second + (1.0 - BETA_TWO) * grads * grads
    direction = new_first / (jnp.sqrt(new_second) + ADAM_EPSILON)
    return (new_first, new_second, params - RATE_SMALL * direction)


def local(
    tokens,
    crop_ids,
    merge_order,
    owner_list,
    w_qkv,
    w_proj,
    w_fc1,
    w_fc2,
    small_params,
    small_first,
    small_second,
    master_blocks,
    first_moment,
    second_moment,
    basis_left,
    basis_right,
    merged_grad,
):
    canvases, quad_side, quad_cols, features = tokens.shape
    head_dim = features // HEADS
    score_scale = head_dim ** (-0.5)
    window_area = WIN * WIN
    quarters = lax.axis_size(("qy", "qx"))
    share_rows = quad_side * quad_cols // quarters
    row_base = lax.axis_index("qy") * quad_side
    col_base = lax.axis_index("qx") * quad_cols
    rolled = jnp.roll(crop_ids, (-SHIFT, -SHIFT), (1, 2))
    local_ids = lax.dynamic_slice(
        rolled, (jnp.int32(0), row_base, col_base), (canvases, quad_side, quad_cols)
    )
    region_row = region_of(
        row_base + jnp.arange(quad_side, dtype=jnp.int32), quad_side * lax.axis_size("qy")
    )
    region_col = region_of(
        col_base + jnp.arange(quad_cols, dtype=jnp.int32), quad_cols * lax.axis_size("qx")
    )
    labels = (local_ids + 1) * 9 + region_row[None, :, None] * 3 + region_col[None, None, :]
    win_labels = to_windows(labels[..., None])[..., 0]
    window_count = win_labels.shape[0]
    gain_one = small_params[0:features]
    offset_one = small_params[features : 2 * features]
    gain_two = small_params[2 * features : 3 * features]
    offset_two = small_params[3 * features : 4 * features]
    table = small_params[4 * features :].reshape(HEADS, -1)
    onehot = (
        relative_index().reshape(-1)[:, None]
        == jnp.arange(table.shape[1], dtype=jnp.int32)[None, :]
    ).astype(jnp.float32)
    rel_bias = jnp.einsum("hr,pr->hp", table, onehot, precision=PRECISE).reshape(
        HEADS, window_area, window_area
    )

    pair_area = 2 * window_area
    place = jnp.arange(PAIR, dtype=jnp.int32)
    pair_labels = jnp.pad(win_labels.reshape(-1, pair_area), ((0, 0), (0, PAIR - pair_area)))
    pair_keys = jnp.where(
        place[None] < pair_area,
        pair_labels * 2 + (place[None] >= window_area).astype(jnp.int32),
        -1 - place[None],
    )
    key_col, key_row = pair_keys[:, :, None], pair_keys[:, None, :]
    valid = (pair_labels >= 9).reshape(-1).astype(jnp.float32)[:, None]
    spread = (
        (place[:, None] % window_area == jnp.arange(window_area, dtype=jnp.int32)[None, :])
        & (place[:, None] < pair_area)
    ).astype(jnp.float32)
    dense_bias = jnp.einsum(
        "hti,ui->htu",
        jnp.einsum("ti,hij->htj", spread, rel_bias, precision=PRECISE),
        spread,
        precision=PRECISE,
    )

    def to_pairs(tensor):
        shaped = tensor.reshape(-1, pair_area, tensor.shape[-1])
        return jnp.pad(shaped, ((0, 0), (0, PAIR - pair_area), (0, 0))).reshape(-1, tensor.shape[-1])

    def from_pairs(tensor):
        shaped = tensor.reshape(-1, PAIR, tensor.shape[-1])
        return shaped[:, :pair_area].reshape(-1, window_area, tensor.shape[-1])

    residual = to_pairs(to_windows(advance(tokens)).astype(jnp.float32))
    normed_one, inverse_one = norm_stats(residual)
    act_one = (normed_one * gain_one + offset_one).astype(jnp.bfloat16)
    mixed = jnp.dot(act_one, w_qkv, preferred_element_type=jnp.float32).astype(jnp.bfloat16)
    mixed_pairs = mixed.reshape(-1, PAIR, mixed.shape[-1])
    attended_pairs, log_total = attention_fwd(mixed_pairs, dense_bias, key_col, key_row, score_scale)
    attended = attended_pairs.reshape(-1, features)
    hidden, act_two, gelu_low, output_flat, stat_block = mlp_fwd(
        attended, residual, valid, w_proj, gain_two, offset_two, w_fc1, w_fc2
    )
    stat_terms = jnp.stack([stat_block[0, 0], stat_block[0, 1], jnp.sum(valid) * features])
    output_low = from_pairs(output_flat)
    restored = retreat(from_windows(output_low, canvases, quad_side, quad_cols))
    flat_out = restored.reshape(canvases, quarters, share_rows, features)
    arrived = lax.all_to_all(flat_out, ("qy", "qx"), 1, 1, tiled=True)
    merged = jnp.take(arrived, merge_order, axis=1, mode="clip").transpose(0, 2, 1, 3).reshape(
        canvases, share_rows, quarters * features
    )
    quarter_ids = jnp.arange(quarters, dtype=jnp.int32)
    source_pick = jnp.sum(
        quarter_ids[:, None] * (merge_order[:, None] == quarter_ids[None, :]).astype(jnp.int32), 0
    )
    incoming = merged_grad.reshape(canvases, share_rows, quarters, features)
    unordered = jnp.take(incoming, source_pick, axis=2, mode="clip").transpose(0, 2, 1, 3)
    returned = lax.all_to_all(unordered, ("qy", "qx"), 1, 1, tiled=True)
    grad_orig = returned.reshape(canvases, quad_side, quad_cols, features)
    grad_out = to_pairs(to_windows(advance(grad_orig)))
    (grad_pre, grad_hidden, grad_branch, grad_attended, small_two, grad_fc1, grad_fc2, grad_proj) = (
        mlp_bwd(grad_out, hidden, act_two, gain_two, w_fc1, w_fc2, w_proj, attended, gelu_low)
    )
    grad_mixed_pairs, dense_grad_bias = attention_bwd(
        mixed_pairs, grad_attended.reshape(-1, PAIR, features), log_total, dense_bias, key_col, key_row, score_scale
    )
    grad_mixed = grad_mixed_pairs.reshape(-1, 3 * features)
    grad_bias = jnp.einsum(
        "ti,htj->hij",
        spread,
        jnp.einsum("htu,uj->htj", dense_grad_bias, spread, precision=PRECISE),
        precision=PRECISE,
    )
    grad_table = jnp.dot(grad_bias.reshape(HEADS, -1), onehot, precision=PRECISE)
    grad_qkv = jnp.einsum("rc,rf->cf", act_one, grad_mixed, preferred_element_type=jnp.float32)
    grad_act_one = jnp.einsum("rf,cf->rc", grad_mixed, w_qkv, preferred_element_type=jnp.float32)
    grad_input = grad_hidden + norm_back(grad_act_one, normed_one, inverse_one, gain_one)
    grad_low = from_pairs(grad_input.astype(jnp.bfloat16))
    grad_tokens = retreat(from_windows(grad_low, canvases, quad_side, quad_cols))
    small_local = jnp.concatenate(
        [
            jnp.sum(grad_act_one * normed_one, 0),
            jnp.sum(grad_act_one, 0),
            small_two[0],
            small_two[1],
            grad_table.reshape(-1),
        ]
    )
    every_block = jnp.concatenate(
        [lane_blocks(grad_qkv), lane_blocks(grad_proj), lane_blocks(grad_fc1), lane_blocks(grad_fc2)],
        0,
    )
    depth = every_block.shape[1] // PARTS
    parted = [
        jnp.take(every_block[:, index * depth : (index + 1) * depth], owner_list, axis=0, mode="clip")
        for index in range(PARTS)
    ]
    owned_grads, small_all = reduce_to_owners(parted, jnp.concatenate([small_local, stat_terms]))
    small_total = small_all[: small_local.shape[0]]
    stat_total = small_all[small_local.shape[0] :]
    new_first, new_second, new_master = rotate_update(
        owned_grads, master_blocks, first_moment, second_moment, basis_left, basis_right
    )
    small_first_new, small_second_new, small_new = small_update(
        small_total, small_params, small_first, small_second
    )
    stats = jnp.stack(
        [jnp.sqrt(stat_total[0] / stat_total[2]), jnp.sqrt(stat_total[1] / (2.0 * stat_total[2]))]
    )
    return (
        merged,
        grad_tokens,
        owned_grads,
        new_master,
        new_first,
        new_second,
        new_master.astype(jnp.bfloat16),
        small_total,
        small_first_new,
        small_second_new,
        small_new,
        stats,
    )


def solution(mesh):
    placed = (
        P("dp", "qy", "qx", None),
        P("dp", None, None),
        P(),
        P(),
        P(),
        P(),
        P(),
        P(),
        P(),
        P(),
        P(),
        P("dp", None, None),
        P("dp", None, None),
        P("dp", None, None),
        P("dp", None, None),
        P("dp", None, None),
        P("dp", ("qy", "qx"), None),
    )
    return jax.shard_map(
        local,
        mesh=mesh,
        in_specs=placed,
        out_specs=(
            P("dp", ("qy", "qx"), None),
            P("dp", "qy", "qx", None),
            P("dp", None, None),
            P("dp", None, None),
            P("dp", None, None),
            P("dp", None, None),
            P("dp", None, None),
            P(),
            P(),
            P(),
            P(),
            P(),
        ),
        check_vma=False,
    )
```

```python
import functools
from functools import partial

import numpy as np

import jax
import jax.numpy as jnp
from jax import lax
from jax.experimental import pallas as pl
from jax.experimental.pallas import tpu as pltpu
from jax.sharding import PartitionSpec as P

HEADS = 12
WIN = 7
SHIFT = 3
BLK = 96


BETA_ONE = 0.5
BETA_TWO = 0.6
ADAM_EPSILON = 1e-08
RATE_BLOCKS = 0.04
RATE_SMALL = 0.2
MASK_FILL = -1e30
NORM_EPSILON = 1e-05
PRECISE = lax.Precision.HIGHEST
ROTATE = lax.Precision.HIGH


def passed_along(value, axis, steps):
    count = lax.axis_size(axis)
    pairs = [(source, (source + steps) % count) for source in range(count)]
    return lax.ppermute(value, axis, pairs)


def partner_of(value, axis, mask):
    count = lax.axis_size(axis)
    pairs = [(source, source ^ mask) for source in range(count)]
    return lax.ppermute(value, axis, pairs)


def bit_of(axis, mask):
    return ((lax.axis_index(axis) & mask) != 0).astype(jnp.int32)


LANES = 128
PARTS = 3
GROUP = 4
LANES = 128
MASK_FILL = -1e30
PAIR = 112
STEP_PAIRS = 8


def _stacked(value, lane4):
    wide = jnp.broadcast_to(value.astype(jnp.float32)[None], (GROUP, PAIR, LANES))
    return jnp.where(lane4, wide, 0.0).reshape(GROUP * PAIR, LANES).astype(jnp.bfloat16)


def _gather_lanes(stack, lane4):
    return jnp.sum(jnp.where(lane4, stack.reshape(GROUP, PAIR, LANES), 0.0), 0)


def _scores(q4, k4, bias4, allowed, scale, lane4):
    raw = lax.dot_general(_stacked(q4, lane4), k4, (((1,), (1,)), ((), ())), preferred_element_type=jnp.float32)
    raw = raw.reshape(GROUP, PAIR, PAIR) * scale + bias4
    return jnp.where(allowed[None], raw, MASK_FILL)


def _lane_masks():
    lane4 = lax.broadcasted_iota(jnp.int32, (GROUP, 1, LANES), 2) // 32 == lax.broadcasted_iota(
        jnp.int32, (GROUP, 1, LANES), 0)
    return lane4, lax.broadcasted_iota(jnp.int32, (1, LANES), 1)


def _fwd_kernel(mix_ref, bias_ref, kc_ref, kr_ref, out_ref, lse_ref, *, scale):
    width = HEADS * 32
    lane4, head_lane = _lane_masks()
    for sub in range(STEP_PAIRS):
        allowed = kc_ref[sub] == kr_ref[sub]
        lse_all = jnp.zeros((PAIR, LANES), jnp.float32)
        for g in range(HEADS // GROUP):
            q4 = mix_ref[sub, :, pl.ds(g * LANES, LANES)]
            k4 = mix_ref[sub, :, pl.ds(width + g * LANES, LANES)]
            v4 = mix_ref[sub, :, pl.ds(2 * width + g * LANES, LANES)]
            s = _scores(q4, k4, bias_ref[pl.ds(g * GROUP, GROUP)], allowed, scale, lane4)
            top = jnp.max(s, -1, keepdims=True)
            e = jnp.exp(s - top)
            total = jnp.sum(e, -1, keepdims=True)
            probs = (e / total).reshape(GROUP * PAIR, PAIR).astype(jnp.bfloat16)
            mixed_out = jnp.dot(probs, v4, preferred_element_type=jnp.float32)
            out_ref[sub, :, pl.ds(g * LANES, LANES)] = _gather_lanes(mixed_out, lane4).astype(out_ref.dtype)
            lse = top + jnp.log(total)
            for j in range(GROUP):
                lse_all = jnp.where(head_lane == g * GROUP + j, lse[j], lse_all)
        lse_ref[sub] = lse_all


def _bwd_kernel(mix_ref, grad_ref, lse_ref, bias_ref, kc_ref, kr_ref, gmix_ref, dbias_ref, *, scale):
    width = HEADS * 32
    lane4, head_lane = _lane_masks()
    step = pl.program_id(0)

    @pl.when(step == 0)
    def _():
        dbias_ref[...] = jnp.zeros_like(dbias_ref)

    for sub in range(STEP_PAIRS):
        allowed = kc_ref[sub] == kr_ref[sub]
        lse_all = lse_ref[sub]
        for g in range(HEADS // GROUP):
            q4 = mix_ref[sub, :, pl.ds(g * LANES, LANES)]
            k4 = mix_ref[sub, :, pl.ds(width + g * LANES, LANES)]
            v4 = mix_ref[sub, :, pl.ds(2 * width + g * LANES, LANES)]
            d4 = grad_ref[sub, :, pl.ds(g * LANES, LANES)]
            heads = pl.ds(g * GROUP, GROUP)
            s = _scores(q4, k4, bias_ref[heads], allowed, scale, lane4)
            lse = jnp.stack([
                jnp.sum(jnp.where(head_lane == g * GROUP + j, lse_all, 0.0), -1, keepdims=True)
                for j in range(GROUP)
            ])
            probs = jnp.exp(s - lse)
            d_stack = _stacked(d4, lane4)
            dprobs = lax.dot_general(d_stack, v4, (((1,), (1,)), ((), ())), preferred_element_type=jnp.float32)
            dprobs = dprobs.reshape(GROUP, PAIR, PAIR)
            inner = jnp.sum(probs * dprobs, -1, keepdims=True)
            dscores = (probs * (dprobs - inner)).reshape(GROUP * PAIR, PAIR).astype(jnp.bfloat16)
            dbias_ref[heads] = dbias_ref[heads] + dscores.astype(jnp.float32).reshape(GROUP, PAIR, PAIR)
            gq = _gather_lanes(jnp.dot(dscores, k4, preferred_element_type=jnp.float32), lane4)
            gk = lax.dot_general(dscores, _stacked(q4, lane4), (((0,), (0,)), ((), ())), preferred_element_type=jnp.float32)
            gv = lax.dot_general(probs.reshape(GROUP * PAIR, PAIR).astype(jnp.bfloat16), d_stack,
                                 (((0,), (0,)), ((), ())), preferred_element_type=jnp.float32)
            gmix_ref[sub, :, pl.ds(g * LANES, LANES)] = (gq * scale).astype(gmix_ref.dtype)
            gmix_ref[sub, :, pl.ds(width + g * LANES, LANES)] = (gk * scale).astype(gmix_ref.dtype)
            gmix_ref[sub, :, pl.ds(2 * width + g * LANES, LANES)] = gv.astype(gmix_ref.dtype)


def _pair_spec(width):
    return pl.BlockSpec((STEP_PAIRS, PAIR, width), lambda p: (p, 0, 0))


def attention_fwd(mixed_pairs, bias, key_col, key_row, scale):
    pairs = mixed_pairs.shape[0]
    kernel = functools.partial(_fwd_kernel, scale=scale)
    return pl.pallas_call(
        kernel,
        grid=(pairs // STEP_PAIRS,),
        out_shape=(
            jax.ShapeDtypeStruct((pairs, PAIR, HEADS * 32), jnp.bfloat16),
            jax.ShapeDtypeStruct((pairs, PAIR, LANES), jnp.float32),
        ),
        in_specs=[_pair_spec(mixed_pairs.shape[2]), pl.BlockSpec(bias.shape, lambda p: (0, 0, 0)),
                  pl.BlockSpec((STEP_PAIRS, PAIR, 1), lambda p: (p, 0, 0)), pl.BlockSpec((STEP_PAIRS, 1, PAIR), lambda p: (p, 0, 0))],
        out_specs=(_pair_spec(HEADS * 32), _pair_spec(LANES)),
        compiler_params=pltpu.CompilerParams(dimension_semantics=("arbitrary",), vmem_limit_bytes=32 * 1024 * 1024),
    )(mixed_pairs, bias, key_col, key_row)


def attention_bwd(mixed_pairs, grad_pairs, lse, bias, key_col, key_row, scale):
    pairs = mixed_pairs.shape[0]
    kernel = functools.partial(_bwd_kernel, scale=scale)
    return pl.pallas_call(
        kernel,
        grid=(pairs // STEP_PAIRS,),
        out_shape=(
            jax.ShapeDtypeStruct(mixed_pairs.shape, jnp.bfloat16),
            jax.ShapeDtypeStruct(bias.shape, jnp.float32),
        ),
        in_specs=[_pair_spec(mixed_pairs.shape[2]), _pair_spec(HEADS * 32), _pair_spec(LANES),
                  pl.BlockSpec(bias.shape, lambda p: (0, 0, 0)),
                  pl.BlockSpec((STEP_PAIRS, PAIR, 1), lambda p: (p, 0, 0)), pl.BlockSpec((STEP_PAIRS, 1, PAIR), lambda p: (p, 0, 0))],
        out_specs=(_pair_spec(mixed_pairs.shape[2]), pl.BlockSpec(bias.shape, lambda p: (0, 0, 0))),
        compiler_params=pltpu.CompilerParams(dimension_semantics=("arbitrary",), vmem_limit_bytes=32 * 1024 * 1024),
    )(mixed_pairs, grad_pairs, lse, bias, key_col, key_row)


def lane_blocks(matrix):
    row_blocks, col_blocks = matrix.shape[0] // BLK, matrix.shape[1] // BLK
    shaped = matrix.reshape(row_blocks, BLK, col_blocks, BLK).transpose(0, 2, 1, 3)
    return shaped.reshape(row_blocks * col_blocks, BLK * BLK // LANES, LANES)


ROWS = 448
SQRT_HALF = float(np.sqrt(0.5))
INV_SQRT_TAU = float(1.0 / np.sqrt(2.0 * np.pi))


def _norm(tensor):
    center = tensor - jnp.mean(tensor, -1, keepdims=True)
    inverse = lax.rsqrt(jnp.mean(center * center, -1, keepdims=True) + NORM_EPSILON)
    return center * inverse, inverse


def _mlp_fwd_kernel(att_ref, res_ref, valid_ref, wp_ref, gain_ref, off_ref, w1_ref, w2_ref,
                    hid_ref, act_ref, gelu_ref, out_ref, stat_ref):
    step = pl.program_id(0)
    branch_one = jnp.dot(att_ref[...], wp_ref[...], preferred_element_type=jnp.float32)
    hidden = res_ref[...] + branch_one
    normed, _ = _norm(hidden)
    act = (normed * gain_ref[...] + off_ref[...]).astype(jnp.bfloat16)
    pre = jnp.dot(act, w1_ref[...], preferred_element_type=jnp.float32)
    gelu = ((0.5 * pre) * (1.0 + lax.erf(pre * SQRT_HALF))).astype(jnp.bfloat16)
    branch_two = jnp.dot(gelu, w2_ref[...], preferred_element_type=jnp.float32)
    output = hidden + branch_two
    valid = valid_ref[...]
    first = jnp.sum(valid * output * output)
    second = jnp.sum(valid * (branch_one * branch_one + branch_two * branch_two))
    lane = lax.broadcasted_iota(jnp.int32, (8, 128), 1)
    row = lax.broadcasted_iota(jnp.int32, (8, 128), 0)
    here = jnp.where((row == 0) & (lane == 0), first, 0.0) + jnp.where((row == 0) & (lane == 1), second, 0.0)

    @pl.when(step == 0)
    def _():
        stat_ref[...] = jnp.zeros_like(stat_ref)

    stat_ref[...] = stat_ref[...] + here
    hid_ref[...] = hidden
    act_ref[...] = act
    gelu_ref[...] = gelu
    out_ref[...] = output.astype(out_ref.dtype)


def _mlp_bwd_kernel(gout_ref, hid_ref, act_ref, gain_ref, w1_ref, w2_ref, wp_ref, att_ref, gelu_ref,
                    gpre_ref, ghid_ref, gbr_ref, gatt_ref, small_ref, gfc1_ref, gfc2_ref, gproj_ref):
    step = pl.program_id(0)
    contract_last = (((1,), (1,)), ((), ()))
    pre = jnp.dot(act_ref[...], w1_ref[...], preferred_element_type=jnp.float32)
    grad_out = gout_ref[...]
    grad_gelu = lax.dot_general(grad_out, w2_ref[...], contract_last, preferred_element_type=jnp.float32)
    cdf = 0.5 * (1.0 + lax.erf(pre * SQRT_HALF))
    pdf = jnp.exp(-0.5 * pre * pre) * INV_SQRT_TAU
    grad_pre = (grad_gelu * (cdf + pre * pdf)).astype(jnp.bfloat16)
    grad_act = lax.dot_general(grad_pre, w1_ref[...], contract_last, preferred_element_type=jnp.float32)
    normed, inverse = _norm(hid_ref[...])
    scaled = grad_act * gain_ref[...]
    mean_one = jnp.mean(scaled, -1, keepdims=True)
    mean_two = jnp.mean(scaled * normed, -1, keepdims=True)
    grad_hidden = grad_out.astype(jnp.float32) + inverse * (scaled - mean_one - normed * mean_two)
    grad_branch = grad_hidden.astype(jnp.bfloat16)
    grad_att = lax.dot_general(grad_branch, wp_ref[...], contract_last, preferred_element_type=jnp.float32)
    sums = jnp.concatenate(
        [jnp.sum(grad_act * normed, 0, keepdims=True), jnp.sum(grad_act, 0, keepdims=True),
         jnp.zeros((6, grad_act.shape[1]), jnp.float32)], 0)

    contract_rows = (((0,), (0,)), ((), ()))
    fc1 = lax.dot_general(act_ref[...], grad_pre, contract_rows, preferred_element_type=jnp.float32)
    fc2 = lax.dot_general(gelu_ref[...], grad_out, contract_rows, preferred_element_type=jnp.float32)
    proj = lax.dot_general(att_ref[...], grad_branch, contract_rows, preferred_element_type=jnp.float32)

    @pl.when(step == 0)
    def _():
        small_ref[...] = jnp.zeros_like(small_ref)
        gfc1_ref[...] = jnp.zeros_like(gfc1_ref)
        gfc2_ref[...] = jnp.zeros_like(gfc2_ref)
        gproj_ref[...] = jnp.zeros_like(gproj_ref)

    small_ref[...] = small_ref[...] + sums
    gfc1_ref[...] = gfc1_ref[...] + fc1
    gfc2_ref[...] = gfc2_ref[...] + fc2
    gproj_ref[...] = gproj_ref[...] + proj
    gpre_ref[...] = grad_pre
    ghid_ref[...] = grad_hidden
    gbr_ref[...] = grad_branch
    gatt_ref[...] = grad_att.astype(gatt_ref.dtype)


def _rows(width):
    return pl.BlockSpec((ROWS, width), lambda i: (i, 0))


def _whole(shape):
    return pl.BlockSpec(shape, lambda i: (0,) * len(shape))


def mlp_fwd(attended, residual, valid, w_proj, gain, offset, w_fc1, w_fc2):
    tokens, width = residual.shape
    hidden_width = w_fc1.shape[1]
    return pl.pallas_call(
        _mlp_fwd_kernel,
        grid=(tokens // ROWS,),
        out_shape=(
            jax.ShapeDtypeStruct((tokens, width), jnp.float32),
            jax.ShapeDtypeStruct((tokens, width), jnp.bfloat16),
            jax.ShapeDtypeStruct((tokens, hidden_width), jnp.bfloat16),
            jax.ShapeDtypeStruct((tokens, width), jnp.bfloat16),
            jax.ShapeDtypeStruct((8, 128), jnp.float32),
        ),
        in_specs=[_rows(width), _rows(width), _rows(1), _whole(w_proj.shape), _whole((1, width)),
                  _whole((1, width)), _whole(w_fc1.shape), _whole(w_fc2.shape)],
        out_specs=(_rows(width), _rows(width), _rows(hidden_width), _rows(width), _whole((8, 128))),
        compiler_params=pltpu.CompilerParams(dimension_semantics=("arbitrary",), vmem_limit_bytes=48 * 1024 * 1024),
    )(attended, residual, valid, w_proj, gain.reshape(1, -1), offset.reshape(1, -1), w_fc1, w_fc2)


def mlp_bwd(grad_out, hidden, act_two, gain, w_fc1, w_fc2, w_proj, attended, gelu_low):
    tokens, width = hidden.shape
    hidden_width = w_fc1.shape[1]
    return pl.pallas_call(
        _mlp_bwd_kernel,
        grid=(tokens // ROWS,),
        out_shape=(
            jax.ShapeDtypeStruct((tokens, hidden_width), jnp.bfloat16),
            jax.ShapeDtypeStruct((tokens, width), jnp.float32),
            jax.ShapeDtypeStruct((tokens, width), jnp.bfloat16),
            jax.ShapeDtypeStruct((tokens, width), jnp.bfloat16),
            jax.ShapeDtypeStruct((8, width), jnp.float32),
            jax.ShapeDtypeStruct(w_fc1.shape, jnp.float32),
            jax.ShapeDtypeStruct(w_fc2.shape, jnp.float32),
            jax.ShapeDtypeStruct(w_proj.shape, jnp.float32),
        ),
        in_specs=[_rows(width), _rows(width), _rows(width), _whole((1, width)), _whole(w_fc1.shape),
                  _whole(w_fc2.shape), _whole(w_proj.shape), _rows(width), _rows(hidden_width)],
        out_specs=(_rows(hidden_width), _rows(width), _rows(width), _rows(width), _whole((8, width)),
                   _whole(w_fc1.shape), _whole(w_fc2.shape), _whole(w_proj.shape)),
        compiler_params=pltpu.CompilerParams(dimension_semantics=("arbitrary",), vmem_limit_bytes=48 * 1024 * 1024),
    )(grad_out, hidden, act_two, gain.reshape(1, -1), w_fc1, w_fc2, w_proj, attended, gelu_low)


def reduce_to_owners(parted, small):
    groups = lax.axis_size("dp")
    dp_bits = groups.bit_length() - 1
    n_qy, n_qx = lax.axis_size("qy"), lax.axis_size("qx")
    count, depth = parted[0].shape[0], parted[0].shape[1]
    per_group = count // groups
    names = [("dp", 1 << power) for power in reversed(range(dp_bits))] + [("qy", 1), ("qx", 1)]
    cross = [("qy", 1)] + [("dp", 1 << power) for power in range(dp_bits)]
    pieces, piece_names, orders = [], [], []
    for index, part in enumerate(parted):
        pieces.append(
            part.reshape([2] * dp_bits + [n_qy, n_qx, per_group * depth // (n_qy * n_qx), LANES])
        )
        piece_names.append(list(names))
        turn = index % len(cross)
        orders.append([("qx", 1)] + cross[turn:] + cross[:turn])
    for stage in range(len(names)):
        for index in range(len(pieces)):
            bit = orders[index][stage]
            place = piece_names[index].index(bit)
            mine = bit_of(*bit)
            keep = lax.dynamic_index_in_dim(pieces[index], mine, place, keepdims=False)
            send = lax.dynamic_index_in_dim(pieces[index], 1 - mine, place, keepdims=False)
            piece_names[index].remove(bit)
            arrived = partner_of(send.astype(jnp.bfloat16), *bit)
            pieces[index] = keep + arrived.astype(jnp.float32)
            if index == 0:
                small = small + partner_of(small, *bit)
                pieces[0], small = lax.optimization_barrier((pieces[0], small))
    chunk = jnp.stack(pieces)
    other = partner_of(chunk, "qy", 1)
    pair = jnp.where(bit_of("qy", 1) == 1, jnp.stack([other, chunk], 1), jnp.stack([chunk, other], 1))
    other = partner_of(pair, "qx", 1)
    quad = jnp.where(bit_of("qx", 1) == 1, jnp.stack([other, pair], 2), jnp.stack([pair, other], 2))
    quad = quad.reshape(len(pieces), per_group, depth, LANES).transpose(1, 0, 2, 3)
    return quad.reshape(per_group, BLK, BLK), small


def cut_along(value, dim, devices):
    before, after = (value.shape[:dim], value.shape[dim + 1 :])
    return jnp.moveaxis(value.reshape(*before, devices, -1, *after), dim, 0)


def sent_and_summed(value, axis, dim):
    pieces = cut_along(value, dim, lax.axis_size(axis))
    arrived = lax.all_to_all(pieces, axis, split_axis=0, concat_axis=0, tiled=True)
    return arrived.astype(jnp.float32).sum(axis=0)


def norm_stats(tensor):
    center = tensor - jnp.mean(tensor, -1, keepdims=True)
    inverse = lax.rsqrt(jnp.mean(center * center, -1, keepdims=True) + NORM_EPSILON)
    return (center * inverse, inverse)


def norm_back(grad_act, normed, inverse, gain):
    scaled = grad_act * gain
    mean_one = jnp.mean(scaled, -1, keepdims=True)
    mean_two = jnp.mean(scaled * normed, -1, keepdims=True)
    return inverse * (scaled - mean_one - normed * mean_two)


def to_windows(tensor):
    canvases, rows_side, cols_side, channels = tensor.shape
    shaped = tensor.reshape(canvases, rows_side // WIN, WIN, cols_side // WIN, WIN, channels)
    return shaped.transpose(0, 1, 3, 2, 4, 5).reshape(
        canvases * (rows_side // WIN) * (cols_side // WIN), WIN * WIN, channels
    )


def from_windows(tensor, canvases, rows_side, cols_side):
    channels = tensor.shape[-1]
    shaped = tensor.reshape(canvases, rows_side // WIN, cols_side // WIN, WIN, WIN, channels)
    return shaped.transpose(0, 1, 3, 2, 4, 5).reshape(canvases, rows_side, cols_side, channels)


def relative_index():
    places = jnp.arange(WIN * WIN, dtype=jnp.int32)
    row_of = places // WIN
    col_of = places % WIN
    return (row_of[:, None] - row_of[None, :] + WIN - 1) * (2 * WIN - 1) + (
        col_of[:, None] - col_of[None, :] + WIN - 1
    )


def region_of(places, full):
    return jnp.where(places < full - WIN, 0, jnp.where(places < full - SHIFT, 1, 2)).astype(
        jnp.int32
    )


def advance(tensor):
    upper = passed_along(tensor[:, :SHIFT], "qy", -1)
    tensor = jnp.concatenate([tensor[:, SHIFT:], upper], 1)
    leftmost = passed_along(tensor[:, :, :SHIFT], "qx", -1)
    return jnp.concatenate([tensor[:, :, SHIFT:], leftmost], 2)


def retreat(tensor):
    lowest = passed_along(tensor[:, -SHIFT:], "qy", 1)
    tensor = jnp.concatenate([lowest, tensor[:, :-SHIFT]], 1)
    rightmost = passed_along(tensor[:, :, -SHIFT:], "qx", 1)
    return jnp.concatenate([rightmost, tensor[:, :, :-SHIFT]], 2)


def blocks_of(matrix):
    row_blocks = matrix.shape[0] // BLK
    col_blocks = matrix.shape[1] // BLK
    return (
        matrix.reshape(row_blocks, BLK, col_blocks, BLK)
        .transpose(0, 2, 1, 3)
        .reshape(row_blocks * col_blocks, BLK, BLK)
    )


def rotate_update(grads, master, first, second, left, right):
    turned = jnp.einsum("sji,sjk->sik", left, grads, precision=ROTATE)
    turned = jnp.einsum("sik,skl->sil", turned, right, precision=ROTATE)
    new_first = BETA_ONE * first + (1.0 - BETA_ONE) * turned
    new_second = BETA_TWO * second + (1.0 - BETA_TWO) * turned * turned
    direction = new_first / (jnp.sqrt(new_second) + ADAM_EPSILON)
    back = jnp.einsum("sij,sjk->sik", left, direction, precision=ROTATE)
    back = jnp.einsum("sik,slk->sil", back, right, precision=ROTATE)
    return (new_first, new_second, master - RATE_BLOCKS * back)


def small_update(grads, params, first, second):
    new_first = BETA_ONE * first + (1.0 - BETA_ONE) * grads
    new_second = BETA_TWO * second + (1.0 - BETA_TWO) * grads * grads
    direction = new_first / (jnp.sqrt(new_second) + ADAM_EPSILON)
    return (new_first, new_second, params - RATE_SMALL * direction)


def local(
    tokens,
    crop_ids,
    merge_order,
    owner_list,
    w_qkv,
    w_proj,
    w_fc1,
    w_fc2,
    small_params,
    small_first,
    small_second,
    master_blocks,
    first_moment,
    second_moment,
    basis_left,
    basis_right,
    merged_grad,
):
    canvases, quad_side, quad_cols, features = tokens.shape
    head_dim = features // HEADS
    score_scale = head_dim ** (-0.5)
    window_area = WIN * WIN
    quarters = lax.axis_size(("qy", "qx"))
    share_rows = quad_side * quad_cols // quarters
    row_base = lax.axis_index("qy") * quad_side
    col_base = lax.axis_index("qx") * quad_cols
    rolled = jnp.roll(crop_ids, (-SHIFT, -SHIFT), (1, 2))
    local_ids = lax.dynamic_slice(
        rolled, (jnp.int32(0), row_base, col_base), (canvases, quad_side, quad_cols)
    )
    region_row = region_of(
        row_base + jnp.arange(quad_side, dtype=jnp.int32), quad_side * lax.axis_size("qy")
    )
    region_col = region_of(
        col_base + jnp.arange(quad_cols, dtype=jnp.int32), quad_cols * lax.axis_size("qx")
    )
    labels = (local_ids + 1) * 9 + region_row[None, :, None] * 3 + region_col[None, None, :]
    win_labels = to_windows(labels[..., None])[..., 0]
    window_count = win_labels.shape[0]
    gain_one = small_params[0:features]
    offset_one = small_params[features : 2 * features]
    gain_two = small_params[2 * features : 3 * features]
    offset_two = small_params[3 * features : 4 * features]
    table = small_params[4 * features :].reshape(HEADS, -1)
    onehot = (
        relative_index().reshape(-1)[:, None]
        == jnp.arange(table.shape[1], dtype=jnp.int32)[None, :]
    ).astype(jnp.float32)
    rel_bias = jnp.einsum("hr,pr->hp", table, onehot, precision=PRECISE).reshape(
        HEADS, window_area, window_area
    )

    pair_area = 2 * window_area
    place = jnp.arange(PAIR, dtype=jnp.int32)
    pair_labels = jnp.pad(win_labels.reshape(-1, pair_area), ((0, 0), (0, PAIR - pair_area)))
    pair_keys = jnp.where(
        place[None] < pair_area,
        pair_labels * 2 + (place[None] >= window_area).astype(jnp.int32),
        -1 - place[None],
    )
    key_col, key_row = pair_keys[:, :, None], pair_keys[:, None, :]
    valid = (pair_labels >= 9).reshape(-1).astype(jnp.float32)[:, None]
    spread = (
        (place[:, None] % window_area == jnp.arange(window_area, dtype=jnp.int32)[None, :])
        & (place[:, None] < pair_area)
    ).astype(jnp.float32)
    dense_bias = jnp.einsum(
        "hti,ui->htu",
        jnp.einsum("ti,hij->htj", spread, rel_bias, precision=PRECISE),
        spread,
        precision=PRECISE,
    )

    def to_pairs(tensor):
        shaped = tensor.reshape(-1, pair_area, tensor.shape[-1])
        return jnp.pad(shaped, ((0, 0), (0, PAIR - pair_area), (0, 0))).reshape(-1, tensor.shape[-1])

    def from_pairs(tensor):
        shaped = tensor.reshape(-1, PAIR, tensor.shape[-1])
        return shaped[:, :pair_area].reshape(-1, window_area, tensor.shape[-1])

    residual = to_pairs(to_windows(advance(tokens)).astype(jnp.float32))
    normed_one, inverse_one = norm_stats(residual)
    act_one = (normed_one * gain_one + offset_one).astype(jnp.bfloat16)
    mixed = jnp.dot(act_one, w_qkv, preferred_element_type=jnp.float32).astype(jnp.bfloat16)
    mixed_pairs = mixed.reshape(-1, PAIR, mixed.shape[-1])
    attended_pairs, log_total = attention_fwd(mixed_pairs, dense_bias, key_col, key_row, score_scale)
    attended = attended_pairs.reshape(-1, features)
    hidden, act_two, gelu_low, output_flat, stat_block = mlp_fwd(
        attended, residual, valid, w_proj, gain_two, offset_two, w_fc1, w_fc2
    )
    stat_terms = jnp.stack([stat_block[0, 0], stat_block[0, 1], jnp.sum(valid) * features])
    output_low = from_pairs(output_flat)
    restored = retreat(from_windows(output_low, canvases, quad_side, quad_cols))
    flat_out = restored.reshape(canvases, quarters, share_rows, features)
    arrived = lax.all_to_all(flat_out, ("qy", "qx"), 1, 1, tiled=True)
    merged = jnp.take(arrived, merge_order, axis=1, mode="clip").transpose(0, 2, 1, 3).reshape(
        canvases, share_rows, quarters * features
    )
    quarter_ids = jnp.arange(quarters, dtype=jnp.int32)
    source_pick = jnp.sum(
        quarter_ids[:, None] * (merge_order[:, None] == quarter_ids[None, :]).astype(jnp.int32), 0
    )
    incoming = merged_grad.reshape(canvases, share_rows, quarters, features)
    unordered = jnp.take(incoming, source_pick, axis=2, mode="clip").transpose(0, 2, 1, 3)
    returned = lax.all_to_all(unordered, ("qy", "qx"), 1, 1, tiled=True)
    grad_orig = returned.reshape(canvases, quad_side, quad_cols, features)
    grad_out = to_pairs(to_windows(advance(grad_orig)))
    (grad_pre, grad_hidden, grad_branch, grad_attended, small_two, grad_fc1, grad_fc2, grad_proj) = (
        mlp_bwd(grad_out, hidden, act_two, gain_two, w_fc1, w_fc2, w_proj, attended, gelu_low)
    )
    grad_mixed_pairs, dense_grad_bias = attention_bwd(
        mixed_pairs, grad_attended.reshape(-1, PAIR, features), log_total, dense_bias, key_col, key_row, score_scale
    )
    grad_mixed = grad_mixed_pairs.reshape(-1, 3 * features)
    grad_bias = jnp.einsum(
        "ti,htj->hij",
        spread,
        jnp.einsum("htu,uj->htj", dense_grad_bias, spread, precision=PRECISE),
        precision=PRECISE,
    )
    grad_table = jnp.dot(grad_bias.reshape(HEADS, -1), onehot, precision=PRECISE)
    grad_qkv = jnp.einsum("rc,rf->cf", act_one, grad_mixed, preferred_element_type=jnp.float32)
    grad_act_one = jnp.einsum("rf,cf->rc", grad_mixed, w_qkv, preferred_element_type=jnp.float32)
    grad_input = grad_hidden + norm_back(grad_act_one, normed_one, inverse_one, gain_one)
    grad_low = from_pairs(grad_input.astype(jnp.bfloat16))
    grad_tokens = retreat(from_windows(grad_low, canvases, quad_side, quad_cols))
    small_local = jnp.concatenate(
        [
            jnp.sum(grad_act_one * normed_one, 0),
            jnp.sum(grad_act_one, 0),
            small_two[0],
            small_two[1],
            grad_table.reshape(-1),
        ]
    )
    every_block = jnp.concatenate(
        [lane_blocks(grad_qkv), lane_blocks(grad_proj), lane_blocks(grad_fc1), lane_blocks(grad_fc2)],
        0,
    )
    depth = every_block.shape[1] // PARTS
    parted = [
        jnp.take(every_block[:, index * depth : (index + 1) * depth], owner_list, axis=0, mode="clip")
        for index in range(PARTS)
    ]
    owned_grads, small_all = reduce_to_owners(parted, jnp.concatenate([small_local, stat_terms]))
    small_total = small_all[: small_local.shape[0]]
    stat_total = small_all[small_local.shape[0] :]
    new_first, new_second, new_master = rotate_update(
        owned_grads, master_blocks, first_moment, second_moment, basis_left, basis_right
    )
    small_first_new, small_second_new, small_new = small_update(
        small_total, small_params, small_first, small_second
    )
    stats = jnp.stack(
        [jnp.sqrt(stat_total[0] / stat_total[2]), jnp.sqrt(stat_total[1] / (2.0 * stat_total[2]))]
    )
    return (
        merged,
        grad_tokens,
        owned_grads,
        new_master,
        new_first,
        new_second,
        new_master.astype(jnp.bfloat16),
        small_total,
        small_first_new,
        small_second_new,
        small_new,
        stats,
    )


def solution(mesh):
    placed = (
        P("dp", "qy", "qx", None),
        P("dp", None, None),
        P(),
        P(),
        P(),
        P(),
        P(),
        P(),
        P(),
        P(),
        P(),
        P("dp", None, None),
        P("dp", None, None),
        P("dp", None, None),
        P("dp", None, None),
        P("dp", None, None),
        P("dp", ("qy", "qx"), None),
    )
    return jax.shard_map(
        local,
        mesh=mesh,
        in_specs=placed,
        out_specs=(
            P("dp", ("qy", "qx"), None),
            P("dp", "qy", "qx", None),
            P("dp", None, None),
            P("dp", None, None),
            P("dp", None, None),
            P("dp", None, None),
            P("dp", None, None),
            P(),
            P(),
            P(),
            P(),
            P(),
        ),
        check_vma=False,
    )
```

```python
import functools
from functools import partial

import numpy as np

import jax
import jax.numpy as jnp
from jax import lax
from jax.experimental import pallas as pl
from jax.experimental.pallas import tpu as pltpu
from jax.sharding import PartitionSpec as P

HEADS = 12
WIN = 7
SHIFT = 3
BLK = 96


BETA_ONE = 0.5
BETA_TWO = 0.6
ADAM_EPSILON = 1e-08
RATE_BLOCKS = 0.04
RATE_SMALL = 0.2
MASK_FILL = -1e30
NORM_EPSILON = 1e-05
PRECISE = lax.Precision.HIGHEST
ROTATE = lax.Precision.HIGH


def passed_along(value, axis, steps):
    count = lax.axis_size(axis)
    pairs = [(source, (source + steps) % count) for source in range(count)]
    return lax.ppermute(value, axis, pairs)


def partner_of(value, axis, mask):
    count = lax.axis_size(axis)
    pairs = [(source, source ^ mask) for source in range(count)]
    return lax.ppermute(value, axis, pairs)


def bit_of(axis, mask):
    return ((lax.axis_index(axis) & mask) != 0).astype(jnp.int32)


LANES = 128
PARTS = 3
GROUP = 4
LANES = 128
MASK_FILL = -1e30
PAIR = 112
STEP_PAIRS = 8


def _stacked(value, lane4):
    wide = jnp.broadcast_to(value.astype(jnp.float32)[None], (GROUP, PAIR, LANES))
    return jnp.where(lane4, wide, 0.0).reshape(GROUP * PAIR, LANES).astype(jnp.bfloat16)


def _gather_lanes(stack, lane4):
    return jnp.sum(jnp.where(lane4, stack.reshape(GROUP, PAIR, LANES), 0.0), 0)


def _scores(q4, k4, bias4, allowed, scale, lane4):
    raw = lax.dot_general(_stacked(q4, lane4), k4, (((1,), (1,)), ((), ())), preferred_element_type=jnp.float32)
    raw = raw.reshape(GROUP, PAIR, PAIR) * scale + bias4
    return jnp.where(allowed[None], raw, MASK_FILL)


def _lane_masks():
    lane4 = lax.broadcasted_iota(jnp.int32, (GROUP, 1, LANES), 2) // 32 == lax.broadcasted_iota(
        jnp.int32, (GROUP, 1, LANES), 0)
    return lane4, lax.broadcasted_iota(jnp.int32, (1, LANES), 1)


def _fwd_kernel(mix_ref, bias_ref, kc_ref, kr_ref, out_ref, lse_ref, *, scale):
    width = HEADS * 32
    lane4, head_lane = _lane_masks()
    for sub in range(STEP_PAIRS):
        allowed = kc_ref[sub] == kr_ref[sub]
        lse_all = jnp.zeros((PAIR, LANES), jnp.float32)
        for g in range(HEADS // GROUP):
            q4 = mix_ref[sub, :, pl.ds(g * LANES, LANES)]
            k4 = mix_ref[sub, :, pl.ds(width + g * LANES, LANES)]
            v4 = mix_ref[sub, :, pl.ds(2 * width + g * LANES, LANES)]
            s = _scores(q4, k4, bias_ref[pl.ds(g * GROUP, GROUP)], allowed, scale, lane4)
            top = jnp.max(s, -1, keepdims=True)
            e = jnp.exp(s - top)
            total = jnp.sum(e, -1, keepdims=True)
            probs = (e / total).reshape(GROUP * PAIR, PAIR).astype(jnp.bfloat16)
            mixed_out = jnp.dot(probs, v4, preferred_element_type=jnp.float32)
            out_ref[sub, :, pl.ds(g * LANES, LANES)] = _gather_lanes(mixed_out, lane4).astype(out_ref.dtype)
            lse = top + jnp.log(total)
            for j in range(GROUP):
                lse_all = jnp.where(head_lane == g * GROUP + j, lse[j], lse_all)
        lse_ref[sub] = lse_all


def _bwd_kernel(mix_ref, grad_ref, lse_ref, bias_ref, kc_ref, kr_ref, gmix_ref, dbias_ref, *, scale):
    width = HEADS * 32
    lane4, head_lane = _lane_masks()
    step = pl.program_id(0)

    @pl.when(step == 0)
    def _():
        dbias_ref[...] = jnp.zeros_like(dbias_ref)

    for sub in range(STEP_PAIRS):
        allowed = kc_ref[sub] == kr_ref[sub]
        lse_all = lse_ref[sub]
        for g in range(HEADS // GROUP):
            q4 = mix_ref[sub, :, pl.ds(g * LANES, LANES)]
            k4 = mix_ref[sub, :, pl.ds(width + g * LANES, LANES)]
            v4 = mix_ref[sub, :, pl.ds(2 * width + g * LANES, LANES)]
            d4 = grad_ref[sub, :, pl.ds(g * LANES, LANES)]
            heads = pl.ds(g * GROUP, GROUP)
            s = _scores(q4, k4, bias_ref[heads], allowed, scale, lane4)
            lse = jnp.stack([
                jnp.sum(jnp.where(head_lane == g * GROUP + j, lse_all, 0.0), -1, keepdims=True)
                for j in range(GROUP)
            ])
            probs = jnp.exp(s - lse)
            d_stack = _stacked(d4, lane4)
            dprobs = lax.dot_general(d_stack, v4, (((1,), (1,)), ((), ())), preferred_element_type=jnp.float32)
            dprobs = dprobs.reshape(GROUP, PAIR, PAIR)
            inner = jnp.sum(probs * dprobs, -1, keepdims=True)
            dscores = (probs * (dprobs - inner)).reshape(GROUP * PAIR, PAIR).astype(jnp.bfloat16)
            dbias_ref[heads] = dbias_ref[heads] + dscores.astype(jnp.float32).reshape(GROUP, PAIR, PAIR)
            gq = _gather_lanes(jnp.dot(dscores, k4, preferred_element_type=jnp.float32), lane4)
            gk = lax.dot_general(dscores, _stacked(q4, lane4), (((0,), (0,)), ((), ())), preferred_element_type=jnp.float32)
            gv = lax.dot_general(probs.reshape(GROUP * PAIR, PAIR).astype(jnp.bfloat16), d_stack,
                                 (((0,), (0,)), ((), ())), preferred_element_type=jnp.float32)
            gmix_ref[sub, :, pl.ds(g * LANES, LANES)] = (gq * scale).astype(gmix_ref.dtype)
            gmix_ref[sub, :, pl.ds(width + g * LANES, LANES)] = (gk * scale).astype(gmix_ref.dtype)
            gmix_ref[sub, :, pl.ds(2 * width + g * LANES, LANES)] = gv.astype(gmix_ref.dtype)


def _pair_spec(width):
    return pl.BlockSpec((STEP_PAIRS, PAIR, width), lambda p: (p, 0, 0))


def attention_fwd(mixed_pairs, bias, key_col, key_row, scale):
    pairs = mixed_pairs.shape[0]
    kernel = functools.partial(_fwd_kernel, scale=scale)
    return pl.pallas_call(
        kernel,
        grid=(pairs // STEP_PAIRS,),
        out_shape=(
            jax.ShapeDtypeStruct((pairs, PAIR, HEADS * 32), jnp.bfloat16),
            jax.ShapeDtypeStruct((pairs, PAIR, LANES), jnp.float32),
        ),
        in_specs=[_pair_spec(mixed_pairs.shape[2]), pl.BlockSpec(bias.shape, lambda p: (0, 0, 0)),
                  pl.BlockSpec((STEP_PAIRS, PAIR, 1), lambda p: (p, 0, 0)), pl.BlockSpec((STEP_PAIRS, 1, PAIR), lambda p: (p, 0, 0))],
        out_specs=(_pair_spec(HEADS * 32), _pair_spec(LANES)),
        compiler_params=pltpu.CompilerParams(dimension_semantics=("arbitrary",), vmem_limit_bytes=32 * 1024 * 1024),
    )(mixed_pairs, bias, key_col, key_row)


def attention_bwd(mixed_pairs, grad_pairs, lse, bias, key_col, key_row, scale):
    pairs = mixed_pairs.shape[0]
    kernel = functools.partial(_bwd_kernel, scale=scale)
    return pl.pallas_call(
        kernel,
        grid=(pairs // STEP_PAIRS,),
        out_shape=(
            jax.ShapeDtypeStruct(mixed_pairs.shape, jnp.bfloat16),
            jax.ShapeDtypeStruct(bias.shape, jnp.float32),
        ),
        in_specs=[_pair_spec(mixed_pairs.shape[2]), _pair_spec(HEADS * 32), _pair_spec(LANES),
                  pl.BlockSpec(bias.shape, lambda p: (0, 0, 0)),
                  pl.BlockSpec((STEP_PAIRS, PAIR, 1), lambda p: (p, 0, 0)), pl.BlockSpec((STEP_PAIRS, 1, PAIR), lambda p: (p, 0, 0))],
        out_specs=(_pair_spec(mixed_pairs.shape[2]), pl.BlockSpec(bias.shape, lambda p: (0, 0, 0))),
        compiler_params=pltpu.CompilerParams(dimension_semantics=("arbitrary",), vmem_limit_bytes=32 * 1024 * 1024),
    )(mixed_pairs, grad_pairs, lse, bias, key_col, key_row)


def lane_blocks(matrix):
    row_blocks, col_blocks = matrix.shape[0] // BLK, matrix.shape[1] // BLK
    shaped = matrix.reshape(row_blocks, BLK, col_blocks, BLK).transpose(0, 2, 1, 3)
    return shaped.reshape(row_blocks * col_blocks, BLK * BLK // LANES, LANES)


ROWS = 224
SQRT_HALF = float(np.sqrt(0.5))
INV_SQRT_TAU = float(1.0 / np.sqrt(2.0 * np.pi))


def _norm(tensor):
    center = tensor - jnp.mean(tensor, -1, keepdims=True)
    inverse = lax.rsqrt(jnp.mean(center * center, -1, keepdims=True) + NORM_EPSILON)
    return center * inverse, inverse


def _mlp_fwd_kernel(att_ref, res_ref, valid_ref, wp_ref, gain_ref, off_ref, w1_ref, w2_ref,
                    hid_ref, act_ref, gelu_ref, out_ref, stat_ref):
    step = pl.program_id(0)
    branch_one = jnp.dot(att_ref[...], wp_ref[...], preferred_element_type=jnp.float32)
    hidden = res_ref[...] + branch_one
    normed, _ = _norm(hidden)
    act = (normed * gain_ref[...] + off_ref[...]).astype(jnp.bfloat16)
    pre = jnp.dot(act, w1_ref[...], preferred_element_type=jnp.float32)
    gelu = ((0.5 * pre) * (1.0 + lax.erf(pre * SQRT_HALF))).astype(jnp.bfloat16)
    branch_two = jnp.dot(gelu, w2_ref[...], preferred_element_type=jnp.float32)
    output = hidden + branch_two
    valid = valid_ref[...]
    first = jnp.sum(valid * output * output)
    second = jnp.sum(valid * (branch_one * branch_one + branch_two * branch_two))
    lane = lax.broadcasted_iota(jnp.int32, (8, 128), 1)
    row = lax.broadcasted_iota(jnp.int32, (8, 128), 0)
    here = jnp.where((row == 0) & (lane == 0), first, 0.0) + jnp.where((row == 0) & (lane == 1), second, 0.0)

    @pl.when(step == 0)
    def _():
        stat_ref[...] = jnp.zeros_like(stat_ref)

    stat_ref[...] = stat_ref[...] + here
    hid_ref[...] = hidden
    act_ref[...] = act
    gelu_ref[...] = gelu
    out_ref[...] = output.astype(out_ref.dtype)


def _mlp_bwd_kernel(gout_ref, hid_ref, act_ref, gain_ref, w1_ref, w2_ref, wp_ref, att_ref, gelu_ref,
                    gpre_ref, ghid_ref, gbr_ref, gatt_ref, small_ref, gfc1_ref, gfc2_ref, gproj_ref):
    step = pl.program_id(0)
    contract_last = (((1,), (1,)), ((), ()))
    pre = jnp.dot(act_ref[...], w1_ref[...], preferred_element_type=jnp.float32)
    grad_out = gout_ref[...]
    grad_gelu = lax.dot_general(grad_out, w2_ref[...], contract_last, preferred_element_type=jnp.float32)
    cdf = 0.5 * (1.0 + lax.erf(pre * SQRT_HALF))
    pdf = jnp.exp(-0.5 * pre * pre) * INV_SQRT_TAU
    grad_pre = (grad_gelu * (cdf + pre * pdf)).astype(jnp.bfloat16)
    grad_act = lax.dot_general(grad_pre, w1_ref[...], contract_last, preferred_element_type=jnp.float32)
    normed, inverse = _norm(hid_ref[...])
    scaled = grad_act * gain_ref[...]
    mean_one = jnp.mean(scaled, -1, keepdims=True)
    mean_two = jnp.mean(scaled * normed, -1, keepdims=True)
    grad_hidden = grad_out.astype(jnp.float32) + inverse * (scaled - mean_one - normed * mean_two)
    grad_branch = grad_hidden.astype(jnp.bfloat16)
    grad_att = lax.dot_general(grad_branch, wp_ref[...], contract_last, preferred_element_type=jnp.float32)
    sums = jnp.concatenate(
        [jnp.sum(grad_act * normed, 0, keepdims=True), jnp.sum(grad_act, 0, keepdims=True),
         jnp.zeros((6, grad_act.shape[1]), jnp.float32)], 0)

    contract_rows = (((0,), (0,)), ((), ()))
    fc1 = lax.dot_general(act_ref[...], grad_pre, contract_rows, preferred_element_type=jnp.float32)
    fc2 = lax.dot_general(gelu_ref[...], grad_out, contract_rows, preferred_element_type=jnp.float32)
    proj = lax.dot_general(att_ref[...], grad_branch, contract_rows, preferred_element_type=jnp.float32)

    @pl.when(step == 0)
    def _():
        small_ref[...] = jnp.zeros_like(small_ref)
        gfc1_ref[...] = jnp.zeros_like(gfc1_ref)
        gfc2_ref[...] = jnp.zeros_like(gfc2_ref)
        gproj_ref[...] = jnp.zeros_like(gproj_ref)

    small_ref[...] = small_ref[...] + sums
    gfc1_ref[...] = gfc1_ref[...] + fc1
    gfc2_ref[...] = gfc2_ref[...] + fc2
    gproj_ref[...] = gproj_ref[...] + proj
    gpre_ref[...] = grad_pre
    ghid_ref[...] = grad_hidden
    gbr_ref[...] = grad_branch
    gatt_ref[...] = grad_att.astype(gatt_ref.dtype)


def _rows(width):
    return pl.BlockSpec((ROWS, width), lambda i: (i, 0))


def _whole(shape):
    return pl.BlockSpec(shape, lambda i: (0,) * len(shape))


def mlp_fwd(attended, residual, valid, w_proj, gain, offset, w_fc1, w_fc2):
    tokens, width = residual.shape
    hidden_width = w_fc1.shape[1]
    return pl.pallas_call(
        _mlp_fwd_kernel,
        grid=(tokens // ROWS,),
        out_shape=(
            jax.ShapeDtypeStruct((tokens, width), jnp.float32),
            jax.ShapeDtypeStruct((tokens, width), jnp.bfloat16),
            jax.ShapeDtypeStruct((tokens, hidden_width), jnp.bfloat16),
            jax.ShapeDtypeStruct((tokens, width), jnp.bfloat16),
            jax.ShapeDtypeStruct((8, 128), jnp.float32),
        ),
        in_specs=[_rows(width), _rows(width), _rows(1), _whole(w_proj.shape), _whole((1, width)),
                  _whole((1, width)), _whole(w_fc1.shape), _whole(w_fc2.shape)],
        out_specs=(_rows(width), _rows(width), _rows(hidden_width), _rows(width), _whole((8, 128))),
        compiler_params=pltpu.CompilerParams(dimension_semantics=("arbitrary",), vmem_limit_bytes=48 * 1024 * 1024),
    )(attended, residual, valid, w_proj, gain.reshape(1, -1), offset.reshape(1, -1), w_fc1, w_fc2)


def mlp_bwd(grad_out, hidden, act_two, gain, w_fc1, w_fc2, w_proj, attended, gelu_low):
    tokens, width = hidden.shape
    hidden_width = w_fc1.shape[1]
    return pl.pallas_call(
        _mlp_bwd_kernel,
        grid=(tokens // ROWS,),
        out_shape=(
            jax.ShapeDtypeStruct((tokens, hidden_width), jnp.bfloat16),
            jax.ShapeDtypeStruct((tokens, width), jnp.float32),
            jax.ShapeDtypeStruct((tokens, width), jnp.bfloat16),
            jax.ShapeDtypeStruct((tokens, width), jnp.bfloat16),
            jax.ShapeDtypeStruct((8, width), jnp.float32),
            jax.ShapeDtypeStruct(w_fc1.shape, jnp.float32),
            jax.ShapeDtypeStruct(w_fc2.shape, jnp.float32),
            jax.ShapeDtypeStruct(w_proj.shape, jnp.float32),
        ),
        in_specs=[_rows(width), _rows(width), _rows(width), _whole((1, width)), _whole(w_fc1.shape),
                  _whole(w_fc2.shape), _whole(w_proj.shape), _rows(width), _rows(hidden_width)],
        out_specs=(_rows(hidden_width), _rows(width), _rows(width), _rows(width), _whole((8, width)),
                   _whole(w_fc1.shape), _whole(w_fc2.shape), _whole(w_proj.shape)),
        compiler_params=pltpu.CompilerParams(dimension_semantics=("arbitrary",), vmem_limit_bytes=48 * 1024 * 1024),
    )(grad_out, hidden, act_two, gain.reshape(1, -1), w_fc1, w_fc2, w_proj, attended, gelu_low)


def reduce_to_owners(parted, small):
    groups = lax.axis_size("dp")
    dp_bits = groups.bit_length() - 1
    n_qy, n_qx = lax.axis_size("qy"), lax.axis_size("qx")
    count, depth = parted[0].shape[0], parted[0].shape[1]
    per_group = count // groups
    names = [("dp", 1 << power) for power in reversed(range(dp_bits))] + [("qy", 1), ("qx", 1)]
    cross = [("qy", 1)] + [("dp", 1 << power) for power in range(dp_bits)]
    pieces, piece_names, orders = [], [], []
    for index, part in enumerate(parted):
        pieces.append(
            part.reshape([2] * dp_bits + [n_qy, n_qx, per_group * depth // (n_qy * n_qx), LANES])
        )
        piece_names.append(list(names))
        turn = index % len(cross)
        orders.append([("qx", 1)] + cross[turn:] + cross[:turn])
    for stage in range(len(names)):
        for index in range(len(pieces)):
            bit = orders[index][stage]
            place = piece_names[index].index(bit)
            mine = bit_of(*bit)
            keep = lax.dynamic_index_in_dim(pieces[index], mine, place, keepdims=False)
            send = lax.dynamic_index_in_dim(pieces[index], 1 - mine, place, keepdims=False)
            piece_names[index].remove(bit)
            arrived = partner_of(send.astype(jnp.bfloat16), *bit)
            pieces[index] = keep + arrived.astype(jnp.float32)
            if index == 0:
                small = small + partner_of(small, *bit)
                pieces[0], small = lax.optimization_barrier((pieces[0], small))
    chunk = jnp.stack(pieces)
    other = partner_of(chunk, "qy", 1)
    pair = jnp.where(bit_of("qy", 1) == 1, jnp.stack([other, chunk], 1), jnp.stack([chunk, other], 1))
    other = partner_of(pair, "qx", 1)
    quad = jnp.where(bit_of("qx", 1) == 1, jnp.stack([other, pair], 2), jnp.stack([pair, other], 2))
    quad = quad.reshape(len(pieces), per_group, depth, LANES).transpose(1, 0, 2, 3)
    return quad.reshape(per_group, BLK, BLK), small


def cut_along(value, dim, devices):
    before, after = (value.shape[:dim], value.shape[dim + 1 :])
    return jnp.moveaxis(value.reshape(*before, devices, -1, *after), dim, 0)


def sent_and_summed(value, axis, dim):
    pieces = cut_along(value, dim, lax.axis_size(axis))
    arrived = lax.all_to_all(pieces, axis, split_axis=0, concat_axis=0, tiled=True)
    return arrived.astype(jnp.float32).sum(axis=0)


def norm_stats(tensor):
    center = tensor - jnp.mean(tensor, -1, keepdims=True)
    inverse = lax.rsqrt(jnp.mean(center * center, -1, keepdims=True) + NORM_EPSILON)
    return (center * inverse, inverse)


def norm_back(grad_act, normed, inverse, gain):
    scaled = grad_act * gain
    mean_one = jnp.mean(scaled, -1, keepdims=True)
    mean_two = jnp.mean(scaled * normed, -1, keepdims=True)
    return inverse * (scaled - mean_one - normed * mean_two)


def to_windows(tensor):
    canvases, rows_side, cols_side, channels = tensor.shape
    shaped = tensor.reshape(canvases, rows_side // WIN, WIN, cols_side // WIN, WIN, channels)
    return shaped.transpose(0, 1, 3, 2, 4, 5).reshape(
        canvases * (rows_side // WIN) * (cols_side // WIN), WIN * WIN, channels
    )


def from_windows(tensor, canvases, rows_side, cols_side):
    channels = tensor.shape[-1]
    shaped = tensor.reshape(canvases, rows_side // WIN, cols_side // WIN, WIN, WIN, channels)
    return shaped.transpose(0, 1, 3, 2, 4, 5).reshape(canvases, rows_side, cols_side, channels)


def relative_index():
    places = jnp.arange(WIN * WIN, dtype=jnp.int32)
    row_of = places // WIN
    col_of = places % WIN
    return (row_of[:, None] - row_of[None, :] + WIN - 1) * (2 * WIN - 1) + (
        col_of[:, None] - col_of[None, :] + WIN - 1
    )


def region_of(places, full):
    return jnp.where(places < full - WIN, 0, jnp.where(places < full - SHIFT, 1, 2)).astype(
        jnp.int32
    )


def advance(tensor):
    upper = passed_along(tensor[:, :SHIFT], "qy", -1)
    tensor = jnp.concatenate([tensor[:, SHIFT:], upper], 1)
    leftmost = passed_along(tensor[:, :, :SHIFT], "qx", -1)
    return jnp.concatenate([tensor[:, :, SHIFT:], leftmost], 2)


def retreat(tensor):
    lowest = passed_along(tensor[:, -SHIFT:], "qy", 1)
    tensor = jnp.concatenate([lowest, tensor[:, :-SHIFT]], 1)
    rightmost = passed_along(tensor[:, :, -SHIFT:], "qx", 1)
    return jnp.concatenate([rightmost, tensor[:, :, :-SHIFT]], 2)


def blocks_of(matrix):
    row_blocks = matrix.shape[0] // BLK
    col_blocks = matrix.shape[1] // BLK
    return (
        matrix.reshape(row_blocks, BLK, col_blocks, BLK)
        .transpose(0, 2, 1, 3)
        .reshape(row_blocks * col_blocks, BLK, BLK)
    )


def rotate_update(grads, master, first, second, left, right):
    turned = jnp.einsum("sji,sjk->sik", left, grads, precision=ROTATE)
    turned = jnp.einsum("sik,skl->sil", turned, right, precision=ROTATE)
    new_first = BETA_ONE * first + (1.0 - BETA_ONE) * turned
    new_second = BETA_TWO * second + (1.0 - BETA_TWO) * turned * turned
    direction = new_first / (jnp.sqrt(new_second) + ADAM_EPSILON)
    back = jnp.einsum("sij,sjk->sik", left, direction, precision=ROTATE)
    back = jnp.einsum("sik,slk->sil", back, right, precision=ROTATE)
    return (new_first, new_second, master - RATE_BLOCKS * back)


def small_update(grads, params, first, second):
    new_first = BETA_ONE * first + (1.0 - BETA_ONE) * grads
    new_second = BETA_TWO * second + (1.0 - BETA_TWO) * grads * grads
    direction = new_first / (jnp.sqrt(new_second) + ADAM_EPSILON)
    return (new_first, new_second, params - RATE_SMALL * direction)


def local(
    tokens,
    crop_ids,
    merge_order,
    owner_list,
    w_qkv,
    w_proj,
    w_fc1,
    w_fc2,
    small_params,
    small_first,
    small_second,
    master_blocks,
    first_moment,
    second_moment,
    basis_left,
    basis_right,
    merged_grad,
):
    canvases, quad_side, quad_cols, features = tokens.shape
    head_dim = features // HEADS
    score_scale = head_dim ** (-0.5)
    window_area = WIN * WIN
    quarters = lax.axis_size(("qy", "qx"))
    share_rows = quad_side * quad_cols // quarters
    row_base = lax.axis_index("qy") * quad_side
    col_base = lax.axis_index("qx") * quad_cols
    rolled = jnp.roll(crop_ids, (-SHIFT, -SHIFT), (1, 2))
    local_ids = lax.dynamic_slice(
        rolled, (jnp.int32(0), row_base, col_base), (canvases, quad_side, quad_cols)
    )
    region_row = region_of(
        row_base + jnp.arange(quad_side, dtype=jnp.int32), quad_side * lax.axis_size("qy")
    )
    region_col = region_of(
        col_base + jnp.arange(quad_cols, dtype=jnp.int32), quad_cols * lax.axis_size("qx")
    )
    labels = (local_ids + 1) * 9 + region_row[None, :, None] * 3 + region_col[None, None, :]
    win_labels = to_windows(labels[..., None])[..., 0]
    window_count = win_labels.shape[0]
    gain_one = small_params[0:features]
    offset_one = small_params[features : 2 * features]
    gain_two = small_params[2 * features : 3 * features]
    offset_two = small_params[3 * features : 4 * features]
    table = small_params[4 * features :].reshape(HEADS, -1)
    onehot = (
        relative_index().reshape(-1)[:, None]
        == jnp.arange(table.shape[1], dtype=jnp.int32)[None, :]
    ).astype(jnp.float32)
    rel_bias = jnp.einsum("hr,pr->hp", table, onehot, precision=PRECISE).reshape(
        HEADS, window_area, window_area
    )

    pair_area = 2 * window_area
    place = jnp.arange(PAIR, dtype=jnp.int32)
    pair_labels = jnp.pad(win_labels.reshape(-1, pair_area), ((0, 0), (0, PAIR - pair_area)))
    pair_keys = jnp.where(
        place[None] < pair_area,
        pair_labels * 2 + (place[None] >= window_area).astype(jnp.int32),
        -1 - place[None],
    )
    key_col, key_row = pair_keys[:, :, None], pair_keys[:, None, :]
    valid = (pair_labels >= 9).reshape(-1).astype(jnp.float32)[:, None]
    spread = (
        (place[:, None] % window_area == jnp.arange(window_area, dtype=jnp.int32)[None, :])
        & (place[:, None] < pair_area)
    ).astype(jnp.float32)
    dense_bias = jnp.einsum(
        "hti,ui->htu",
        jnp.einsum("ti,hij->htj", spread, rel_bias, precision=PRECISE),
        spread,
        precision=PRECISE,
    )

    def to_pairs(tensor):
        shaped = tensor.reshape(-1, pair_area, tensor.shape[-1])
        return jnp.pad(shaped, ((0, 0), (0, PAIR - pair_area), (0, 0))).reshape(-1, tensor.shape[-1])

    def from_pairs(tensor):
        shaped = tensor.reshape(-1, PAIR, tensor.shape[-1])
        return shaped[:, :pair_area].reshape(-1, window_area, tensor.shape[-1])

    residual = to_pairs(to_windows(advance(tokens)).astype(jnp.float32))
    normed_one, inverse_one = norm_stats(residual)
    act_one = (normed_one * gain_one + offset_one).astype(jnp.bfloat16)
    mixed = jnp.dot(act_one, w_qkv, preferred_element_type=jnp.float32).astype(jnp.bfloat16)
    mixed_pairs = mixed.reshape(-1, PAIR, mixed.shape[-1])
    attended_pairs, log_total = attention_fwd(mixed_pairs, dense_bias, key_col, key_row, score_scale)
    attended = attended_pairs.reshape(-1, features)
    hidden, act_two, gelu_low, output_flat, stat_block = mlp_fwd(
        attended, residual, valid, w_proj, gain_two, offset_two, w_fc1, w_fc2
    )
    stat_terms = jnp.stack([stat_block[0, 0], stat_block[0, 1], jnp.sum(valid) * features])
    output_low = from_pairs(output_flat)
    restored = retreat(from_windows(output_low, canvases, quad_side, quad_cols))
    flat_out = restored.reshape(canvases, quarters, share_rows, features)
    arrived = lax.all_to_all(flat_out, ("qy", "qx"), 1, 1, tiled=True)
    merged = jnp.take(arrived, merge_order, axis=1, mode="clip").transpose(0, 2, 1, 3).reshape(
        canvases, share_rows, quarters * features
    )
    quarter_ids = jnp.arange(quarters, dtype=jnp.int32)
    source_pick = jnp.sum(
        quarter_ids[:, None] * (merge_order[:, None] == quarter_ids[None, :]).astype(jnp.int32), 0
    )
    incoming = merged_grad.reshape(canvases, share_rows, quarters, features)
    unordered = jnp.take(incoming, source_pick, axis=2, mode="clip").transpose(0, 2, 1, 3)
    returned = lax.all_to_all(unordered, ("qy", "qx"), 1, 1, tiled=True)
    grad_orig = returned.reshape(canvases, quad_side, quad_cols, features)
    grad_out = to_pairs(to_windows(advance(grad_orig)))
    (grad_pre, grad_hidden, grad_branch, grad_attended, small_two, grad_fc1, grad_fc2, grad_proj) = (
        mlp_bwd(grad_out, hidden, act_two, gain_two, w_fc1, w_fc2, w_proj, attended, gelu_low)
    )
    grad_mixed_pairs, dense_grad_bias = attention_bwd(
        mixed_pairs, grad_attended.reshape(-1, PAIR, features), log_total, dense_bias, key_col, key_row, score_scale
    )
    grad_mixed = grad_mixed_pairs.reshape(-1, 3 * features)
    grad_bias = jnp.einsum(
        "ti,htj->hij",
        spread,
        jnp.einsum("htu,uj->htj", dense_grad_bias, spread, precision=PRECISE),
        precision=PRECISE,
    )
    grad_table = jnp.dot(grad_bias.reshape(HEADS, -1), onehot, precision=PRECISE)
    grad_qkv = jnp.einsum("rc,rf->cf", act_one, grad_mixed, preferred_element_type=jnp.float32)
    grad_act_one = jnp.einsum("rf,cf->rc", grad_mixed, w_qkv, preferred_element_type=jnp.float32)
    grad_input = grad_hidden + norm_back(grad_act_one, normed_one, inverse_one, gain_one)
    grad_low = from_pairs(grad_input.astype(jnp.bfloat16))
    grad_tokens = retreat(from_windows(grad_low, canvases, quad_side, quad_cols))
    small_local = jnp.concatenate(
        [
            jnp.sum(grad_act_one * normed_one, 0),
            jnp.sum(grad_act_one, 0),
            small_two[0],
            small_two[1],
            grad_table.reshape(-1),
        ]
    )
    every_block = jnp.concatenate(
        [lane_blocks(grad_qkv), lane_blocks(grad_proj), lane_blocks(grad_fc1), lane_blocks(grad_fc2)],
        0,
    )
    depth = every_block.shape[1] // PARTS
    parted = [
        jnp.take(every_block[:, index * depth : (index + 1) * depth], owner_list, axis=0, mode="clip")
        for index in range(PARTS)
    ]
    owned_grads, small_all = reduce_to_owners(parted, jnp.concatenate([small_local, stat_terms]))
    small_total = small_all[: small_local.shape[0]]
    stat_total = small_all[small_local.shape[0] :]
    new_first, new_second, new_master = rotate_update(
        owned_grads, master_blocks, first_moment, second_moment, basis_left, basis_right
    )
    small_first_new, small_second_new, small_new = small_update(
        small_total, small_params, small_first, small_second
    )
    stats = jnp.stack(
        [jnp.sqrt(stat_total[0] / stat_total[2]), jnp.sqrt(stat_total[1] / (2.0 * stat_total[2]))]
    )
    return (
        merged,
        grad_tokens,
        owned_grads,
        new_master,
        new_first,
        new_second,
        new_master.astype(jnp.bfloat16),
        small_total,
        small_first_new,
        small_second_new,
        small_new,
        stats,
    )


def solution(mesh):
    placed = (
        P("dp", "qy", "qx", None),
        P("dp", None, None),
        P(),
        P(),
        P(),
        P(),
        P(),
        P(),
        P(),
        P(),
        P(),
        P("dp", None, None),
        P("dp", None, None),
        P("dp", None, None),
        P("dp", None, None),
        P("dp", None, None),
        P("dp", ("qy", "qx"), None),
    )
    return jax.shard_map(
        local,
        mesh=mesh,
        in_specs=placed,
        out_specs=(
            P("dp", ("qy", "qx"), None),
            P("dp", "qy", "qx", None),
            P("dp", None, None),
            P("dp", None, None),
            P("dp", None, None),
            P("dp", None, None),
            P("dp", None, None),
            P(),
            P(),
            P(),
            P(),
            P(),
        ),
        check_vma=False,
    )
```

```python
import functools
from functools import partial

import numpy as np

import jax
import jax.numpy as jnp
from jax import lax
from jax.experimental import pallas as pl
from jax.experimental.pallas import tpu as pltpu
from jax.sharding import PartitionSpec as P

HEADS = 12
WIN = 7
SHIFT = 3
BLK = 96


BETA_ONE = 0.5
BETA_TWO = 0.6
ADAM_EPSILON = 1e-08
RATE_BLOCKS = 0.04
RATE_SMALL = 0.2
MASK_FILL = -1e30
NORM_EPSILON = 1e-05
PRECISE = lax.Precision.HIGHEST
ROTATE = lax.Precision.HIGH


def passed_along(value, axis, steps):
    count = lax.axis_size(axis)
    pairs = [(source, (source + steps) % count) for source in range(count)]
    return lax.ppermute(value, axis, pairs)


def partner_of(value, axis, mask):
    count = lax.axis_size(axis)
    pairs = [(source, source ^ mask) for source in range(count)]
    return lax.ppermute(value, axis, pairs)


def bit_of(axis, mask):
    return ((lax.axis_index(axis) & mask) != 0).astype(jnp.int32)


LANES = 128
PARTS = 3
GROUP = 4
LANES = 128
MASK_FILL = -1e30
PAIR = 112
STEP_PAIRS = 4


def _stacked(value, lane4):
    wide = jnp.broadcast_to(value.astype(jnp.float32)[None], (GROUP, PAIR, LANES))
    return jnp.where(lane4, wide, 0.0).reshape(GROUP * PAIR, LANES).astype(jnp.bfloat16)


def _gather_lanes(stack, lane4):
    return jnp.sum(jnp.where(lane4, stack.reshape(GROUP, PAIR, LANES), 0.0), 0)


def _scores(q4, k4, bias4, allowed, scale, lane4):
    raw = lax.dot_general(_stacked(q4, lane4), k4, (((1,), (1,)), ((), ())), preferred_element_type=jnp.float32)
    raw = raw.reshape(GROUP, PAIR, PAIR) * scale + bias4
    return jnp.where(allowed[None], raw, MASK_FILL)


def _lane_masks():
    lane4 = lax.broadcasted_iota(jnp.int32, (GROUP, 1, LANES), 2) // 32 == lax.broadcasted_iota(
        jnp.int32, (GROUP, 1, LANES), 0)
    return lane4, lax.broadcasted_iota(jnp.int32, (1, LANES), 1)


def _fwd_kernel(mix_ref, bias_ref, kc_ref, kr_ref, out_ref, lse_ref, *, scale):
    width = HEADS * 32
    lane4, head_lane = _lane_masks()
    for sub in range(STEP_PAIRS):
        allowed = kc_ref[sub] == kr_ref[sub]
        lse_all = jnp.zeros((PAIR, LANES), jnp.float32)
        for g in range(HEADS // GROUP):
            q4 = mix_ref[sub, :, pl.ds(g * LANES, LANES)]
            k4 = mix_ref[sub, :, pl.ds(width + g * LANES, LANES)]
            v4 = mix_ref[sub, :, pl.ds(2 * width + g * LANES, LANES)]
            s = _scores(q4, k4, bias_ref[pl.ds(g * GROUP, GROUP)], allowed, scale, lane4)
            top = jnp.max(s, -1, keepdims=True)
            e = jnp.exp(s - top)
            total = jnp.sum(e, -1, keepdims=True)
            probs = (e / total).reshape(GROUP * PAIR, PAIR).astype(jnp.bfloat16)
            mixed_out = jnp.dot(probs, v4, preferred_element_type=jnp.float32)
            out_ref[sub, :, pl.ds(g * LANES, LANES)] = _gather_lanes(mixed_out, lane4).astype(out_ref.dtype)
            lse = top + jnp.log(total)
            for j in range(GROUP):
                lse_all = jnp.where(head_lane == g * GROUP + j, lse[j], lse_all)
        lse_ref[sub] = lse_all


def _bwd_kernel(mix_ref, grad_ref, lse_ref, bias_ref, kc_ref, kr_ref, gmix_ref, dbias_ref, *, scale):
    width = HEADS * 32
    lane4, head_lane = _lane_masks()
    step = pl.program_id(0)

    @pl.when(step == 0)
    def _():
        dbias_ref[...] = jnp.zeros_like(dbias_ref)

    for sub in range(STEP_PAIRS):
        allowed = kc_ref[sub] == kr_ref[sub]
        lse_all = lse_ref[sub]
        for g in range(HEADS // GROUP):
            q4 = mix_ref[sub, :, pl.ds(g * LANES, LANES)]
            k4 = mix_ref[sub, :, pl.ds(width + g * LANES, LANES)]
            v4 = mix_ref[sub, :, pl.ds(2 * width + g * LANES, LANES)]
            d4 = grad_ref[sub, :, pl.ds(g * LANES, LANES)]
            heads = pl.ds(g * GROUP, GROUP)
            s = _scores(q4, k4, bias_ref[heads], allowed, scale, lane4)
            lse = jnp.stack([
                jnp.sum(jnp.where(head_lane == g * GROUP + j, lse_all, 0.0), -1, keepdims=True)
                for j in range(GROUP)
            ])
            probs = jnp.exp(s - lse)
            d_stack = _stacked(d4, lane4)
            dprobs = lax.dot_general(d_stack, v4, (((1,), (1,)), ((), ())), preferred_element_type=jnp.float32)
            dprobs = dprobs.reshape(GROUP, PAIR, PAIR)
            inner = jnp.sum(probs * dprobs, -1, keepdims=True)
            dscores = (probs * (dprobs - inner)).reshape(GROUP * PAIR, PAIR).astype(jnp.bfloat16)
            dbias_ref[heads] = dbias_ref[heads] + dscores.astype(jnp.float32).reshape(GROUP, PAIR, PAIR)
            gq = _gather_lanes(jnp.dot(dscores, k4, preferred_element_type=jnp.float32), lane4)
            gk = lax.dot_general(dscores, _stacked(q4, lane4), (((0,), (0,)), ((), ())), preferred_element_type=jnp.float32)
            gv = lax.dot_general(probs.reshape(GROUP * PAIR, PAIR).astype(jnp.bfloat16), d_stack,
                                 (((0,), (0,)), ((), ())), preferred_element_type=jnp.float32)
            gmix_ref[sub, :, pl.ds(g * LANES, LANES)] = (gq * scale).astype(gmix_ref.dtype)
            gmix_ref[sub, :, pl.ds(width + g * LANES, LANES)] = (gk * scale).astype(gmix_ref.dtype)
            gmix_ref[sub, :, pl.ds(2 * width + g * LANES, LANES)] = gv.astype(gmix_ref.dtype)


def _pair_spec(width):
    return pl.BlockSpec((STEP_PAIRS, PAIR, width), lambda p: (p, 0, 0))


def attention_fwd(mixed_pairs, bias, key_col, key_row, scale):
    pairs = mixed_pairs.shape[0]
    kernel = functools.partial(_fwd_kernel, scale=scale)
    return pl.pallas_call(
        kernel,
        grid=(pairs // STEP_PAIRS,),
        out_shape=(
            jax.ShapeDtypeStruct((pairs, PAIR, HEADS * 32), jnp.bfloat16),
            jax.ShapeDtypeStruct((pairs, PAIR, LANES), jnp.float32),
        ),
        in_specs=[_pair_spec(mixed_pairs.shape[2]), pl.BlockSpec(bias.shape, lambda p: (0, 0, 0)),
                  pl.BlockSpec((STEP_PAIRS, PAIR, 1), lambda p: (p, 0, 0)), pl.BlockSpec((STEP_PAIRS, 1, PAIR), lambda p: (p, 0, 0))],
        out_specs=(_pair_spec(HEADS * 32), _pair_spec(LANES)),
        compiler_params=pltpu.CompilerParams(dimension_semantics=("arbitrary",), vmem_limit_bytes=32 * 1024 * 1024),
    )(mixed_pairs, bias, key_col, key_row)


def attention_bwd(mixed_pairs, grad_pairs, lse, bias, key_col, key_row, scale):
    pairs = mixed_pairs.shape[0]
    kernel = functools.partial(_bwd_kernel, scale=scale)
    return pl.pallas_call(
        kernel,
        grid=(pairs // STEP_PAIRS,),
        out_shape=(
            jax.ShapeDtypeStruct(mixed_pairs.shape, jnp.bfloat16),
            jax.ShapeDtypeStruct(bias.shape, jnp.float32),
        ),
        in_specs=[_pair_spec(mixed_pairs.shape[2]), _pair_spec(HEADS * 32), _pair_spec(LANES),
                  pl.BlockSpec(bias.shape, lambda p: (0, 0, 0)),
                  pl.BlockSpec((STEP_PAIRS, PAIR, 1), lambda p: (p, 0, 0)), pl.BlockSpec((STEP_PAIRS, 1, PAIR), lambda p: (p, 0, 0))],
        out_specs=(_pair_spec(mixed_pairs.shape[2]), pl.BlockSpec(bias.shape, lambda p: (0, 0, 0))),
        compiler_params=pltpu.CompilerParams(dimension_semantics=("arbitrary",), vmem_limit_bytes=32 * 1024 * 1024),
    )(mixed_pairs, grad_pairs, lse, bias, key_col, key_row)


def lane_blocks(matrix):
    row_blocks, col_blocks = matrix.shape[0] // BLK, matrix.shape[1] // BLK
    shaped = matrix.reshape(row_blocks, BLK, col_blocks, BLK).transpose(0, 2, 1, 3)
    return shaped.reshape(row_blocks * col_blocks, BLK * BLK // LANES, LANES)


ROWS = 448
SQRT_HALF = float(np.sqrt(0.5))
INV_SQRT_TAU = float(1.0 / np.sqrt(2.0 * np.pi))


def _norm(tensor):
    center = tensor - jnp.mean(tensor, -1, keepdims=True)
    inverse = lax.rsqrt(jnp.mean(center * center, -1, keepdims=True) + NORM_EPSILON)
    return center * inverse, inverse


def _mlp_fwd_kernel(att_ref, res_ref, valid_ref, wp_ref, gain_ref, off_ref, w1_ref, w2_ref,
                    hid_ref, act_ref, gelu_ref, out_ref, stat_ref):
    step = pl.program_id(0)
    branch_one = jnp.dot(att_ref[...], wp_ref[...], preferred_element_type=jnp.float32)
    hidden = res_ref[...] + branch_one
    normed, _ = _norm(hidden)
    act = (normed * gain_ref[...] + off_ref[...]).astype(jnp.bfloat16)
    pre = jnp.dot(act, w1_ref[...], preferred_element_type=jnp.float32)
    gelu = ((0.5 * pre) * (1.0 + lax.erf(pre * SQRT_HALF))).astype(jnp.bfloat16)
    branch_two = jnp.dot(gelu, w2_ref[...], preferred_element_type=jnp.float32)
    output = hidden + branch_two
    valid = valid_ref[...]
    first = jnp.sum(valid * output * output)
    second = jnp.sum(valid * (branch_one * branch_one + branch_two * branch_two))
    lane = lax.broadcasted_iota(jnp.int32, (8, 128), 1)
    row = lax.broadcasted_iota(jnp.int32, (8, 128), 0)
    here = jnp.where((row == 0) & (lane == 0), first, 0.0) + jnp.where((row == 0) & (lane == 1), second, 0.0)

    @pl.when(step == 0)
    def _():
        stat_ref[...] = jnp.zeros_like(stat_ref)

    stat_ref[...] = stat_ref[...] + here
    hid_ref[...] = hidden
    act_ref[...] = act
    gelu_ref[...] = gelu
    out_ref[...] = output.astype(out_ref.dtype)


def _mlp_bwd_kernel(gout_ref, hid_ref, act_ref, gain_ref, w1_ref, w2_ref, wp_ref, att_ref, gelu_ref,
                    gpre_ref, ghid_ref, gbr_ref, gatt_ref, small_ref, gfc1_ref, gfc2_ref, gproj_ref):
    step = pl.program_id(0)
    contract_last = (((1,), (1,)), ((), ()))
    pre = jnp.dot(act_ref[...], w1_ref[...], preferred_element_type=jnp.float32)
    grad_out = gout_ref[...]
    grad_gelu = lax.dot_general(grad_out, w2_ref[...], contract_last, preferred_element_type=jnp.float32)
    cdf = 0.5 * (1.0 + lax.erf(pre * SQRT_HALF))
    pdf = jnp.exp(-0.5 * pre * pre) * INV_SQRT_TAU
    grad_pre = (grad_gelu * (cdf + pre * pdf)).astype(jnp.bfloat16)
    grad_act = lax.dot_general(grad_pre, w1_ref[...], contract_last, preferred_element_type=jnp.float32)
    normed, inverse = _norm(hid_ref[...])
    scaled = grad_act * gain_ref[...]
    mean_one = jnp.mean(scaled, -1, keepdims=True)
    mean_two = jnp.mean(scaled * normed, -1, keepdims=True)
    grad_hidden = grad_out.astype(jnp.float32) + inverse * (scaled - mean_one - normed * mean_two)
    grad_branch = grad_hidden.astype(jnp.bfloat16)
    grad_att = lax.dot_general(grad_branch, wp_ref[...], contract_last, preferred_element_type=jnp.float32)
    sums = jnp.concatenate(
        [jnp.sum(grad_act * normed, 0, keepdims=True), jnp.sum(grad_act, 0, keepdims=True),
         jnp.zeros((6, grad_act.shape[1]), jnp.float32)], 0)

    contract_rows = (((0,), (0,)), ((), ()))
    fc1 = lax.dot_general(act_ref[...], grad_pre, contract_rows, preferred_element_type=jnp.float32)
    fc2 = lax.dot_general(gelu_ref[...], grad_out, contract_rows, preferred_element_type=jnp.float32)
    proj = lax.dot_general(att_ref[...], grad_branch, contract_rows, preferred_element_type=jnp.float32)

    @pl.when(step == 0)
    def _():
        small_ref[...] = jnp.zeros_like(small_ref)
        gfc1_ref[...] = jnp.zeros_like(gfc1_ref)
        gfc2_ref[...] = jnp.zeros_like(gfc2_ref)
        gproj_ref[...] = jnp.zeros_like(gproj_ref)

    small_ref[...] = small_ref[...] + sums
    gfc1_ref[...] = gfc1_ref[...] + fc1
    gfc2_ref[...] = gfc2_ref[...] + fc2
    gproj_ref[...] = gproj_ref[...] + proj
    gpre_ref[...] = grad_pre
    ghid_ref[...] = grad_hidden
    gbr_ref[...] = grad_branch
    gatt_ref[...] = grad_att.astype(gatt_ref.dtype)


def _rows(width):
    return pl.BlockSpec((ROWS, width), lambda i: (i, 0))


def _whole(shape):
    return pl.BlockSpec(shape, lambda i: (0,) * len(shape))


def mlp_fwd(attended, residual, valid, w_proj, gain, offset, w_fc1, w_fc2):
    tokens, width = residual.shape
    hidden_width = w_fc1.shape[1]
    return pl.pallas_call(
        _mlp_fwd_kernel,
        grid=(tokens // ROWS,),
        out_shape=(
            jax.ShapeDtypeStruct((tokens, width), jnp.float32),
            jax.ShapeDtypeStruct((tokens, width), jnp.bfloat16),
            jax.ShapeDtypeStruct((tokens, hidden_width), jnp.bfloat16),
            jax.ShapeDtypeStruct((tokens, width), jnp.bfloat16),
            jax.ShapeDtypeStruct((8, 128), jnp.float32),
        ),
        in_specs=[_rows(width), _rows(width), _rows(1), _whole(w_proj.shape), _whole((1, width)),
                  _whole((1, width)), _whole(w_fc1.shape), _whole(w_fc2.shape)],
        out_specs=(_rows(width), _rows(width), _rows(hidden_width), _rows(width), _whole((8, 128))),
        compiler_params=pltpu.CompilerParams(dimension_semantics=("arbitrary",), vmem_limit_bytes=48 * 1024 * 1024),
    )(attended, residual, valid, w_proj, gain.reshape(1, -1), offset.reshape(1, -1), w_fc1, w_fc2)


def mlp_bwd(grad_out, hidden, act_two, gain, w_fc1, w_fc2, w_proj, attended, gelu_low):
    tokens, width = hidden.shape
    hidden_width = w_fc1.shape[1]
    return pl.pallas_call(
        _mlp_bwd_kernel,
        grid=(tokens // ROWS,),
        out_shape=(
            jax.ShapeDtypeStruct((tokens, hidden_width), jnp.bfloat16),
            jax.ShapeDtypeStruct((tokens, width), jnp.float32),
            jax.ShapeDtypeStruct((tokens, width), jnp.bfloat16),
            jax.ShapeDtypeStruct((tokens, width), jnp.bfloat16),
            jax.ShapeDtypeStruct((8, width), jnp.float32),
            jax.ShapeDtypeStruct(w_fc1.shape, jnp.float32),
            jax.ShapeDtypeStruct(w_fc2.shape, jnp.float32),
            jax.ShapeDtypeStruct(w_proj.shape, jnp.float32),
        ),
        in_specs=[_rows(width), _rows(width), _rows(width), _whole((1, width)), _whole(w_fc1.shape),
                  _whole(w_fc2.shape), _whole(w_proj.shape), _rows(width), _rows(hidden_width)],
        out_specs=(_rows(hidden_width), _rows(width), _rows(width), _rows(width), _whole((8, width)),
                   _whole(w_fc1.shape), _whole(w_fc2.shape), _whole(w_proj.shape)),
        compiler_params=pltpu.CompilerParams(dimension_semantics=("arbitrary",), vmem_limit_bytes=48 * 1024 * 1024),
    )(grad_out, hidden, act_two, gain.reshape(1, -1), w_fc1, w_fc2, w_proj, attended, gelu_low)


def reduce_to_owners(parted, small):
    groups = lax.axis_size("dp")
    dp_bits = groups.bit_length() - 1
    n_qy, n_qx = lax.axis_size("qy"), lax.axis_size("qx")
    count, depth = parted[0].shape[0], parted[0].shape[1]
    per_group = count // groups
    names = [("dp", 1 << power) for power in reversed(range(dp_bits))] + [("qy", 1), ("qx", 1)]
    cross = [("qy", 1)] + [("dp", 1 << power) for power in range(dp_bits)]
    pieces, piece_names, orders = [], [], []
    for index, part in enumerate(parted):
        pieces.append(
            part.reshape([2] * dp_bits + [n_qy, n_qx, per_group * depth // (n_qy * n_qx), LANES])
        )
        piece_names.append(list(names))
        turn = index % len(cross)
        orders.append([("qx", 1)] + cross[turn:] + cross[:turn])
    for stage in range(len(names)):
        for index in range(len(pieces)):
            bit = orders[index][stage]
            place = piece_names[index].index(bit)
            mine = bit_of(*bit)
            keep = lax.dynamic_index_in_dim(pieces[index], mine, place, keepdims=False)
            send = lax.dynamic_index_in_dim(pieces[index], 1 - mine, place, keepdims=False)
            piece_names[index].remove(bit)
            arrived = partner_of(send.astype(jnp.bfloat16), *bit)
            pieces[index] = keep + arrived.astype(jnp.float32)
            if index == 0:
                small = small + partner_of(small, *bit)
                pieces[0], small = lax.optimization_barrier((pieces[0], small))
    chunk = jnp.stack(pieces)
    other = partner_of(chunk, "qy", 1)
    pair = jnp.where(bit_of("qy", 1) == 1, jnp.stack([other, chunk], 1), jnp.stack([chunk, other], 1))
    other = partner_of(pair, "qx", 1)
    quad = jnp.where(bit_of("qx", 1) == 1, jnp.stack([other, pair], 2), jnp.stack([pair, other], 2))
    quad = quad.reshape(len(pieces), per_group, depth, LANES).transpose(1, 0, 2, 3)
    return quad.reshape(per_group, BLK, BLK), small


def cut_along(value, dim, devices):
    before, after = (value.shape[:dim], value.shape[dim + 1 :])
    return jnp.moveaxis(value.reshape(*before, devices, -1, *after), dim, 0)


def sent_and_summed(value, axis, dim):
    pieces = cut_along(value, dim, lax.axis_size(axis))
    arrived = lax.all_to_all(pieces, axis, split_axis=0, concat_axis=0, tiled=True)
    return arrived.astype(jnp.float32).sum(axis=0)


def norm_stats(tensor):
    center = tensor - jnp.mean(tensor, -1, keepdims=True)
    inverse = lax.rsqrt(jnp.mean(center * center, -1, keepdims=True) + NORM_EPSILON)
    return (center * inverse, inverse)


def norm_back(grad_act, normed, inverse, gain):
    scaled = grad_act * gain
    mean_one = jnp.mean(scaled, -1, keepdims=True)
    mean_two = jnp.mean(scaled * normed, -1, keepdims=True)
    return inverse * (scaled - mean_one - normed * mean_two)


def to_windows(tensor):
    canvases, rows_side, cols_side, channels = tensor.shape
    shaped = tensor.reshape(canvases, rows_side // WIN, WIN, cols_side // WIN, WIN, channels)
    return shaped.transpose(0, 1, 3, 2, 4, 5).reshape(
        canvases * (rows_side // WIN) * (cols_side // WIN), WIN * WIN, channels
    )


def from_windows(tensor, canvases, rows_side, cols_side):
    channels = tensor.shape[-1]
    shaped = tensor.reshape(canvases, rows_side // WIN, cols_side // WIN, WIN, WIN, channels)
    return shaped.transpose(0, 1, 3, 2, 4, 5).reshape(canvases, rows_side, cols_side, channels)


def relative_index():
    places = jnp.arange(WIN * WIN, dtype=jnp.int32)
    row_of = places // WIN
    col_of = places % WIN
    return (row_of[:, None] - row_of[None, :] + WIN - 1) * (2 * WIN - 1) + (
        col_of[:, None] - col_of[None, :] + WIN - 1
    )


def region_of(places, full):
    return jnp.where(places < full - WIN, 0, jnp.where(places < full - SHIFT, 1, 2)).astype(
        jnp.int32
    )


def advance(tensor):
    upper = passed_along(tensor[:, :SHIFT], "qy", -1)
    tensor = jnp.concatenate([tensor[:, SHIFT:], upper], 1)
    leftmost = passed_along(tensor[:, :, :SHIFT], "qx", -1)
    return jnp.concatenate([tensor[:, :, SHIFT:], leftmost], 2)


def retreat(tensor):
    lowest = passed_along(tensor[:, -SHIFT:], "qy", 1)
    tensor = jnp.concatenate([lowest, tensor[:, :-SHIFT]], 1)
    rightmost = passed_along(tensor[:, :, -SHIFT:], "qx", 1)
    return jnp.concatenate([rightmost, tensor[:, :, :-SHIFT]], 2)


def blocks_of(matrix):
    row_blocks = matrix.shape[0] // BLK
    col_blocks = matrix.shape[1] // BLK
    return (
        matrix.reshape(row_blocks, BLK, col_blocks, BLK)
        .transpose(0, 2, 1, 3)
        .reshape(row_blocks * col_blocks, BLK, BLK)
    )


def rotate_update(grads, master, first, second, left, right):
    turned = jnp.einsum("sji,sjk->sik", left, grads, precision=ROTATE)
    turned = jnp.einsum("sik,skl->sil", turned, right, precision=ROTATE)
    new_first = BETA_ONE * first + (1.0 - BETA_ONE) * turned
    new_second = BETA_TWO * second + (1.0 - BETA_TWO) * turned * turned
    direction = new_first / (jnp.sqrt(new_second) + ADAM_EPSILON)
    back = jnp.einsum("sij,sjk->sik", left, direction, precision=ROTATE)
    back = jnp.einsum("sik,slk->sil", back, right, precision=ROTATE)
    return (new_first, new_second, master - RATE_BLOCKS * back)


def small_update(grads, params, first, second):
    new_first = BETA_ONE * first + (1.0 - BETA_ONE) * grads
    new_second = BETA_TWO * second + (1.0 - BETA_TWO) * grads * grads
    direction = new_first / (jnp.sqrt(new_second) + ADAM_EPSILON)
    return (new_first, new_second, params - RATE_SMALL * direction)


def local(
    tokens,
    crop_ids,
    merge_order,
    owner_list,
    w_qkv,
    w_proj,
    w_fc1,
    w_fc2,
    small_params,
    small_first,
    small_second,
    master_blocks,
    first_moment,
    second_moment,
    basis_left,
    basis_right,
    merged_grad,
):
    canvases, quad_side, quad_cols, features = tokens.shape
    head_dim = features // HEADS
    score_scale = head_dim ** (-0.5)
    window_area = WIN * WIN
    quarters = lax.axis_size(("qy", "qx"))
    share_rows = quad_side * quad_cols // quarters
    row_base = lax.axis_index("qy") * quad_side
    col_base = lax.axis_index("qx") * quad_cols
    rolled = jnp.roll(crop_ids, (-SHIFT, -SHIFT), (1, 2))
    local_ids = lax.dynamic_slice(
        rolled, (jnp.int32(0), row_base, col_base), (canvases, quad_side, quad_cols)
    )
    region_row = region_of(
        row_base + jnp.arange(quad_side, dtype=jnp.int32), quad_side * lax.axis_size("qy")
    )
    region_col = region_of(
        col_base + jnp.arange(quad_cols, dtype=jnp.int32), quad_cols * lax.axis_size("qx")
    )
    labels = (local_ids + 1) * 9 + region_row[None, :, None] * 3 + region_col[None, None, :]
    win_labels = to_windows(labels[..., None])[..., 0]
    window_count = win_labels.shape[0]
    gain_one = small_params[0:features]
    offset_one = small_params[features : 2 * features]
    gain_two = small_params[2 * features : 3 * features]
    offset_two = small_params[3 * features : 4 * features]
    table = small_params[4 * features :].reshape(HEADS, -1)
    onehot = (
        relative_index().reshape(-1)[:, None]
        == jnp.arange(table.shape[1], dtype=jnp.int32)[None, :]
    ).astype(jnp.float32)
    rel_bias = jnp.einsum("hr,pr->hp", table, onehot, precision=PRECISE).reshape(
        HEADS, window_area, window_area
    )

    pair_area = 2 * window_area
    place = jnp.arange(PAIR, dtype=jnp.int32)
    pair_labels = jnp.pad(win_labels.reshape(-1, pair_area), ((0, 0), (0, PAIR - pair_area)))
    pair_keys = jnp.where(
        place[None] < pair_area,
        pair_labels * 2 + (place[None] >= window_area).astype(jnp.int32),
        -1 - place[None],
    )
    key_col, key_row = pair_keys[:, :, None], pair_keys[:, None, :]
    valid = (pair_labels >= 9).reshape(-1).astype(jnp.float32)[:, None]
    spread = (
        (place[:, None] % window_area == jnp.arange(window_area, dtype=jnp.int32)[None, :])
        & (place[:, None] < pair_area)
    ).astype(jnp.float32)
    dense_bias = jnp.einsum(
        "hti,ui->htu",
        jnp.einsum("ti,hij->htj", spread, rel_bias, precision=PRECISE),
        spread,
        precision=PRECISE,
    )

    def to_pairs(tensor):
        shaped = tensor.reshape(-1, pair_area, tensor.shape[-1])
        return jnp.pad(shaped, ((0, 0), (0, PAIR - pair_area), (0, 0))).reshape(-1, tensor.shape[-1])

    def from_pairs(tensor):
        shaped = tensor.reshape(-1, PAIR, tensor.shape[-1])
        return shaped[:, :pair_area].reshape(-1, window_area, tensor.shape[-1])

    residual = to_pairs(to_windows(advance(tokens)).astype(jnp.float32))
    normed_one, inverse_one = norm_stats(residual)
    act_one = (normed_one * gain_one + offset_one).astype(jnp.bfloat16)
    mixed = jnp.dot(act_one, w_qkv, preferred_element_type=jnp.float32).astype(jnp.bfloat16)
    mixed_pairs = mixed.reshape(-1, PAIR, mixed.shape[-1])
    attended_pairs, log_total = attention_fwd(mixed_pairs, dense_bias, key_col, key_row, score_scale)
    attended = attended_pairs.reshape(-1, features)
    hidden, act_two, gelu_low, output_flat, stat_block = mlp_fwd(
        attended, residual, valid, w_proj, gain_two, offset_two, w_fc1, w_fc2
    )
    stat_terms = jnp.stack([stat_block[0, 0], stat_block[0, 1], jnp.sum(valid) * features])
    output_low = from_pairs(output_flat)
    restored = retreat(from_windows(output_low, canvases, quad_side, quad_cols))
    flat_out = restored.reshape(canvases, quarters, share_rows, features)
    arrived = lax.all_to_all(flat_out, ("qy", "qx"), 1, 1, tiled=True)
    merged = jnp.take(arrived, merge_order, axis=1, mode="clip").transpose(0, 2, 1, 3).reshape(
        canvases, share_rows, quarters * features
    )
    quarter_ids = jnp.arange(quarters, dtype=jnp.int32)
    source_pick = jnp.sum(
        quarter_ids[:, None] * (merge_order[:, None] == quarter_ids[None, :]).astype(jnp.int32), 0
    )
    incoming = merged_grad.reshape(canvases, share_rows, quarters, features)
    unordered = jnp.take(incoming, source_pick, axis=2, mode="clip").transpose(0, 2, 1, 3)
    returned = lax.all_to_all(unordered, ("qy", "qx"), 1, 1, tiled=True)
    grad_orig = returned.reshape(canvases, quad_side, quad_cols, features)
    grad_out = to_pairs(to_windows(advance(grad_orig)))
    (grad_pre, grad_hidden, grad_branch, grad_attended, small_two, grad_fc1, grad_fc2, grad_proj) = (
        mlp_bwd(grad_out, hidden, act_two, gain_two, w_fc1, w_fc2, w_proj, attended, gelu_low)
    )
    grad_mixed_pairs, dense_grad_bias = attention_bwd(
        mixed_pairs, grad_attended.reshape(-1, PAIR, features), log_total, dense_bias, key_col, key_row, score_scale
    )
    grad_mixed = grad_mixed_pairs.reshape(-1, 3 * features)
    grad_bias = jnp.einsum(
        "ti,htj->hij",
        spread,
        jnp.einsum("htu,uj->htj", dense_grad_bias, spread, precision=PRECISE),
        precision=PRECISE,
    )
    grad_table = jnp.dot(grad_bias.reshape(HEADS, -1), onehot, precision=PRECISE)
    grad_qkv = jnp.einsum("rc,rf->cf", act_one, grad_mixed, preferred_element_type=jnp.float32)
    grad_act_one = jnp.einsum("rf,cf->rc", grad_mixed, w_qkv, preferred_element_type=jnp.float32)
    grad_input = grad_hidden + norm_back(grad_act_one, normed_one, inverse_one, gain_one)
    grad_low = from_pairs(grad_input.astype(jnp.bfloat16))
    grad_tokens = retreat(from_windows(grad_low, canvases, quad_side, quad_cols))
    small_local = jnp.concatenate(
        [
            jnp.sum(grad_act_one * normed_one, 0),
            jnp.sum(grad_act_one, 0),
            small_two[0],
            small_two[1],
            grad_table.reshape(-1),
        ]
    )
    every_block = jnp.concatenate(
        [lane_blocks(grad_qkv), lane_blocks(grad_proj), lane_blocks(grad_fc1), lane_blocks(grad_fc2)],
        0,
    )
    depth = every_block.shape[1] // PARTS
    parted = [
        jnp.take(every_block[:, index * depth : (index + 1) * depth], owner_list, axis=0, mode="clip")
        for index in range(PARTS)
    ]
    owned_grads, small_all = reduce_to_owners(parted, jnp.concatenate([small_local, stat_terms]))
    small_total = small_all[: small_local.shape[0]]
    stat_total = small_all[small_local.shape[0] :]
    new_first, new_second, new_master = rotate_update(
        owned_grads, master_blocks, first_moment, second_moment, basis_left, basis_right
    )
    small_first_new, small_second_new, small_new = small_update(
        small_total, small_params, small_first, small_second
    )
    stats = jnp.stack(
        [jnp.sqrt(stat_total[0] / stat_total[2]), jnp.sqrt(stat_total[1] / (2.0 * stat_total[2]))]
    )
    return (
        merged,
        grad_tokens,
        owned_grads,
        new_master,
        new_first,
        new_second,
        new_master.astype(jnp.bfloat16),
        small_total,
        small_first_new,
        small_second_new,
        small_new,
        stats,
    )


def solution(mesh):
    placed = (
        P("dp", "qy", "qx", None),
        P("dp", None, None),
        P(),
        P(),
        P(),
        P(),
        P(),
        P(),
        P(),
        P(),
        P(),
        P("dp", None, None),
        P("dp", None, None),
        P("dp", None, None),
        P("dp", None, None),
        P("dp", None, None),
        P("dp", ("qy", "qx"), None),
    )
    return jax.shard_map(
        local,
        mesh=mesh,
        in_specs=placed,
        out_specs=(
            P("dp", ("qy", "qx"), None),
            P("dp", "qy", "qx", None),
            P("dp", None, None),
            P("dp", None, None),
            P("dp", None, None),
            P("dp", None, None),
            P("dp", None, None),
            P(),
            P(),
            P(),
            P(),
            P(),
        ),
        check_vma=False,
    )
```
